32 devices in a mesh: groups: 2 (over y), ctx: 4 (over z), tp: 2 (over x), dp: 2 (over core).
Axes of the slice: x: 2, y: 2, z: 4, core: 2. Of those that a mesh axis runs over, the one named last changes fastest.
Arguments:
- tokens: bfloat16 [1024, 5120], P(('groups', 'ctx'), ('tp', 'dp')), parts along dimension 0, may hold values from -6 to 6
- lengths: int32 [8], P('groups'), parts along dimension 0, may hold values from 1 to 256, 512 in all
- request_adapter_ids: int32 [8], P('groups'), parts along dimension 0, may hold values from 0 to 7
- adapter_store_slot: int32 [8], replicated, may hold values from 0 to 7, each once
- xchan_input_weight: bfloat16 [5120, 4096], P('ctx', ('tp', 'dp')), may hold values from -0.078125 to 0.078125
- bc_input_weight: bfloat16 [5120, 512], P('ctx', ('tp', 'dp')), may hold values from -0.078125 to 0.078125
- step_input_weight: bfloat16 [5120, 64], P('ctx', ('tp', 'dp')), may hold values from -0.078125 to 0.078125
- convolution_x_taps: float32 [4, 4096], P(None, ('tp', 'dp')), may hold values from -3 to 3
- convolution_bc_taps: float32 [4, 512], P(None, ('tp', 'dp')), may hold values from -3 to 3
- step_bias: float32 [64], P(('tp', 'dp')), may hold values from -2 to 1
- decay_log_rate: float32 [64], P(('tp', 'dp')), may hold values from -16 to -2
- head_skip_gain: float32 [64], P(('tp', 'dp')), may hold values from 0.5 to 1.5
- output_norm_gain: float32 [4096], P(('tp', 'dp')), may hold values from 0.1 to 1.9
- output_weight: bfloat16 [4096, 5120], P(('tp', 'dp'), 'ctx'), may hold values from -0.09375 to 0.09375
- adapter_down_input: bfloat16 [8, 5120, 64], P('ctx', ('tp', 'dp')), may hold values from -0.078125 to 0.078125
- adapter_up_xchan: bfloat16 [8, 64, 4096], P('ctx', None, ('tp', 'dp')), may hold values from -0.75 to 0.75
- adapter_up_bc: bfloat16 [8, 64, 512], P('ctx', None, ('tp', 'dp')), may hold values from -0.75 to 0.75
- adapter_down_output: bfloat16 [8, 4096, 64], P('ctx', ('tp', 'dp')), may hold values from -0.09375 to 0.09375
- adapter_up_output: bfloat16 [8, 64, 5120], P('ctx', None, ('tp', 'dp')), may hold values from -0.75 to 0.75
Outputs:
- mixed: bfloat16 [1024, 5120], P(('groups', 'ctx'), ('tp', 'dp')), parts along dimension 0
The draws below stay inside these ranges and needn't reach their ends.
There are 2 independent parts, one for each index of `groups`. The reference program is written for one: setup_inputs(seed, part) draws one part's arguments, and reference() takes and returns one part's arrays. A program takes and returns all parts, laid end to end along the dimension named above; an argument that names none is the same for every part. Nothing has to cross between parts.
Inputs may be any that keep to these rules, and one draw needn't show every extreme that they name: The 4 lengths add up to 512; the longest is exactly 256. `adapter_store_slot`: each slot once; the adapter in slot k is stored on index k // 2 of ctx, at its place k % 2 there.
All inputs are finite; a program needn't handle non-finite values.
Results may differ from the reference program's by a relative error of at most 0.023.
Values may be sent and summed in bfloat16 or wider, within the bound.
No kernel may reach another device: no remote copies, remote signals or barrier semaphores. Data moves between devices by JAX's collectives and lax.ppermute only.
A program may use at most 64 MiB of HBM per device.

```python
import math
import jax
import jax.numpy as jnp
import numpy as np
from jax import lax

MODEL_WIDTH = 5120
HEAD_SIZE = 64
STATE_SIZE = 256
KC = 4
HEAD_TOTAL = 64
ADAPTER_RANK = 64
REQS = 4
TOK_DEV = 128
HPD = 16
LEN = 512
ADAPTER_COUNT = 8
N_CTX = 4


def draw_decay_log_rate(key, part):
    picker = jax.random.uniform(jax.random.fold_in(key, 11), (HEAD_TOTAL,))
    slow_rates = jax.random.uniform(jax.random.fold_in(key, 12), (HEAD_TOTAL,), minval=math.log(0.02 / LEN), maxval=math.log(0.3 / LEN))
    fast_rates = jax.random.uniform(jax.random.fold_in(key, 13), (HEAD_TOTAL,), minval=math.log(0.03), maxval=math.log(0.12))
    share = 0.5
    return jnp.where(picker < share, slow_rates, fast_rates).astype(jnp.float32)


def set_ends(array, rng, low, largest):
    spot = [jax.random.randint(jax.random.fold_in(rng, axis), (), 0, length) for axis, length in enumerate(array.shape)]
    widest = array.shape.index(max(array.shape))
    next_to = spot[:widest] + [(spot[widest] + 1) % array.shape[widest]] + spot[widest + 1:]
    return array.at[tuple(spot)].set(low).at[tuple(next_to)].set(largest)


def levels(key, dims, pieces, low, top_value):
    level = 1.0
    for axis_at, shards_of in pieces:
        draws = jax.random.uniform(jax.random.fold_in(jax.random.fold_in(key, 6), axis_at), (shards_of,), jnp.float32, low / len(pieces), top_value / len(pieces))
        level = level * jnp.repeat(jnp.exp(draws), dims[axis_at] // shards_of).reshape((-1,) + (1,) * (len(dims) - 1 - axis_at))
    return level


def profile(number_of, total, limit, lean):
    loads = [(1 << 20) // math.isqrt(rank ** lean) + 1 for rank in range(2, number_of + 1)]
    surplus, counts = total - limit - (number_of - 1), [1] * (number_of - 1)
    while surplus > 0:
        candidates = [i for i in range(number_of - 1) if counts[i] < limit]
        mass, left = sum([loads[i] for i in candidates]), surplus
        for i in candidates:
            extra = min(limit - counts[i], max(1, left * loads[i] // mass), surplus)
            counts[i] = counts[i] + extra
            surplus = surplus - extra
    return np.array([limit] + counts)


def ragged_sizes(own_key, amount, total, reach, slope):
    if amount == 2:
        one = jax.random.randint(own_key, (), max(1, total - reach), min(reach, total - 1) + 1)
        return jnp.stack([one, total - one])
    sizes = jnp.asarray(profile(amount, total, reach, slope), jnp.int32)
    twos = (amount - 1) // 2
    donor, taker = sizes[1:1 + 2 * twos:2], sizes[2:2 + 2 * twos:2]
    room = jnp.minimum(donor - 1, reach - taker)
    passed = jax.random.randint(jax.random.fold_in(own_key, 1), (twos,), 0, 1 << 20) % (room + 1)
    sizes = sizes.at[1:1 + 2 * twos:2].set(donor - passed).at[2:2 + 2 * twos:2].set(taker + passed)
    return sizes[jax.random.permutation(jax.random.fold_in(own_key, 2), amount)]


def gaussian(own_key, dims, spread, limit, shards=(), kind=jnp.bfloat16):
    factor_of = levels(own_key, dims, shards, -0.22, 0.18) if shards else 1.0
    result = jax.random.normal(own_key, dims, jnp.float32) * spread * factor_of
    return jnp.minimum(jnp.maximum(result, -limit), limit).astype(kind)


def setup_inputs(seed: int = 0, part: int = 0) -> dict:
    keys = jax.random.split(jax.random.key(seed), 20)
    own_keys = jax.random.split(jax.random.fold_in(keys[19], part), 20)
    tokens = gaussian(own_keys[0], (LEN, MODEL_WIDTH), 1.0, 6.0, ((0, 4), (1, 4)))
    lengths = ragged_sizes(own_keys[1], REQS, LEN, LEN // 2, 2).astype(jnp.int32)
    request_adapter_ids = set_ends(jax.random.randint(own_keys[2], (REQS,), 0, ADAPTER_COUNT), jax.random.fold_in(own_keys[2], 1), 0, ADAPTER_COUNT - 1).astype(jnp.int32)
    adapter_store_slot = jax.random.permutation(keys[3], ADAPTER_COUNT).astype(jnp.int32)
    xchan_input_weight = gaussian(keys[4], (MODEL_WIDTH, HEAD_TOTAL * HEAD_SIZE), MODEL_WIDTH ** -0.5, 0.078125, ((0, 4), (1, 4)))
    bc_input_weight = gaussian(keys[5], (MODEL_WIDTH, 2 * STATE_SIZE), MODEL_WIDTH ** -0.5, 0.078125, ((0, 4), (1, 4)))
    step_input_weight = gaussian(keys[6], (MODEL_WIDTH, HEAD_TOTAL), MODEL_WIDTH ** -0.5, 0.078125, ((0, 4), (1, 4)))
    convolution_x_taps = gaussian(keys[7], (KC, HEAD_TOTAL * HEAD_SIZE), 0.5, 3.0, ((1, 4),), jnp.float32)
    convolution_bc_taps = gaussian(keys[8], (KC, 2 * STATE_SIZE), 0.5, 3.0, ((1, 4),), jnp.float32)
    step_bias = jnp.clip(-2.0 + 3.0 * jax.random.uniform(keys[9], (HEAD_TOTAL,), jnp.float32) ** levels(keys[9], (HEAD_TOTAL,), ((0, 4),), -0.2, 0.2), -2.0, 1.0)
    decay_log_rate = draw_decay_log_rate(jax.random.fold_in(keys[19], 71), part)
    head_skip_gain = jnp.clip(0.5 + 1.0 * jax.random.uniform(keys[11], (HEAD_TOTAL,), jnp.float32) ** levels(keys[11], (HEAD_TOTAL,), ((0, 4),), -0.2, 0.2), 0.5, 1.5)
    output_norm_gain = jnp.clip(1.0 + 0.18 * jax.random.normal(keys[12], (HEAD_TOTAL * HEAD_SIZE,), jnp.float32), 0.1, 1.9)
    output_weight = gaussian(keys[13], (HEAD_TOTAL * HEAD_SIZE, MODEL_WIDTH), (HEAD_TOTAL * HEAD_SIZE) ** -0.5, 0.09375, ((0, 4), (1, 4)))
    adapter_down_input = gaussian(keys[14], (ADAPTER_COUNT, MODEL_WIDTH, ADAPTER_RANK), MODEL_WIDTH ** -0.5, 0.078125, ((0, 4), (1, 4)))
    adapter_up_xchan = gaussian(keys[15], (ADAPTER_COUNT, ADAPTER_RANK, HEAD_TOTAL * HEAD_SIZE), ADAPTER_RANK ** -0.5, 0.75, ((0, 4), (2, 4)))
    adapter_up_bc = gaussian(keys[16], (ADAPTER_COUNT, ADAPTER_RANK, 2 * STATE_SIZE), ADAPTER_RANK ** -0.5, 0.75, ((0, 4), (2, 4)))
    adapter_down_output = gaussian(keys[17], (ADAPTER_COUNT, HEAD_TOTAL * HEAD_SIZE, ADAPTER_RANK), (HEAD_TOTAL * HEAD_SIZE) ** -0.5, 0.09375, ((0, 4), (1, 4)))
    adapter_up_output = gaussian(keys[18], (ADAPTER_COUNT, ADAPTER_RANK, MODEL_WIDTH), ADAPTER_RANK ** -0.5, 0.75, ((0, 4), (2, 4)))
    return dict(tokens=tokens, lengths=lengths, request_adapter_ids=request_adapter_ids, adapter_store_slot=adapter_store_slot, xchan_input_weight=xchan_input_weight, bc_input_weight=bc_input_weight, step_input_weight=step_input_weight, convolution_x_taps=convolution_x_taps, convolution_bc_taps=convolution_bc_taps, step_bias=step_bias, decay_log_rate=decay_log_rate, head_skip_gain=head_skip_gain, output_norm_gain=output_norm_gain, output_weight=output_weight, adapter_down_input=adapter_down_input, adapter_up_xchan=adapter_up_xchan, adapter_up_bc=adapter_up_bc, adapter_down_output=adapter_down_output, adapter_up_output=adapter_up_output)


FULL_PRECISION = lax.Precision.HIGHEST
NORM_EPSILON = 1e-06

def segment_of(positions, request_ends):
    inside = (positions[:, None] >= request_ends[None, :]).astype(jnp.int32)
    counted = lax.optimization_barrier(jnp.sum(inside, axis=1, dtype=jnp.int32))
    return jnp.where(positions < 0, jnp.int32(-1), counted).astype(jnp.int32)

def span_parts(x_heads, b_proj, c_proj, step_size, log_decay, segment, previous):
    length = x_heads.shape[0]
    cumulative = jnp.cumsum(log_decay, axis=0)
    final_log = cumulative[length - 1]
    places = jnp.arange(length, dtype=jnp.int32)
    same_request = jnp.logical_and(segment[:, None] == segment[None, :], places[None, :] <= places[:, None]).astype(jnp.float32)
    log_gap = cumulative.T[:, :, None] - cumulative.T[:, None, :]
    decay_table = jnp.exp(jnp.minimum(log_gap, 0.0)) * same_request[None]
    scores = lax.dot_general(c_proj, b_proj, (((1,), (1,)), ((), ())), preferred_element_type=jnp.float32)
    weights = scores[None] * decay_table * step_size.T[:, None, :]
    inner_out = jnp.einsum('hts,shd->thd', weights, x_heads, precision=FULL_PRECISION)
    at_end = (segment == segment[length - 1]).astype(jnp.float32)
    state_weight = jnp.exp(final_log[None, :] - cumulative) * at_end[:, None] * step_size
    local_state = jnp.einsum('sh,shd,sn->hdn', state_weight, x_heads, b_proj.astype(jnp.float32), precision=FULL_PRECISION)
    enter_weight = jnp.exp(cumulative) * (segment == previous).astype(jnp.float32)[:, None]
    carry_decay = jnp.exp(final_log) * (segment[length - 1] == previous).astype(jnp.float32)
    return (inner_out, local_state, enter_weight, carry_decay)

def reference(tokens, lengths, request_adapter_ids, adapter_store_slot, xchan_input_weight, bc_input_weight, step_input_weight, convolution_x_taps, convolution_bc_taps, step_bias, decay_log_rate, head_skip_gain, output_norm_gain, output_weight, adapter_down_input, adapter_up_xchan, adapter_up_bc, adapter_down_output, adapter_up_output):
    width = HEAD_TOTAL * HEAD_SIZE
    input_rows = tokens
    request_ends = jnp.cumsum(lengths, dtype=jnp.int32).astype(jnp.int32)
    positions = jnp.arange(LEN, dtype=jnp.int32)
    segment = segment_of(positions, request_ends)
    adapter_picker_matrix = (segment[:, None] == jnp.arange(REQS, dtype=jnp.int32)[None, :]).astype(jnp.float32)
    slot_indices = adapter_store_slot[request_adapter_ids].astype(jnp.int32)
    rank_hidden = jnp.zeros((LEN, ADAPTER_RANK), jnp.float32)
    for request_item in range(REQS):
        rank_hidden = rank_hidden + adapter_picker_matrix[:, request_item:request_item + 1] * jnp.dot(input_rows, adapter_down_input[slot_indices[request_item]], preferred_element_type=jnp.float32)
    rank_hidden = rank_hidden.astype(jnp.bfloat16)
    xchan_values = jnp.dot(input_rows, xchan_input_weight, preferred_element_type=jnp.float32)
    bc_channel_values = jnp.dot(input_rows, bc_input_weight, preferred_element_type=jnp.float32)
    step_raw = jnp.dot(input_rows, step_input_weight, preferred_element_type=jnp.float32)
    for request_item in range(REQS):
        selected_adapter = adapter_picker_matrix[:, request_item:request_item + 1]
        xchan_values = xchan_values + selected_adapter * jnp.dot(rank_hidden, adapter_up_xchan[slot_indices[request_item]], preferred_element_type=jnp.float32)
        bc_channel_values = bc_channel_values + selected_adapter * jnp.dot(rank_hidden, adapter_up_bc[slot_indices[request_item]], preferred_element_type=jnp.float32)
    values = jnp.concatenate([xchan_values, bc_channel_values], axis=1)
    kernel = jnp.concatenate([convolution_x_taps, convolution_bc_taps], axis=1)
    padded = jnp.concatenate([jnp.zeros((KC - 1, values.shape[1]), jnp.float32), values], axis=0)
    padded_segment = segment_of(jnp.arange(LEN + KC - 1, dtype=jnp.int32) - (KC - 1), request_ends)
    convolved = jnp.zeros_like(values)
    for tap in range(KC):
        keep = (padded_segment[tap:tap + LEN] == segment).astype(jnp.float32)
        convolved = convolved + kernel[tap][None, :] * padded[tap:tap + LEN] * keep[:, None]
    act = jax.nn.silu(convolved)
    x_all = act[:, :width].reshape(LEN, HEAD_TOTAL, HEAD_SIZE)
    b_all = act[:, width:width + STATE_SIZE].astype(jnp.bfloat16)
    c_all = act[:, width + STATE_SIZE:].astype(jnp.bfloat16)
    step_size = jax.nn.softplus(step_raw + step_bias[None, :])
    log_decay = -step_size * jnp.exp(decay_log_rate)[None, :]

    def advance(entering, block_index):
        start = block_index * TOK_DEV
        x_heads = lax.dynamic_slice_in_dim(x_all, start, TOK_DEV, 0)
        b_proj = lax.dynamic_slice_in_dim(b_all, start, TOK_DEV, 0)
        c_proj = lax.dynamic_slice_in_dim(c_all, start, TOK_DEV, 0)
        step_block = lax.dynamic_slice_in_dim(step_size, start, TOK_DEV, 0)
        decay_block = lax.dynamic_slice_in_dim(log_decay, start, TOK_DEV, 0)
        segment_block = lax.dynamic_slice_in_dim(segment, start, TOK_DEV, 0)
        previous = segment_of(jnp.reshape(start - 1, (1,)).astype(jnp.int32), request_ends)[0]
        inner_out, local_state, enter_weight, carry_decay = span_parts(x_heads, b_proj, c_proj, step_block, decay_block, segment_block, previous)
        entered = jnp.einsum('tn,hdn->thd', c_proj.astype(jnp.float32), entering, precision=FULL_PRECISION) * enter_weight[:, :, None]
        output = inner_out + entered + head_skip_gain[None, :, None] * x_heads
        leaving = carry_decay[:, None, None] * entering + local_state
        return (leaving, output)
    initial = jnp.zeros((HEAD_TOTAL, HEAD_SIZE, STATE_SIZE), jnp.float32)
    final_state, outputs = lax.scan(advance, initial, jnp.arange(N_CTX, dtype=jnp.int32))
    mixer_out = outputs.reshape(LEN, width)
    grouped = mixer_out.reshape(LEN, HEAD_TOTAL // HPD, HPD * HEAD_SIZE)
    scale = lax.rsqrt(lax.optimization_barrier(jnp.mean(grouped * grouped, axis=2, keepdims=True)) + NORM_EPSILON)
    normalized_rows = ((grouped * scale).reshape(LEN, width) * output_norm_gain[None, :]).astype(jnp.bfloat16)
    group = HPD * HEAD_SIZE
    token_total = jnp.zeros((LEN, MODEL_WIDTH), jnp.float32)
    for member in range(HEAD_TOTAL // HPD):
        piece = jnp.dot(normalized_rows[:, member * group:(member + 1) * group], output_weight[member * group:(member + 1) * group], preferred_element_type=jnp.float32)
        token_total = token_total + piece.astype(jnp.bfloat16).astype(jnp.float32)
    rank_hidden_output = jnp.zeros((LEN, ADAPTER_RANK), jnp.float32)
    for request_item in range(REQS):
        rank_hidden_output = rank_hidden_output + adapter_picker_matrix[:, request_item:request_item + 1] * jnp.dot(normalized_rows, adapter_down_output[slot_indices[request_item]], preferred_element_type=jnp.float32)
    rank_hidden_output = rank_hidden_output.astype(jnp.bfloat16)
    for request_item in range(REQS):
        token_total = token_total + adapter_picker_matrix[:, request_item:request_item + 1] * jnp.dot(rank_hidden_output, adapter_up_output[slot_indices[request_item]], preferred_element_type=jnp.float32)
    return token_total.astype(jnp.bfloat16)
```

```python
import jax
import jax.numpy as jnp
from jax import lax
from jax.sharding import PartitionSpec as P

FULL_PRECISION = lax.Precision.HIGHEST
NORM_EPSILON = 1e-06


def from_root(block, axis, source):
    block = jnp.where(lax.axis_index(axis) == source, block, jnp.zeros_like(block))
    return lax.psum(block, axis)


def passed_along(shard, axis, by):
    size = lax.axis_size(axis)
    pairs = [(i, i + by) for i in range(size) if 0 <= i + by < size]
    return lax.ppermute(shard, axis, pairs)


def prefix(shard, axis, combine, identity):
    size, place = (lax.axis_size(axis), lax.axis_index(axis))
    everything = jax.tree.map(
        lambda part, kind: lax.all_gather(part.astype(kind), axis),
        shard,
        (jnp.bfloat16, jnp.bfloat16),
    )
    start = jax.tree.map(
        lambda part, zero: jnp.broadcast_to(jnp.asarray(zero, part.dtype), part.shape),
        shard,
        identity,
    )

    def lap(k, before):
        reached = k < place
        new = combine(
            before, jax.tree.map(lambda part, own: part[k].astype(own.dtype), everything, shard)
        )
        return jax.tree.map(lambda a, b: jnp.where(reached, a, b), new, before)

    return lax.fori_loop(0, size, lap, start)


def segment_of(positions, request_ends):
    inside = (positions[:, None] >= request_ends[None, :]).astype(jnp.int32)
    counted = jnp.sum(inside, axis=1, dtype=jnp.int32)
    return jnp.where(positions < 0, jnp.int32(-1), counted)


def span_parts(x_heads, b_proj, c_proj, step_size, log_decay, segment, previous):
    length = x_heads.shape[0]
    cumulative = jnp.cumsum(log_decay, axis=0)
    final_log = cumulative[length - 1]
    places = jnp.arange(length, dtype=jnp.int32)
    same_request = jnp.logical_and(
        segment[:, None] == segment[None, :], places[None, :] <= places[:, None]
    ).astype(jnp.float32)
    log_gap = cumulative.T[:, :, None] - cumulative.T[:, None, :]
    decay_table = jnp.exp(jnp.minimum(log_gap, 0.0)) * same_request[None]
    scores = lax.dot_general(
        c_proj, b_proj, (((1,), (1,)), ((), ())), preferred_element_type=jnp.float32
    )
    weights = scores[None] * decay_table * step_size.T[:, None, :]
    inner_out = jnp.einsum("hts,shd->thd", weights, x_heads, precision=FULL_PRECISION)
    at_end = (segment == segment[length - 1]).astype(jnp.float32)
    state_weight = jnp.exp(final_log[None, :] - cumulative) * at_end[:, None] * step_size
    local_state = jnp.einsum(
        "sh,shd,sn->hdn",
        state_weight,
        x_heads,
        b_proj.astype(jnp.float32),
        precision=FULL_PRECISION,
    )
    enter_weight = jnp.exp(cumulative) * (segment == previous).astype(jnp.float32)[:, None]
    carry_decay = jnp.exp(final_log) * (segment[length - 1] == previous).astype(jnp.float32)
    return (inner_out, local_state, enter_weight, carry_decay)


def select_rows(wide, adapter_picker_matrix):
    shaped = wide.reshape(wide.shape[0], adapter_picker_matrix.shape[1], -1)
    return jnp.sum(shaped * adapter_picker_matrix[:, :, None], axis=1)


def masked_wide(values, onehot_b):
    return (values[:, None, :] * onehot_b[:, :, None]).reshape(values.shape[0], -1)


def general_body(
    tokens,
    lengths,
    request_adapter_ids,
    adapter_store_slot,
    xchan_input_weight,
    bc_input_weight,
    step_input_weight,
    convolution_x_taps,
    convolution_bc_taps,
    step_bias,
    decay_log_rate,
    head_skip_gain,
    output_norm_gain,
    output_weight,
    adapter_down_input,
    adapter_up_xchan,
    adapter_up_bc,
    adapter_down_output,
    adapter_up_output,
):
    length = tokens.shape[0]
    request_list = lengths.shape[0]
    taps = convolution_x_taps.shape[0]
    bank_entries = adapter_down_input.shape[0]
    head_count = step_bias.shape[0]
    channels = xchan_input_weight.shape[1]
    start_pos = lax.axis_index("ctx") * length
    request_ends = jnp.cumsum(lengths, dtype=jnp.int32)
    positions = start_pos + jnp.arange(length, dtype=jnp.int32)
    segment = segment_of(positions, request_ends)
    previous = segment_of(jnp.reshape(start_pos - 1, (1,)), request_ends)[0]
    adapter_picker_matrix = (
        segment[:, None] == jnp.arange(request_list, dtype=jnp.int32)[None, :]
    ).astype(jnp.float32)
    onehot_b = adapter_picker_matrix.astype(jnp.bfloat16)
    slot_indices = adapter_store_slot[request_adapter_ids]
    initial_stacks = (
        jnp.zeros(
            (adapter_down_input.shape[1], request_list, adapter_down_input.shape[2]), jnp.bfloat16
        ),
        jnp.zeros((request_list,) + adapter_up_xchan.shape[1:], jnp.bfloat16),
        jnp.zeros((request_list,) + adapter_up_bc.shape[1:], jnp.bfloat16),
        jnp.zeros(
            (adapter_down_output.shape[1], request_list, adapter_down_output.shape[2]), jnp.bfloat16
        ),
        jnp.zeros((request_list,) + adapter_up_output.shape[1:], jnp.bfloat16),
    )
    stack_dims = (1, 0, 0, 1, 0)

    def fetch(request_item, current):
        slot = slot_indices[request_item]
        owner = slot // bank_entries
        within = slot % bank_entries
        a_in, b_x, b_bc, a_out, b_out = [
            lax.dynamic_index_in_dim(adapter_bank, within, 0, keepdims=False)
            for adapter_bank in (
                adapter_down_input,
                adapter_up_xchan,
                adapter_up_bc,
                adapter_down_output,
                adapter_up_output,
            )
        ]
        received = (
            from_root(a_in, "ctx", owner),
            from_root(b_x, "ctx", owner),
            from_root(b_bc, "ctx", owner),
            from_root(a_out, "ctx", owner),
            from_root(b_out, "ctx", owner),
        )
        return tuple(
            (
                lax.dynamic_update_index_in_dim(stack, panel, request_item, along)
                for stack, panel, along in zip(current, received, stack_dims)
            )
        )

    stacks = lax.fori_loop(0, request_list, fetch, initial_stacks)
    rank_value = adapter_down_input.shape[2]
    down_in = stacks[0].reshape(stacks[0].shape[0], request_list * rank_value)
    up_x = stacks[1].reshape(request_list * rank_value, -1)
    up_bc = stacks[2].reshape(request_list * rank_value, -1)
    down_out = stacks[3].reshape(stacks[3].shape[0], request_list * rank_value)
    up_out = stacks[4].reshape(request_list * rank_value, -1)
    lowrank_part = select_rows(
        jnp.dot(tokens, down_in, preferred_element_type=jnp.float32), adapter_picker_matrix
    )
    rank_hidden = lax.psum(lowrank_part.astype(jnp.bfloat16), ("tp", "dp"))
    lowrank_wide = masked_wide(rank_hidden, onehot_b)
    full_tokens = lax.all_gather(tokens, ("tp", "dp"), axis=1, tiled=True)
    pieces = (
        lax.all_gather(xchan_input_weight, "ctx", axis=0, tiled=True),
        lax.all_gather(bc_input_weight, "ctx", axis=0, tiled=True),
        lax.all_gather(step_input_weight, "ctx", axis=0, tiled=True),
    )
    xchan_values, bc_channel_values, step_raw = tuple(
        (jnp.dot(full_tokens, piece, preferred_element_type=jnp.float32) for piece in pieces)
    )
    xchan_values = xchan_values + jnp.dot(lowrank_wide, up_x, preferred_element_type=jnp.float32)
    bc_channel_values = bc_channel_values + jnp.dot(
        lowrank_wide, up_bc, preferred_element_type=jnp.float32
    )
    values = jnp.concatenate([xchan_values, bc_channel_values], axis=1)
    kernel = jnp.concatenate([convolution_x_taps, convolution_bc_taps], axis=1)
    tail_rows = passed_along(values[length - (taps - 1) :], "ctx", 1)
    extended = jnp.concatenate([tail_rows, values], axis=0)
    extended_segment = segment_of(
        start_pos - (taps - 1) + jnp.arange(length + taps - 1, dtype=jnp.int32), request_ends
    )
    convolved = jnp.zeros_like(values)
    for tap in range(taps):
        keep = (extended_segment[tap : tap + length] == segment).astype(jnp.float32)
        convolved = convolved + kernel[tap][None, :] * extended[tap : tap + length] * keep[:, None]
    act = jax.nn.silu(convolved)
    x_heads = act[:, :channels].reshape(length, head_count, -1)
    bc_local = act[:, channels:].astype(jnp.bfloat16)
    bc_all = lax.all_gather(bc_local, ("tp", "dp"), axis=1, tiled=True)
    state_width = bc_all.shape[1] // 2
    b_proj = bc_all[:, :state_width]
    c_proj = bc_all[:, state_width:]
    step_size = jax.nn.softplus(step_raw + step_bias[None, :])
    log_decay = -step_size * jnp.exp(decay_log_rate)[None, :]
    inner_out, local_state, enter_weight, carry_decay = span_parts(
        x_heads, b_proj, c_proj, step_size, log_decay, segment, previous
    )

    def compose(earlier, later):
        return (earlier[0] * later[0], later[0][:, None, None] * earlier[1] + later[1])

    carried = prefix(
        (carry_decay, local_state),
        "ctx",
        compose,
        (jnp.ones_like(carry_decay), jnp.zeros_like(local_state)),
    )
    entering = carried[1]
    entered = (
        jnp.einsum("tn,hdn->thd", c_proj.astype(jnp.float32), entering, precision=FULL_PRECISION)
        * enter_weight[:, :, None]
    )
    mixer_out = (inner_out + entered + head_skip_gain[None, :, None] * x_heads).reshape(
        length, channels
    )
    scale = lax.rsqrt(jnp.mean(mixer_out * mixer_out, axis=1, keepdims=True) + NORM_EPSILON)
    normalized_rows = (mixer_out * scale * output_norm_gain[None, :]).astype(jnp.bfloat16)
    term = jnp.dot(
        normalized_rows,
        lax.all_gather(output_weight, "ctx", axis=1, tiled=True),
        preferred_element_type=jnp.float32,
    )
    base = lax.psum_scatter(
        term.astype(jnp.bfloat16), ("tp", "dp"), scatter_dimension=1, tiled=True
    ).astype(jnp.float32)
    lowrank_out_part = select_rows(
        jnp.dot(normalized_rows, down_out, preferred_element_type=jnp.float32),
        adapter_picker_matrix,
    )
    rank_hidden_output = lax.psum(lowrank_out_part.astype(jnp.bfloat16), ("tp", "dp"))
    adapter_term = jnp.dot(
        masked_wide(rank_hidden_output, onehot_b), up_out, preferred_element_type=jnp.float32
    )
    return (base + adapter_term).astype(jnp.bfloat16)


def transposed(block):
    side = lax.axis_size("ctx")
    pairs = [(row * side + col, col * side + row) for row in range(side) for col in range(side)]
    return lax.ppermute(block, ("ctx", "tp", "dp"), pairs)


def owned_rows(values, owned):
    return jnp.concatenate(
        [values * owned[:, i : i + 1].astype(values.dtype) for i in range(owned.shape[1])], axis=1
    )


def square_body(
    tokens,
    lengths,
    request_adapter_ids,
    adapter_store_slot,
    xchan_input_weight,
    bc_input_weight,
    step_input_weight,
    convolution_x_taps,
    convolution_bc_taps,
    step_bias,
    decay_log_rate,
    head_skip_gain,
    output_norm_gain,
    output_weight,
    adapter_down_input,
    adapter_up_xchan,
    adapter_up_bc,
    adapter_down_output,
    adapter_up_output,
):
    length = tokens.shape[0]
    side = lax.axis_size("ctx")
    stream = side * length
    taps = convolution_x_taps.shape[0]
    bank_entries = adapter_down_input.shape[0]
    rank_value = adapter_down_input.shape[2]
    head_count = step_bias.shape[0]
    channels = xchan_input_weight.shape[1]
    bc_width = bc_input_weight.shape[1]
    here = lax.axis_index("ctx")
    lane = lax.axis_index(("tp", "dp"))
    start_pos = here * length
    request_ends = jnp.cumsum(lengths, dtype=jnp.int32)
    every_position = jnp.arange(stream, dtype=jnp.int32)
    every_segment = segment_of(every_position, request_ends)
    slot_indices = adapter_store_slot[request_adapter_ids]
    request_count = lengths.shape[0]
    stream_onehot = every_segment[:, None] == jnp.arange(request_count, dtype=jnp.int32)[None, :]
    slot_of_position = jnp.sum(
        jnp.where(stream_onehot, slot_indices[None, :], 0), axis=1, dtype=jnp.int32
    )
    entry_ids = jnp.arange(bank_entries, dtype=jnp.int32)[None, :]
    owned_here = slot_of_position[:, None] == here * bank_entries + entry_ids
    owned_lane = slot_of_position[:, None] == lane * bank_entries + entry_ids
    positions = start_pos + jnp.arange(length, dtype=jnp.int32)
    segment = segment_of(positions, request_ends)
    previous = segment_of(jnp.reshape(start_pos - 1, (1,)), request_ends)[0]

    stream_rows = lax.all_gather(transposed(tokens), ("tp", "dp"), axis=0, tiled=True)
    down_in_t = transposed(adapter_down_input)
    up_out_t = transposed(adapter_up_output)
    down_part = jnp.einsum(
        "pf,efr->per", stream_rows, down_in_t, preferred_element_type=jnp.float32
    )
    down_pick = jnp.sum(
        down_part * owned_lane[:, :, None].astype(jnp.float32), axis=1
    )
    rank_hidden = lax.psum(down_pick, ("ctx", "tp", "dp"))
    hidden_wide = owned_rows(rank_hidden, owned_here).astype(jnp.bfloat16)
    xchan_part = jnp.dot(
        stream_rows, xchan_input_weight, preferred_element_type=jnp.float32
    ) + jnp.dot(
        hidden_wide,
        adapter_up_xchan.reshape(bank_entries * rank_value, -1),
        preferred_element_type=jnp.float32,
    )
    bc_part = jnp.dot(stream_rows, bc_input_weight, preferred_element_type=jnp.float32) + jnp.dot(
        hidden_wide,
        adapter_up_bc.reshape(bank_entries * rank_value, -1),
        preferred_element_type=jnp.float32,
    )
    step_part = jnp.dot(stream_rows, step_input_weight, preferred_element_type=jnp.float32)
    summed = lax.psum_scatter(
        jnp.concatenate([xchan_part, bc_part, step_part], axis=1),
        "ctx",
        scatter_dimension=0,
        tiled=True,
    )
    values = summed[:, : channels + bc_width]
    step_raw = summed[:, channels + bc_width :]

    kernel = jnp.concatenate([convolution_x_taps, convolution_bc_taps], axis=1)
    tail_rows = passed_along(values[length - (taps - 1) :], "ctx", 1)
    extended = jnp.concatenate([tail_rows, values], axis=0)
    extended_segment = segment_of(
        start_pos - (taps - 1) + jnp.arange(length + taps - 1, dtype=jnp.int32), request_ends
    )
    convolved = jnp.zeros_like(values)
    for tap in range(taps):
        keep = (extended_segment[tap : tap + length] == segment).astype(jnp.float32)
        convolved = convolved + kernel[tap][None, :] * extended[tap : tap + length] * keep[:, None]
    act = jax.nn.silu(convolved)
    x_heads = act[:, :channels].reshape(length, head_count, -1)
    bc_local = act[:, channels:].astype(jnp.bfloat16)
    bc_all = lax.all_gather(bc_local, ("tp", "dp"), axis=1, tiled=True)
    state_width = bc_all.shape[1] // 2
    b_proj = bc_all[:, :state_width]
    c_proj = bc_all[:, state_width:]
    step_size = jax.nn.softplus(step_raw + step_bias[None, :])
    log_decay = -step_size * jnp.exp(decay_log_rate)[None, :]
    inner_out, local_state, enter_weight, carry_decay = span_parts(
        x_heads, b_proj, c_proj, step_size, log_decay, segment, previous
    )

    def compose(earlier, later):
        return (earlier[0] * later[0], later[0][:, None, None] * earlier[1] + later[1])

    carried = prefix(
        (carry_decay, local_state),
        "ctx",
        compose,
        (jnp.ones_like(carry_decay), jnp.zeros_like(local_state)),
    )
    entering = carried[1]
    entered = (
        jnp.einsum("tn,hdn->thd", c_proj.astype(jnp.float32), entering, precision=FULL_PRECISION)
        * enter_weight[:, :, None]
    )
    mixer_out = (inner_out + entered + head_skip_gain[None, :, None] * x_heads).reshape(
        length, channels
    )
    scale = lax.rsqrt(jnp.mean(mixer_out * mixer_out, axis=1, keepdims=True) + NORM_EPSILON)
    normalized_rows = (mixer_out * scale * output_norm_gain[None, :]).astype(jnp.bfloat16)

    normed_stream = lax.all_gather(normalized_rows, "ctx", axis=0, tiled=True)
    out_down_part = jnp.einsum(
        "pc,ecr->per", normed_stream, adapter_down_output, preferred_element_type=jnp.float32
    )
    out_down_pick = jnp.sum(out_down_part * owned_here[:, :, None].astype(jnp.float32), axis=1)
    rank_hidden_output = lax.psum(out_down_pick, ("ctx", "tp", "dp"))
    base_part = jnp.dot(
        normed_stream, output_weight, preferred_element_type=jnp.float32
    ).astype(jnp.bfloat16).astype(jnp.float32)
    adapter_part = jnp.dot(
        owned_rows(rank_hidden_output, owned_lane).astype(jnp.bfloat16),
        up_out_t.reshape(bank_entries * rank_value, -1),
        preferred_element_type=jnp.float32,
    )
    mixed_t = lax.psum_scatter(
        base_part + adapter_part, ("tp", "dp"), scatter_dimension=0, tiled=True
    ).astype(jnp.bfloat16)
    return transposed(mixed_t)


def solution(mesh):
    body = square_body if mesh.shape["ctx"] == mesh.shape["tp"] * mesh.shape["dp"] else general_body
    placed = (
        P(("groups", "ctx"), ("tp", "dp")),
        P("groups"),
        P("groups"),
        P(),
        P("ctx", ("tp", "dp")),
        P("ctx", ("tp", "dp")),
        P("ctx", ("tp", "dp")),
        P(None, ("tp", "dp")),
        P(None, ("tp", "dp")),
        P(("tp", "dp")),
        P(("tp", "dp")),
        P(("tp", "dp")),
        P(("tp", "dp")),
        P(("tp", "dp"), "ctx"),
        P("ctx", ("tp", "dp"), None),
        P("ctx", None, ("tp", "dp")),
        P("ctx", None, ("tp", "dp")),
        P("ctx", ("tp", "dp"), None),
        P("ctx", None, ("tp", "dp")),
    )
    return jax.shard_map(
        body,
        mesh=mesh,
        in_specs=placed,
        out_specs=P(("groups", "ctx"), ("tp", "dp")),
        check_vma=False,
    )
```

```python
import jax
import jax.numpy as jnp
from jax import lax
from jax.sharding import PartitionSpec as P

FULL_PRECISION = lax.Precision.HIGHEST
NORM_EPSILON = 1e-06


def from_root(block, axis, source):
    block = jnp.where(lax.axis_index(axis) == source, block, jnp.zeros_like(block))
    return lax.psum(block, axis)


def passed_along(shard, axis, by):
    size = lax.axis_size(axis)
    pairs = [(i, i + by) for i in range(size) if 0 <= i + by < size]
    return lax.ppermute(shard, axis, pairs)


def prefix(shard, axis, combine, identity):
    size, place = (lax.axis_size(axis), lax.axis_index(axis))
    everything = jax.tree.map(
        lambda part, kind: lax.all_gather(part.astype(kind), axis),
        shard,
        (jnp.bfloat16, jnp.bfloat16),
    )
    start = jax.tree.map(
        lambda part, zero: jnp.broadcast_to(jnp.asarray(zero, part.dtype), part.shape),
        shard,
        identity,
    )

    def lap(k, before):
        reached = k < place
        new = combine(
            before, jax.tree.map(lambda part, own: part[k].astype(own.dtype), everything, shard)
        )
        return jax.tree.map(lambda a, b: jnp.where(reached, a, b), new, before)

    return lax.fori_loop(0, size, lap, start)


def segment_of(positions, request_ends):
    inside = (positions[:, None] >= request_ends[None, :]).astype(jnp.int32)
    counted = jnp.sum(inside, axis=1, dtype=jnp.int32)
    return jnp.where(positions < 0, jnp.int32(-1), counted)


def span_parts(x_heads, b_proj, c_proj, step_size, log_decay, segment, previous):
    length = x_heads.shape[0]
    cumulative = jnp.cumsum(log_decay, axis=0)
    final_log = cumulative[length - 1]
    places = jnp.arange(length, dtype=jnp.int32)
    same_request = jnp.logical_and(
        segment[:, None] == segment[None, :], places[None, :] <= places[:, None]
    ).astype(jnp.float32)
    log_gap = cumulative.T[:, :, None] - cumulative.T[:, None, :]
    decay_table = jnp.exp(jnp.minimum(log_gap, 0.0)) * same_request[None]
    scores = lax.dot_general(
        c_proj, b_proj, (((1,), (1,)), ((), ())), preferred_element_type=jnp.float32
    )
    weights = scores[None] * decay_table * step_size.T[:, None, :]
    inner_out = jnp.einsum("hts,shd->thd", weights, x_heads, precision=FULL_PRECISION)
    at_end = (segment == segment[length - 1]).astype(jnp.float32)
    state_weight = jnp.exp(final_log[None, :] - cumulative) * at_end[:, None] * step_size
    local_state = jnp.einsum(
        "sh,shd,sn->hdn",
        state_weight,
        x_heads,
        b_proj.astype(jnp.float32),
        precision=FULL_PRECISION,
    )
    enter_weight = jnp.exp(cumulative) * (segment == previous).astype(jnp.float32)[:, None]
    carry_decay = jnp.exp(final_log) * (segment[length - 1] == previous).astype(jnp.float32)
    return (inner_out, local_state, enter_weight, carry_decay)


def select_rows(wide, adapter_picker_matrix):
    shaped = wide.reshape(wide.shape[0], adapter_picker_matrix.shape[1], -1)
    return jnp.sum(shaped * adapter_picker_matrix[:, :, None], axis=1)


def masked_wide(values, onehot_b):
    return (values[:, None, :] * onehot_b[:, :, None]).reshape(values.shape[0], -1)


def general_body(
    tokens,
    lengths,
    request_adapter_ids,
    adapter_store_slot,
    xchan_input_weight,
    bc_input_weight,
    step_input_weight,
    convolution_x_taps,
    convolution_bc_taps,
    step_bias,
    decay_log_rate,
    head_skip_gain,
    output_norm_gain,
    output_weight,
    adapter_down_input,
    adapter_up_xchan,
    adapter_up_bc,
    adapter_down_output,
    adapter_up_output,
):
    length = tokens.shape[0]
    request_list = lengths.shape[0]
    taps = convolution_x_taps.shape[0]
    bank_entries = adapter_down_input.shape[0]
    head_count = step_bias.shape[0]
    channels = xchan_input_weight.shape[1]
    start_pos = lax.axis_index("ctx") * length
    request_ends = jnp.cumsum(lengths, dtype=jnp.int32)
    positions = start_pos + jnp.arange(length, dtype=jnp.int32)
    segment = segment_of(positions, request_ends)
    previous = segment_of(jnp.reshape(start_pos - 1, (1,)), request_ends)[0]
    adapter_picker_matrix = (
        segment[:, None] == jnp.arange(request_list, dtype=jnp.int32)[None, :]
    ).astype(jnp.float32)
    onehot_b = adapter_picker_matrix.astype(jnp.bfloat16)
    slot_indices = adapter_store_slot[request_adapter_ids]
    initial_stacks = (
        jnp.zeros(
            (adapter_down_input.shape[1], request_list, adapter_down_input.shape[2]), jnp.bfloat16
        ),
        jnp.zeros((request_list,) + adapter_up_xchan.shape[1:], jnp.bfloat16),
        jnp.zeros((request_list,) + adapter_up_bc.shape[1:], jnp.bfloat16),
        jnp.zeros(
            (adapter_down_output.shape[1], request_list, adapter_down_output.shape[2]), jnp.bfloat16
        ),
        jnp.zeros((request_list,) + adapter_up_output.shape[1:], jnp.bfloat16),
    )
    stack_dims = (1, 0, 0, 1, 0)

    def fetch(request_item, current):
        slot = slot_indices[request_item]
        owner = slot // bank_entries
        within = slot % bank_entries
        a_in, b_x, b_bc, a_out, b_out = [
            lax.dynamic_index_in_dim(adapter_bank, within, 0, keepdims=False)
            for adapter_bank in (
                adapter_down_input,
                adapter_up_xchan,
                adapter_up_bc,
                adapter_down_output,
                adapter_up_output,
            )
        ]
        received = (
            from_root(a_in, "ctx", owner),
            from_root(b_x, "ctx", owner),
            from_root(b_bc, "ctx", owner),
            from_root(a_out, "ctx", owner),
            from_root(b_out, "ctx", owner),
        )
        return tuple(
            (
                lax.dynamic_update_index_in_dim(stack, panel, request_item, along)
                for stack, panel, along in zip(current, received, stack_dims)
            )
        )

    stacks = lax.fori_loop(0, request_list, fetch, initial_stacks)
    rank_value = adapter_down_input.shape[2]
    down_in = stacks[0].reshape(stacks[0].shape[0], request_list * rank_value)
    up_x = stacks[1].reshape(request_list * rank_value, -1)
    up_bc = stacks[2].reshape(request_list * rank_value, -1)
    down_out = stacks[3].reshape(stacks[3].shape[0], request_list * rank_value)
    up_out = stacks[4].reshape(request_list * rank_value, -1)
    lowrank_part = select_rows(
        jnp.dot(tokens, down_in, preferred_element_type=jnp.float32), adapter_picker_matrix
    )
    rank_hidden = lax.psum(lowrank_part.astype(jnp.bfloat16), ("tp", "dp"))
    lowrank_wide = masked_wide(rank_hidden, onehot_b)
    full_tokens = lax.all_gather(tokens, ("tp", "dp"), axis=1, tiled=True)
    pieces = (
        lax.all_gather(xchan_input_weight, "ctx", axis=0, tiled=True),
        lax.all_gather(bc_input_weight, "ctx", axis=0, tiled=True),
        lax.all_gather(step_input_weight, "ctx", axis=0, tiled=True),
    )
    xchan_values, bc_channel_values, step_raw = tuple(
        (jnp.dot(full_tokens, piece, preferred_element_type=jnp.float32) for piece in pieces)
    )
    xchan_values = xchan_values + jnp.dot(lowrank_wide, up_x, preferred_element_type=jnp.float32)
    bc_channel_values = bc_channel_values + jnp.dot(
        lowrank_wide, up_bc, preferred_element_type=jnp.float32
    )
    values = jnp.concatenate([xchan_values, bc_channel_values], axis=1)
    kernel = jnp.concatenate([convolution_x_taps, convolution_bc_taps], axis=1)
    tail_rows = passed_along(values[length - (taps - 1) :], "ctx", 1)
    extended = jnp.concatenate([tail_rows, values], axis=0)
    extended_segment = segment_of(
        start_pos - (taps - 1) + jnp.arange(length + taps - 1, dtype=jnp.int32), request_ends
    )
    convolved = jnp.zeros_like(values)
    for tap in range(taps):
        keep = (extended_segment[tap : tap + length] == segment).astype(jnp.float32)
        convolved = convolved + kernel[tap][None, :] * extended[tap : tap + length] * keep[:, None]
    act = jax.nn.silu(convolved)
    x_heads = act[:, :channels].reshape(length, head_count, -1)
    bc_local = act[:, channels:].astype(jnp.bfloat16)
    bc_all = lax.all_gather(bc_local, ("tp", "dp"), axis=1, tiled=True)
    state_width = bc_all.shape[1] // 2
    b_proj = bc_all[:, :state_width]
    c_proj = bc_all[:, state_width:]
    step_size = jax.nn.softplus(step_raw + step_bias[None, :])
    log_decay = -step_size * jnp.exp(decay_log_rate)[None, :]
    inner_out, local_state, enter_weight, carry_decay = span_parts(
        x_heads, b_proj, c_proj, step_size, log_decay, segment, previous
    )

    def compose(earlier, later):
        return (earlier[0] * later[0], later[0][:, None, None] * earlier[1] + later[1])

    carried = prefix(
        (carry_decay, local_state),
        "ctx",
        compose,
        (jnp.ones_like(carry_decay), jnp.zeros_like(local_state)),
    )
    entering = carried[1]
    entered = (
        jnp.einsum("tn,hdn->thd", c_proj.astype(jnp.float32), entering, precision=FULL_PRECISION)
        * enter_weight[:, :, None]
    )
    mixer_out = (inner_out + entered + head_skip_gain[None, :, None] * x_heads).reshape(
        length, channels
    )
    scale = lax.rsqrt(jnp.mean(mixer_out * mixer_out, axis=1, keepdims=True) + NORM_EPSILON)
    normalized_rows = (mixer_out * scale * output_norm_gain[None, :]).astype(jnp.bfloat16)
    term = jnp.dot(
        normalized_rows,
        lax.all_gather(output_weight, "ctx", axis=1, tiled=True),
        preferred_element_type=jnp.float32,
    )
    base = lax.psum_scatter(
        term.astype(jnp.bfloat16), ("tp", "dp"), scatter_dimension=1, tiled=True
    ).astype(jnp.float32)
    lowrank_out_part = select_rows(
        jnp.dot(normalized_rows, down_out, preferred_element_type=jnp.float32),
        adapter_picker_matrix,
    )
    rank_hidden_output = lax.psum(lowrank_out_part.astype(jnp.bfloat16), ("tp", "dp"))
    adapter_term = jnp.dot(
        masked_wide(rank_hidden_output, onehot_b), up_out, preferred_element_type=jnp.float32
    )
    return (base + adapter_term).astype(jnp.bfloat16)


def moved(block, shift, kind):
    side = lax.axis_size("ctx")
    if kind == "ctx":
        pairs = [(a, (a + shift) % side) for a in range(side)]
        return lax.ppermute(block, "ctx", pairs)
    if kind == "rows":
        pairs = [(a * side + b, b * side + (a + shift) % side) for a in range(side) for b in range(side)]
    else:
        pairs = [(a * side + b, ((b + shift) % side) * side + a) for a in range(side) for b in range(side)]
    return lax.ppermute(block, ("ctx", "tp", "dp"), pairs)


def transposed(block):
    return moved(block, 0, "rows")


def in_order(pieces, place):
    stacked = jnp.stack(pieces[::-1], axis=0)
    ordered = jnp.roll(stacked, place + 1, axis=0)
    return ordered.reshape((-1,) + pieces[0].shape[1:])


def block_rows(values, index, length):
    return lax.dynamic_slice_in_dim(values, index * length, length, 0)


def owned_rows(values, owned):
    return jnp.concatenate(
        [values * owned[:, i : i + 1].astype(values.dtype) for i in range(owned.shape[1])], axis=1
    )


def square_body(
    tokens,
    lengths,
    request_adapter_ids,
    adapter_store_slot,
    xchan_input_weight,
    bc_input_weight,
    step_input_weight,
    convolution_x_taps,
    convolution_bc_taps,
    step_bias,
    decay_log_rate,
    head_skip_gain,
    output_norm_gain,
    output_weight,
    adapter_down_input,
    adapter_up_xchan,
    adapter_up_bc,
    adapter_down_output,
    adapter_up_output,
):
    length = tokens.shape[0]
    side = lax.axis_size("ctx")
    stream = side * length
    taps = convolution_x_taps.shape[0]
    bank_entries = adapter_down_input.shape[0]
    rank_value = adapter_down_input.shape[2]
    head_count = step_bias.shape[0]
    channels = xchan_input_weight.shape[1]
    bc_width = bc_input_weight.shape[1]
    here = lax.axis_index("ctx")
    lane = lax.axis_index(("tp", "dp"))
    start_pos = here * length
    request_ends = jnp.cumsum(lengths, dtype=jnp.int32)
    every_position = jnp.arange(stream, dtype=jnp.int32)
    every_segment = segment_of(every_position, request_ends)
    slot_indices = adapter_store_slot[request_adapter_ids]
    request_count = lengths.shape[0]
    stream_onehot = every_segment[:, None] == jnp.arange(request_count, dtype=jnp.int32)[None, :]
    slot_of_position = jnp.sum(
        jnp.where(stream_onehot, slot_indices[None, :], 0), axis=1, dtype=jnp.int32
    )
    entry_ids = jnp.arange(bank_entries, dtype=jnp.int32)[None, :]
    owned_here = slot_of_position[:, None] == here * bank_entries + entry_ids
    owned_lane = slot_of_position[:, None] == lane * bank_entries + entry_ids
    positions = start_pos + jnp.arange(length, dtype=jnp.int32)
    segment = segment_of(positions, request_ends)
    previous = segment_of(jnp.reshape(start_pos - 1, (1,)), request_ends)[0]

    stream_rows = in_order([moved(tokens, s, "rows") for s in range(side)], lane)
    down_in_t = transposed(adapter_down_input)
    up_out_t = transposed(adapter_up_output)
    down_part = jnp.einsum(
        "pf,efr->per", stream_rows, down_in_t, preferred_element_type=jnp.float32
    )
    down_pick = jnp.sum(
        down_part * owned_lane[:, :, None].astype(jnp.float32), axis=1
    )
    rank_hidden = sum(moved(down_pick, s, "rows") for s in range(side))
    hidden_wide = owned_rows(rank_hidden, owned_here).astype(jnp.bfloat16)
    xchan_part = jnp.dot(
        stream_rows, xchan_input_weight, preferred_element_type=jnp.float32
    ) + jnp.dot(
        hidden_wide,
        adapter_up_xchan.reshape(bank_entries * rank_value, -1),
        preferred_element_type=jnp.float32,
    )
    bc_part = jnp.dot(stream_rows, bc_input_weight, preferred_element_type=jnp.float32) + jnp.dot(
        hidden_wide,
        adapter_up_bc.reshape(bank_entries * rank_value, -1),
        preferred_element_type=jnp.float32,
    )
    step_part = jnp.dot(stream_rows, step_input_weight, preferred_element_type=jnp.float32)
    projected = jnp.concatenate([xchan_part, bc_part, step_part], axis=1)
    summed = block_rows(projected, here, length)
    for s in range(1, side):
        summed = summed + moved(block_rows(projected, (here + s) % side, length), s, "ctx")
    values = summed[:, : channels + bc_width]
    step_raw = summed[:, channels + bc_width :]

    kernel = jnp.concatenate([convolution_x_taps, convolution_bc_taps], axis=1)
    tail_rows = passed_along(values[length - (taps - 1) :], "ctx", 1)
    extended = jnp.concatenate([tail_rows, values], axis=0)
    extended_segment = segment_of(
        start_pos - (taps - 1) + jnp.arange(length + taps - 1, dtype=jnp.int32), request_ends
    )
    convolved = jnp.zeros_like(values)
    for tap in range(taps):
        keep = (extended_segment[tap : tap + length] == segment).astype(jnp.float32)
        convolved = convolved + kernel[tap][None, :] * extended[tap : tap + length] * keep[:, None]
    act = jax.nn.silu(convolved)
    x_heads = act[:, :channels].reshape(length, head_count, -1)
    bc_local = act[:, channels:].astype(jnp.bfloat16)
    bc_all = lax.all_gather(bc_local, ("tp", "dp"), axis=1, tiled=True)
    state_width = bc_all.shape[1] // 2
    b_proj = bc_all[:, :state_width]
    c_proj = bc_all[:, state_width:]
    step_size = jax.nn.softplus(step_raw + step_bias[None, :])
    log_decay = -step_size * jnp.exp(decay_log_rate)[None, :]
    inner_out, local_state, enter_weight, carry_decay = span_parts(
        x_heads, b_proj, c_proj, step_size, log_decay, segment, previous
    )

    entering = jnp.zeros_like(local_state)
    for s in range(side - 1, 0, -1):
        pairs = [(a, a + s) for a in range(side - s)]
        decay_in = lax.ppermute(carry_decay.astype(jnp.bfloat16), "ctx", pairs)
        state_in = lax.ppermute(local_state.astype(jnp.bfloat16), "ctx", pairs)
        entering = decay_in.astype(jnp.float32)[:, None, None] * entering + state_in.astype(
            jnp.float32
        )
    entered = (
        jnp.einsum("tn,hdn->thd", c_proj.astype(jnp.float32), entering, precision=FULL_PRECISION)
        * enter_weight[:, :, None]
    )
    mixer_out = (inner_out + entered + head_skip_gain[None, :, None] * x_heads).reshape(
        length, channels
    )
    scale = lax.rsqrt(jnp.mean(mixer_out * mixer_out, axis=1, keepdims=True) + NORM_EPSILON)
    normalized_rows = (mixer_out * scale * output_norm_gain[None, :]).astype(jnp.bfloat16)

    normed_stream = in_order(
        [normalized_rows] + [moved(normalized_rows, s, "ctx") for s in range(1, side)], here
    )
    out_down_part = jnp.einsum(
        "pc,ecr->per", normed_stream, adapter_down_output, preferred_element_type=jnp.float32
    )
    out_down_pick = jnp.sum(out_down_part * owned_here[:, :, None].astype(jnp.float32), axis=1)
    rank_hidden_output = sum(moved(out_down_pick, s, "cols") for s in range(side))
    base_part = jnp.dot(
        normed_stream, output_weight, preferred_element_type=jnp.float32
    ).astype(jnp.bfloat16).astype(jnp.float32)
    adapter_part = jnp.dot(
        owned_rows(rank_hidden_output, owned_lane).astype(jnp.bfloat16),
        up_out_t.reshape(bank_entries * rank_value, -1),
        preferred_element_type=jnp.float32,
    )
    out_part = base_part + adapter_part
    mixed = sum(
        moved(block_rows(out_part, (lane + s) % side, length), s, "cols") for s in range(side)
    )
    return mixed.astype(jnp.bfloat16)


def solution(mesh):
    body = square_body if mesh.shape["ctx"] == mesh.shape["tp"] * mesh.shape["dp"] else general_body
    placed = (
        P(("groups", "ctx"), ("tp", "dp")),
        P("groups"),
        P("groups"),
        P(),
        P("ctx", ("tp", "dp")),
        P("ctx", ("tp", "dp")),
        P("ctx", ("tp", "dp")),
        P(None, ("tp", "dp")),
        P(None, ("tp", "dp")),
        P(("tp", "dp")),
        P(("tp", "dp")),
        P(("tp", "dp")),
        P(("tp", "dp")),
        P(("tp", "dp"), "ctx"),
        P("ctx", ("tp", "dp"), None),
        P("ctx", None, ("tp", "dp")),
        P("ctx", None, ("tp", "dp")),
        P("ctx", ("tp", "dp"), None),
        P("ctx", None, ("tp", "dp")),
    )
    return jax.shard_map(
        body,
        mesh=mesh,
        in_specs=placed,
        out_specs=P(("groups", "ctx"), ("tp", "dp")),
        check_vma=False,
    )
```

```python
import jax
import jax.numpy as jnp
from jax import lax
from jax.sharding import PartitionSpec as P

FULL_PRECISION = lax.Precision.HIGHEST
NORM_EPSILON = 1e-06


def from_root(block, axis, source):
    block = jnp.where(lax.axis_index(axis) == source, block, jnp.zeros_like(block))
    return lax.psum(block, axis)


def passed_along(shard, axis, by):
    size = lax.axis_size(axis)
    pairs = [(i, i + by) for i in range(size) if 0 <= i + by < size]
    return lax.ppermute(shard, axis, pairs)


def prefix(shard, axis, combine, identity):
    size, place = (lax.axis_size(axis), lax.axis_index(axis))
    everything = jax.tree.map(
        lambda part, kind: lax.all_gather(part.astype(kind), axis),
        shard,
        (jnp.bfloat16, jnp.bfloat16),
    )
    start = jax.tree.map(
        lambda part, zero: jnp.broadcast_to(jnp.asarray(zero, part.dtype), part.shape),
        shard,
        identity,
    )

    def lap(k, before):
        reached = k < place
        new = combine(
            before, jax.tree.map(lambda part, own: part[k].astype(own.dtype), everything, shard)
        )
        return jax.tree.map(lambda a, b: jnp.where(reached, a, b), new, before)

    return lax.fori_loop(0, size, lap, start)


def segment_of(positions, request_ends):
    inside = (positions[:, None] >= request_ends[None, :]).astype(jnp.int32)
    counted = jnp.sum(inside, axis=1, dtype=jnp.int32)
    return jnp.where(positions < 0, jnp.int32(-1), counted)


def span_parts(x_heads, b_proj, c_proj, step_size, log_decay, segment, previous):
    length = x_heads.shape[0]
    cumulative = jnp.cumsum(log_decay, axis=0)
    final_log = cumulative[length - 1]
    places = jnp.arange(length, dtype=jnp.int32)
    same_request = jnp.logical_and(
        segment[:, None] == segment[None, :], places[None, :] <= places[:, None]
    ).astype(jnp.float32)
    log_gap = cumulative.T[:, :, None] - cumulative.T[:, None, :]
    decay_table = jnp.exp(jnp.minimum(log_gap, 0.0)) * same_request[None]
    scores = lax.dot_general(
        c_proj, b_proj, (((1,), (1,)), ((), ())), preferred_element_type=jnp.float32
    )
    weights = scores[None] * decay_table * step_size.T[:, None, :]
    inner_out = jnp.einsum("hts,shd->thd", weights, x_heads, precision=FULL_PRECISION)
    at_end = (segment == segment[length - 1]).astype(jnp.float32)
    state_weight = jnp.exp(final_log[None, :] - cumulative) * at_end[:, None] * step_size
    local_state = jnp.einsum(
        "sh,shd,sn->hdn",
        state_weight,
        x_heads,
        b_proj.astype(jnp.float32),
        precision=FULL_PRECISION,
    )
    enter_weight = jnp.exp(cumulative) * (segment == previous).astype(jnp.float32)[:, None]
    carry_decay = jnp.exp(final_log) * (segment[length - 1] == previous).astype(jnp.float32)
    return (inner_out, local_state, enter_weight, carry_decay)


def select_rows(wide, adapter_picker_matrix):
    shaped = wide.reshape(wide.shape[0], adapter_picker_matrix.shape[1], -1)
    return jnp.sum(shaped * adapter_picker_matrix[:, :, None], axis=1)


def masked_wide(values, onehot_b):
    return (values[:, None, :] * onehot_b[:, :, None]).reshape(values.shape[0], -1)


def general_body(
    tokens,
    lengths,
    request_adapter_ids,
    adapter_store_slot,
    xchan_input_weight,
    bc_input_weight,
    step_input_weight,
    convolution_x_taps,
    convolution_bc_taps,
    step_bias,
    decay_log_rate,
    head_skip_gain,
    output_norm_gain,
    output_weight,
    adapter_down_input,
    adapter_up_xchan,
    adapter_up_bc,
    adapter_down_output,
    adapter_up_output,
):
    length = tokens.shape[0]
    request_list = lengths.shape[0]
    taps = convolution_x_taps.shape[0]
    bank_entries = adapter_down_input.shape[0]
    head_count = step_bias.shape[0]
    channels = xchan_input_weight.shape[1]
    start_pos = lax.axis_index("ctx") * length
    request_ends = jnp.cumsum(lengths, dtype=jnp.int32)
    positions = start_pos + jnp.arange(length, dtype=jnp.int32)
    segment = segment_of(positions, request_ends)
    previous = segment_of(jnp.reshape(start_pos - 1, (1,)), request_ends)[0]
    adapter_picker_matrix = (
        segment[:, None] == jnp.arange(request_list, dtype=jnp.int32)[None, :]
    ).astype(jnp.float32)
    onehot_b = adapter_picker_matrix.astype(jnp.bfloat16)
    slot_indices = adapter_store_slot[request_adapter_ids]
    initial_stacks = (
        jnp.zeros(
            (adapter_down_input.shape[1], request_list, adapter_down_input.shape[2]), jnp.bfloat16
        ),
        jnp.zeros((request_list,) + adapter_up_xchan.shape[1:], jnp.bfloat16),
        jnp.zeros((request_list,) + adapter_up_bc.shape[1:], jnp.bfloat16),
        jnp.zeros(
            (adapter_down_output.shape[1], request_list, adapter_down_output.shape[2]), jnp.bfloat16
        ),
        jnp.zeros((request_list,) + adapter_up_output.shape[1:], jnp.bfloat16),
    )
    stack_dims = (1, 0, 0, 1, 0)

    def fetch(request_item, current):
        slot = slot_indices[request_item]
        owner = slot // bank_entries
        within = slot % bank_entries
        a_in, b_x, b_bc, a_out, b_out = [
            lax.dynamic_index_in_dim(adapter_bank, within, 0, keepdims=False)
            for adapter_bank in (
                adapter_down_input,
                adapter_up_xchan,
                adapter_up_bc,
                adapter_down_output,
                adapter_up_output,
            )
        ]
        received = (
            from_root(a_in, "ctx", owner),
            from_root(b_x, "ctx", owner),
            from_root(b_bc, "ctx", owner),
            from_root(a_out, "ctx", owner),
            from_root(b_out, "ctx", owner),
        )
        return tuple(
            (
                lax.dynamic_update_index_in_dim(stack, panel, request_item, along)
                for stack, panel, along in zip(current, received, stack_dims)
            )
        )

    stacks = lax.fori_loop(0, request_list, fetch, initial_stacks)
    rank_value = adapter_down_input.shape[2]
    down_in = stacks[0].reshape(stacks[0].shape[0], request_list * rank_value)
    up_x = stacks[1].reshape(request_list * rank_value, -1)
    up_bc = stacks[2].reshape(request_list * rank_value, -1)
    down_out = stacks[3].reshape(stacks[3].shape[0], request_list * rank_value)
    up_out = stacks[4].reshape(request_list * rank_value, -1)
    lowrank_part = select_rows(
        jnp.dot(tokens, down_in, preferred_element_type=jnp.float32), adapter_picker_matrix
    )
    rank_hidden = lax.psum(lowrank_part.astype(jnp.bfloat16), ("tp", "dp"))
    lowrank_wide = masked_wide(rank_hidden, onehot_b)
    full_tokens = lax.all_gather(tokens, ("tp", "dp"), axis=1, tiled=True)
    pieces = (
        lax.all_gather(xchan_input_weight, "ctx", axis=0, tiled=True),
        lax.all_gather(bc_input_weight, "ctx", axis=0, tiled=True),
        lax.all_gather(step_input_weight, "ctx", axis=0, tiled=True),
    )
    xchan_values, bc_channel_values, step_raw = tuple(
        (jnp.dot(full_tokens, piece, preferred_element_type=jnp.float32) for piece in pieces)
    )
    xchan_values = xchan_values + jnp.dot(lowrank_wide, up_x, preferred_element_type=jnp.float32)
    bc_channel_values = bc_channel_values + jnp.dot(
        lowrank_wide, up_bc, preferred_element_type=jnp.float32
    )
    values = jnp.concatenate([xchan_values, bc_channel_values], axis=1)
    kernel = jnp.concatenate([convolution_x_taps, convolution_bc_taps], axis=1)
    tail_rows = passed_along(values[length - (taps - 1) :], "ctx", 1)
    extended = jnp.concatenate([tail_rows, values], axis=0)
    extended_segment = segment_of(
        start_pos - (taps - 1) + jnp.arange(length + taps - 1, dtype=jnp.int32), request_ends
    )
    convolved = jnp.zeros_like(values)
    for tap in range(taps):
        keep = (extended_segment[tap : tap + length] == segment).astype(jnp.float32)
        convolved = convolved + kernel[tap][None, :] * extended[tap : tap + length] * keep[:, None]
    act = jax.nn.silu(convolved)
    x_heads = act[:, :channels].reshape(length, head_count, -1)
    bc_local = act[:, channels:].astype(jnp.bfloat16)
    bc_all = lax.all_gather(bc_local, ("tp", "dp"), axis=1, tiled=True)
    state_width = bc_all.shape[1] // 2
    b_proj = bc_all[:, :state_width]
    c_proj = bc_all[:, state_width:]
    step_size = jax.nn.softplus(step_raw + step_bias[None, :])
    log_decay = -step_size * jnp.exp(decay_log_rate)[None, :]
    inner_out, local_state, enter_weight, carry_decay = span_parts(
        x_heads, b_proj, c_proj, step_size, log_decay, segment, previous
    )

    def compose(earlier, later):
        return (earlier[0] * later[0], later[0][:, None, None] * earlier[1] + later[1])

    carried = prefix(
        (carry_decay, local_state),
        "ctx",
        compose,
        (jnp.ones_like(carry_decay), jnp.zeros_like(local_state)),
    )
    entering = carried[1]
    entered = (
        jnp.einsum("tn,hdn->thd", c_proj.astype(jnp.float32), entering, precision=FULL_PRECISION)
        * enter_weight[:, :, None]
    )
    mixer_out = (inner_out + entered + head_skip_gain[None, :, None] * x_heads).reshape(
        length, channels
    )
    scale = lax.rsqrt(jnp.mean(mixer_out * mixer_out, axis=1, keepdims=True) + NORM_EPSILON)
    normalized_rows = (mixer_out * scale * output_norm_gain[None, :]).astype(jnp.bfloat16)
    term = jnp.dot(
        normalized_rows,
        lax.all_gather(output_weight, "ctx", axis=1, tiled=True),
        preferred_element_type=jnp.float32,
    )
    base = lax.psum_scatter(
        term.astype(jnp.bfloat16), ("tp", "dp"), scatter_dimension=1, tiled=True
    ).astype(jnp.float32)
    lowrank_out_part = select_rows(
        jnp.dot(normalized_rows, down_out, preferred_element_type=jnp.float32),
        adapter_picker_matrix,
    )
    rank_hidden_output = lax.psum(lowrank_out_part.astype(jnp.bfloat16), ("tp", "dp"))
    adapter_term = jnp.dot(
        masked_wide(rank_hidden_output, onehot_b), up_out, preferred_element_type=jnp.float32
    )
    return (base + adapter_term).astype(jnp.bfloat16)


def moved(block, shift, kind):
    side = lax.axis_size("ctx")
    if kind == "ctx":
        pairs = [(a, (a + shift) % side) for a in range(side)]
        return lax.ppermute(block, "ctx", pairs)
    if kind == "lane":
        pairs = [(a, (a + shift) % side) for a in range(side)]
        return lax.ppermute(block, ("tp", "dp"), pairs)
    if kind == "rows":
        pairs = [(a * side + b, b * side + (a + shift) % side) for a in range(side) for b in range(side)]
    else:
        pairs = [(a * side + b, ((b + shift) % side) * side + a) for a in range(side) for b in range(side)]
    return lax.ppermute(block, ("ctx", "tp", "dp"), pairs)


def transposed(block):
    return moved(block, 0, "rows")


def in_order(pieces, place):
    stacked = jnp.stack(pieces[::-1], axis=0)
    ordered = jnp.roll(stacked, place + 1, axis=0)
    return ordered.reshape((-1,) + pieces[0].shape[1:])


def block_rows(values, index, length):
    return lax.dynamic_slice_in_dim(values, index * length, length, 0)


def owned_rows(values, owned):
    return jnp.concatenate(
        [values * owned[:, i : i + 1].astype(values.dtype) for i in range(owned.shape[1])], axis=1
    )


def square_body(
    tokens,
    lengths,
    request_adapter_ids,
    adapter_store_slot,
    xchan_input_weight,
    bc_input_weight,
    step_input_weight,
    convolution_x_taps,
    convolution_bc_taps,
    step_bias,
    decay_log_rate,
    head_skip_gain,
    output_norm_gain,
    output_weight,
    adapter_down_input,
    adapter_up_xchan,
    adapter_up_bc,
    adapter_down_output,
    adapter_up_output,
):
    length = tokens.shape[0]
    side = lax.axis_size("ctx")
    stream = side * length
    taps = convolution_x_taps.shape[0]
    bank_entries = adapter_down_input.shape[0]
    rank_value = adapter_down_input.shape[2]
    head_count = step_bias.shape[0]
    channels = xchan_input_weight.shape[1]
    bc_width = bc_input_weight.shape[1]
    here = lax.axis_index("ctx")
    lane = lax.axis_index(("tp", "dp"))
    start_pos = here * length
    request_ends = jnp.cumsum(lengths, dtype=jnp.int32)
    every_position = jnp.arange(stream, dtype=jnp.int32)
    every_segment = segment_of(every_position, request_ends)
    slot_indices = adapter_store_slot[request_adapter_ids]
    request_count = lengths.shape[0]
    stream_onehot = every_segment[:, None] == jnp.arange(request_count, dtype=jnp.int32)[None, :]
    slot_of_position = jnp.sum(
        jnp.where(stream_onehot, slot_indices[None, :], 0), axis=1, dtype=jnp.int32
    )
    entry_ids = jnp.arange(bank_entries, dtype=jnp.int32)[None, :]
    owned_here = slot_of_position[:, None] == here * bank_entries + entry_ids
    owned_lane = slot_of_position[:, None] == lane * bank_entries + entry_ids
    positions = start_pos + jnp.arange(length, dtype=jnp.int32)
    segment = segment_of(positions, request_ends)
    previous = segment_of(jnp.reshape(start_pos - 1, (1,)), request_ends)[0]

    tokens_t = transposed(tokens)
    stream_rows = in_order(
        [tokens_t] + [moved(tokens_t, s, "lane") for s in range(1, side)], lane
    )
    down_in_t = transposed(adapter_down_input)
    up_out_t = transposed(adapter_up_output)
    down_part = jnp.einsum(
        "pf,efr->per", stream_rows, down_in_t, preferred_element_type=jnp.float32
    )
    down_pick = jnp.sum(
        down_part * owned_lane[:, :, None].astype(jnp.float32), axis=1
    )
    rank_hidden = sum(moved(down_pick, s, "rows") for s in range(side))
    hidden_wide = owned_rows(rank_hidden, owned_here).astype(jnp.bfloat16)
    xchan_part = jnp.dot(
        stream_rows, xchan_input_weight, preferred_element_type=jnp.float32
    ) + jnp.dot(
        hidden_wide,
        adapter_up_xchan.reshape(bank_entries * rank_value, -1),
        preferred_element_type=jnp.float32,
    )
    bc_part = jnp.dot(stream_rows, bc_input_weight, preferred_element_type=jnp.float32) + jnp.dot(
        hidden_wide,
        adapter_up_bc.reshape(bank_entries * rank_value, -1),
        preferred_element_type=jnp.float32,
    )
    step_part = jnp.dot(stream_rows, step_input_weight, preferred_element_type=jnp.float32)
    projected = jnp.concatenate([xchan_part, bc_part, step_part], axis=1)
    summed = block_rows(projected, here, length)
    for s in range(1, side):
        summed = summed + moved(block_rows(projected, (here + s) % side, length), s, "ctx")
    values = summed[:, : channels + bc_width]
    step_raw = summed[:, channels + bc_width :]

    kernel = jnp.concatenate([convolution_x_taps, convolution_bc_taps], axis=1)
    tail_rows = passed_along(values[length - (taps - 1) :], "ctx", 1)
    extended = jnp.concatenate([tail_rows, values], axis=0)
    extended_segment = segment_of(
        start_pos - (taps - 1) + jnp.arange(length + taps - 1, dtype=jnp.int32), request_ends
    )
    convolved = jnp.zeros_like(values)
    for tap in range(taps):
        keep = (extended_segment[tap : tap + length] == segment).astype(jnp.float32)
        convolved = convolved + kernel[tap][None, :] * extended[tap : tap + length] * keep[:, None]
    act = jax.nn.silu(convolved)
    x_heads = act[:, :channels].reshape(length, head_count, -1)
    bc_local = act[:, channels:].astype(jnp.bfloat16)
    bc_all = lax.all_gather(bc_local, ("tp", "dp"), axis=1, tiled=True)
    state_width = bc_all.shape[1] // 2
    b_proj = bc_all[:, :state_width]
    c_proj = bc_all[:, state_width:]
    step_size = jax.nn.softplus(step_raw + step_bias[None, :])
    log_decay = -step_size * jnp.exp(decay_log_rate)[None, :]
    inner_out, local_state, enter_weight, carry_decay = span_parts(
        x_heads, b_proj, c_proj, step_size, log_decay, segment, previous
    )

    entering = jnp.zeros_like(local_state)
    for s in range(side - 1, 0, -1):
        pairs = [(a, a + s) for a in range(side - s)]
        decay_in = lax.ppermute(carry_decay.astype(jnp.bfloat16), "ctx", pairs)
        state_in = lax.ppermute(local_state.astype(jnp.bfloat16), "ctx", pairs)
        entering = decay_in.astype(jnp.float32)[:, None, None] * entering + state_in.astype(
            jnp.float32
        )
    entered = (
        jnp.einsum("tn,hdn->thd", c_proj.astype(jnp.float32), entering, precision=FULL_PRECISION)
        * enter_weight[:, :, None]
    )
    mixer_out = (inner_out + entered + head_skip_gain[None, :, None] * x_heads).reshape(
        length, channels
    )
    scale = lax.rsqrt(jnp.mean(mixer_out * mixer_out, axis=1, keepdims=True) + NORM_EPSILON)
    normalized_rows = (mixer_out * scale * output_norm_gain[None, :]).astype(jnp.bfloat16)

    normed_stream = in_order(
        [normalized_rows] + [moved(normalized_rows, s, "ctx") for s in range(1, side)], here
    )
    out_down_part = jnp.einsum(
        "pc,ecr->per", normed_stream, adapter_down_output, preferred_element_type=jnp.float32
    )
    out_down_pick = jnp.sum(out_down_part * owned_here[:, :, None].astype(jnp.float32), axis=1)
    rank_hidden_output = transposed(
        out_down_pick + sum(moved(out_down_pick, s, "lane") for s in range(1, side))
    )
    base_part = jnp.dot(
        normed_stream, output_weight, preferred_element_type=jnp.float32
    ).astype(jnp.bfloat16).astype(jnp.float32)
    adapter_part = jnp.dot(
        owned_rows(rank_hidden_output, owned_lane).astype(jnp.bfloat16),
        up_out_t.reshape(bank_entries * rank_value, -1),
        preferred_element_type=jnp.float32,
    )
    out_part = base_part + adapter_part
    mixed_t = block_rows(out_part, lane, length)
    for s in range(1, side):
        mixed_t = mixed_t + moved(block_rows(out_part, (lane + s) % side, length), s, "lane")
    return transposed(mixed_t.astype(jnp.bfloat16))


def solution(mesh):
    body = square_body if mesh.shape["ctx"] == mesh.shape["tp"] * mesh.shape["dp"] else general_body
    placed = (
        P(("groups", "ctx"), ("tp", "dp")),
        P("groups"),
        P("groups"),
        P(),
        P("ctx", ("tp", "dp")),
        P("ctx", ("tp", "dp")),
        P("ctx", ("tp", "dp")),
        P(None, ("tp", "dp")),
        P(None, ("tp", "dp")),
        P(("tp", "dp")),
        P(("tp", "dp")),
        P(("tp", "dp")),
        P(("tp", "dp")),
        P(("tp", "dp"), "ctx"),
        P("ctx", ("tp", "dp"), None),
        P("ctx", None, ("tp", "dp")),
        P("ctx", None, ("tp", "dp")),
        P("ctx", ("tp", "dp"), None),
        P("ctx", None, ("tp", "dp")),
    )
    return jax.shard_map(
        body,
        mesh=mesh,
        in_specs=placed,
        out_specs=P(("groups", "ctx"), ("tp", "dp")),
        check_vma=False,
    )
```

```python
import jax
import jax.numpy as jnp
from jax import lax
from jax.sharding import PartitionSpec as P

FULL_PRECISION = lax.Precision.HIGHEST
NORM_EPSILON = 1e-06


def from_root(block, axis, source):
    block = jnp.where(lax.axis_index(axis) == source, block, jnp.zeros_like(block))
    return lax.psum(block, axis)


def passed_along(shard, axis, by):
    size = lax.axis_size(axis)
    pairs = [(i, i + by) for i in range(size) if 0 <= i + by < size]
    return lax.ppermute(shard, axis, pairs)


def prefix(shard, axis, combine, identity):
    size, place = (lax.axis_size(axis), lax.axis_index(axis))
    everything = jax.tree.map(
        lambda part, kind: lax.all_gather(part.astype(kind), axis),
        shard,
        (jnp.bfloat16, jnp.bfloat16),
    )
    start = jax.tree.map(
        lambda part, zero: jnp.broadcast_to(jnp.asarray(zero, part.dtype), part.shape),
        shard,
        identity,
    )

    def lap(k, before):
        reached = k < place
        new = combine(
            before, jax.tree.map(lambda part, own: part[k].astype(own.dtype), everything, shard)
        )
        return jax.tree.map(lambda a, b: jnp.where(reached, a, b), new, before)

    return lax.fori_loop(0, size, lap, start)


def segment_of(positions, request_ends):
    inside = (positions[:, None] >= request_ends[None, :]).astype(jnp.int32)
    counted = jnp.sum(inside, axis=1, dtype=jnp.int32)
    return jnp.where(positions < 0, jnp.int32(-1), counted)


def span_parts(x_heads, b_proj, c_proj, step_size, log_decay, segment, previous):
    length = x_heads.shape[0]
    cumulative = jnp.cumsum(log_decay, axis=0)
    final_log = cumulative[length - 1]
    places = jnp.arange(length, dtype=jnp.int32)
    same_request = jnp.logical_and(
        segment[:, None] == segment[None, :], places[None, :] <= places[:, None]
    ).astype(jnp.float32)
    log_gap = cumulative.T[:, :, None] - cumulative.T[:, None, :]
    decay_table = jnp.exp(jnp.minimum(log_gap, 0.0)) * same_request[None]
    scores = lax.dot_general(
        c_proj, b_proj, (((1,), (1,)), ((), ())), preferred_element_type=jnp.float32
    )
    weights = scores[None] * decay_table * step_size.T[:, None, :]
    inner_out = jnp.einsum("hts,shd->thd", weights, x_heads, precision=FULL_PRECISION)
    at_end = (segment == segment[length - 1]).astype(jnp.float32)
    state_weight = jnp.exp(final_log[None, :] - cumulative) * at_end[:, None] * step_size
    local_state = jnp.einsum(
        "sh,shd,sn->hdn",
        state_weight,
        x_heads,
        b_proj.astype(jnp.float32),
        precision=FULL_PRECISION,
    )
    enter_weight = jnp.exp(cumulative) * (segment == previous).astype(jnp.float32)[:, None]
    carry_decay = jnp.exp(final_log) * (segment[length - 1] == previous).astype(jnp.float32)
    return (inner_out, local_state, enter_weight, carry_decay)


def select_rows(wide, adapter_picker_matrix):
    shaped = wide.reshape(wide.shape[0], adapter_picker_matrix.shape[1], -1)
    return jnp.sum(shaped * adapter_picker_matrix[:, :, None], axis=1)


def masked_wide(values, onehot_b):
    return (values[:, None, :] * onehot_b[:, :, None]).reshape(values.shape[0], -1)


def general_body(
    tokens,
    lengths,
    request_adapter_ids,
    adapter_store_slot,
    xchan_input_weight,
    bc_input_weight,
    step_input_weight,
    convolution_x_taps,
    convolution_bc_taps,
    step_bias,
    decay_log_rate,
    head_skip_gain,
    output_norm_gain,
    output_weight,
    adapter_down_input,
    adapter_up_xchan,
    adapter_up_bc,
    adapter_down_output,
    adapter_up_output,
):
    length = tokens.shape[0]
    request_list = lengths.shape[0]
    taps = convolution_x_taps.shape[0]
    bank_entries = adapter_down_input.shape[0]
    head_count = step_bias.shape[0]
    channels = xchan_input_weight.shape[1]
    start_pos = lax.axis_index("ctx") * length
    request_ends = jnp.cumsum(lengths, dtype=jnp.int32)
    positions = start_pos + jnp.arange(length, dtype=jnp.int32)
    segment = segment_of(positions, request_ends)
    previous = segment_of(jnp.reshape(start_pos - 1, (1,)), request_ends)[0]
    adapter_picker_matrix = (
        segment[:, None] == jnp.arange(request_list, dtype=jnp.int32)[None, :]
    ).astype(jnp.float32)
    onehot_b = adapter_picker_matrix.astype(jnp.bfloat16)
    slot_indices = adapter_store_slot[request_adapter_ids]
    initial_stacks = (
        jnp.zeros(
            (adapter_down_input.shape[1], request_list, adapter_down_input.shape[2]), jnp.bfloat16
        ),
        jnp.zeros((request_list,) + adapter_up_xchan.shape[1:], jnp.bfloat16),
        jnp.zeros((request_list,) + adapter_up_bc.shape[1:], jnp.bfloat16),
        jnp.zeros(
            (adapter_down_output.shape[1], request_list, adapter_down_output.shape[2]), jnp.bfloat16
        ),
        jnp.zeros((request_list,) + adapter_up_output.shape[1:], jnp.bfloat16),
    )
    stack_dims = (1, 0, 0, 1, 0)

    def fetch(request_item, current):
        slot = slot_indices[request_item]
        owner = slot // bank_entries
        within = slot % bank_entries
        a_in, b_x, b_bc, a_out, b_out = [
            lax.dynamic_index_in_dim(adapter_bank, within, 0, keepdims=False)
            for adapter_bank in (
                adapter_down_input,
                adapter_up_xchan,
                adapter_up_bc,
                adapter_down_output,
                adapter_up_output,
            )
        ]
        received = (
            from_root(a_in, "ctx", owner),
            from_root(b_x, "ctx", owner),
            from_root(b_bc, "ctx", owner),
            from_root(a_out, "ctx", owner),
            from_root(b_out, "ctx", owner),
        )
        return tuple(
            (
                lax.dynamic_update_index_in_dim(stack, panel, request_item, along)
                for stack, panel, along in zip(current, received, stack_dims)
            )
        )

    stacks = lax.fori_loop(0, request_list, fetch, initial_stacks)
    rank_value = adapter_down_input.shape[2]
    down_in = stacks[0].reshape(stacks[0].shape[0], request_list * rank_value)
    up_x = stacks[1].reshape(request_list * rank_value, -1)
    up_bc = stacks[2].reshape(request_list * rank_value, -1)
    down_out = stacks[3].reshape(stacks[3].shape[0], request_list * rank_value)
    up_out = stacks[4].reshape(request_list * rank_value, -1)
    lowrank_part = select_rows(
        jnp.dot(tokens, down_in, preferred_element_type=jnp.float32), adapter_picker_matrix
    )
    rank_hidden = lax.psum(lowrank_part.astype(jnp.bfloat16), ("tp", "dp"))
    lowrank_wide = masked_wide(rank_hidden, onehot_b)
    full_tokens = lax.all_gather(tokens, ("tp", "dp"), axis=1, tiled=True)
    pieces = (
        lax.all_gather(xchan_input_weight, "ctx", axis=0, tiled=True),
        lax.all_gather(bc_input_weight, "ctx", axis=0, tiled=True),
        lax.all_gather(step_input_weight, "ctx", axis=0, tiled=True),
    )
    xchan_values, bc_channel_values, step_raw = tuple(
        (jnp.dot(full_tokens, piece, preferred_element_type=jnp.float32) for piece in pieces)
    )
    xchan_values = xchan_values + jnp.dot(lowrank_wide, up_x, preferred_element_type=jnp.float32)
    bc_channel_values = bc_channel_values + jnp.dot(
        lowrank_wide, up_bc, preferred_element_type=jnp.float32
    )
    values = jnp.concatenate([xchan_values, bc_channel_values], axis=1)
    kernel = jnp.concatenate([convolution_x_taps, convolution_bc_taps], axis=1)
    tail_rows = passed_along(values[length - (taps - 1) :], "ctx", 1)
    extended = jnp.concatenate([tail_rows, values], axis=0)
    extended_segment = segment_of(
        start_pos - (taps - 1) + jnp.arange(length + taps - 1, dtype=jnp.int32), request_ends
    )
    convolved = jnp.zeros_like(values)
    for tap in range(taps):
        keep = (extended_segment[tap : tap + length] == segment).astype(jnp.float32)
        convolved = convolved + kernel[tap][None, :] * extended[tap : tap + length] * keep[:, None]
    act = jax.nn.silu(convolved)
    x_heads = act[:, :channels].reshape(length, head_count, -1)
    bc_local = act[:, channels:].astype(jnp.bfloat16)
    bc_all = lax.all_gather(bc_local, ("tp", "dp"), axis=1, tiled=True)
    state_width = bc_all.shape[1] // 2
    b_proj = bc_all[:, :state_width]
    c_proj = bc_all[:, state_width:]
    step_size = jax.nn.softplus(step_raw + step_bias[None, :])
    log_decay = -step_size * jnp.exp(decay_log_rate)[None, :]
    inner_out, local_state, enter_weight, carry_decay = span_parts(
        x_heads, b_proj, c_proj, step_size, log_decay, segment, previous
    )

    def compose(earlier, later):
        return (earlier[0] * later[0], later[0][:, None, None] * earlier[1] + later[1])

    carried = prefix(
        (carry_decay, local_state),
        "ctx",
        compose,
        (jnp.ones_like(carry_decay), jnp.zeros_like(local_state)),
    )
    entering = carried[1]
    entered = (
        jnp.einsum("tn,hdn->thd", c_proj.astype(jnp.float32), entering, precision=FULL_PRECISION)
        * enter_weight[:, :, None]
    )
    mixer_out = (inner_out + entered + head_skip_gain[None, :, None] * x_heads).reshape(
        length, channels
    )
    scale = lax.rsqrt(jnp.mean(mixer_out * mixer_out, axis=1, keepdims=True) + NORM_EPSILON)
    normalized_rows = (mixer_out * scale * output_norm_gain[None, :]).astype(jnp.bfloat16)
    term = jnp.dot(
        normalized_rows,
        lax.all_gather(output_weight, "ctx", axis=1, tiled=True),
        preferred_element_type=jnp.float32,
    )
    base = lax.psum_scatter(
        term.astype(jnp.bfloat16), ("tp", "dp"), scatter_dimension=1, tiled=True
    ).astype(jnp.float32)
    lowrank_out_part = select_rows(
        jnp.dot(normalized_rows, down_out, preferred_element_type=jnp.float32),
        adapter_picker_matrix,
    )
    rank_hidden_output = lax.psum(lowrank_out_part.astype(jnp.bfloat16), ("tp", "dp"))
    adapter_term = jnp.dot(
        masked_wide(rank_hidden_output, onehot_b), up_out, preferred_element_type=jnp.float32
    )
    return (base + adapter_term).astype(jnp.bfloat16)


def moved(block, shift, kind):
    side = lax.axis_size("ctx")
    if kind == "ctx":
        pairs = [(a, (a + shift) % side) for a in range(side)]
        return lax.ppermute(block, "ctx", pairs)
    if kind == "lane":
        pairs = [(a, (a + shift) % side) for a in range(side)]
        return lax.ppermute(block, ("tp", "dp"), pairs)
    if kind == "rows":
        pairs = [(a * side + b, b * side + (a + shift) % side) for a in range(side) for b in range(side)]
    else:
        pairs = [(a * side + b, ((b + shift) % side) * side + a) for a in range(side) for b in range(side)]
    return lax.ppermute(block, ("ctx", "tp", "dp"), pairs)


def transposed(block):
    return moved(block, 0, "rows")


def in_order(pieces, place):
    stacked = jnp.stack(pieces[::-1], axis=0)
    ordered = jnp.roll(stacked, place + 1, axis=0)
    return ordered.reshape((-1,) + pieces[0].shape[1:])


def block_rows(values, index, length):
    return lax.dynamic_slice_in_dim(values, index * length, length, 0)


def owned_rows(values, owned):
    return jnp.concatenate(
        [values * owned[:, i : i + 1].astype(values.dtype) for i in range(owned.shape[1])], axis=1
    )


def square_body(
    tokens,
    lengths,
    request_adapter_ids,
    adapter_store_slot,
    xchan_input_weight,
    bc_input_weight,
    step_input_weight,
    convolution_x_taps,
    convolution_bc_taps,
    step_bias,
    decay_log_rate,
    head_skip_gain,
    output_norm_gain,
    output_weight,
    adapter_down_input,
    adapter_up_xchan,
    adapter_up_bc,
    adapter_down_output,
    adapter_up_output,
):
    length = tokens.shape[0]
    side = lax.axis_size("ctx")
    stream = side * length
    taps = convolution_x_taps.shape[0]
    bank_entries = adapter_down_input.shape[0]
    rank_value = adapter_down_input.shape[2]
    head_count = step_bias.shape[0]
    channels = xchan_input_weight.shape[1]
    bc_width = bc_input_weight.shape[1]
    here = lax.axis_index("ctx")
    lane = lax.axis_index(("tp", "dp"))
    start_pos = here * length
    request_ends = jnp.cumsum(lengths, dtype=jnp.int32)
    every_position = jnp.arange(stream, dtype=jnp.int32)
    every_segment = segment_of(every_position, request_ends)
    slot_indices = adapter_store_slot[request_adapter_ids]
    request_count = lengths.shape[0]
    stream_onehot = every_segment[:, None] == jnp.arange(request_count, dtype=jnp.int32)[None, :]
    slot_of_position = jnp.sum(
        jnp.where(stream_onehot, slot_indices[None, :], 0), axis=1, dtype=jnp.int32
    )
    entry_ids = jnp.arange(bank_entries, dtype=jnp.int32)[None, :]
    owned_here = slot_of_position[:, None] == here * bank_entries + entry_ids
    owned_lane = slot_of_position[:, None] == lane * bank_entries + entry_ids
    positions = start_pos + jnp.arange(length, dtype=jnp.int32)
    segment = segment_of(positions, request_ends)
    previous = segment_of(jnp.reshape(start_pos - 1, (1,)), request_ends)[0]

    tokens_t = transposed(tokens)
    stream_rows = in_order(
        [tokens_t] + [moved(tokens_t, s, "lane") for s in range(1, side)], lane
    )
    down_in_t = transposed(adapter_down_input)
    up_out_t = transposed(adapter_up_output)
    down_part = jnp.einsum(
        "pf,efr->per", stream_rows, down_in_t, preferred_element_type=jnp.float32
    )
    down_pick = jnp.sum(
        down_part * owned_lane[:, :, None].astype(jnp.float32), axis=1
    )
    rank_hidden = sum(moved(down_pick, s, "rows") for s in range(side))
    hidden_wide = owned_rows(rank_hidden, owned_here).astype(jnp.bfloat16)
    xchan_part = jnp.dot(
        stream_rows, xchan_input_weight, preferred_element_type=jnp.float32
    ) + jnp.dot(
        hidden_wide,
        adapter_up_xchan.reshape(bank_entries * rank_value, -1),
        preferred_element_type=jnp.float32,
    )
    bc_part = jnp.dot(stream_rows, bc_input_weight, preferred_element_type=jnp.float32) + jnp.dot(
        hidden_wide,
        adapter_up_bc.reshape(bank_entries * rank_value, -1),
        preferred_element_type=jnp.float32,
    )
    step_part = jnp.dot(stream_rows, step_input_weight, preferred_element_type=jnp.float32)
    projected = jnp.concatenate([xchan_part, bc_part, step_part], axis=1)
    summed = block_rows(projected, here, length)
    for s in range(1, side):
        sent = block_rows(projected, (here + s) % side, length).astype(jnp.bfloat16)
        summed = summed + moved(sent, s, "ctx").astype(jnp.float32)
    values = summed[:, : channels + bc_width]
    step_raw = summed[:, channels + bc_width :]

    kernel = jnp.concatenate([convolution_x_taps, convolution_bc_taps], axis=1)
    tail_rows = passed_along(values[length - (taps - 1) :], "ctx", 1)
    extended = jnp.concatenate([tail_rows, values], axis=0)
    extended_segment = segment_of(
        start_pos - (taps - 1) + jnp.arange(length + taps - 1, dtype=jnp.int32), request_ends
    )
    convolved = jnp.zeros_like(values)
    for tap in range(taps):
        keep = (extended_segment[tap : tap + length] == segment).astype(jnp.float32)
        convolved = convolved + kernel[tap][None, :] * extended[tap : tap + length] * keep[:, None]
    act = jax.nn.silu(convolved)
    x_heads = act[:, :channels].reshape(length, head_count, -1)
    bc_local = act[:, channels:].astype(jnp.bfloat16)
    bc_all = lax.all_gather(bc_local, ("tp", "dp"), axis=1, tiled=True)
    state_width = bc_all.shape[1] // 2
    b_proj = bc_all[:, :state_width]
    c_proj = bc_all[:, state_width:]
    step_size = jax.nn.softplus(step_raw + step_bias[None, :])
    log_decay = -step_size * jnp.exp(decay_log_rate)[None, :]
    inner_out, local_state, enter_weight, carry_decay = span_parts(
        x_heads, b_proj, c_proj, step_size, log_decay, segment, previous
    )

    entering = jnp.zeros_like(local_state)
    for s in range(side - 1, 0, -1):
        pairs = [(a, a + s) for a in range(side - s)]
        decay_in = lax.ppermute(carry_decay.astype(jnp.bfloat16), "ctx", pairs)
        state_in = lax.ppermute(local_state.astype(jnp.bfloat16), "ctx", pairs)
        entering = decay_in.astype(jnp.float32)[:, None, None] * entering + state_in.astype(
            jnp.float32
        )
    entered = (
        jnp.einsum("tn,hdn->thd", c_proj.astype(jnp.float32), entering, precision=FULL_PRECISION)
        * enter_weight[:, :, None]
    )
    mixer_out = (inner_out + entered + head_skip_gain[None, :, None] * x_heads).reshape(
        length, channels
    )
    scale = lax.rsqrt(jnp.mean(mixer_out * mixer_out, axis=1, keepdims=True) + NORM_EPSILON)
    normalized_rows = (mixer_out * scale * output_norm_gain[None, :]).astype(jnp.bfloat16)

    normed_stream = in_order(
        [normalized_rows] + [moved(normalized_rows, s, "ctx") for s in range(1, side)], here
    )
    out_down_part = jnp.einsum(
        "pc,ecr->per", normed_stream, adapter_down_output, preferred_element_type=jnp.float32
    )
    out_down_pick = jnp.sum(out_down_part * owned_here[:, :, None].astype(jnp.float32), axis=1)
    rank_hidden_output = transposed(
        out_down_pick + sum(moved(out_down_pick, s, "lane") for s in range(1, side))
    )
    base_part = jnp.dot(
        normed_stream, output_weight, preferred_element_type=jnp.float32
    ).astype(jnp.bfloat16).astype(jnp.float32)
    adapter_part = jnp.dot(
        owned_rows(rank_hidden_output, owned_lane).astype(jnp.bfloat16),
        up_out_t.reshape(bank_entries * rank_value, -1),
        preferred_element_type=jnp.float32,
    )
    out_part = base_part + adapter_part
    mixed_t = block_rows(out_part, lane, length)
    for s in range(1, side):
        sent = block_rows(out_part, (lane + s) % side, length).astype(jnp.bfloat16)
        mixed_t = mixed_t + moved(sent, s, "lane").astype(jnp.float32)
    return transposed(mixed_t.astype(jnp.bfloat16))


def solution(mesh):
    body = square_body if mesh.shape["ctx"] == mesh.shape["tp"] * mesh.shape["dp"] else general_body
    placed = (
        P(("groups", "ctx"), ("tp", "dp")),
        P("groups"),
        P("groups"),
        P(),
        P("ctx", ("tp", "dp")),
        P("ctx", ("tp", "dp")),
        P("ctx", ("tp", "dp")),
        P(None, ("tp", "dp")),
        P(None, ("tp", "dp")),
        P(("tp", "dp")),
        P(("tp", "dp")),
        P(("tp", "dp")),
        P(("tp", "dp")),
        P(("tp", "dp"), "ctx"),
        P("ctx", ("tp", "dp"), None),
        P("ctx", None, ("tp", "dp")),
        P("ctx", None, ("tp", "dp")),
        P("ctx", ("tp", "dp"), None),
        P("ctx", None, ("tp", "dp")),
    )
    return jax.shard_map(
        body,
        mesh=mesh,
        in_specs=placed,
        out_specs=P(("groups", "ctx"), ("tp", "dp")),
        check_vma=False,
    )
```

```python
import jax
import jax.numpy as jnp
from jax import lax
from jax.sharding import PartitionSpec as P

FULL_PRECISION = lax.Precision.HIGHEST
NORM_EPSILON = 1e-06


def from_root(block, axis, source):
    block = jnp.where(lax.axis_index(axis) == source, block, jnp.zeros_like(block))
    return lax.psum(block, axis)


def passed_along(shard, axis, by):
    size = lax.axis_size(axis)
    pairs = [(i, i + by) for i in range(size) if 0 <= i + by < size]
    return lax.ppermute(shard, axis, pairs)


def prefix(shard, axis, combine, identity):
    size, place = (lax.axis_size(axis), lax.axis_index(axis))
    everything = jax.tree.map(
        lambda part, kind: lax.all_gather(part.astype(kind), axis),
        shard,
        (jnp.bfloat16, jnp.bfloat16),
    )
    start = jax.tree.map(
        lambda part, zero: jnp.broadcast_to(jnp.asarray(zero, part.dtype), part.shape),
        shard,
        identity,
    )

    def lap(k, before):
        reached = k < place
        new = combine(
            before, jax.tree.map(lambda part, own: part[k].astype(own.dtype), everything, shard)
        )
        return jax.tree.map(lambda a, b: jnp.where(reached, a, b), new, before)

    return lax.fori_loop(0, size, lap, start)


def segment_of(positions, request_ends):
    inside = (positions[:, None] >= request_ends[None, :]).astype(jnp.int32)
    counted = jnp.sum(inside, axis=1, dtype=jnp.int32)
    return jnp.where(positions < 0, jnp.int32(-1), counted)


def span_parts(x_heads, b_proj, c_proj, step_size, log_decay, segment, previous):
    length = x_heads.shape[0]
    cumulative = jnp.cumsum(log_decay, axis=0)
    final_log = cumulative[length - 1]
    places = jnp.arange(length, dtype=jnp.int32)
    same_request = jnp.logical_and(
        segment[:, None] == segment[None, :], places[None, :] <= places[:, None]
    ).astype(jnp.float32)
    log_gap = cumulative.T[:, :, None] - cumulative.T[:, None, :]
    decay_table = jnp.exp(jnp.minimum(log_gap, 0.0)) * same_request[None]
    scores = lax.dot_general(
        c_proj, b_proj, (((1,), (1,)), ((), ())), preferred_element_type=jnp.float32
    )
    weights = scores[None] * decay_table * step_size.T[:, None, :]
    inner_out = jnp.einsum("hts,shd->thd", weights, x_heads, precision=FULL_PRECISION)
    at_end = (segment == segment[length - 1]).astype(jnp.float32)
    state_weight = jnp.exp(final_log[None, :] - cumulative) * at_end[:, None] * step_size
    local_state = jnp.einsum(
        "sh,shd,sn->hdn",
        state_weight,
        x_heads,
        b_proj.astype(jnp.float32),
        precision=FULL_PRECISION,
    )
    enter_weight = jnp.exp(cumulative) * (segment == previous).astype(jnp.float32)[:, None]
    carry_decay = jnp.exp(final_log) * (segment[length - 1] == previous).astype(jnp.float32)
    return (inner_out, local_state, enter_weight, carry_decay)


def select_rows(wide, adapter_picker_matrix):
    shaped = wide.reshape(wide.shape[0], adapter_picker_matrix.shape[1], -1)
    return jnp.sum(shaped * adapter_picker_matrix[:, :, None], axis=1)


def masked_wide(values, onehot_b):
    return (values[:, None, :] * onehot_b[:, :, None]).reshape(values.shape[0], -1)


def general_body(
    tokens,
    lengths,
    request_adapter_ids,
    adapter_store_slot,
    xchan_input_weight,
    bc_input_weight,
    step_input_weight,
    convolution_x_taps,
    convolution_bc_taps,
    step_bias,
    decay_log_rate,
    head_skip_gain,
    output_norm_gain,
    output_weight,
    adapter_down_input,
    adapter_up_xchan,
    adapter_up_bc,
    adapter_down_output,
    adapter_up_output,
):
    length = tokens.shape[0]
    request_list = lengths.shape[0]
    taps = convolution_x_taps.shape[0]
    bank_entries = adapter_down_input.shape[0]
    head_count = step_bias.shape[0]
    channels = xchan_input_weight.shape[1]
    start_pos = lax.axis_index("ctx") * length
    request_ends = jnp.cumsum(lengths, dtype=jnp.int32)
    positions = start_pos + jnp.arange(length, dtype=jnp.int32)
    segment = segment_of(positions, request_ends)
    previous = segment_of(jnp.reshape(start_pos - 1, (1,)), request_ends)[0]
    adapter_picker_matrix = (
        segment[:, None] == jnp.arange(request_list, dtype=jnp.int32)[None, :]
    ).astype(jnp.float32)
    onehot_b = adapter_picker_matrix.astype(jnp.bfloat16)
    slot_indices = adapter_store_slot[request_adapter_ids]
    initial_stacks = (
        jnp.zeros(
            (adapter_down_input.shape[1], request_list, adapter_down_input.shape[2]), jnp.bfloat16
        ),
        jnp.zeros((request_list,) + adapter_up_xchan.shape[1:], jnp.bfloat16),
        jnp.zeros((request_list,) + adapter_up_bc.shape[1:], jnp.bfloat16),
        jnp.zeros(
            (adapter_down_output.shape[1], request_list, adapter_down_output.shape[2]), jnp.bfloat16
        ),
        jnp.zeros((request_list,) + adapter_up_output.shape[1:], jnp.bfloat16),
    )
    stack_dims = (1, 0, 0, 1, 0)

    def fetch(request_item, current):
        slot = slot_indices[request_item]
        owner = slot // bank_entries
        within = slot % bank_entries
        a_in, b_x, b_bc, a_out, b_out = [
            lax.dynamic_index_in_dim(adapter_bank, within, 0, keepdims=False)
            for adapter_bank in (
                adapter_down_input,
                adapter_up_xchan,
                adapter_up_bc,
                adapter_down_output,
                adapter_up_output,
            )
        ]
        received = (
            from_root(a_in, "ctx", owner),
            from_root(b_x, "ctx", owner),
            from_root(b_bc, "ctx", owner),
            from_root(a_out, "ctx", owner),
            from_root(b_out, "ctx", owner),
        )
        return tuple(
            (
                lax.dynamic_update_index_in_dim(stack, panel, request_item, along)
                for stack, panel, along in zip(current, received, stack_dims)
            )
        )

    stacks = lax.fori_loop(0, request_list, fetch, initial_stacks)
    rank_value = adapter_down_input.shape[2]
    down_in = stacks[0].reshape(stacks[0].shape[0], request_list * rank_value)
    up_x = stacks[1].reshape(request_list * rank_value, -1)
    up_bc = stacks[2].reshape(request_list * rank_value, -1)
    down_out = stacks[3].reshape(stacks[3].shape[0], request_list * rank_value)
    up_out = stacks[4].reshape(request_list * rank_value, -1)
    lowrank_part = select_rows(
        jnp.dot(tokens, down_in, preferred_element_type=jnp.float32), adapter_picker_matrix
    )
    rank_hidden = lax.psum(lowrank_part.astype(jnp.bfloat16), ("tp", "dp"))
    lowrank_wide = masked_wide(rank_hidden, onehot_b)
    full_tokens = lax.all_gather(tokens, ("tp", "dp"), axis=1, tiled=True)
    pieces = (
        lax.all_gather(xchan_input_weight, "ctx", axis=0, tiled=True),
        lax.all_gather(bc_input_weight, "ctx", axis=0, tiled=True),
        lax.all_gather(step_input_weight, "ctx", axis=0, tiled=True),
    )
    xchan_values, bc_channel_values, step_raw = tuple(
        (jnp.dot(full_tokens, piece, preferred_element_type=jnp.float32) for piece in pieces)
    )
    xchan_values = xchan_values + jnp.dot(lowrank_wide, up_x, preferred_element_type=jnp.float32)
    bc_channel_values = bc_channel_values + jnp.dot(
        lowrank_wide, up_bc, preferred_element_type=jnp.float32
    )
    values = jnp.concatenate([xchan_values, bc_channel_values], axis=1)
    kernel = jnp.concatenate([convolution_x_taps, convolution_bc_taps], axis=1)
    tail_rows = passed_along(values[length - (taps - 1) :], "ctx", 1)
    extended = jnp.concatenate([tail_rows, values], axis=0)
    extended_segment = segment_of(
        start_pos - (taps - 1) + jnp.arange(length + taps - 1, dtype=jnp.int32), request_ends
    )
    convolved = jnp.zeros_like(values)
    for tap in range(taps):
        keep = (extended_segment[tap : tap + length] == segment).astype(jnp.float32)
        convolved = convolved + kernel[tap][None, :] * extended[tap : tap + length] * keep[:, None]
    act = jax.nn.silu(convolved)
    x_heads = act[:, :channels].reshape(length, head_count, -1)
    bc_local = act[:, channels:].astype(jnp.bfloat16)
    bc_all = lax.all_gather(bc_local, ("tp", "dp"), axis=1, tiled=True)
    state_width = bc_all.shape[1] // 2
    b_proj = bc_all[:, :state_width]
    c_proj = bc_all[:, state_width:]
    step_size = jax.nn.softplus(step_raw + step_bias[None, :])
    log_decay = -step_size * jnp.exp(decay_log_rate)[None, :]
    inner_out, local_state, enter_weight, carry_decay = span_parts(
        x_heads, b_proj, c_proj, step_size, log_decay, segment, previous
    )

    def compose(earlier, later):
        return (earlier[0] * later[0], later[0][:, None, None] * earlier[1] + later[1])

    carried = prefix(
        (carry_decay, local_state),
        "ctx",
        compose,
        (jnp.ones_like(carry_decay), jnp.zeros_like(local_state)),
    )
    entering = carried[1]
    entered = (
        jnp.einsum("tn,hdn->thd", c_proj.astype(jnp.float32), entering, precision=FULL_PRECISION)
        * enter_weight[:, :, None]
    )
    mixer_out = (inner_out + entered + head_skip_gain[None, :, None] * x_heads).reshape(
        length, channels
    )
    scale = lax.rsqrt(jnp.mean(mixer_out * mixer_out, axis=1, keepdims=True) + NORM_EPSILON)
    normalized_rows = (mixer_out * scale * output_norm_gain[None, :]).astype(jnp.bfloat16)
    term = jnp.dot(
        normalized_rows,
        lax.all_gather(output_weight, "ctx", axis=1, tiled=True),
        preferred_element_type=jnp.float32,
    )
    base = lax.psum_scatter(
        term.astype(jnp.bfloat16), ("tp", "dp"), scatter_dimension=1, tiled=True
    ).astype(jnp.float32)
    lowrank_out_part = select_rows(
        jnp.dot(normalized_rows, down_out, preferred_element_type=jnp.float32),
        adapter_picker_matrix,
    )
    rank_hidden_output = lax.psum(lowrank_out_part.astype(jnp.bfloat16), ("tp", "dp"))
    adapter_term = jnp.dot(
        masked_wide(rank_hidden_output, onehot_b), up_out, preferred_element_type=jnp.float32
    )
    return (base + adapter_term).astype(jnp.bfloat16)


def moved(block, shift, kind):
    side = lax.axis_size("ctx")
    if kind == "ctx":
        pairs = [(a, (a + shift) % side) for a in range(side)]
        return lax.ppermute(block, "ctx", pairs)
    if kind == "lane":
        pairs = [(a, (a + shift) % side) for a in range(side)]
        return lax.ppermute(block, ("tp", "dp"), pairs)
    if kind == "rows":
        pairs = [(a * side + b, b * side + (a + shift) % side) for a in range(side) for b in range(side)]
    else:
        pairs = [(a * side + b, ((b + shift) % side) * side + a) for a in range(side) for b in range(side)]
    return lax.ppermute(block, ("ctx", "tp", "dp"), pairs)


def transposed(block):
    return moved(block, 0, "rows")


def in_order(pieces, place):
    stacked = jnp.stack(pieces[::-1], axis=0)
    ordered = jnp.roll(stacked, place + 1, axis=0)
    return ordered.reshape((-1,) + pieces[0].shape[1:])


def block_rows(values, index, length):
    return lax.dynamic_slice_in_dim(values, index * length, length, 0)


def owned_rows(values, owned):
    return jnp.concatenate(
        [values * owned[:, i : i + 1].astype(values.dtype) for i in range(owned.shape[1])], axis=1
    )


def square_body(
    tokens,
    lengths,
    request_adapter_ids,
    adapter_store_slot,
    xchan_input_weight,
    bc_input_weight,
    step_input_weight,
    convolution_x_taps,
    convolution_bc_taps,
    step_bias,
    decay_log_rate,
    head_skip_gain,
    output_norm_gain,
    output_weight,
    adapter_down_input,
    adapter_up_xchan,
    adapter_up_bc,
    adapter_down_output,
    adapter_up_output,
):
    length = tokens.shape[0]
    side = lax.axis_size("ctx")
    taps = convolution_x_taps.shape[0]
    bank_entries = adapter_down_input.shape[0]
    rank_value = adapter_down_input.shape[2]
    head_count = step_bias.shape[0]
    channels = xchan_input_weight.shape[1]
    bc_width = bc_input_weight.shape[1]
    here = lax.axis_index("ctx")
    lane = lax.axis_index(("tp", "dp"))
    start_pos = here * length
    request_ends = jnp.cumsum(lengths, dtype=jnp.int32)
    positions = start_pos + jnp.arange(length, dtype=jnp.int32)
    segment = segment_of(positions, request_ends)
    previous = segment_of(jnp.reshape(start_pos - 1, (1,)), request_ends)[0]
    slot_indices = adapter_store_slot[request_adapter_ids]
    request_count = lengths.shape[0]
    local_onehot = segment[:, None] == jnp.arange(request_count, dtype=jnp.int32)[None, :]
    slot_of_position = jnp.sum(
        jnp.where(local_onehot, slot_indices[None, :], 0), axis=1, dtype=jnp.int32
    )
    slot_owned = slot_of_position[:, None] == jnp.arange(side * bank_entries, dtype=jnp.int32)[None, :]

    panels = (
        adapter_down_input,
        adapter_up_xchan,
        adapter_up_bc,
        adapter_down_output,
        adapter_up_output,
    )
    packed = jnp.concatenate([panel.reshape(bank_entries, -1) for panel in panels], axis=1)
    store = in_order([packed] + [moved(packed, s, "ctx") for s in range(1, side)], here)
    offsets = [0]
    for panel in panels:
        offsets.append(offsets[-1] + panel[0].size)
    down_in_all, up_x_all, up_bc_all, down_out_all, up_out_all = [
        store[:, offsets[i] : offsets[i + 1]].reshape((side * bank_entries,) + panel.shape[1:])
        for i, panel in enumerate(panels)
    ]

    def lane_total(part):
        return part + sum(moved(part, s, "lane") for s in range(1, side))

    def picked(rows, bank):
        every = jnp.einsum("pf,afr->par", rows, bank, preferred_element_type=jnp.float32)
        return jnp.sum(every * slot_owned[:, :, None].astype(jnp.float32), axis=1)

    def spread(hidden):
        return owned_rows(hidden, slot_owned).astype(jnp.bfloat16)

    hidden_wide = spread(lane_total(picked(tokens, down_in_all)))

    tokens_t = transposed(tokens)
    stream_rows = in_order(
        [tokens_t] + [moved(tokens_t, s, "lane") for s in range(1, side)], lane
    )
    projected = jnp.concatenate(
        [
            jnp.dot(stream_rows, xchan_input_weight, preferred_element_type=jnp.float32),
            jnp.dot(stream_rows, bc_input_weight, preferred_element_type=jnp.float32),
            jnp.dot(stream_rows, step_input_weight, preferred_element_type=jnp.float32),
        ],
        axis=1,
    )
    summed = block_rows(projected, here, length)
    for s in range(1, side):
        sent = block_rows(projected, (here + s) % side, length).astype(jnp.bfloat16)
        summed = summed + moved(sent, s, "ctx").astype(jnp.float32)
    adapter_values = jnp.concatenate(
        [
            jnp.dot(
                hidden_wide,
                up_x_all.reshape(side * bank_entries * rank_value, -1),
                preferred_element_type=jnp.float32,
            ),
            jnp.dot(
                hidden_wide,
                up_bc_all.reshape(side * bank_entries * rank_value, -1),
                preferred_element_type=jnp.float32,
            ),
        ],
        axis=1,
    )
    values = summed[:, : channels + bc_width] + adapter_values
    step_raw = summed[:, channels + bc_width :]

    kernel = jnp.concatenate([convolution_x_taps, convolution_bc_taps], axis=1)
    tail_rows = passed_along(values[length - (taps - 1) :], "ctx", 1)
    extended = jnp.concatenate([tail_rows, values], axis=0)
    extended_segment = segment_of(
        start_pos - (taps - 1) + jnp.arange(length + taps - 1, dtype=jnp.int32), request_ends
    )
    convolved = jnp.zeros_like(values)
    for tap in range(taps):
        keep = (extended_segment[tap : tap + length] == segment).astype(jnp.float32)
        convolved = convolved + kernel[tap][None, :] * extended[tap : tap + length] * keep[:, None]
    act = jax.nn.silu(convolved)
    x_heads = act[:, :channels].reshape(length, head_count, -1)
    bc_local = act[:, channels:].astype(jnp.bfloat16)
    bc_all = lax.all_gather(bc_local, ("tp", "dp"), axis=1, tiled=True)
    state_width = bc_all.shape[1] // 2
    b_proj = bc_all[:, :state_width]
    c_proj = bc_all[:, state_width:]
    step_size = jax.nn.softplus(step_raw + step_bias[None, :])
    log_decay = -step_size * jnp.exp(decay_log_rate)[None, :]
    inner_out, local_state, enter_weight, carry_decay = span_parts(
        x_heads, b_proj, c_proj, step_size, log_decay, segment, previous
    )
    entering = jnp.zeros_like(local_state)
    for s in range(side - 1, 0, -1):
        pairs = [(a, a + s) for a in range(side - s)]
        decay_in = lax.ppermute(carry_decay.astype(jnp.bfloat16), "ctx", pairs)
        state_in = lax.ppermute(local_state.astype(jnp.bfloat16), "ctx", pairs)
        entering = decay_in.astype(jnp.float32)[:, None, None] * entering + state_in.astype(
            jnp.float32
        )
    entered = (
        jnp.einsum("tn,hdn->thd", c_proj.astype(jnp.float32), entering, precision=FULL_PRECISION)
        * enter_weight[:, :, None]
    )
    mixer_out = (inner_out + entered + head_skip_gain[None, :, None] * x_heads).reshape(
        length, channels
    )
    scale = lax.rsqrt(jnp.mean(mixer_out * mixer_out, axis=1, keepdims=True) + NORM_EPSILON)
    normalized_rows = (mixer_out * scale * output_norm_gain[None, :]).astype(jnp.bfloat16)

    output_wide = spread(lane_total(picked(normalized_rows, down_out_all)))
    adapter_output = jnp.dot(
        output_wide,
        up_out_all.reshape(side * bank_entries * rank_value, -1),
        preferred_element_type=jnp.float32,
    )
    normed_stream = in_order(
        [normalized_rows] + [moved(normalized_rows, s, "ctx") for s in range(1, side)], here
    )
    base_part = jnp.dot(normed_stream, output_weight, preferred_element_type=jnp.float32).astype(
        jnp.bfloat16
    )
    mixed_t = block_rows(base_part, lane, length).astype(jnp.float32)
    for s in range(1, side):
        mixed_t = mixed_t + moved(
            block_rows(base_part, (lane + s) % side, length), s, "lane"
        ).astype(jnp.float32)
    mixed = transposed(mixed_t.astype(jnp.bfloat16)).astype(jnp.float32) + adapter_output
    return mixed.astype(jnp.bfloat16)


def solution(mesh):
    body = square_body if mesh.shape["ctx"] == mesh.shape["tp"] * mesh.shape["dp"] else general_body
    placed = (
        P(("groups", "ctx"), ("tp", "dp")),
        P("groups"),
        P("groups"),
        P(),
        P("ctx", ("tp", "dp")),
        P("ctx", ("tp", "dp")),
        P("ctx", ("tp", "dp")),
        P(None, ("tp", "dp")),
        P(None, ("tp", "dp")),
        P(("tp", "dp")),
        P(("tp", "dp")),
        P(("tp", "dp")),
        P(("tp", "dp")),
        P(("tp", "dp"), "ctx"),
        P("ctx", ("tp", "dp"), None),
        P("ctx", None, ("tp", "dp")),
        P("ctx", None, ("tp", "dp")),
        P("ctx", ("tp", "dp"), None),
        P("ctx", None, ("tp", "dp")),
    )
    return jax.shard_map(
        body,
        mesh=mesh,
        in_specs=placed,
        out_specs=P(("groups", "ctx"), ("tp", "dp")),
        check_vma=False,
    )
```

```python
import jax
import jax.numpy as jnp
from jax import lax
from jax.sharding import PartitionSpec as P

FULL_PRECISION = lax.Precision.HIGHEST
NORM_EPSILON = 1e-06


def from_root(block, axis, source):
    block = jnp.where(lax.axis_index(axis) == source, block, jnp.zeros_like(block))
    return lax.psum(block, axis)


def passed_along(shard, axis, by):
    size = lax.axis_size(axis)
    pairs = [(i, i + by) for i in range(size) if 0 <= i + by < size]
    return lax.ppermute(shard, axis, pairs)


def prefix(shard, axis, combine, identity):
    size, place = (lax.axis_size(axis), lax.axis_index(axis))
    everything = jax.tree.map(
        lambda part, kind: lax.all_gather(part.astype(kind), axis),
        shard,
        (jnp.bfloat16, jnp.bfloat16),
    )
    start = jax.tree.map(
        lambda part, zero: jnp.broadcast_to(jnp.asarray(zero, part.dtype), part.shape),
        shard,
        identity,
    )

    def lap(k, before):
        reached = k < place
        new = combine(
            before, jax.tree.map(lambda part, own: part[k].astype(own.dtype), everything, shard)
        )
        return jax.tree.map(lambda a, b: jnp.where(reached, a, b), new, before)

    return lax.fori_loop(0, size, lap, start)


def segment_of(positions, request_ends):
    inside = (positions[:, None] >= request_ends[None, :]).astype(jnp.int32)
    counted = jnp.sum(inside, axis=1, dtype=jnp.int32)
    return jnp.where(positions < 0, jnp.int32(-1), counted)


def span_parts(x_heads, b_proj, c_proj, step_size, log_decay, segment, previous):
    length = x_heads.shape[0]
    cumulative = jnp.cumsum(log_decay, axis=0)
    final_log = cumulative[length - 1]
    places = jnp.arange(length, dtype=jnp.int32)
    same_request = jnp.logical_and(
        segment[:, None] == segment[None, :], places[None, :] <= places[:, None]
    ).astype(jnp.float32)
    log_gap = cumulative.T[:, :, None] - cumulative.T[:, None, :]
    decay_table = jnp.exp(jnp.minimum(log_gap, 0.0)) * same_request[None]
    scores = lax.dot_general(
        c_proj, b_proj, (((1,), (1,)), ((), ())), preferred_element_type=jnp.float32
    )
    weights = scores[None] * decay_table * step_size.T[:, None, :]
    inner_out = jnp.einsum("hts,shd->thd", weights, x_heads, precision=FULL_PRECISION)
    at_end = (segment == segment[length - 1]).astype(jnp.float32)
    state_weight = jnp.exp(final_log[None, :] - cumulative) * at_end[:, None] * step_size
    local_state = jnp.einsum(
        "sh,shd,sn->hdn",
        state_weight,
        x_heads,
        b_proj.astype(jnp.float32),
        precision=FULL_PRECISION,
    )
    enter_weight = jnp.exp(cumulative) * (segment == previous).astype(jnp.float32)[:, None]
    carry_decay = jnp.exp(final_log) * (segment[length - 1] == previous).astype(jnp.float32)
    return (inner_out, local_state, enter_weight, carry_decay)


def select_rows(wide, adapter_picker_matrix):
    shaped = wide.reshape(wide.shape[0], adapter_picker_matrix.shape[1], -1)
    return jnp.sum(shaped * adapter_picker_matrix[:, :, None], axis=1)


def masked_wide(values, onehot_b):
    return (values[:, None, :] * onehot_b[:, :, None]).reshape(values.shape[0], -1)


def general_body(
    tokens,
    lengths,
    request_adapter_ids,
    adapter_store_slot,
    xchan_input_weight,
    bc_input_weight,
    step_input_weight,
    convolution_x_taps,
    convolution_bc_taps,
    step_bias,
    decay_log_rate,
    head_skip_gain,
    output_norm_gain,
    output_weight,
    adapter_down_input,
    adapter_up_xchan,
    adapter_up_bc,
    adapter_down_output,
    adapter_up_output,
):
    length = tokens.shape[0]
    request_list = lengths.shape[0]
    taps = convolution_x_taps.shape[0]
    bank_entries = adapter_down_input.shape[0]
    head_count = step_bias.shape[0]
    channels = xchan_input_weight.shape[1]
    start_pos = lax.axis_index("ctx") * length
    request_ends = jnp.cumsum(lengths, dtype=jnp.int32)
    positions = start_pos + jnp.arange(length, dtype=jnp.int32)
    segment = segment_of(positions, request_ends)
    previous = segment_of(jnp.reshape(start_pos - 1, (1,)), request_ends)[0]
    adapter_picker_matrix = (
        segment[:, None] == jnp.arange(request_list, dtype=jnp.int32)[None, :]
    ).astype(jnp.float32)
    onehot_b = adapter_picker_matrix.astype(jnp.bfloat16)
    slot_indices = adapter_store_slot[request_adapter_ids]
    initial_stacks = (
        jnp.zeros(
            (adapter_down_input.shape[1], request_list, adapter_down_input.shape[2]), jnp.bfloat16
        ),
        jnp.zeros((request_list,) + adapter_up_xchan.shape[1:], jnp.bfloat16),
        jnp.zeros((request_list,) + adapter_up_bc.shape[1:], jnp.bfloat16),
        jnp.zeros(
            (adapter_down_output.shape[1], request_list, adapter_down_output.shape[2]), jnp.bfloat16
        ),
        jnp.zeros((request_list,) + adapter_up_output.shape[1:], jnp.bfloat16),
    )
    stack_dims = (1, 0, 0, 1, 0)

    def fetch(request_item, current):
        slot = slot_indices[request_item]
        owner = slot // bank_entries
        within = slot % bank_entries
        a_in, b_x, b_bc, a_out, b_out = [
            lax.dynamic_index_in_dim(adapter_bank, within, 0, keepdims=False)
            for adapter_bank in (
                adapter_down_input,
                adapter_up_xchan,
                adapter_up_bc,
                adapter_down_output,
                adapter_up_output,
            )
        ]
        received = (
            from_root(a_in, "ctx", owner),
            from_root(b_x, "ctx", owner),
            from_root(b_bc, "ctx", owner),
            from_root(a_out, "ctx", owner),
            from_root(b_out, "ctx", owner),
        )
        return tuple(
            (
                lax.dynamic_update_index_in_dim(stack, panel, request_item, along)
                for stack, panel, along in zip(current, received, stack_dims)
            )
        )

    stacks = lax.fori_loop(0, request_list, fetch, initial_stacks)
    rank_value = adapter_down_input.shape[2]
    down_in = stacks[0].reshape(stacks[0].shape[0], request_list * rank_value)
    up_x = stacks[1].reshape(request_list * rank_value, -1)
    up_bc = stacks[2].reshape(request_list * rank_value, -1)
    down_out = stacks[3].reshape(stacks[3].shape[0], request_list * rank_value)
    up_out = stacks[4].reshape(request_list * rank_value, -1)
    lowrank_part = select_rows(
        jnp.dot(tokens, down_in, preferred_element_type=jnp.float32), adapter_picker_matrix
    )
    rank_hidden = lax.psum(lowrank_part.astype(jnp.bfloat16), ("tp", "dp"))
    lowrank_wide = masked_wide(rank_hidden, onehot_b)
    full_tokens = lax.all_gather(tokens, ("tp", "dp"), axis=1, tiled=True)
    pieces = (
        lax.all_gather(xchan_input_weight, "ctx", axis=0, tiled=True),
        lax.all_gather(bc_input_weight, "ctx", axis=0, tiled=True),
        lax.all_gather(step_input_weight, "ctx", axis=0, tiled=True),
    )
    xchan_values, bc_channel_values, step_raw = tuple(
        (jnp.dot(full_tokens, piece, preferred_element_type=jnp.float32) for piece in pieces)
    )
    xchan_values = xchan_values + jnp.dot(lowrank_wide, up_x, preferred_element_type=jnp.float32)
    bc_channel_values = bc_channel_values + jnp.dot(
        lowrank_wide, up_bc, preferred_element_type=jnp.float32
    )
    values = jnp.concatenate([xchan_values, bc_channel_values], axis=1)
    kernel = jnp.concatenate([convolution_x_taps, convolution_bc_taps], axis=1)
    tail_rows = passed_along(values[length - (taps - 1) :], "ctx", 1)
    extended = jnp.concatenate([tail_rows, values], axis=0)
    extended_segment = segment_of(
        start_pos - (taps - 1) + jnp.arange(length + taps - 1, dtype=jnp.int32), request_ends
    )
    convolved = jnp.zeros_like(values)
    for tap in range(taps):
        keep = (extended_segment[tap : tap + length] == segment).astype(jnp.float32)
        convolved = convolved + kernel[tap][None, :] * extended[tap : tap + length] * keep[:, None]
    act = jax.nn.silu(convolved)
    x_heads = act[:, :channels].reshape(length, head_count, -1)
    bc_local = act[:, channels:].astype(jnp.bfloat16)
    bc_all = lax.all_gather(bc_local, ("tp", "dp"), axis=1, tiled=True)
    state_width = bc_all.shape[1] // 2
    b_proj = bc_all[:, :state_width]
    c_proj = bc_all[:, state_width:]
    step_size = jax.nn.softplus(step_raw + step_bias[None, :])
    log_decay = -step_size * jnp.exp(decay_log_rate)[None, :]
    inner_out, local_state, enter_weight, carry_decay = span_parts(
        x_heads, b_proj, c_proj, step_size, log_decay, segment, previous
    )

    def compose(earlier, later):
        return (earlier[0] * later[0], later[0][:, None, None] * earlier[1] + later[1])

    carried = prefix(
        (carry_decay, local_state),
        "ctx",
        compose,
        (jnp.ones_like(carry_decay), jnp.zeros_like(local_state)),
    )
    entering = carried[1]
    entered = (
        jnp.einsum("tn,hdn->thd", c_proj.astype(jnp.float32), entering, precision=FULL_PRECISION)
        * enter_weight[:, :, None]
    )
    mixer_out = (inner_out + entered + head_skip_gain[None, :, None] * x_heads).reshape(
        length, channels
    )
    scale = lax.rsqrt(jnp.mean(mixer_out * mixer_out, axis=1, keepdims=True) + NORM_EPSILON)
    normalized_rows = (mixer_out * scale * output_norm_gain[None, :]).astype(jnp.bfloat16)
    term = jnp.dot(
        normalized_rows,
        lax.all_gather(output_weight, "ctx", axis=1, tiled=True),
        preferred_element_type=jnp.float32,
    )
    base = lax.psum_scatter(
        term.astype(jnp.bfloat16), ("tp", "dp"), scatter_dimension=1, tiled=True
    ).astype(jnp.float32)
    lowrank_out_part = select_rows(
        jnp.dot(normalized_rows, down_out, preferred_element_type=jnp.float32),
        adapter_picker_matrix,
    )
    rank_hidden_output = lax.psum(lowrank_out_part.astype(jnp.bfloat16), ("tp", "dp"))
    adapter_term = jnp.dot(
        masked_wide(rank_hidden_output, onehot_b), up_out, preferred_element_type=jnp.float32
    )
    return (base + adapter_term).astype(jnp.bfloat16)


def moved(block, shift, kind):
    side = lax.axis_size("ctx")
    if kind == "ctx":
        pairs = [(a, (a + shift) % side) for a in range(side)]
        return lax.ppermute(block, "ctx", pairs)
    if kind == "lane":
        pairs = [(a, (a + shift) % side) for a in range(side)]
        return lax.ppermute(block, ("tp", "dp"), pairs)
    if kind == "rows":
        pairs = [(a * side + b, b * side + (a + shift) % side) for a in range(side) for b in range(side)]
    else:
        pairs = [(a * side + b, ((b + shift) % side) * side + a) for a in range(side) for b in range(side)]
    return lax.ppermute(block, ("ctx", "tp", "dp"), pairs)


def transposed(block):
    return moved(block, 0, "rows")


def in_order(pieces, place):
    stacked = jnp.stack(pieces[::-1], axis=0)
    ordered = jnp.roll(stacked, place + 1, axis=0)
    return ordered.reshape((-1,) + pieces[0].shape[1:])


def block_rows(values, index, length):
    return lax.dynamic_slice_in_dim(values, index * length, length, 0)


def owned_rows(values, owned):
    return jnp.concatenate(
        [values * owned[:, i : i + 1].astype(values.dtype) for i in range(owned.shape[1])], axis=1
    )


def square_body(
    tokens,
    lengths,
    request_adapter_ids,
    adapter_store_slot,
    xchan_input_weight,
    bc_input_weight,
    step_input_weight,
    convolution_x_taps,
    convolution_bc_taps,
    step_bias,
    decay_log_rate,
    head_skip_gain,
    output_norm_gain,
    output_weight,
    adapter_down_input,
    adapter_up_xchan,
    adapter_up_bc,
    adapter_down_output,
    adapter_up_output,
):
    length = tokens.shape[0]
    side = lax.axis_size("ctx")
    stream = side * length
    taps = convolution_x_taps.shape[0]
    bank_entries = adapter_down_input.shape[0]
    rank_value = adapter_down_input.shape[2]
    head_count = step_bias.shape[0]
    channels = xchan_input_weight.shape[1]
    bc_width = bc_input_weight.shape[1]
    here = lax.axis_index("ctx")
    lane = lax.axis_index(("tp", "dp"))
    start_pos = here * length
    request_ends = jnp.cumsum(lengths, dtype=jnp.int32)
    every_position = jnp.arange(stream, dtype=jnp.int32)
    every_segment = segment_of(every_position, request_ends)
    slot_indices = adapter_store_slot[request_adapter_ids]
    request_count = lengths.shape[0]
    stream_onehot = every_segment[:, None] == jnp.arange(request_count, dtype=jnp.int32)[None, :]
    slot_of_position = jnp.sum(
        jnp.where(stream_onehot, slot_indices[None, :], 0), axis=1, dtype=jnp.int32
    )
    entry_ids = jnp.arange(bank_entries, dtype=jnp.int32)[None, :]
    owned_here = slot_of_position[:, None] == here * bank_entries + entry_ids
    owned_lane = slot_of_position[:, None] == lane * bank_entries + entry_ids
    positions = start_pos + jnp.arange(length, dtype=jnp.int32)
    segment = segment_of(positions, request_ends)
    previous = segment_of(jnp.reshape(start_pos - 1, (1,)), request_ends)[0]

    tokens_t = transposed(tokens)
    stream_rows = in_order(
        [tokens_t] + [moved(tokens_t, s, "lane") for s in range(1, side)], lane
    )
    down_in_t = transposed(adapter_down_input)
    up_out_t = transposed(adapter_up_output)
    down_part = jnp.einsum(
        "pf,efr->per", stream_rows, down_in_t, preferred_element_type=jnp.float32
    )
    down_pick = jnp.sum(
        down_part * owned_lane[:, :, None].astype(jnp.float32), axis=1
    )
    rank_hidden = sum(moved(down_pick, s, "rows") for s in range(side))
    hidden_wide = owned_rows(rank_hidden, owned_here).astype(jnp.bfloat16)
    xchan_part = jnp.dot(
        stream_rows, xchan_input_weight, preferred_element_type=jnp.float32
    ) + jnp.dot(
        hidden_wide,
        adapter_up_xchan.reshape(bank_entries * rank_value, -1),
        preferred_element_type=jnp.float32,
    )
    bc_part = jnp.dot(stream_rows, bc_input_weight, preferred_element_type=jnp.float32) + jnp.dot(
        hidden_wide,
        adapter_up_bc.reshape(bank_entries * rank_value, -1),
        preferred_element_type=jnp.float32,
    )
    step_part = jnp.dot(stream_rows, step_input_weight, preferred_element_type=jnp.float32)
    projected = jnp.concatenate([xchan_part, bc_part, step_part], axis=1)
    padded = jnp.concatenate(
        [jnp.zeros((taps - 1, projected.shape[1]), projected.dtype), projected], axis=0
    )

    def with_tail(index):
        return lax.dynamic_slice_in_dim(padded, index * length, length + taps - 1, 0)

    summed = with_tail(here)
    for s in range(1, side):
        sent = with_tail((here + s) % side).astype(jnp.bfloat16)
        summed = summed + moved(sent, s, "ctx").astype(jnp.float32)
    extended = summed[:, : channels + bc_width]
    values = extended[taps - 1 :]
    step_raw = summed[taps - 1 :, channels + bc_width :]

    kernel = jnp.concatenate([convolution_x_taps, convolution_bc_taps], axis=1)
    extended_segment = segment_of(
        start_pos - (taps - 1) + jnp.arange(length + taps - 1, dtype=jnp.int32), request_ends
    )
    convolved = jnp.zeros_like(values)
    for tap in range(taps):
        keep = (extended_segment[tap : tap + length] == segment).astype(jnp.float32)
        convolved = convolved + kernel[tap][None, :] * extended[tap : tap + length] * keep[:, None]
    act = jax.nn.silu(convolved)
    x_heads = act[:, :channels].reshape(length, head_count, -1)
    bc_local = act[:, channels:].astype(jnp.bfloat16)
    bc_all = lax.all_gather(bc_local, ("tp", "dp"), axis=1, tiled=True)
    state_width = bc_all.shape[1] // 2
    b_proj = bc_all[:, :state_width]
    c_proj = bc_all[:, state_width:]
    step_size = jax.nn.softplus(step_raw + step_bias[None, :])
    log_decay = -step_size * jnp.exp(decay_log_rate)[None, :]
    inner_out, local_state, enter_weight, carry_decay = span_parts(
        x_heads, b_proj, c_proj, step_size, log_decay, segment, previous
    )

    decay_row = jnp.broadcast_to(carry_decay[:, None, None], (head_count, 1, local_state.shape[2]))
    state_and_decay = jnp.concatenate([decay_row, local_state], axis=1).astype(jnp.bfloat16)
    entering = jnp.zeros_like(local_state)
    for s in range(side - 1, 0, -1):
        pairs = [(a, a + s) for a in range(side - s)]
        both_in = lax.ppermute(state_and_decay, "ctx", pairs).astype(jnp.float32)
        entering = both_in[:, :1, : local_state.shape[2]][:, :, :1] * entering + both_in[:, 1:]
    entered = (
        jnp.einsum("tn,hdn->thd", c_proj.astype(jnp.float32), entering, precision=FULL_PRECISION)
        * enter_weight[:, :, None]
    )
    mixer_out = (inner_out + entered + head_skip_gain[None, :, None] * x_heads).reshape(
        length, channels
    )
    scale = lax.rsqrt(jnp.mean(mixer_out * mixer_out, axis=1, keepdims=True) + NORM_EPSILON)
    normalized_rows = (mixer_out * scale * output_norm_gain[None, :]).astype(jnp.bfloat16)

    normed_stream = in_order(
        [normalized_rows] + [moved(normalized_rows, s, "ctx") for s in range(1, side)], here
    )
    out_down_part = jnp.einsum(
        "pc,ecr->per", normed_stream, adapter_down_output, preferred_element_type=jnp.float32
    )
    out_down_pick = jnp.sum(out_down_part * owned_here[:, :, None].astype(jnp.float32), axis=1)
    rank_hidden_output = transposed(
        out_down_pick + sum(moved(out_down_pick, s, "lane") for s in range(1, side))
    )
    base_part = jnp.dot(
        normed_stream, output_weight, preferred_element_type=jnp.float32
    ).astype(jnp.bfloat16).astype(jnp.float32)
    adapter_part = jnp.dot(
        owned_rows(rank_hidden_output, owned_lane).astype(jnp.bfloat16),
        up_out_t.reshape(bank_entries * rank_value, -1),
        preferred_element_type=jnp.float32,
    )
    out_part = base_part + adapter_part
    mixed_t = block_rows(out_part, lane, length)
    for s in range(1, side):
        sent = block_rows(out_part, (lane + s) % side, length).astype(jnp.bfloat16)
        mixed_t = mixed_t + moved(sent, s, "lane").astype(jnp.float32)
    return transposed(mixed_t.astype(jnp.bfloat16))


def solution(mesh):
    body = square_body if mesh.shape["ctx"] == mesh.shape["tp"] * mesh.shape["dp"] else general_body
    placed = (
        P(("groups", "ctx"), ("tp", "dp")),
        P("groups"),
        P("groups"),
        P(),
        P("ctx", ("tp", "dp")),
        P("ctx", ("tp", "dp")),
        P("ctx", ("tp", "dp")),
        P(None, ("tp", "dp")),
        P(None, ("tp", "dp")),
        P(("tp", "dp")),
        P(("tp", "dp")),
        P(("tp", "dp")),
        P(("tp", "dp")),
        P(("tp", "dp"), "ctx"),
        P("ctx", ("tp", "dp"), None),
        P("ctx", None, ("tp", "dp")),
        P("ctx", None, ("tp", "dp")),
        P("ctx", ("tp", "dp"), None),
        P("ctx", None, ("tp", "dp")),
    )
    return jax.shard_map(
        body,
        mesh=mesh,
        in_specs=placed,
        out_specs=P(("groups", "ctx"), ("tp", "dp")),
        check_vma=False,
    )
```

```python
import jax
import jax.numpy as jnp
from jax import lax
from jax.sharding import PartitionSpec as P

FULL_PRECISION = lax.Precision.HIGHEST
NORM_EPSILON = 1e-06


def from_root(block, axis, source):
    block = jnp.where(lax.axis_index(axis) == source, block, jnp.zeros_like(block))
    return lax.psum(block, axis)


def passed_along(shard, axis, by):
    size = lax.axis_size(axis)
    pairs = [(i, i + by) for i in range(size) if 0 <= i + by < size]
    return lax.ppermute(shard, axis, pairs)


def prefix(shard, axis, combine, identity):
    size, place = (lax.axis_size(axis), lax.axis_index(axis))
    everything = jax.tree.map(
        lambda part, kind: lax.all_gather(part.astype(kind), axis),
        shard,
        (jnp.bfloat16, jnp.bfloat16),
    )
    start = jax.tree.map(
        lambda part, zero: jnp.broadcast_to(jnp.asarray(zero, part.dtype), part.shape),
        shard,
        identity,
    )

    def lap(k, before):
        reached = k < place
        new = combine(
            before, jax.tree.map(lambda part, own: part[k].astype(own.dtype), everything, shard)
        )
        return jax.tree.map(lambda a, b: jnp.where(reached, a, b), new, before)

    return lax.fori_loop(0, size, lap, start)


def segment_of(positions, request_ends):
    inside = (positions[:, None] >= request_ends[None, :]).astype(jnp.int32)
    counted = jnp.sum(inside, axis=1, dtype=jnp.int32)
    return jnp.where(positions < 0, jnp.int32(-1), counted)


def span_parts(x_heads, b_proj, c_proj, step_size, log_decay, segment, previous):
    length = x_heads.shape[0]
    cumulative = jnp.cumsum(log_decay, axis=0)
    final_log = cumulative[length - 1]
    places = jnp.arange(length, dtype=jnp.int32)
    same_request = jnp.logical_and(
        segment[:, None] == segment[None, :], places[None, :] <= places[:, None]
    ).astype(jnp.float32)
    log_gap = cumulative.T[:, :, None] - cumulative.T[:, None, :]
    decay_table = jnp.exp(jnp.minimum(log_gap, 0.0)) * same_request[None]
    scores = lax.dot_general(
        c_proj, b_proj, (((1,), (1,)), ((), ())), preferred_element_type=jnp.float32
    )
    weights = scores[None] * decay_table * step_size.T[:, None, :]
    inner_out = jnp.einsum("hts,shd->thd", weights, x_heads, precision=FULL_PRECISION)
    at_end = (segment == segment[length - 1]).astype(jnp.float32)
    state_weight = jnp.exp(final_log[None, :] - cumulative) * at_end[:, None] * step_size
    local_state = jnp.einsum(
        "sh,shd,sn->hdn",
        state_weight,
        x_heads,
        b_proj.astype(jnp.float32),
        precision=FULL_PRECISION,
    )
    enter_weight = jnp.exp(cumulative) * (segment == previous).astype(jnp.float32)[:, None]
    carry_decay = jnp.exp(final_log) * (segment[length - 1] == previous).astype(jnp.float32)
    return (inner_out, local_state, enter_weight, carry_decay)


def select_rows(wide, adapter_picker_matrix):
    shaped = wide.reshape(wide.shape[0], adapter_picker_matrix.shape[1], -1)
    return jnp.sum(shaped * adapter_picker_matrix[:, :, None], axis=1)


def masked_wide(values, onehot_b):
    return (values[:, None, :] * onehot_b[:, :, None]).reshape(values.shape[0], -1)


def general_body(
    tokens,
    lengths,
    request_adapter_ids,
    adapter_store_slot,
    xchan_input_weight,
    bc_input_weight,
    step_input_weight,
    convolution_x_taps,
    convolution_bc_taps,
    step_bias,
    decay_log_rate,
    head_skip_gain,
    output_norm_gain,
    output_weight,
    adapter_down_input,
    adapter_up_xchan,
    adapter_up_bc,
    adapter_down_output,
    adapter_up_output,
):
    length = tokens.shape[0]
    request_list = lengths.shape[0]
    taps = convolution_x_taps.shape[0]
    bank_entries = adapter_down_input.shape[0]
    head_count = step_bias.shape[0]
    channels = xchan_input_weight.shape[1]
    start_pos = lax.axis_index("ctx") * length
    request_ends = jnp.cumsum(lengths, dtype=jnp.int32)
    positions = start_pos + jnp.arange(length, dtype=jnp.int32)
    segment = segment_of(positions, request_ends)
    previous = segment_of(jnp.reshape(start_pos - 1, (1,)), request_ends)[0]
    adapter_picker_matrix = (
        segment[:, None] == jnp.arange(request_list, dtype=jnp.int32)[None, :]
    ).astype(jnp.float32)
    onehot_b = adapter_picker_matrix.astype(jnp.bfloat16)
    slot_indices = adapter_store_slot[request_adapter_ids]
    initial_stacks = (
        jnp.zeros(
            (adapter_down_input.shape[1], request_list, adapter_down_input.shape[2]), jnp.bfloat16
        ),
        jnp.zeros((request_list,) + adapter_up_xchan.shape[1:], jnp.bfloat16),
        jnp.zeros((request_list,) + adapter_up_bc.shape[1:], jnp.bfloat16),
        jnp.zeros(
            (adapter_down_output.shape[1], request_list, adapter_down_output.shape[2]), jnp.bfloat16
        ),
        jnp.zeros((request_list,) + adapter_up_output.shape[1:], jnp.bfloat16),
    )
    stack_dims = (1, 0, 0, 1, 0)

    def fetch(request_item, current):
        slot = slot_indices[request_item]
        owner = slot // bank_entries
        within = slot % bank_entries
        a_in, b_x, b_bc, a_out, b_out = [
            lax.dynamic_index_in_dim(adapter_bank, within, 0, keepdims=False)
            for adapter_bank in (
                adapter_down_input,
                adapter_up_xchan,
                adapter_up_bc,
                adapter_down_output,
                adapter_up_output,
            )
        ]
        received = (
            from_root(a_in, "ctx", owner),
            from_root(b_x, "ctx", owner),
            from_root(b_bc, "ctx", owner),
            from_root(a_out, "ctx", owner),
            from_root(b_out, "ctx", owner),
        )
        return tuple(
            (
                lax.dynamic_update_index_in_dim(stack, panel, request_item, along)
                for stack, panel, along in zip(current, received, stack_dims)
            )
        )

    stacks = lax.fori_loop(0, request_list, fetch, initial_stacks)
    rank_value = adapter_down_input.shape[2]
    down_in = stacks[0].reshape(stacks[0].shape[0], request_list * rank_value)
    up_x = stacks[1].reshape(request_list * rank_value, -1)
    up_bc = stacks[2].reshape(request_list * rank_value, -1)
    down_out = stacks[3].reshape(stacks[3].shape[0], request_list * rank_value)
    up_out = stacks[4].reshape(request_list * rank_value, -1)
    lowrank_part = select_rows(
        jnp.dot(tokens, down_in, preferred_element_type=jnp.float32), adapter_picker_matrix
    )
    rank_hidden = lax.psum(lowrank_part.astype(jnp.bfloat16), ("tp", "dp"))
    lowrank_wide = masked_wide(rank_hidden, onehot_b)
    full_tokens = lax.all_gather(tokens, ("tp", "dp"), axis=1, tiled=True)
    pieces = (
        lax.all_gather(xchan_input_weight, "ctx", axis=0, tiled=True),
        lax.all_gather(bc_input_weight, "ctx", axis=0, tiled=True),
        lax.all_gather(step_input_weight, "ctx", axis=0, tiled=True),
    )
    xchan_values, bc_channel_values, step_raw = tuple(
        (jnp.dot(full_tokens, piece, preferred_element_type=jnp.float32) for piece in pieces)
    )
    xchan_values = xchan_values + jnp.dot(lowrank_wide, up_x, preferred_element_type=jnp.float32)
    bc_channel_values = bc_channel_values + jnp.dot(
        lowrank_wide, up_bc, preferred_element_type=jnp.float32
    )
    values = jnp.concatenate([xchan_values, bc_channel_values], axis=1)
    kernel = jnp.concatenate([convolution_x_taps, convolution_bc_taps], axis=1)
    tail_rows = passed_along(values[length - (taps - 1) :], "ctx", 1)
    extended = jnp.concatenate([tail_rows, values], axis=0)
    extended_segment = segment_of(
        start_pos - (taps - 1) + jnp.arange(length + taps - 1, dtype=jnp.int32), request_ends
    )
    convolved = jnp.zeros_like(values)
    for tap in range(taps):
        keep = (extended_segment[tap : tap + length] == segment).astype(jnp.float32)
        convolved = convolved + kernel[tap][None, :] * extended[tap : tap + length] * keep[:, None]
    act = jax.nn.silu(convolved)
    x_heads = act[:, :channels].reshape(length, head_count, -1)
    bc_local = act[:, channels:].astype(jnp.bfloat16)
    bc_all = lax.all_gather(bc_local, ("tp", "dp"), axis=1, tiled=True)
    state_width = bc_all.shape[1] // 2
    b_proj = bc_all[:, :state_width]
    c_proj = bc_all[:, state_width:]
    step_size = jax.nn.softplus(step_raw + step_bias[None, :])
    log_decay = -step_size * jnp.exp(decay_log_rate)[None, :]
    inner_out, local_state, enter_weight, carry_decay = span_parts(
        x_heads, b_proj, c_proj, step_size, log_decay, segment, previous
    )

    def compose(earlier, later):
        return (earlier[0] * later[0], later[0][:, None, None] * earlier[1] + later[1])

    carried = prefix(
        (carry_decay, local_state),
        "ctx",
        compose,
        (jnp.ones_like(carry_decay), jnp.zeros_like(local_state)),
    )
    entering = carried[1]
    entered = (
        jnp.einsum("tn,hdn->thd", c_proj.astype(jnp.float32), entering, precision=FULL_PRECISION)
        * enter_weight[:, :, None]
    )
    mixer_out = (inner_out + entered + head_skip_gain[None, :, None] * x_heads).reshape(
        length, channels
    )
    scale = lax.rsqrt(jnp.mean(mixer_out * mixer_out, axis=1, keepdims=True) + NORM_EPSILON)
    normalized_rows = (mixer_out * scale * output_norm_gain[None, :]).astype(jnp.bfloat16)
    term = jnp.dot(
        normalized_rows,
        lax.all_gather(output_weight, "ctx", axis=1, tiled=True),
        preferred_element_type=jnp.float32,
    )
    base = lax.psum_scatter(
        term.astype(jnp.bfloat16), ("tp", "dp"), scatter_dimension=1, tiled=True
    ).astype(jnp.float32)
    lowrank_out_part = select_rows(
        jnp.dot(normalized_rows, down_out, preferred_element_type=jnp.float32),
        adapter_picker_matrix,
    )
    rank_hidden_output = lax.psum(lowrank_out_part.astype(jnp.bfloat16), ("tp", "dp"))
    adapter_term = jnp.dot(
        masked_wide(rank_hidden_output, onehot_b), up_out, preferred_element_type=jnp.float32
    )
    return (base + adapter_term).astype(jnp.bfloat16)


def moved(block, shift, kind):
    side = lax.axis_size("ctx")
    if kind == "ctx":
        pairs = [(a, (a + shift) % side) for a in range(side)]
        return lax.ppermute(block, "ctx", pairs)
    if kind == "lane":
        pairs = [(a, (a + shift) % side) for a in range(side)]
        return lax.ppermute(block, ("tp", "dp"), pairs)
    if kind == "rows":
        pairs = [(a * side + b, b * side + (a + shift) % side) for a in range(side) for b in range(side)]
    else:
        pairs = [(a * side + b, ((b + shift) % side) * side + a) for a in range(side) for b in range(side)]
    return lax.ppermute(block, ("ctx", "tp", "dp"), pairs)


def transposed(block):
    return moved(block, 0, "rows")


def in_order(pieces, place):
    stacked = jnp.stack(pieces[::-1], axis=0)
    ordered = jnp.roll(stacked, place + 1, axis=0)
    return ordered.reshape((-1,) + pieces[0].shape[1:])


def block_rows(values, index, length):
    return lax.dynamic_slice_in_dim(values, index * length, length, 0)


def owned_rows(values, owned):
    return jnp.concatenate(
        [values * owned[:, i : i + 1].astype(values.dtype) for i in range(owned.shape[1])], axis=1
    )


def square_body(
    tokens,
    lengths,
    request_adapter_ids,
    adapter_store_slot,
    xchan_input_weight,
    bc_input_weight,
    step_input_weight,
    convolution_x_taps,
    convolution_bc_taps,
    step_bias,
    decay_log_rate,
    head_skip_gain,
    output_norm_gain,
    output_weight,
    adapter_down_input,
    adapter_up_xchan,
    adapter_up_bc,
    adapter_down_output,
    adapter_up_output,
):
    length = tokens.shape[0]
    side = lax.axis_size("ctx")
    stream = side * length
    taps = convolution_x_taps.shape[0]
    bank_entries = adapter_down_input.shape[0]
    rank_value = adapter_down_input.shape[2]
    head_count = step_bias.shape[0]
    channels = xchan_input_weight.shape[1]
    bc_width = bc_input_weight.shape[1]
    here = lax.axis_index("ctx")
    lane = lax.axis_index(("tp", "dp"))
    start_pos = here * length
    request_ends = jnp.cumsum(lengths, dtype=jnp.int32)
    every_position = jnp.arange(stream, dtype=jnp.int32)
    every_segment = segment_of(every_position, request_ends)
    slot_indices = adapter_store_slot[request_adapter_ids]
    request_count = lengths.shape[0]
    stream_onehot = every_segment[:, None] == jnp.arange(request_count, dtype=jnp.int32)[None, :]
    slot_of_position = jnp.sum(
        jnp.where(stream_onehot, slot_indices[None, :], 0), axis=1, dtype=jnp.int32
    )
    entry_ids = jnp.arange(bank_entries, dtype=jnp.int32)[None, :]
    owned_here = slot_of_position[:, None] == here * bank_entries + entry_ids
    owned_lane = slot_of_position[:, None] == lane * bank_entries + entry_ids
    positions = start_pos + jnp.arange(length, dtype=jnp.int32)
    segment = segment_of(positions, request_ends)
    previous = segment_of(jnp.reshape(start_pos - 1, (1,)), request_ends)[0]

    tokens_t = transposed(tokens)
    stream_rows = in_order(
        [tokens_t] + [moved(tokens_t, s, "lane") for s in range(1, side)], lane
    )
    down_in_t = transposed(adapter_down_input)
    up_out_t = transposed(adapter_up_output)
    down_part = jnp.einsum(
        "pf,efr->per", stream_rows, down_in_t, preferred_element_type=jnp.float32
    )
    down_pick = jnp.sum(
        down_part * owned_lane[:, :, None].astype(jnp.float32), axis=1
    )
    rank_hidden = sum(moved(down_pick, s, "rows") for s in range(side))
    hidden_wide = owned_rows(rank_hidden, owned_here).astype(jnp.bfloat16)
    xchan_part = jnp.dot(
        stream_rows, xchan_input_weight, preferred_element_type=jnp.float32
    ) + jnp.dot(
        hidden_wide,
        adapter_up_xchan.reshape(bank_entries * rank_value, -1),
        preferred_element_type=jnp.float32,
    )
    bc_part = jnp.dot(stream_rows, bc_input_weight, preferred_element_type=jnp.float32) + jnp.dot(
        hidden_wide,
        adapter_up_bc.reshape(bank_entries * rank_value, -1),
        preferred_element_type=jnp.float32,
    )
    step_part = jnp.dot(stream_rows, step_input_weight, preferred_element_type=jnp.float32)
    projected = jnp.concatenate([xchan_part, bc_part, step_part], axis=1)
    summed = block_rows(projected, here, length)
    for s in range(1, side):
        sent = block_rows(projected, (here + s) % side, length).astype(jnp.bfloat16)
        summed = summed + moved(sent, s, "ctx").astype(jnp.float32)
    values = summed[:, : channels + bc_width]
    step_raw = summed[:, channels + bc_width :]

    kernel = jnp.concatenate([convolution_x_taps, convolution_bc_taps], axis=1)
    tail_rows = passed_along(values[length - (taps - 1) :], "ctx", 1)
    extended = jnp.concatenate([tail_rows, values], axis=0)
    extended_segment = segment_of(
        start_pos - (taps - 1) + jnp.arange(length + taps - 1, dtype=jnp.int32), request_ends
    )
    convolved = jnp.zeros_like(values)
    for tap in range(taps):
        keep = (extended_segment[tap : tap + length] == segment).astype(jnp.float32)
        convolved = convolved + kernel[tap][None, :] * extended[tap : tap + length] * keep[:, None]
    act = jax.nn.silu(convolved)
    x_heads = act[:, :channels].reshape(length, head_count, -1)
    bc_local = act[:, channels:].astype(jnp.bfloat16)
    bc_pieces = [bc_local] + [moved(bc_local, s, "lane") for s in range(1, side)]
    bc_all = jnp.transpose(in_order([piece.T for piece in bc_pieces], lane))
    state_width = bc_all.shape[1] // 2
    b_proj = bc_all[:, :state_width]
    c_proj = bc_all[:, state_width:]
    step_size = jax.nn.softplus(step_raw + step_bias[None, :])
    log_decay = -step_size * jnp.exp(decay_log_rate)[None, :]
    inner_out, local_state, enter_weight, carry_decay = span_parts(
        x_heads, b_proj, c_proj, step_size, log_decay, segment, previous
    )

    decay_row = jnp.broadcast_to(carry_decay[:, None, None], (head_count, 1, local_state.shape[2]))
    state_and_decay = jnp.concatenate([decay_row, local_state], axis=1).astype(jnp.bfloat16)
    entering = jnp.zeros_like(local_state)
    for s in range(side - 1, 0, -1):
        pairs = [(a, a + s) for a in range(side - s)]
        both_in = lax.ppermute(state_and_decay, "ctx", pairs).astype(jnp.float32)
        entering = both_in[:, :1, :1] * entering + both_in[:, 1:]
    entered = (
        jnp.einsum("tn,hdn->thd", c_proj.astype(jnp.float32), entering, precision=FULL_PRECISION)
        * enter_weight[:, :, None]
    )
    mixer_out = (inner_out + entered + head_skip_gain[None, :, None] * x_heads).reshape(
        length, channels
    )
    scale = lax.rsqrt(jnp.mean(mixer_out * mixer_out, axis=1, keepdims=True) + NORM_EPSILON)
    normalized_rows = (mixer_out * scale * output_norm_gain[None, :]).astype(jnp.bfloat16)

    normed_stream = in_order(
        [normalized_rows] + [moved(normalized_rows, s, "ctx") for s in range(1, side)], here
    )
    out_down_part = jnp.einsum(
        "pc,ecr->per", normed_stream, adapter_down_output, preferred_element_type=jnp.float32
    )
    out_down_pick = jnp.sum(out_down_part * owned_here[:, :, None].astype(jnp.float32), axis=1)
    rank_hidden_output = transposed(
        out_down_pick + sum(moved(out_down_pick, s, "lane") for s in range(1, side))
    )
    base_part = jnp.dot(
        normed_stream, output_weight, preferred_element_type=jnp.float32
    ).astype(jnp.bfloat16).astype(jnp.float32)
    adapter_part = jnp.dot(
        owned_rows(rank_hidden_output, owned_lane).astype(jnp.bfloat16),
        up_out_t.reshape(bank_entries * rank_value, -1),
        preferred_element_type=jnp.float32,
    )
    out_part = base_part + adapter_part
    mixed_t = block_rows(out_part, lane, length)
    for s in range(1, side):
        sent = block_rows(out_part, (lane + s) % side, length).astype(jnp.bfloat16)
        mixed_t = mixed_t + moved(sent, s, "lane").astype(jnp.float32)
    return transposed(mixed_t.astype(jnp.bfloat16))


def solution(mesh):
    body = square_body if mesh.shape["ctx"] == mesh.shape["tp"] * mesh.shape["dp"] else general_body
    placed = (
        P(("groups", "ctx"), ("tp", "dp")),
        P("groups"),
        P("groups"),
        P(),
        P("ctx", ("tp", "dp")),
        P("ctx", ("tp", "dp")),
        P("ctx", ("tp", "dp")),
        P(None, ("tp", "dp")),
        P(None, ("tp", "dp")),
        P(("tp", "dp")),
        P(("tp", "dp")),
        P(("tp", "dp")),
        P(("tp", "dp")),
        P(("tp", "dp"), "ctx"),
        P("ctx", ("tp", "dp"), None),
        P("ctx", None, ("tp", "dp")),
        P("ctx", None, ("tp", "dp")),
        P("ctx", ("tp", "dp"), None),
        P("ctx", None, ("tp", "dp")),
    )
    return jax.shard_map(
        body,
        mesh=mesh,
        in_specs=placed,
        out_specs=P(("groups", "ctx"), ("tp", "dp")),
        check_vma=False,
    )
```

```python
import jax
import jax.numpy as jnp
from jax import lax
from jax.sharding import PartitionSpec as P

FULL_PRECISION = lax.Precision.HIGHEST
NORM_EPSILON = 1e-06


def from_root(block, axis, source):
    block = jnp.where(lax.axis_index(axis) == source, block, jnp.zeros_like(block))
    return lax.psum(block, axis)


def passed_along(shard, axis, by):
    size = lax.axis_size(axis)
    pairs = [(i, i + by) for i in range(size) if 0 <= i + by < size]
    return lax.ppermute(shard, axis, pairs)


def prefix(shard, axis, combine, identity):
    size, place = (lax.axis_size(axis), lax.axis_index(axis))
    everything = jax.tree.map(
        lambda part, kind: lax.all_gather(part.astype(kind), axis),
        shard,
        (jnp.bfloat16, jnp.bfloat16),
    )
    start = jax.tree.map(
        lambda part, zero: jnp.broadcast_to(jnp.asarray(zero, part.dtype), part.shape),
        shard,
        identity,
    )

    def lap(k, before):
        reached = k < place
        new = combine(
            before, jax.tree.map(lambda part, own: part[k].astype(own.dtype), everything, shard)
        )
        return jax.tree.map(lambda a, b: jnp.where(reached, a, b), new, before)

    return lax.fori_loop(0, size, lap, start)


def segment_of(positions, request_ends):
    inside = (positions[:, None] >= request_ends[None, :]).astype(jnp.int32)
    counted = jnp.sum(inside, axis=1, dtype=jnp.int32)
    return jnp.where(positions < 0, jnp.int32(-1), counted)


def span_parts(x_heads, b_proj, c_proj, step_size, log_decay, segment, previous):
    length = x_heads.shape[0]
    cumulative = jnp.cumsum(log_decay, axis=0)
    final_log = cumulative[length - 1]
    places = jnp.arange(length, dtype=jnp.int32)
    same_request = jnp.logical_and(
        segment[:, None] == segment[None, :], places[None, :] <= places[:, None]
    ).astype(jnp.float32)
    log_gap = cumulative.T[:, :, None] - cumulative.T[:, None, :]
    decay_table = jnp.exp(jnp.minimum(log_gap, 0.0)) * same_request[None]
    scores = lax.dot_general(
        c_proj, b_proj, (((1,), (1,)), ((), ())), preferred_element_type=jnp.float32
    )
    weights = scores[None] * decay_table * step_size.T[:, None, :]
    inner_out = jnp.einsum("hts,shd->thd", weights, x_heads, precision=FULL_PRECISION)
    at_end = (segment == segment[length - 1]).astype(jnp.float32)
    state_weight = jnp.exp(final_log[None, :] - cumulative) * at_end[:, None] * step_size
    local_state = jnp.einsum(
        "sh,shd,sn->hdn",
        state_weight,
        x_heads,
        b_proj.astype(jnp.float32),
        precision=FULL_PRECISION,
    )
    enter_weight = jnp.exp(cumulative) * (segment == previous).astype(jnp.float32)[:, None]
    carry_decay = jnp.exp(final_log) * (segment[length - 1] == previous).astype(jnp.float32)
    return (inner_out, local_state, enter_weight, carry_decay)


def select_rows(wide, adapter_picker_matrix):
    shaped = wide.reshape(wide.shape[0], adapter_picker_matrix.shape[1], -1)
    return jnp.sum(shaped * adapter_picker_matrix[:, :, None], axis=1)


def masked_wide(values, onehot_b):
    return (values[:, None, :] * onehot_b[:, :, None]).reshape(values.shape[0], -1)


def general_body(
    tokens,
    lengths,
    request_adapter_ids,
    adapter_store_slot,
    xchan_input_weight,
    bc_input_weight,
    step_input_weight,
    convolution_x_taps,
    convolution_bc_taps,
    step_bias,
    decay_log_rate,
    head_skip_gain,
    output_norm_gain,
    output_weight,
    adapter_down_input,
    adapter_up_xchan,
    adapter_up_bc,
    adapter_down_output,
    adapter_up_output,
):
    length = tokens.shape[0]
    request_list = lengths.shape[0]
    taps = convolution_x_taps.shape[0]
    bank_entries = adapter_down_input.shape[0]
    head_count = step_bias.shape[0]
    channels = xchan_input_weight.shape[1]
    start_pos = lax.axis_index("ctx") * length
    request_ends = jnp.cumsum(lengths, dtype=jnp.int32)
    positions = start_pos + jnp.arange(length, dtype=jnp.int32)
    segment = segment_of(positions, request_ends)
    previous = segment_of(jnp.reshape(start_pos - 1, (1,)), request_ends)[0]
    adapter_picker_matrix = (
        segment[:, None] == jnp.arange(request_list, dtype=jnp.int32)[None, :]
    ).astype(jnp.float32)
    onehot_b = adapter_picker_matrix.astype(jnp.bfloat16)
    slot_indices = adapter_store_slot[request_adapter_ids]
    initial_stacks = (
        jnp.zeros(
            (adapter_down_input.shape[1], request_list, adapter_down_input.shape[2]), jnp.bfloat16
        ),
        jnp.zeros((request_list,) + adapter_up_xchan.shape[1:], jnp.bfloat16),
        jnp.zeros((request_list,) + adapter_up_bc.shape[1:], jnp.bfloat16),
        jnp.zeros(
            (adapter_down_output.shape[1], request_list, adapter_down_output.shape[2]), jnp.bfloat16
        ),
        jnp.zeros((request_list,) + adapter_up_output.shape[1:], jnp.bfloat16),
    )
    stack_dims = (1, 0, 0, 1, 0)

    def fetch(request_item, current):
        slot = slot_indices[request_item]
        owner = slot // bank_entries
        within = slot % bank_entries
        a_in, b_x, b_bc, a_out, b_out = [
            lax.dynamic_index_in_dim(adapter_bank, within, 0, keepdims=False)
            for adapter_bank in (
                adapter_down_input,
                adapter_up_xchan,
                adapter_up_bc,
                adapter_down_output,
                adapter_up_output,
            )
        ]
        received = (
            from_root(a_in, "ctx", owner),
            from_root(b_x, "ctx", owner),
            from_root(b_bc, "ctx", owner),
            from_root(a_out, "ctx", owner),
            from_root(b_out, "ctx", owner),
        )
        return tuple(
            (
                lax.dynamic_update_index_in_dim(stack, panel, request_item, along)
                for stack, panel, along in zip(current, received, stack_dims)
            )
        )

    stacks = lax.fori_loop(0, request_list, fetch, initial_stacks)
    rank_value = adapter_down_input.shape[2]
    down_in = stacks[0].reshape(stacks[0].shape[0], request_list * rank_value)
    up_x = stacks[1].reshape(request_list * rank_value, -1)
    up_bc = stacks[2].reshape(request_list * rank_value, -1)
    down_out = stacks[3].reshape(stacks[3].shape[0], request_list * rank_value)
    up_out = stacks[4].reshape(request_list * rank_value, -1)
    lowrank_part = select_rows(
        jnp.dot(tokens, down_in, preferred_element_type=jnp.float32), adapter_picker_matrix
    )
    rank_hidden = lax.psum(lowrank_part.astype(jnp.bfloat16), ("tp", "dp"))
    lowrank_wide = masked_wide(rank_hidden, onehot_b)
    full_tokens = lax.all_gather(tokens, ("tp", "dp"), axis=1, tiled=True)
    pieces = (
        lax.all_gather(xchan_input_weight, "ctx", axis=0, tiled=True),
        lax.all_gather(bc_input_weight, "ctx", axis=0, tiled=True),
        lax.all_gather(step_input_weight, "ctx", axis=0, tiled=True),
    )
    xchan_values, bc_channel_values, step_raw = tuple(
        (jnp.dot(full_tokens, piece, preferred_element_type=jnp.float32) for piece in pieces)
    )
    xchan_values = xchan_values + jnp.dot(lowrank_wide, up_x, preferred_element_type=jnp.float32)
    bc_channel_values = bc_channel_values + jnp.dot(
        lowrank_wide, up_bc, preferred_element_type=jnp.float32
    )
    values = jnp.concatenate([xchan_values, bc_channel_values], axis=1)
    kernel = jnp.concatenate([convolution_x_taps, convolution_bc_taps], axis=1)
    tail_rows = passed_along(values[length - (taps - 1) :], "ctx", 1)
    extended = jnp.concatenate([tail_rows, values], axis=0)
    extended_segment = segment_of(
        start_pos - (taps - 1) + jnp.arange(length + taps - 1, dtype=jnp.int32), request_ends
    )
    convolved = jnp.zeros_like(values)
    for tap in range(taps):
        keep = (extended_segment[tap : tap + length] == segment).astype(jnp.float32)
        convolved = convolved + kernel[tap][None, :] * extended[tap : tap + length] * keep[:, None]
    act = jax.nn.silu(convolved)
    x_heads = act[:, :channels].reshape(length, head_count, -1)
    bc_local = act[:, channels:].astype(jnp.bfloat16)
    bc_all = lax.all_gather(bc_local, ("tp", "dp"), axis=1, tiled=True)
    state_width = bc_all.shape[1] // 2
    b_proj = bc_all[:, :state_width]
    c_proj = bc_all[:, state_width:]
    step_size = jax.nn.softplus(step_raw + step_bias[None, :])
    log_decay = -step_size * jnp.exp(decay_log_rate)[None, :]
    inner_out, local_state, enter_weight, carry_decay = span_parts(
        x_heads, b_proj, c_proj, step_size, log_decay, segment, previous
    )

    def compose(earlier, later):
        return (earlier[0] * later[0], later[0][:, None, None] * earlier[1] + later[1])

    carried = prefix(
        (carry_decay, local_state),
        "ctx",
        compose,
        (jnp.ones_like(carry_decay), jnp.zeros_like(local_state)),
    )
    entering = carried[1]
    entered = (
        jnp.einsum("tn,hdn->thd", c_proj.astype(jnp.float32), entering, precision=FULL_PRECISION)
        * enter_weight[:, :, None]
    )
    mixer_out = (inner_out + entered + head_skip_gain[None, :, None] * x_heads).reshape(
        length, channels
    )
    scale = lax.rsqrt(jnp.mean(mixer_out * mixer_out, axis=1, keepdims=True) + NORM_EPSILON)
    normalized_rows = (mixer_out * scale * output_norm_gain[None, :]).astype(jnp.bfloat16)
    term = jnp.dot(
        normalized_rows,
        lax.all_gather(output_weight, "ctx", axis=1, tiled=True),
        preferred_element_type=jnp.float32,
    )
    base = lax.psum_scatter(
        term.astype(jnp.bfloat16), ("tp", "dp"), scatter_dimension=1, tiled=True
    ).astype(jnp.float32)
    lowrank_out_part = select_rows(
        jnp.dot(normalized_rows, down_out, preferred_element_type=jnp.float32),
        adapter_picker_matrix,
    )
    rank_hidden_output = lax.psum(lowrank_out_part.astype(jnp.bfloat16), ("tp", "dp"))
    adapter_term = jnp.dot(
        masked_wide(rank_hidden_output, onehot_b), up_out, preferred_element_type=jnp.float32
    )
    return (base + adapter_term).astype(jnp.bfloat16)


def moved(block, shift, kind):
    side = lax.axis_size("ctx")
    if kind == "ctx":
        pairs = [(a, (a + shift) % side) for a in range(side)]
        return lax.ppermute(block, "ctx", pairs)
    if kind == "lane":
        pairs = [(a, (a + shift) % side) for a in range(side)]
        return lax.ppermute(block, ("tp", "dp"), pairs)
    if kind == "rows":
        pairs = [(a * side + b, b * side + (a + shift) % side) for a in range(side) for b in range(side)]
    else:
        pairs = [(a * side + b, ((b + shift) % side) * side + a) for a in range(side) for b in range(side)]
    return lax.ppermute(block, ("ctx", "tp", "dp"), pairs)


def transposed(block):
    return moved(block, 0, "rows")


def in_order(pieces, place):
    stacked = jnp.stack(pieces[::-1], axis=0)
    ordered = jnp.roll(stacked, place + 1, axis=0)
    return ordered.reshape((-1,) + pieces[0].shape[1:])


def block_rows(values, index, length):
    return lax.dynamic_slice_in_dim(values, index * length, length, 0)


def owned_rows(values, owned):
    return jnp.concatenate(
        [values * owned[:, i : i + 1].astype(values.dtype) for i in range(owned.shape[1])], axis=1
    )


def square_body(
    tokens,
    lengths,
    request_adapter_ids,
    adapter_store_slot,
    xchan_input_weight,
    bc_input_weight,
    step_input_weight,
    convolution_x_taps,
    convolution_bc_taps,
    step_bias,
    decay_log_rate,
    head_skip_gain,
    output_norm_gain,
    output_weight,
    adapter_down_input,
    adapter_up_xchan,
    adapter_up_bc,
    adapter_down_output,
    adapter_up_output,
):
    length = tokens.shape[0]
    side = lax.axis_size("ctx")
    stream = side * length
    taps = convolution_x_taps.shape[0]
    bank_entries = adapter_down_input.shape[0]
    rank_value = adapter_down_input.shape[2]
    head_count = step_bias.shape[0]
    channels = xchan_input_weight.shape[1]
    bc_width = bc_input_weight.shape[1]
    here = lax.axis_index("ctx")
    lane = lax.axis_index(("tp", "dp"))
    start_pos = here * length
    request_ends = jnp.cumsum(lengths, dtype=jnp.int32)
    every_position = jnp.arange(stream, dtype=jnp.int32)
    every_segment = segment_of(every_position, request_ends)
    slot_indices = adapter_store_slot[request_adapter_ids]
    request_count = lengths.shape[0]
    stream_onehot = every_segment[:, None] == jnp.arange(request_count, dtype=jnp.int32)[None, :]
    slot_of_position = jnp.sum(
        jnp.where(stream_onehot, slot_indices[None, :], 0), axis=1, dtype=jnp.int32
    )
    entry_ids = jnp.arange(bank_entries, dtype=jnp.int32)[None, :]
    owned_here = slot_of_position[:, None] == here * bank_entries + entry_ids
    owned_lane = slot_of_position[:, None] == lane * bank_entries + entry_ids
    positions = start_pos + jnp.arange(length, dtype=jnp.int32)
    segment = segment_of(positions, request_ends)
    previous = segment_of(jnp.reshape(start_pos - 1, (1,)), request_ends)[0]

    tokens_t = transposed(tokens)
    stream_rows = in_order(
        [tokens_t] + [moved(tokens_t, s, "lane") for s in range(1, side)], lane
    )
    both_t = transposed(
        jnp.concatenate(
            [
                adapter_down_input.reshape(bank_entries, -1),
                adapter_up_output.reshape(bank_entries, -1),
            ],
            axis=1,
        )
    )
    down_in_t = both_t[:, : adapter_down_input[0].size].reshape(adapter_down_input.shape)
    up_out_t = both_t[:, adapter_down_input[0].size :].reshape(adapter_up_output.shape)
    down_part = jnp.einsum(
        "pf,efr->per", stream_rows, down_in_t, preferred_element_type=jnp.float32
    )
    down_pick = jnp.sum(
        down_part * owned_lane[:, :, None].astype(jnp.float32), axis=1
    )
    rank_hidden = sum(moved(down_pick, s, "rows") for s in range(side))
    hidden_wide = owned_rows(rank_hidden, owned_here).astype(jnp.bfloat16)
    xchan_part = jnp.dot(
        stream_rows, xchan_input_weight, preferred_element_type=jnp.float32
    ) + jnp.dot(
        hidden_wide,
        adapter_up_xchan.reshape(bank_entries * rank_value, -1),
        preferred_element_type=jnp.float32,
    )
    bc_part = jnp.dot(stream_rows, bc_input_weight, preferred_element_type=jnp.float32) + jnp.dot(
        hidden_wide,
        adapter_up_bc.reshape(bank_entries * rank_value, -1),
        preferred_element_type=jnp.float32,
    )
    step_part = jnp.dot(stream_rows, step_input_weight, preferred_element_type=jnp.float32)
    projected = jnp.concatenate([xchan_part, bc_part, step_part], axis=1)
    summed = block_rows(projected, here, length)
    for s in range(1, side):
        sent = block_rows(projected, (here + s) % side, length).astype(jnp.bfloat16)
        summed = summed + moved(sent, s, "ctx").astype(jnp.float32)
    values = summed[:, : channels + bc_width]
    step_raw = summed[:, channels + bc_width :]

    kernel = jnp.concatenate([convolution_x_taps, convolution_bc_taps], axis=1)
    tail_rows = passed_along(values[length - (taps - 1) :], "ctx", 1)
    extended = jnp.concatenate([tail_rows, values], axis=0)
    extended_segment = segment_of(
        start_pos - (taps - 1) + jnp.arange(length + taps - 1, dtype=jnp.int32), request_ends
    )
    convolved = jnp.zeros_like(values)
    for tap in range(taps):
        keep = (extended_segment[tap : tap + length] == segment).astype(jnp.float32)
        convolved = convolved + kernel[tap][None, :] * extended[tap : tap + length] * keep[:, None]
    act = jax.nn.silu(convolved)
    x_heads = act[:, :channels].reshape(length, head_count, -1)
    bc_local = act[:, channels:].astype(jnp.bfloat16)
    bc_pieces = [bc_local] + [moved(bc_local, s, "lane") for s in range(1, side)]
    bc_all = jnp.transpose(in_order([piece.T for piece in bc_pieces], lane))
    state_width = bc_all.shape[1] // 2
    b_proj = bc_all[:, :state_width]
    c_proj = bc_all[:, state_width:]
    step_size = jax.nn.softplus(step_raw + step_bias[None, :])
    log_decay = -step_size * jnp.exp(decay_log_rate)[None, :]
    inner_out, local_state, enter_weight, carry_decay = span_parts(
        x_heads, b_proj, c_proj, step_size, log_decay, segment, previous
    )

    decay_row = jnp.broadcast_to(carry_decay[:, None, None], (head_count, 1, local_state.shape[2]))
    state_and_decay = jnp.concatenate([decay_row, local_state], axis=1).astype(jnp.bfloat16)
    entering = jnp.zeros_like(local_state)
    for s in range(side - 1, 0, -1):
        pairs = [(a, a + s) for a in range(side - s)]
        both_in = lax.ppermute(state_and_decay, "ctx", pairs).astype(jnp.float32)
        entering = both_in[:, :1, :1] * entering + both_in[:, 1:]
    entered = (
        jnp.einsum("tn,hdn->thd", c_proj.astype(jnp.float32), entering, precision=FULL_PRECISION)
        * enter_weight[:, :, None]
    )
    mixer_out = (inner_out + entered + head_skip_gain[None, :, None] * x_heads).reshape(
        length, channels
    )
    scale = lax.rsqrt(jnp.mean(mixer_out * mixer_out, axis=1, keepdims=True) + NORM_EPSILON)
    normalized_rows = (mixer_out * scale * output_norm_gain[None, :]).astype(jnp.bfloat16)

    normed_stream = in_order(
        [normalized_rows] + [moved(normalized_rows, s, "ctx") for s in range(1, side)], here
    )
    out_down_part = jnp.einsum(
        "pc,ecr->per", normed_stream, adapter_down_output, preferred_element_type=jnp.float32
    )
    out_down_pick = jnp.sum(out_down_part * owned_here[:, :, None].astype(jnp.float32), axis=1)
    rank_hidden_output = transposed(
        out_down_pick + sum(moved(out_down_pick, s, "lane") for s in range(1, side))
    )
    base_part = jnp.dot(
        normed_stream, output_weight, preferred_element_type=jnp.float32
    ).astype(jnp.bfloat16).astype(jnp.float32)
    adapter_part = jnp.dot(
        owned_rows(rank_hidden_output, owned_lane).astype(jnp.bfloat16),
        up_out_t.reshape(bank_entries * rank_value, -1),
        preferred_element_type=jnp.float32,
    )
    out_part = base_part + adapter_part
    mixed_t = block_rows(out_part, lane, length)
    for s in range(1, side):
        sent = block_rows(out_part, (lane + s) % side, length).astype(jnp.bfloat16)
        mixed_t = mixed_t + moved(sent, s, "lane").astype(jnp.float32)
    return transposed(mixed_t.astype(jnp.bfloat16))


def solution(mesh):
    body = square_body if mesh.shape["ctx"] == mesh.shape["tp"] * mesh.shape["dp"] else general_body
    placed = (
        P(("groups", "ctx"), ("tp", "dp")),
        P("groups"),
        P("groups"),
        P(),
        P("ctx", ("tp", "dp")),
        P("ctx", ("tp", "dp")),
        P("ctx", ("tp", "dp")),
        P(None, ("tp", "dp")),
        P(None, ("tp", "dp")),
        P(("tp", "dp")),
        P(("tp", "dp")),
        P(("tp", "dp")),
        P(("tp", "dp")),
        P(("tp", "dp"), "ctx"),
        P("ctx", ("tp", "dp"), None),
        P("ctx", None, ("tp", "dp")),
        P("ctx", None, ("tp", "dp")),
        P("ctx", ("tp", "dp"), None),
        P("ctx", None, ("tp", "dp")),
    )
    return jax.shard_map(
        body,
        mesh=mesh,
        in_specs=placed,
        out_specs=P(("groups", "ctx"), ("tp", "dp")),
        check_vma=False,
    )
```

```python
import jax
import jax.numpy as jnp
from jax import lax
from jax.sharding import PartitionSpec as P

FULL_PRECISION = lax.Precision.HIGHEST
NORM_EPSILON = 1e-06


def from_root(block, axis, source):
    block = jnp.where(lax.axis_index(axis) == source, block, jnp.zeros_like(block))
    return lax.psum(block, axis)


def passed_along(shard, axis, by):
    size = lax.axis_size(axis)
    pairs = [(i, i + by) for i in range(size) if 0 <= i + by < size]
    return lax.ppermute(shard, axis, pairs)


def prefix(shard, axis, combine, identity):
    size, place = (lax.axis_size(axis), lax.axis_index(axis))
    everything = jax.tree.map(
        lambda part, kind: lax.all_gather(part.astype(kind), axis),
        shard,
        (jnp.bfloat16, jnp.bfloat16),
    )
    start = jax.tree.map(
        lambda part, zero: jnp.broadcast_to(jnp.asarray(zero, part.dtype), part.shape),
        shard,
        identity,
    )

    def lap(k, before):
        reached = k < place
        new = combine(
            before, jax.tree.map(lambda part, own: part[k].astype(own.dtype), everything, shard)
        )
        return jax.tree.map(lambda a, b: jnp.where(reached, a, b), new, before)

    return lax.fori_loop(0, size, lap, start)


def segment_of(positions, request_ends):
    inside = (positions[:, None] >= request_ends[None, :]).astype(jnp.int32)
    counted = jnp.sum(inside, axis=1, dtype=jnp.int32)
    return jnp.where(positions < 0, jnp.int32(-1), counted)


def span_parts(x_heads, b_proj, c_proj, step_size, log_decay, segment, previous):
    length = x_heads.shape[0]
    cumulative = jnp.cumsum(log_decay, axis=0)
    final_log = cumulative[length - 1]
    places = jnp.arange(length, dtype=jnp.int32)
    same_request = jnp.logical_and(
        segment[:, None] == segment[None, :], places[None, :] <= places[:, None]
    ).astype(jnp.float32)
    log_gap = cumulative.T[:, :, None] - cumulative.T[:, None, :]
    decay_table = jnp.exp(jnp.minimum(log_gap, 0.0)) * same_request[None]
    scores = lax.dot_general(
        c_proj, b_proj, (((1,), (1,)), ((), ())), preferred_element_type=jnp.float32
    )
    weights = scores[None] * decay_table * step_size.T[:, None, :]
    inner_out = jnp.einsum("hts,shd->thd", weights, x_heads, precision=FULL_PRECISION)
    at_end = (segment == segment[length - 1]).astype(jnp.float32)
    state_weight = jnp.exp(final_log[None, :] - cumulative) * at_end[:, None] * step_size
    local_state = jnp.einsum(
        "sh,shd,sn->hdn",
        state_weight,
        x_heads,
        b_proj.astype(jnp.float32),
        precision=FULL_PRECISION,
    )
    enter_weight = jnp.exp(cumulative) * (segment == previous).astype(jnp.float32)[:, None]
    carry_decay = jnp.exp(final_log) * (segment[length - 1] == previous).astype(jnp.float32)
    return (inner_out, local_state, enter_weight, carry_decay)


def select_rows(wide, adapter_picker_matrix):
    shaped = wide.reshape(wide.shape[0], adapter_picker_matrix.shape[1], -1)
    return jnp.sum(shaped * adapter_picker_matrix[:, :, None], axis=1)


def masked_wide(values, onehot_b):
    return (values[:, None, :] * onehot_b[:, :, None]).reshape(values.shape[0], -1)


def general_body(
    tokens,
    lengths,
    request_adapter_ids,
    adapter_store_slot,
    xchan_input_weight,
    bc_input_weight,
    step_input_weight,
    convolution_x_taps,
    convolution_bc_taps,
    step_bias,
    decay_log_rate,
    head_skip_gain,
    output_norm_gain,
    output_weight,
    adapter_down_input,
    adapter_up_xchan,
    adapter_up_bc,
    adapter_down_output,
    adapter_up_output,
):
    length = tokens.shape[0]
    request_list = lengths.shape[0]
    taps = convolution_x_taps.shape[0]
    bank_entries = adapter_down_input.shape[0]
    head_count = step_bias.shape[0]
    channels = xchan_input_weight.shape[1]
    start_pos = lax.axis_index("ctx") * length
    request_ends = jnp.cumsum(lengths, dtype=jnp.int32)
    positions = start_pos + jnp.arange(length, dtype=jnp.int32)
    segment = segment_of(positions, request_ends)
    previous = segment_of(jnp.reshape(start_pos - 1, (1,)), request_ends)[0]
    adapter_picker_matrix = (
        segment[:, None] == jnp.arange(request_list, dtype=jnp.int32)[None, :]
    ).astype(jnp.float32)
    onehot_b = adapter_picker_matrix.astype(jnp.bfloat16)
    slot_indices = adapter_store_slot[request_adapter_ids]
    initial_stacks = (
        jnp.zeros(
            (adapter_down_input.shape[1], request_list, adapter_down_input.shape[2]), jnp.bfloat16
        ),
        jnp.zeros((request_list,) + adapter_up_xchan.shape[1:], jnp.bfloat16),
        jnp.zeros((request_list,) + adapter_up_bc.shape[1:], jnp.bfloat16),
        jnp.zeros(
            (adapter_down_output.shape[1], request_list, adapter_down_output.shape[2]), jnp.bfloat16
        ),
        jnp.zeros((request_list,) + adapter_up_output.shape[1:], jnp.bfloat16),
    )
    stack_dims = (1, 0, 0, 1, 0)

    def fetch(request_item, current):
        slot = slot_indices[request_item]
        owner = slot // bank_entries
        within = slot % bank_entries
        a_in, b_x, b_bc, a_out, b_out = [
            lax.dynamic_index_in_dim(adapter_bank, within, 0, keepdims=False)
            for adapter_bank in (
                adapter_down_input,
                adapter_up_xchan,
                adapter_up_bc,
                adapter_down_output,
                adapter_up_output,
            )
        ]
        received = (
            from_root(a_in, "ctx", owner),
            from_root(b_x, "ctx", owner),
            from_root(b_bc, "ctx", owner),
            from_root(a_out, "ctx", owner),
            from_root(b_out, "ctx", owner),
        )
        return tuple(
            (
                lax.dynamic_update_index_in_dim(stack, panel, request_item, along)
                for stack, panel, along in zip(current, received, stack_dims)
            )
        )

    stacks = lax.fori_loop(0, request_list, fetch, initial_stacks)
    rank_value = adapter_down_input.shape[2]
    down_in = stacks[0].reshape(stacks[0].shape[0], request_list * rank_value)
    up_x = stacks[1].reshape(request_list * rank_value, -1)
    up_bc = stacks[2].reshape(request_list * rank_value, -1)
    down_out = stacks[3].reshape(stacks[3].shape[0], request_list * rank_value)
    up_out = stacks[4].reshape(request_list * rank_value, -1)
    lowrank_part = select_rows(
        jnp.dot(tokens, down_in, preferred_element_type=jnp.float32), adapter_picker_matrix
    )
    rank_hidden = lax.psum(lowrank_part.astype(jnp.bfloat16), ("tp", "dp"))
    lowrank_wide = masked_wide(rank_hidden, onehot_b)
    full_tokens = lax.all_gather(tokens, ("tp", "dp"), axis=1, tiled=True)
    pieces = (
        lax.all_gather(xchan_input_weight, "ctx", axis=0, tiled=True),
        lax.all_gather(bc_input_weight, "ctx", axis=0, tiled=True),
        lax.all_gather(step_input_weight, "ctx", axis=0, tiled=True),
    )
    xchan_values, bc_channel_values, step_raw = tuple(
        (jnp.dot(full_tokens, piece, preferred_element_type=jnp.float32) for piece in pieces)
    )
    xchan_values = xchan_values + jnp.dot(lowrank_wide, up_x, preferred_element_type=jnp.float32)
    bc_channel_values = bc_channel_values + jnp.dot(
        lowrank_wide, up_bc, preferred_element_type=jnp.float32
    )
    values = jnp.concatenate([xchan_values, bc_channel_values], axis=1)
    kernel = jnp.concatenate([convolution_x_taps, convolution_bc_taps], axis=1)
    tail_rows = passed_along(values[length - (taps - 1) :], "ctx", 1)
    extended = jnp.concatenate([tail_rows, values], axis=0)
    extended_segment = segment_of(
        start_pos - (taps - 1) + jnp.arange(length + taps - 1, dtype=jnp.int32), request_ends
    )
    convolved = jnp.zeros_like(values)
    for tap in range(taps):
        keep = (extended_segment[tap : tap + length] == segment).astype(jnp.float32)
        convolved = convolved + kernel[tap][None, :] * extended[tap : tap + length] * keep[:, None]
    act = jax.nn.silu(convolved)
    x_heads = act[:, :channels].reshape(length, head_count, -1)
    bc_local = act[:, channels:].astype(jnp.bfloat16)
    bc_all = lax.all_gather(bc_local, ("tp", "dp"), axis=1, tiled=True)
    state_width = bc_all.shape[1] // 2
    b_proj = bc_all[:, :state_width]
    c_proj = bc_all[:, state_width:]
    step_size = jax.nn.softplus(step_raw + step_bias[None, :])
    log_decay = -step_size * jnp.exp(decay_log_rate)[None, :]
    inner_out, local_state, enter_weight, carry_decay = span_parts(
        x_heads, b_proj, c_proj, step_size, log_decay, segment, previous
    )

    def compose(earlier, later):
        return (earlier[0] * later[0], later[0][:, None, None] * earlier[1] + later[1])

    carried = prefix(
        (carry_decay, local_state),
        "ctx",
        compose,
        (jnp.ones_like(carry_decay), jnp.zeros_like(local_state)),
    )
    entering = carried[1]
    entered = (
        jnp.einsum("tn,hdn->thd", c_proj.astype(jnp.float32), entering, precision=FULL_PRECISION)
        * enter_weight[:, :, None]
    )
    mixer_out = (inner_out + entered + head_skip_gain[None, :, None] * x_heads).reshape(
        length, channels
    )
    scale = lax.rsqrt(jnp.mean(mixer_out * mixer_out, axis=1, keepdims=True) + NORM_EPSILON)
    normalized_rows = (mixer_out * scale * output_norm_gain[None, :]).astype(jnp.bfloat16)
    term = jnp.dot(
        normalized_rows,
        lax.all_gather(output_weight, "ctx", axis=1, tiled=True),
        preferred_element_type=jnp.float32,
    )
    base = lax.psum_scatter(
        term.astype(jnp.bfloat16), ("tp", "dp"), scatter_dimension=1, tiled=True
    ).astype(jnp.float32)
    lowrank_out_part = select_rows(
        jnp.dot(normalized_rows, down_out, preferred_element_type=jnp.float32),
        adapter_picker_matrix,
    )
    rank_hidden_output = lax.psum(lowrank_out_part.astype(jnp.bfloat16), ("tp", "dp"))
    adapter_term = jnp.dot(
        masked_wide(rank_hidden_output, onehot_b), up_out, preferred_element_type=jnp.float32
    )
    return (base + adapter_term).astype(jnp.bfloat16)


def moved(block, shift, kind):
    side = lax.axis_size("ctx")
    if kind == "ctx":
        pairs = [(a, (a + shift) % side) for a in range(side)]
        return lax.ppermute(block, "ctx", pairs)
    if kind == "lane":
        pairs = [(a, (a + shift) % side) for a in range(side)]
        return lax.ppermute(block, ("tp", "dp"), pairs)
    if kind == "rows":
        pairs = [(a * side + b, b * side + (a + shift) % side) for a in range(side) for b in range(side)]
    else:
        pairs = [(a * side + b, ((b + shift) % side) * side + a) for a in range(side) for b in range(side)]
    return lax.ppermute(block, ("ctx", "tp", "dp"), pairs)


def transposed(block):
    return moved(block, 0, "rows")


def in_order(pieces, place):
    stacked = jnp.stack(pieces[::-1], axis=0)
    ordered = jnp.roll(stacked, place + 1, axis=0)
    return ordered.reshape((-1,) + pieces[0].shape[1:])


def block_rows(values, index, length):
    return lax.dynamic_slice_in_dim(values, index * length, length, 0)


def owned_rows(values, owned):
    return jnp.concatenate(
        [values * owned[:, i : i + 1].astype(values.dtype) for i in range(owned.shape[1])], axis=1
    )


def square_body(
    tokens,
    lengths,
    request_adapter_ids,
    adapter_store_slot,
    xchan_input_weight,
    bc_input_weight,
    step_input_weight,
    convolution_x_taps,
    convolution_bc_taps,
    step_bias,
    decay_log_rate,
    head_skip_gain,
    output_norm_gain,
    output_weight,
    adapter_down_input,
    adapter_up_xchan,
    adapter_up_bc,
    adapter_down_output,
    adapter_up_output,
):
    length = tokens.shape[0]
    side = lax.axis_size("ctx")
    stream = side * length
    taps = convolution_x_taps.shape[0]
    bank_entries = adapter_down_input.shape[0]
    rank_value = adapter_down_input.shape[2]
    head_count = step_bias.shape[0]
    channels = xchan_input_weight.shape[1]
    bc_width = bc_input_weight.shape[1]
    here = lax.axis_index("ctx")
    lane = lax.axis_index(("tp", "dp"))
    start_pos = here * length
    request_ends = jnp.cumsum(lengths, dtype=jnp.int32)
    every_position = jnp.arange(stream, dtype=jnp.int32)
    every_segment = segment_of(every_position, request_ends)
    slot_indices = adapter_store_slot[request_adapter_ids]
    request_count = lengths.shape[0]
    stream_onehot = every_segment[:, None] == jnp.arange(request_count, dtype=jnp.int32)[None, :]
    slot_of_position = jnp.sum(
        jnp.where(stream_onehot, slot_indices[None, :], 0), axis=1, dtype=jnp.int32
    )
    entry_ids = jnp.arange(bank_entries, dtype=jnp.int32)[None, :]
    owned_here = slot_of_position[:, None] == here * bank_entries + entry_ids
    owned_lane = slot_of_position[:, None] == lane * bank_entries + entry_ids
    positions = start_pos + jnp.arange(length, dtype=jnp.int32)
    segment = segment_of(positions, request_ends)
    previous = segment_of(jnp.reshape(start_pos - 1, (1,)), request_ends)[0]

    tokens_t = transposed(tokens)
    stream_rows = in_order(
        [tokens_t] + [moved(tokens_t, s, "lane") for s in range(1, side)], lane
    )
    local_owned = lax.dynamic_slice_in_dim(slot_of_position, start_pos, length, 0)
    down_pick = jnp.zeros((length, rank_value), jnp.float32)
    for s in range(side):
        piece = adapter_down_input if s == 0 else moved(adapter_down_input, s, "ctx")
        first = ((here - s) % side) * bank_entries
        every = jnp.einsum("pf,efr->per", tokens, piece, preferred_element_type=jnp.float32)
        chosen = local_owned[:, None] == first + jnp.arange(bank_entries, dtype=jnp.int32)[None, :]
        down_pick = down_pick + jnp.sum(every * chosen[:, :, None].astype(jnp.float32), axis=1)
    rank_local = (
        down_pick + sum(moved(down_pick, s, "lane") for s in range(1, side))
    ).astype(jnp.bfloat16)
    rank_hidden = in_order(
        [rank_local] + [moved(rank_local, s, "ctx") for s in range(1, side)], here
    )
    up_out_t = transposed(adapter_up_output)
    hidden_wide = owned_rows(rank_hidden, owned_here)
    xchan_part = jnp.dot(
        stream_rows, xchan_input_weight, preferred_element_type=jnp.float32
    ) + jnp.dot(
        hidden_wide,
        adapter_up_xchan.reshape(bank_entries * rank_value, -1),
        preferred_element_type=jnp.float32,
    )
    bc_part = jnp.dot(stream_rows, bc_input_weight, preferred_element_type=jnp.float32) + jnp.dot(
        hidden_wide,
        adapter_up_bc.reshape(bank_entries * rank_value, -1),
        preferred_element_type=jnp.float32,
    )
    step_part = jnp.dot(stream_rows, step_input_weight, preferred_element_type=jnp.float32)
    projected = jnp.concatenate([xchan_part, bc_part, step_part], axis=1)
    summed = block_rows(projected, here, length)
    for s in range(1, side):
        sent = block_rows(projected, (here + s) % side, length).astype(jnp.bfloat16)
        summed = summed + moved(sent, s, "ctx").astype(jnp.float32)
    values = summed[:, : channels + bc_width]
    step_raw = summed[:, channels + bc_width :]

    kernel = jnp.concatenate([convolution_x_taps, convolution_bc_taps], axis=1)
    tail_rows = passed_along(values[length - (taps - 1) :], "ctx", 1)
    extended = jnp.concatenate([tail_rows, values], axis=0)
    extended_segment = segment_of(
        start_pos - (taps - 1) + jnp.arange(length + taps - 1, dtype=jnp.int32), request_ends
    )
    convolved = jnp.zeros_like(values)
    for tap in range(taps):
        keep = (extended_segment[tap : tap + length] == segment).astype(jnp.float32)
        convolved = convolved + kernel[tap][None, :] * extended[tap : tap + length] * keep[:, None]
    act = jax.nn.silu(convolved)
    x_heads = act[:, :channels].reshape(length, head_count, -1)
    bc_local = act[:, channels:].astype(jnp.bfloat16)
    bc_pieces = [bc_local] + [moved(bc_local, s, "lane") for s in range(1, side)]
    bc_all = jnp.transpose(in_order([piece.T for piece in bc_pieces], lane))
    state_width = bc_all.shape[1] // 2
    b_proj = bc_all[:, :state_width]
    c_proj = bc_all[:, state_width:]
    step_size = jax.nn.softplus(step_raw + step_bias[None, :])
    log_decay = -step_size * jnp.exp(decay_log_rate)[None, :]
    inner_out, local_state, enter_weight, carry_decay = span_parts(
        x_heads, b_proj, c_proj, step_size, log_decay, segment, previous
    )

    decay_row = jnp.broadcast_to(carry_decay[:, None, None], (head_count, 1, local_state.shape[2]))
    state_and_decay = jnp.concatenate([decay_row, local_state], axis=1).astype(jnp.bfloat16)
    entering = jnp.zeros_like(local_state)
    for s in range(side - 1, 0, -1):
        pairs = [(a, a + s) for a in range(side - s)]
        both_in = lax.ppermute(state_and_decay, "ctx", pairs).astype(jnp.float32)
        entering = both_in[:, :1, :1] * entering + both_in[:, 1:]
    entered = (
        jnp.einsum("tn,hdn->thd", c_proj.astype(jnp.float32), entering, precision=FULL_PRECISION)
        * enter_weight[:, :, None]
    )
    mixer_out = (inner_out + entered + head_skip_gain[None, :, None] * x_heads).reshape(
        length, channels
    )
    scale = lax.rsqrt(jnp.mean(mixer_out * mixer_out, axis=1, keepdims=True) + NORM_EPSILON)
    normalized_rows = (mixer_out * scale * output_norm_gain[None, :]).astype(jnp.bfloat16)

    normed_stream = in_order(
        [normalized_rows] + [moved(normalized_rows, s, "ctx") for s in range(1, side)], here
    )
    out_down_part = jnp.einsum(
        "pc,ecr->per", normed_stream, adapter_down_output, preferred_element_type=jnp.float32
    )
    out_down_pick = jnp.sum(out_down_part * owned_here[:, :, None].astype(jnp.float32), axis=1)
    rank_hidden_output = transposed(
        out_down_pick + sum(moved(out_down_pick, s, "lane") for s in range(1, side))
    )
    base_part = jnp.dot(
        normed_stream, output_weight, preferred_element_type=jnp.float32
    ).astype(jnp.bfloat16).astype(jnp.float32)
    adapter_part = jnp.dot(
        owned_rows(rank_hidden_output, owned_lane).astype(jnp.bfloat16),
        up_out_t.reshape(bank_entries * rank_value, -1),
        preferred_element_type=jnp.float32,
    )
    out_part = base_part + adapter_part
    mixed_t = block_rows(out_part, lane, length)
    for s in range(1, side):
        sent = block_rows(out_part, (lane + s) % side, length).astype(jnp.bfloat16)
        mixed_t = mixed_t + moved(sent, s, "lane").astype(jnp.float32)
    return transposed(mixed_t.astype(jnp.bfloat16))


def solution(mesh):
    body = square_body if mesh.shape["ctx"] == mesh.shape["tp"] * mesh.shape["dp"] else general_body
    placed = (
        P(("groups", "ctx"), ("tp", "dp")),
        P("groups"),
        P("groups"),
        P(),
        P("ctx", ("tp", "dp")),
        P("ctx", ("tp", "dp")),
        P("ctx", ("tp", "dp")),
        P(None, ("tp", "dp")),
        P(None, ("tp", "dp")),
        P(("tp", "dp")),
        P(("tp", "dp")),
        P(("tp", "dp")),
        P(("tp", "dp")),
        P(("tp", "dp"), "ctx"),
        P("ctx", ("tp", "dp"), None),
        P("ctx", None, ("tp", "dp")),
        P("ctx", None, ("tp", "dp")),
        P("ctx", ("tp", "dp"), None),
        P("ctx", None, ("tp", "dp")),
    )
    return jax.shard_map(
        body,
        mesh=mesh,
        in_specs=placed,
        out_specs=P(("groups", "ctx"), ("tp", "dp")),
        check_vma=False,
    )
```

```python
import jax
import jax.numpy as jnp
from jax import lax
from jax.sharding import PartitionSpec as P

FULL_PRECISION = lax.Precision.HIGHEST
NORM_EPSILON = 1e-06


def from_root(block, axis, source):
    block = jnp.where(lax.axis_index(axis) == source, block, jnp.zeros_like(block))
    return lax.psum(block, axis)


def passed_along(shard, axis, by):
    size = lax.axis_size(axis)
    pairs = [(i, i + by) for i in range(size) if 0 <= i + by < size]
    return lax.ppermute(shard, axis, pairs)


def prefix(shard, axis, combine, identity):
    size, place = (lax.axis_size(axis), lax.axis_index(axis))
    everything = jax.tree.map(
        lambda part, kind: lax.all_gather(part.astype(kind), axis),
        shard,
        (jnp.bfloat16, jnp.bfloat16),
    )
    start = jax.tree.map(
        lambda part, zero: jnp.broadcast_to(jnp.asarray(zero, part.dtype), part.shape),
        shard,
        identity,
    )

    def lap(k, before):
        reached = k < place
        new = combine(
            before, jax.tree.map(lambda part, own: part[k].astype(own.dtype), everything, shard)
        )
        return jax.tree.map(lambda a, b: jnp.where(reached, a, b), new, before)

    return lax.fori_loop(0, size, lap, start)


def segment_of(positions, request_ends):
    inside = (positions[:, None] >= request_ends[None, :]).astype(jnp.int32)
    counted = jnp.sum(inside, axis=1, dtype=jnp.int32)
    return jnp.where(positions < 0, jnp.int32(-1), counted)


def span_parts(x_heads, b_proj, c_proj, step_size, log_decay, segment, previous):
    length = x_heads.shape[0]
    cumulative = jnp.cumsum(log_decay, axis=0)
    final_log = cumulative[length - 1]
    places = jnp.arange(length, dtype=jnp.int32)
    same_request = jnp.logical_and(
        segment[:, None] == segment[None, :], places[None, :] <= places[:, None]
    ).astype(jnp.float32)
    log_gap = cumulative.T[:, :, None] - cumulative.T[:, None, :]
    decay_table = jnp.exp(jnp.minimum(log_gap, 0.0)) * same_request[None]
    scores = lax.dot_general(
        c_proj, b_proj, (((1,), (1,)), ((), ())), preferred_element_type=jnp.float32
    )
    weights = scores[None] * decay_table * step_size.T[:, None, :]
    inner_out = jnp.einsum("hts,shd->thd", weights, x_heads, precision=FULL_PRECISION)
    at_end = (segment == segment[length - 1]).astype(jnp.float32)
    state_weight = jnp.exp(final_log[None, :] - cumulative) * at_end[:, None] * step_size
    local_state = jnp.einsum(
        "sh,shd,sn->hdn",
        state_weight,
        x_heads,
        b_proj.astype(jnp.float32),
        precision=FULL_PRECISION,
    )
    enter_weight = jnp.exp(cumulative) * (segment == previous).astype(jnp.float32)[:, None]
    carry_decay = jnp.exp(final_log) * (segment[length - 1] == previous).astype(jnp.float32)
    return (inner_out, local_state, enter_weight, carry_decay)


def select_rows(wide, adapter_picker_matrix):
    shaped = wide.reshape(wide.shape[0], adapter_picker_matrix.shape[1], -1)
    return jnp.sum(shaped * adapter_picker_matrix[:, :, None], axis=1)


def masked_wide(values, onehot_b):
    return (values[:, None, :] * onehot_b[:, :, None]).reshape(values.shape[0], -1)


def general_body(
    tokens,
    lengths,
    request_adapter_ids,
    adapter_store_slot,
    xchan_input_weight,
    bc_input_weight,
    step_input_weight,
    convolution_x_taps,
    convolution_bc_taps,
    step_bias,
    decay_log_rate,
    head_skip_gain,
    output_norm_gain,
    output_weight,
    adapter_down_input,
    adapter_up_xchan,
    adapter_up_bc,
    adapter_down_output,
    adapter_up_output,
):
    length = tokens.shape[0]
    request_list = lengths.shape[0]
    taps = convolution_x_taps.shape[0]
    bank_entries = adapter_down_input.shape[0]
    head_count = step_bias.shape[0]
    channels = xchan_input_weight.shape[1]
    start_pos = lax.axis_index("ctx") * length
    request_ends = jnp.cumsum(lengths, dtype=jnp.int32)
    positions = start_pos + jnp.arange(length, dtype=jnp.int32)
    segment = segment_of(positions, request_ends)
    previous = segment_of(jnp.reshape(start_pos - 1, (1,)), request_ends)[0]
    adapter_picker_matrix = (
        segment[:, None] == jnp.arange(request_list, dtype=jnp.int32)[None, :]
    ).astype(jnp.float32)
    onehot_b = adapter_picker_matrix.astype(jnp.bfloat16)
    slot_indices = adapter_store_slot[request_adapter_ids]
    initial_stacks = (
        jnp.zeros(
            (adapter_down_input.shape[1], request_list, adapter_down_input.shape[2]), jnp.bfloat16
        ),
        jnp.zeros((request_list,) + adapter_up_xchan.shape[1:], jnp.bfloat16),
        jnp.zeros((request_list,) + adapter_up_bc.shape[1:], jnp.bfloat16),
        jnp.zeros(
            (adapter_down_output.shape[1], request_list, adapter_down_output.shape[2]), jnp.bfloat16
        ),
        jnp.zeros((request_list,) + adapter_up_output.shape[1:], jnp.bfloat16),
    )
    stack_dims = (1, 0, 0, 1, 0)

    def fetch(request_item, current):
        slot = slot_indices[request_item]
        owner = slot // bank_entries
        within = slot % bank_entries
        a_in, b_x, b_bc, a_out, b_out = [
            lax.dynamic_index_in_dim(adapter_bank, within, 0, keepdims=False)
            for adapter_bank in (
                adapter_down_input,
                adapter_up_xchan,
                adapter_up_bc,
                adapter_down_output,
                adapter_up_output,
            )
        ]
        received = (
            from_root(a_in, "ctx", owner),
            from_root(b_x, "ctx", owner),
            from_root(b_bc, "ctx", owner),
            from_root(a_out, "ctx", owner),
            from_root(b_out, "ctx", owner),
        )
        return tuple(
            (
                lax.dynamic_update_index_in_dim(stack, panel, request_item, along)
                for stack, panel, along in zip(current, received, stack_dims)
            )
        )

    stacks = lax.fori_loop(0, request_list, fetch, initial_stacks)
    rank_value = adapter_down_input.shape[2]
    down_in = stacks[0].reshape(stacks[0].shape[0], request_list * rank_value)
    up_x = stacks[1].reshape(request_list * rank_value, -1)
    up_bc = stacks[2].reshape(request_list * rank_value, -1)
    down_out = stacks[3].reshape(stacks[3].shape[0], request_list * rank_value)
    up_out = stacks[4].reshape(request_list * rank_value, -1)
    lowrank_part = select_rows(
        jnp.dot(tokens, down_in, preferred_element_type=jnp.float32), adapter_picker_matrix
    )
    rank_hidden = lax.psum(lowrank_part.astype(jnp.bfloat16), ("tp", "dp"))
    lowrank_wide = masked_wide(rank_hidden, onehot_b)
    full_tokens = lax.all_gather(tokens, ("tp", "dp"), axis=1, tiled=True)
    pieces = (
        lax.all_gather(xchan_input_weight, "ctx", axis=0, tiled=True),
        lax.all_gather(bc_input_weight, "ctx", axis=0, tiled=True),
        lax.all_gather(step_input_weight, "ctx", axis=0, tiled=True),
    )
    xchan_values, bc_channel_values, step_raw = tuple(
        (jnp.dot(full_tokens, piece, preferred_element_type=jnp.float32) for piece in pieces)
    )
    xchan_values = xchan_values + jnp.dot(lowrank_wide, up_x, preferred_element_type=jnp.float32)
    bc_channel_values = bc_channel_values + jnp.dot(
        lowrank_wide, up_bc, preferred_element_type=jnp.float32
    )
    values = jnp.concatenate([xchan_values, bc_channel_values], axis=1)
    kernel = jnp.concatenate([convolution_x_taps, convolution_bc_taps], axis=1)
    tail_rows = passed_along(values[length - (taps - 1) :], "ctx", 1)
    extended = jnp.concatenate([tail_rows, values], axis=0)
    extended_segment = segment_of(
        start_pos - (taps - 1) + jnp.arange(length + taps - 1, dtype=jnp.int32), request_ends
    )
    convolved = jnp.zeros_like(values)
    for tap in range(taps):
        keep = (extended_segment[tap : tap + length] == segment).astype(jnp.float32)
        convolved = convolved + kernel[tap][None, :] * extended[tap : tap + length] * keep[:, None]
    act = jax.nn.silu(convolved)
    x_heads = act[:, :channels].reshape(length, head_count, -1)
    bc_local = act[:, channels:].astype(jnp.bfloat16)
    bc_all = lax.all_gather(bc_local, ("tp", "dp"), axis=1, tiled=True)
    state_width = bc_all.shape[1] // 2
    b_proj = bc_all[:, :state_width]
    c_proj = bc_all[:, state_width:]
    step_size = jax.nn.softplus(step_raw + step_bias[None, :])
    log_decay = -step_size * jnp.exp(decay_log_rate)[None, :]
    inner_out, local_state, enter_weight, carry_decay = span_parts(
        x_heads, b_proj, c_proj, step_size, log_decay, segment, previous
    )

    def compose(earlier, later):
        return (earlier[0] * later[0], later[0][:, None, None] * earlier[1] + later[1])

    carried = prefix(
        (carry_decay, local_state),
        "ctx",
        compose,
        (jnp.ones_like(carry_decay), jnp.zeros_like(local_state)),
    )
    entering = carried[1]
    entered = (
        jnp.einsum("tn,hdn->thd", c_proj.astype(jnp.float32), entering, precision=FULL_PRECISION)
        * enter_weight[:, :, None]
    )
    mixer_out = (inner_out + entered + head_skip_gain[None, :, None] * x_heads).reshape(
        length, channels
    )
    scale = lax.rsqrt(jnp.mean(mixer_out * mixer_out, axis=1, keepdims=True) + NORM_EPSILON)
    normalized_rows = (mixer_out * scale * output_norm_gain[None, :]).astype(jnp.bfloat16)
    term = jnp.dot(
        normalized_rows,
        lax.all_gather(output_weight, "ctx", axis=1, tiled=True),
        preferred_element_type=jnp.float32,
    )
    base = lax.psum_scatter(
        term.astype(jnp.bfloat16), ("tp", "dp"), scatter_dimension=1, tiled=True
    ).astype(jnp.float32)
    lowrank_out_part = select_rows(
        jnp.dot(normalized_rows, down_out, preferred_element_type=jnp.float32),
        adapter_picker_matrix,
    )
    rank_hidden_output = lax.psum(lowrank_out_part.astype(jnp.bfloat16), ("tp", "dp"))
    adapter_term = jnp.dot(
        masked_wide(rank_hidden_output, onehot_b), up_out, preferred_element_type=jnp.float32
    )
    return (base + adapter_term).astype(jnp.bfloat16)


def moved(block, shift, kind):
    side = lax.axis_size("ctx")
    if kind == "ctx":
        pairs = [(a, (a + shift) % side) for a in range(side)]
        return lax.ppermute(block, "ctx", pairs)
    if kind == "lane":
        pairs = [(a, (a + shift) % side) for a in range(side)]
        return lax.ppermute(block, ("tp", "dp"), pairs)
    if kind == "rows":
        pairs = [(a * side + b, b * side + (a + shift) % side) for a in range(side) for b in range(side)]
    else:
        pairs = [(a * side + b, ((b + shift) % side) * side + a) for a in range(side) for b in range(side)]
    return lax.ppermute(block, ("ctx", "tp", "dp"), pairs)


def transposed(block):
    return moved(block, 0, "rows")


def in_order(pieces, place):
    stacked = jnp.stack(pieces[::-1], axis=0)
    ordered = jnp.roll(stacked, place + 1, axis=0)
    return ordered.reshape((-1,) + pieces[0].shape[1:])


def block_rows(values, index, length):
    return lax.dynamic_slice_in_dim(values, index * length, length, 0)


def owned_rows(values, owned):
    return jnp.concatenate(
        [values * owned[:, i : i + 1].astype(values.dtype) for i in range(owned.shape[1])], axis=1
    )


def square_body(
    tokens,
    lengths,
    request_adapter_ids,
    adapter_store_slot,
    xchan_input_weight,
    bc_input_weight,
    step_input_weight,
    convolution_x_taps,
    convolution_bc_taps,
    step_bias,
    decay_log_rate,
    head_skip_gain,
    output_norm_gain,
    output_weight,
    adapter_down_input,
    adapter_up_xchan,
    adapter_up_bc,
    adapter_down_output,
    adapter_up_output,
):
    length = tokens.shape[0]
    side = lax.axis_size("ctx")
    stream = side * length
    taps = convolution_x_taps.shape[0]
    bank_entries = adapter_down_input.shape[0]
    rank_value = adapter_down_input.shape[2]
    head_count = step_bias.shape[0]
    channels = xchan_input_weight.shape[1]
    bc_width = bc_input_weight.shape[1]
    here = lax.axis_index("ctx")
    lane = lax.axis_index(("tp", "dp"))
    start_pos = here * length
    request_ends = jnp.cumsum(lengths, dtype=jnp.int32)
    every_position = jnp.arange(stream, dtype=jnp.int32)
    every_segment = segment_of(every_position, request_ends)
    slot_indices = adapter_store_slot[request_adapter_ids]
    request_count = lengths.shape[0]
    stream_onehot = every_segment[:, None] == jnp.arange(request_count, dtype=jnp.int32)[None, :]
    slot_of_position = jnp.sum(
        jnp.where(stream_onehot, slot_indices[None, :], 0), axis=1, dtype=jnp.int32
    )
    entry_ids = jnp.arange(bank_entries, dtype=jnp.int32)[None, :]
    owned_here = slot_of_position[:, None] == here * bank_entries + entry_ids
    owned_lane = slot_of_position[:, None] == lane * bank_entries + entry_ids
    positions = start_pos + jnp.arange(length, dtype=jnp.int32)
    segment = segment_of(positions, request_ends)
    previous = segment_of(jnp.reshape(start_pos - 1, (1,)), request_ends)[0]

    tokens_t = transposed(tokens)
    stream_rows = in_order(
        [tokens_t] + [moved(tokens_t, s, "lane") for s in range(1, side)], lane
    )
    local_owned = lax.dynamic_slice_in_dim(slot_of_position, start_pos, length, 0)
    down_pick = jnp.zeros((length, rank_value), jnp.float32)
    for s in range(side):
        piece = adapter_down_input if s == 0 else moved(adapter_down_input, s, "ctx")
        first = ((here - s) % side) * bank_entries
        every = jnp.einsum("pf,efr->per", tokens, piece, preferred_element_type=jnp.float32)
        chosen = local_owned[:, None] == first + jnp.arange(bank_entries, dtype=jnp.int32)[None, :]
        down_pick = down_pick + jnp.sum(every * chosen[:, :, None].astype(jnp.float32), axis=1)
    rank_local = (
        down_pick + sum(moved(down_pick, s, "lane") for s in range(1, side))
    ).astype(jnp.bfloat16)
    rank_hidden = in_order(
        [rank_local] + [moved(rank_local, s, "ctx") for s in range(1, side)], here
    )
    up_out_t = transposed(adapter_up_output)
    hidden_wide = owned_rows(rank_hidden, owned_here)
    xchan_part = jnp.dot(
        stream_rows, xchan_input_weight, preferred_element_type=jnp.float32
    ) + jnp.dot(
        hidden_wide,
        adapter_up_xchan.reshape(bank_entries * rank_value, -1),
        preferred_element_type=jnp.float32,
    )
    bc_part = jnp.dot(stream_rows, bc_input_weight, preferred_element_type=jnp.float32) + jnp.dot(
        hidden_wide,
        adapter_up_bc.reshape(bank_entries * rank_value, -1),
        preferred_element_type=jnp.float32,
    )
    step_part = jnp.dot(stream_rows, step_input_weight, preferred_element_type=jnp.float32)
    projected = jnp.concatenate([xchan_part, bc_part, step_part], axis=1)
    summed = block_rows(projected, here, length)
    for s in range(1, side):
        sent = block_rows(projected, (here + s) % side, length).astype(jnp.bfloat16)
        summed = summed + moved(sent, s, "ctx").astype(jnp.float32)
    values = summed[:, : channels + bc_width]
    step_raw = summed[:, channels + bc_width :]

    kernel = jnp.concatenate([convolution_x_taps, convolution_bc_taps], axis=1)
    tail_rows = passed_along(values[length - (taps - 1) :], "ctx", 1)
    extended = jnp.concatenate([tail_rows, values], axis=0)
    extended_segment = segment_of(
        start_pos - (taps - 1) + jnp.arange(length + taps - 1, dtype=jnp.int32), request_ends
    )
    convolved = jnp.zeros_like(values)
    for tap in range(taps):
        keep = (extended_segment[tap : tap + length] == segment).astype(jnp.float32)
        convolved = convolved + kernel[tap][None, :] * extended[tap : tap + length] * keep[:, None]
    act = jax.nn.silu(convolved)
    x_heads = act[:, :channels].reshape(length, head_count, -1)
    bc_local = act[:, channels:].astype(jnp.bfloat16)
    bc_pieces = [bc_local] + [moved(bc_local, s, "lane") for s in range(1, side)]
    bc_all = jnp.transpose(in_order([piece.T for piece in bc_pieces], lane))
    state_width = bc_all.shape[1] // 2
    b_proj = bc_all[:, :state_width]
    c_proj = bc_all[:, state_width:]
    step_size = jax.nn.softplus(step_raw + step_bias[None, :])
    log_decay = -step_size * jnp.exp(decay_log_rate)[None, :]
    inner_out, local_state, enter_weight, carry_decay = span_parts(
        x_heads, b_proj, c_proj, step_size, log_decay, segment, previous
    )

    decay_row = jnp.broadcast_to(carry_decay[:, None, None], (head_count, 1, local_state.shape[2]))
    state_and_decay = jnp.concatenate([decay_row, local_state], axis=1).astype(jnp.bfloat16)
    entering = jnp.zeros_like(local_state)
    for s in range(side - 1, 0, -1):
        pairs = [(a, a + s) for a in range(side - s)]
        both_in = lax.ppermute(state_and_decay, "ctx", pairs).astype(jnp.float32)
        entering = both_in[:, :1, :1] * entering + both_in[:, 1:]
    entered = (
        jnp.einsum("tn,hdn->thd", c_proj.astype(jnp.float32), entering, precision=FULL_PRECISION)
        * enter_weight[:, :, None]
    )
    mixer_out = (inner_out + entered + head_skip_gain[None, :, None] * x_heads).reshape(
        length, channels
    )
    scale = lax.rsqrt(jnp.mean(mixer_out * mixer_out, axis=1, keepdims=True) + NORM_EPSILON)
    normalized_rows = (mixer_out * scale * output_norm_gain[None, :]).astype(jnp.bfloat16)

    out_pick = jnp.zeros((length, rank_value), jnp.float32)
    for s in range(side):
        piece = adapter_down_output if s == 0 else moved(adapter_down_output, s, "ctx")
        first = ((here - s) % side) * bank_entries
        every = jnp.einsum(
            "pf,efr->per", normalized_rows, piece, preferred_element_type=jnp.float32
        )
        chosen = local_owned[:, None] == first + jnp.arange(bank_entries, dtype=jnp.int32)[None, :]
        out_pick = out_pick + jnp.sum(every * chosen[:, :, None].astype(jnp.float32), axis=1)
    out_local = (
        out_pick + sum(moved(out_pick, s, "lane") for s in range(1, side))
    ).astype(jnp.bfloat16)
    rank_hidden_output = in_order(
        [out_local] + [moved(out_local, s, "ctx") for s in range(1, side)], here
    )
    normed_stream = in_order(
        [normalized_rows] + [moved(normalized_rows, s, "ctx") for s in range(1, side)], here
    )
    base_part = jnp.dot(
        normed_stream, output_weight, preferred_element_type=jnp.float32
    ).astype(jnp.bfloat16).astype(jnp.float32)
    adapter_part = jnp.dot(
        owned_rows(rank_hidden_output, owned_lane),
        up_out_t.reshape(bank_entries * rank_value, -1),
        preferred_element_type=jnp.float32,
    )
    out_part = base_part + adapter_part
    mixed_t = block_rows(out_part, lane, length)
    for s in range(1, side):
        sent = block_rows(out_part, (lane + s) % side, length).astype(jnp.bfloat16)
        mixed_t = mixed_t + moved(sent, s, "lane").astype(jnp.float32)
    return transposed(mixed_t.astype(jnp.bfloat16))


def solution(mesh):
    body = square_body if mesh.shape["ctx"] == mesh.shape["tp"] * mesh.shape["dp"] else general_body
    placed = (
        P(("groups", "ctx"), ("tp", "dp")),
        P("groups"),
        P("groups"),
        P(),
        P("ctx", ("tp", "dp")),
        P("ctx", ("tp", "dp")),
        P("ctx", ("tp", "dp")),
        P(None, ("tp", "dp")),
        P(None, ("tp", "dp")),
        P(("tp", "dp")),
        P(("tp", "dp")),
        P(("tp", "dp")),
        P(("tp", "dp")),
        P(("tp", "dp"), "ctx"),
        P("ctx", ("tp", "dp"), None),
        P("ctx", None, ("tp", "dp")),
        P("ctx", None, ("tp", "dp")),
        P("ctx", ("tp", "dp"), None),
        P("ctx", None, ("tp", "dp")),
    )
    return jax.shard_map(
        body,
        mesh=mesh,
        in_specs=placed,
        out_specs=P(("groups", "ctx"), ("tp", "dp")),
        check_vma=False,
    )
```

```python
import jax
import jax.numpy as jnp
from jax import lax
from jax.sharding import PartitionSpec as P

FULL_PRECISION = lax.Precision.HIGHEST
NORM_EPSILON = 1e-06


def from_root(block, axis, source):
    block = jnp.where(lax.axis_index(axis) == source, block, jnp.zeros_like(block))
    return lax.psum(block, axis)


def passed_along(shard, axis, by):
    size = lax.axis_size(axis)
    pairs = [(i, i + by) for i in range(size) if 0 <= i + by < size]
    return lax.ppermute(shard, axis, pairs)


def prefix(shard, axis, combine, identity):
    size, place = (lax.axis_size(axis), lax.axis_index(axis))
    everything = jax.tree.map(
        lambda part, kind: lax.all_gather(part.astype(kind), axis),
        shard,
        (jnp.bfloat16, jnp.bfloat16),
    )
    start = jax.tree.map(
        lambda part, zero: jnp.broadcast_to(jnp.asarray(zero, part.dtype), part.shape),
        shard,
        identity,
    )

    def lap(k, before):
        reached = k < place
        new = combine(
            before, jax.tree.map(lambda part, own: part[k].astype(own.dtype), everything, shard)
        )
        return jax.tree.map(lambda a, b: jnp.where(reached, a, b), new, before)

    return lax.fori_loop(0, size, lap, start)


def segment_of(positions, request_ends):
    inside = (positions[:, None] >= request_ends[None, :]).astype(jnp.int32)
    counted = jnp.sum(inside, axis=1, dtype=jnp.int32)
    return jnp.where(positions < 0, jnp.int32(-1), counted)


def span_parts(x_heads, b_proj, c_proj, step_size, log_decay, segment, previous):
    length = x_heads.shape[0]
    cumulative = jnp.cumsum(log_decay, axis=0)
    final_log = cumulative[length - 1]
    places = jnp.arange(length, dtype=jnp.int32)
    same_request = jnp.logical_and(
        segment[:, None] == segment[None, :], places[None, :] <= places[:, None]
    ).astype(jnp.float32)
    log_gap = cumulative.T[:, :, None] - cumulative.T[:, None, :]
    decay_table = jnp.exp(jnp.minimum(log_gap, 0.0)) * same_request[None]
    scores = lax.dot_general(
        c_proj, b_proj, (((1,), (1,)), ((), ())), preferred_element_type=jnp.float32
    )
    weights = scores[None] * decay_table * step_size.T[:, None, :]
    inner_out = jnp.einsum("hts,shd->thd", weights, x_heads, precision=FULL_PRECISION)
    at_end = (segment == segment[length - 1]).astype(jnp.float32)
    state_weight = jnp.exp(final_log[None, :] - cumulative) * at_end[:, None] * step_size
    local_state = jnp.einsum(
        "sh,shd,sn->hdn",
        state_weight,
        x_heads,
        b_proj.astype(jnp.float32),
        precision=FULL_PRECISION,
    )
    enter_weight = jnp.exp(cumulative) * (segment == previous).astype(jnp.float32)[:, None]
    carry_decay = jnp.exp(final_log) * (segment[length - 1] == previous).astype(jnp.float32)
    return (inner_out, local_state, enter_weight, carry_decay)


def select_rows(wide, adapter_picker_matrix):
    shaped = wide.reshape(wide.shape[0], adapter_picker_matrix.shape[1], -1)
    return jnp.sum(shaped * adapter_picker_matrix[:, :, None], axis=1)


def masked_wide(values, onehot_b):
    return (values[:, None, :] * onehot_b[:, :, None]).reshape(values.shape[0], -1)


def general_body(
    tokens,
    lengths,
    request_adapter_ids,
    adapter_store_slot,
    xchan_input_weight,
    bc_input_weight,
    step_input_weight,
    convolution_x_taps,
    convolution_bc_taps,
    step_bias,
    decay_log_rate,
    head_skip_gain,
    output_norm_gain,
    output_weight,
    adapter_down_input,
    adapter_up_xchan,
    adapter_up_bc,
    adapter_down_output,
    adapter_up_output,
):
    length = tokens.shape[0]
    request_list = lengths.shape[0]
    taps = convolution_x_taps.shape[0]
    bank_entries = adapter_down_input.shape[0]
    head_count = step_bias.shape[0]
    channels = xchan_input_weight.shape[1]
    start_pos = lax.axis_index("ctx") * length
    request_ends = jnp.cumsum(lengths, dtype=jnp.int32)
    positions = start_pos + jnp.arange(length, dtype=jnp.int32)
    segment = segment_of(positions, request_ends)
    previous = segment_of(jnp.reshape(start_pos - 1, (1,)), request_ends)[0]
    adapter_picker_matrix = (
        segment[:, None] == jnp.arange(request_list, dtype=jnp.int32)[None, :]
    ).astype(jnp.float32)
    onehot_b = adapter_picker_matrix.astype(jnp.bfloat16)
    slot_indices = adapter_store_slot[request_adapter_ids]
    initial_stacks = (
        jnp.zeros(
            (adapter_down_input.shape[1], request_list, adapter_down_input.shape[2]), jnp.bfloat16
        ),
        jnp.zeros((request_list,) + adapter_up_xchan.shape[1:], jnp.bfloat16),
        jnp.zeros((request_list,) + adapter_up_bc.shape[1:], jnp.bfloat16),
        jnp.zeros(
            (adapter_down_output.shape[1], request_list, adapter_down_output.shape[2]), jnp.bfloat16
        ),
        jnp.zeros((request_list,) + adapter_up_output.shape[1:], jnp.bfloat16),
    )
    stack_dims = (1, 0, 0, 1, 0)

    def fetch(request_item, current):
        slot = slot_indices[request_item]
        owner = slot // bank_entries
        within = slot % bank_entries
        a_in, b_x, b_bc, a_out, b_out = [
            lax.dynamic_index_in_dim(adapter_bank, within, 0, keepdims=False)
            for adapter_bank in (
                adapter_down_input,
                adapter_up_xchan,
                adapter_up_bc,
                adapter_down_output,
                adapter_up_output,
            )
        ]
        received = (
            from_root(a_in, "ctx", owner),
            from_root(b_x, "ctx", owner),
            from_root(b_bc, "ctx", owner),
            from_root(a_out, "ctx", owner),
            from_root(b_out, "ctx", owner),
        )
        return tuple(
            (
                lax.dynamic_update_index_in_dim(stack, panel, request_item, along)
                for stack, panel, along in zip(current, received, stack_dims)
            )
        )

    stacks = lax.fori_loop(0, request_list, fetch, initial_stacks)
    rank_value = adapter_down_input.shape[2]
    down_in = stacks[0].reshape(stacks[0].shape[0], request_list * rank_value)
    up_x = stacks[1].reshape(request_list * rank_value, -1)
    up_bc = stacks[2].reshape(request_list * rank_value, -1)
    down_out = stacks[3].reshape(stacks[3].shape[0], request_list * rank_value)
    up_out = stacks[4].reshape(request_list * rank_value, -1)
    lowrank_part = select_rows(
        jnp.dot(tokens, down_in, preferred_element_type=jnp.float32), adapter_picker_matrix
    )
    rank_hidden = lax.psum(lowrank_part.astype(jnp.bfloat16), ("tp", "dp"))
    lowrank_wide = masked_wide(rank_hidden, onehot_b)
    full_tokens = lax.all_gather(tokens, ("tp", "dp"), axis=1, tiled=True)
    pieces = (
        lax.all_gather(xchan_input_weight, "ctx", axis=0, tiled=True),
        lax.all_gather(bc_input_weight, "ctx", axis=0, tiled=True),
        lax.all_gather(step_input_weight, "ctx", axis=0, tiled=True),
    )
    xchan_values, bc_channel_values, step_raw = tuple(
        (jnp.dot(full_tokens, piece, preferred_element_type=jnp.float32) for piece in pieces)
    )
    xchan_values = xchan_values + jnp.dot(lowrank_wide, up_x, preferred_element_type=jnp.float32)
    bc_channel_values = bc_channel_values + jnp.dot(
        lowrank_wide, up_bc, preferred_element_type=jnp.float32
    )
    values = jnp.concatenate([xchan_values, bc_channel_values], axis=1)
    kernel = jnp.concatenate([convolution_x_taps, convolution_bc_taps], axis=1)
    tail_rows = passed_along(values[length - (taps - 1) :], "ctx", 1)
    extended = jnp.concatenate([tail_rows, values], axis=0)
    extended_segment = segment_of(
        start_pos - (taps - 1) + jnp.arange(length + taps - 1, dtype=jnp.int32), request_ends
    )
    convolved = jnp.zeros_like(values)
    for tap in range(taps):
        keep = (extended_segment[tap : tap + length] == segment).astype(jnp.float32)
        convolved = convolved + kernel[tap][None, :] * extended[tap : tap + length] * keep[:, None]
    act = jax.nn.silu(convolved)
    x_heads = act[:, :channels].reshape(length, head_count, -1)
    bc_local = act[:, channels:].astype(jnp.bfloat16)
    bc_all = lax.all_gather(bc_local, ("tp", "dp"), axis=1, tiled=True)
    state_width = bc_all.shape[1] // 2
    b_proj = bc_all[:, :state_width]
    c_proj = bc_all[:, state_width:]
    step_size = jax.nn.softplus(step_raw + step_bias[None, :])
    log_decay = -step_size * jnp.exp(decay_log_rate)[None, :]
    inner_out, local_state, enter_weight, carry_decay = span_parts(
        x_heads, b_proj, c_proj, step_size, log_decay, segment, previous
    )

    def compose(earlier, later):
        return (earlier[0] * later[0], later[0][:, None, None] * earlier[1] + later[1])

    carried = prefix(
        (carry_decay, local_state),
        "ctx",
        compose,
        (jnp.ones_like(carry_decay), jnp.zeros_like(local_state)),
    )
    entering = carried[1]
    entered = (
        jnp.einsum("tn,hdn->thd", c_proj.astype(jnp.float32), entering, precision=FULL_PRECISION)
        * enter_weight[:, :, None]
    )
    mixer_out = (inner_out + entered + head_skip_gain[None, :, None] * x_heads).reshape(
        length, channels
    )
    scale = lax.rsqrt(jnp.mean(mixer_out * mixer_out, axis=1, keepdims=True) + NORM_EPSILON)
    normalized_rows = (mixer_out * scale * output_norm_gain[None, :]).astype(jnp.bfloat16)
    term = jnp.dot(
        normalized_rows,
        lax.all_gather(output_weight, "ctx", axis=1, tiled=True),
        preferred_element_type=jnp.float32,
    )
    base = lax.psum_scatter(
        term.astype(jnp.bfloat16), ("tp", "dp"), scatter_dimension=1, tiled=True
    ).astype(jnp.float32)
    lowrank_out_part = select_rows(
        jnp.dot(normalized_rows, down_out, preferred_element_type=jnp.float32),
        adapter_picker_matrix,
    )
    rank_hidden_output = lax.psum(lowrank_out_part.astype(jnp.bfloat16), ("tp", "dp"))
    adapter_term = jnp.dot(
        masked_wide(rank_hidden_output, onehot_b), up_out, preferred_element_type=jnp.float32
    )
    return (base + adapter_term).astype(jnp.bfloat16)


def moved(block, shift, kind):
    side = lax.axis_size("ctx")
    if kind == "ctx":
        pairs = [(a, (a + shift) % side) for a in range(side)]
        return lax.ppermute(block, "ctx", pairs)
    if kind == "lane":
        pairs = [(a, (a + shift) % side) for a in range(side)]
        return lax.ppermute(block, ("tp", "dp"), pairs)
    if kind == "rows":
        pairs = [(a * side + b, b * side + (a + shift) % side) for a in range(side) for b in range(side)]
    else:
        pairs = [(a * side + b, ((b + shift) % side) * side + a) for a in range(side) for b in range(side)]
    return lax.ppermute(block, ("ctx", "tp", "dp"), pairs)


def transposed(block):
    return moved(block, 0, "rows")


def in_order(pieces, place):
    stacked = jnp.stack(pieces[::-1], axis=0)
    ordered = jnp.roll(stacked, place + 1, axis=0)
    return ordered.reshape((-1,) + pieces[0].shape[1:])


def block_rows(values, index, length):
    return lax.dynamic_slice_in_dim(values, index * length, length, 0)


def owned_rows(values, owned):
    return jnp.concatenate(
        [values * owned[:, i : i + 1].astype(values.dtype) for i in range(owned.shape[1])], axis=1
    )


def square_body(
    tokens,
    lengths,
    request_adapter_ids,
    adapter_store_slot,
    xchan_input_weight,
    bc_input_weight,
    step_input_weight,
    convolution_x_taps,
    convolution_bc_taps,
    step_bias,
    decay_log_rate,
    head_skip_gain,
    output_norm_gain,
    output_weight,
    adapter_down_input,
    adapter_up_xchan,
    adapter_up_bc,
    adapter_down_output,
    adapter_up_output,
):
    length = tokens.shape[0]
    side = lax.axis_size("ctx")
    stream = side * length
    taps = convolution_x_taps.shape[0]
    bank_entries = adapter_down_input.shape[0]
    rank_value = adapter_down_input.shape[2]
    head_count = step_bias.shape[0]
    channels = xchan_input_weight.shape[1]
    bc_width = bc_input_weight.shape[1]
    here = lax.axis_index("ctx")
    lane = lax.axis_index(("tp", "dp"))
    start_pos = here * length
    request_ends = jnp.cumsum(lengths, dtype=jnp.int32)
    every_position = jnp.arange(stream, dtype=jnp.int32)
    every_segment = segment_of(every_position, request_ends)
    slot_indices = adapter_store_slot[request_adapter_ids]
    request_count = lengths.shape[0]
    stream_onehot = every_segment[:, None] == jnp.arange(request_count, dtype=jnp.int32)[None, :]
    slot_of_position = jnp.sum(
        jnp.where(stream_onehot, slot_indices[None, :], 0), axis=1, dtype=jnp.int32
    )
    entry_ids = jnp.arange(bank_entries, dtype=jnp.int32)[None, :]
    owned_here = slot_of_position[:, None] == here * bank_entries + entry_ids
    owned_lane = slot_of_position[:, None] == lane * bank_entries + entry_ids
    positions = start_pos + jnp.arange(length, dtype=jnp.int32)
    segment = segment_of(positions, request_ends)
    previous = segment_of(jnp.reshape(start_pos - 1, (1,)), request_ends)[0]

    tokens_t, down_in_local = lax.optimization_barrier((transposed(tokens), adapter_down_input))
    stream_rows = in_order(
        [tokens_t] + [moved(tokens_t, s, "lane") for s in range(1, side)], lane
    )
    local_owned = lax.dynamic_slice_in_dim(slot_of_position, start_pos, length, 0)
    down_pick = jnp.zeros((length, rank_value), jnp.float32)
    for s in range(side):
        piece = down_in_local if s == 0 else moved(down_in_local, s, "ctx")
        first = ((here - s) % side) * bank_entries
        every = jnp.einsum("pf,efr->per", tokens, piece, preferred_element_type=jnp.float32)
        chosen = local_owned[:, None] == first + jnp.arange(bank_entries, dtype=jnp.int32)[None, :]
        down_pick = down_pick + jnp.sum(every * chosen[:, :, None].astype(jnp.float32), axis=1)
    rank_local = (
        down_pick + sum(moved(down_pick, s, "lane") for s in range(1, side))
    ).astype(jnp.bfloat16)
    rank_hidden = in_order(
        [rank_local] + [moved(rank_local, s, "ctx") for s in range(1, side)], here
    )
    up_out_t = transposed(adapter_up_output)
    hidden_wide = owned_rows(rank_hidden, owned_here)
    xchan_part = jnp.dot(
        stream_rows, xchan_input_weight, preferred_element_type=jnp.float32
    ) + jnp.dot(
        hidden_wide,
        adapter_up_xchan.reshape(bank_entries * rank_value, -1),
        preferred_element_type=jnp.float32,
    )
    bc_part = jnp.dot(stream_rows, bc_input_weight, preferred_element_type=jnp.float32) + jnp.dot(
        hidden_wide,
        adapter_up_bc.reshape(bank_entries * rank_value, -1),
        preferred_element_type=jnp.float32,
    )
    step_part = jnp.dot(stream_rows, step_input_weight, preferred_element_type=jnp.float32)
    projected = jnp.concatenate([xchan_part, bc_part, step_part], axis=1)
    summed = block_rows(projected, here, length)
    for s in range(1, side):
        sent = block_rows(projected, (here + s) % side, length).astype(jnp.bfloat16)
        summed = summed + moved(sent, s, "ctx").astype(jnp.float32)
    values = summed[:, : channels + bc_width]
    step_raw = summed[:, channels + bc_width :]

    kernel = jnp.concatenate([convolution_x_taps, convolution_bc_taps], axis=1)
    tail_rows = passed_along(values[length - (taps - 1) :], "ctx", 1)
    extended = jnp.concatenate([tail_rows, values], axis=0)
    extended_segment = segment_of(
        start_pos - (taps - 1) + jnp.arange(length + taps - 1, dtype=jnp.int32), request_ends
    )
    convolved = jnp.zeros_like(values)
    for tap in range(taps):
        keep = (extended_segment[tap : tap + length] == segment).astype(jnp.float32)
        convolved = convolved + kernel[tap][None, :] * extended[tap : tap + length] * keep[:, None]
    act = jax.nn.silu(convolved)
    x_heads = act[:, :channels].reshape(length, head_count, -1)
    bc_local = act[:, channels:].astype(jnp.bfloat16)
    bc_pieces = [bc_local] + [moved(bc_local, s, "lane") for s in range(1, side)]
    bc_all = jnp.transpose(in_order([piece.T for piece in bc_pieces], lane))
    state_width = bc_all.shape[1] // 2
    b_proj = bc_all[:, :state_width]
    c_proj = bc_all[:, state_width:]
    step_size = jax.nn.softplus(step_raw + step_bias[None, :])
    log_decay = -step_size * jnp.exp(decay_log_rate)[None, :]
    inner_out, local_state, enter_weight, carry_decay = span_parts(
        x_heads, b_proj, c_proj, step_size, log_decay, segment, previous
    )

    decay_row = jnp.broadcast_to(carry_decay[:, None, None], (head_count, 1, local_state.shape[2]))
    state_and_decay = jnp.concatenate([decay_row, local_state], axis=1).astype(jnp.bfloat16)
    entering = jnp.zeros_like(local_state)
    for s in range(side - 1, 0, -1):
        pairs = [(a, a + s) for a in range(side - s)]
        both_in = lax.ppermute(state_and_decay, "ctx", pairs).astype(jnp.float32)
        entering = both_in[:, :1, :1] * entering + both_in[:, 1:]
    entered = (
        jnp.einsum("tn,hdn->thd", c_proj.astype(jnp.float32), entering, precision=FULL_PRECISION)
        * enter_weight[:, :, None]
    )
    mixer_out = (inner_out + entered + head_skip_gain[None, :, None] * x_heads).reshape(
        length, channels
    )
    scale = lax.rsqrt(jnp.mean(mixer_out * mixer_out, axis=1, keepdims=True) + NORM_EPSILON)
    normalized_rows = (mixer_out * scale * output_norm_gain[None, :]).astype(jnp.bfloat16)

    normed_stream = in_order(
        [normalized_rows] + [moved(normalized_rows, s, "ctx") for s in range(1, side)], here
    )
    out_down_part = jnp.einsum(
        "pc,ecr->per", normed_stream, adapter_down_output, preferred_element_type=jnp.float32
    )
    out_down_pick = jnp.sum(out_down_part * owned_here[:, :, None].astype(jnp.float32), axis=1)
    rank_hidden_output = transposed(
        out_down_pick + sum(moved(out_down_pick, s, "lane") for s in range(1, side))
    )
    base_part = jnp.dot(
        normed_stream, output_weight, preferred_element_type=jnp.float32
    ).astype(jnp.bfloat16).astype(jnp.float32)
    adapter_part = jnp.dot(
        owned_rows(rank_hidden_output, owned_lane).astype(jnp.bfloat16),
        up_out_t.reshape(bank_entries * rank_value, -1),
        preferred_element_type=jnp.float32,
    )
    out_part = base_part + adapter_part
    mixed_t = block_rows(out_part, lane, length)
    for s in range(1, side):
        sent = block_rows(out_part, (lane + s) % side, length).astype(jnp.bfloat16)
        mixed_t = mixed_t + moved(sent, s, "lane").astype(jnp.float32)
    return transposed(mixed_t.astype(jnp.bfloat16))


def solution(mesh):
    body = square_body if mesh.shape["ctx"] == mesh.shape["tp"] * mesh.shape["dp"] else general_body
    placed = (
        P(("groups", "ctx"), ("tp", "dp")),
        P("groups"),
        P("groups"),
        P(),
        P("ctx", ("tp", "dp")),
        P("ctx", ("tp", "dp")),
        P("ctx", ("tp", "dp")),
        P(None, ("tp", "dp")),
        P(None, ("tp", "dp")),
        P(("tp", "dp")),
        P(("tp", "dp")),
        P(("tp", "dp")),
        P(("tp", "dp")),
        P(("tp", "dp"), "ctx"),
        P("ctx", ("tp", "dp"), None),
        P("ctx", None, ("tp", "dp")),
        P("ctx", None, ("tp", "dp")),
        P("ctx", ("tp", "dp"), None),
        P("ctx", None, ("tp", "dp")),
    )
    return jax.shard_map(
        body,
        mesh=mesh,
        in_specs=placed,
        out_specs=P(("groups", "ctx"), ("tp", "dp")),
        check_vma=False,
    )
```

```python
import jax
import jax.numpy as jnp
from jax import lax
from jax.sharding import PartitionSpec as P

FULL_PRECISION = lax.Precision.HIGHEST
NORM_EPSILON = 1e-06


def from_root(block, axis, source):
    block = jnp.where(lax.axis_index(axis) == source, block, jnp.zeros_like(block))
    return lax.psum(block, axis)


def passed_along(shard, axis, by):
    size = lax.axis_size(axis)
    pairs = [(i, i + by) for i in range(size) if 0 <= i + by < size]
    return lax.ppermute(shard, axis, pairs)


def prefix(shard, axis, combine, identity):
    size, place = (lax.axis_size(axis), lax.axis_index(axis))
    everything = jax.tree.map(
        lambda part, kind: lax.all_gather(part.astype(kind), axis),
        shard,
        (jnp.bfloat16, jnp.bfloat16),
    )
    start = jax.tree.map(
        lambda part, zero: jnp.broadcast_to(jnp.asarray(zero, part.dtype), part.shape),
        shard,
        identity,
    )

    def lap(k, before):
        reached = k < place
        new = combine(
            before, jax.tree.map(lambda part, own: part[k].astype(own.dtype), everything, shard)
        )
        return jax.tree.map(lambda a, b: jnp.where(reached, a, b), new, before)

    return lax.fori_loop(0, size, lap, start)


def segment_of(positions, request_ends):
    inside = (positions[:, None] >= request_ends[None, :]).astype(jnp.int32)
    counted = jnp.sum(inside, axis=1, dtype=jnp.int32)
    return jnp.where(positions < 0, jnp.int32(-1), counted)


def span_parts(x_heads, b_proj, c_proj, step_size, log_decay, segment, previous):
    length = x_heads.shape[0]
    cumulative = jnp.cumsum(log_decay, axis=0)
    final_log = cumulative[length - 1]
    places = jnp.arange(length, dtype=jnp.int32)
    same_request = jnp.logical_and(
        segment[:, None] == segment[None, :], places[None, :] <= places[:, None]
    ).astype(jnp.float32)
    log_gap = cumulative.T[:, :, None] - cumulative.T[:, None, :]
    decay_table = jnp.exp(jnp.minimum(log_gap, 0.0)) * same_request[None]
    scores = lax.dot_general(
        c_proj, b_proj, (((1,), (1,)), ((), ())), preferred_element_type=jnp.float32
    )
    weights = scores[None] * decay_table * step_size.T[:, None, :]
    inner_out = jnp.einsum("hts,shd->thd", weights, x_heads, precision=FULL_PRECISION)
    at_end = (segment == segment[length - 1]).astype(jnp.float32)
    state_weight = jnp.exp(final_log[None, :] - cumulative) * at_end[:, None] * step_size
    local_state = jnp.einsum(
        "sh,shd,sn->hdn",
        state_weight,
        x_heads,
        b_proj.astype(jnp.float32),
        precision=FULL_PRECISION,
    )
    enter_weight = jnp.exp(cumulative) * (segment == previous).astype(jnp.float32)[:, None]
    carry_decay = jnp.exp(final_log) * (segment[length - 1] == previous).astype(jnp.float32)
    return (inner_out, local_state, enter_weight, carry_decay)


def select_rows(wide, adapter_picker_matrix):
    shaped = wide.reshape(wide.shape[0], adapter_picker_matrix.shape[1], -1)
    return jnp.sum(shaped * adapter_picker_matrix[:, :, None], axis=1)


def masked_wide(values, onehot_b):
    return (values[:, None, :] * onehot_b[:, :, None]).reshape(values.shape[0], -1)


def general_body(
    tokens,
    lengths,
    request_adapter_ids,
    adapter_store_slot,
    xchan_input_weight,
    bc_input_weight,
    step_input_weight,
    convolution_x_taps,
    convolution_bc_taps,
    step_bias,
    decay_log_rate,
    head_skip_gain,
    output_norm_gain,
    output_weight,
    adapter_down_input,
    adapter_up_xchan,
    adapter_up_bc,
    adapter_down_output,
    adapter_up_output,
):
    length = tokens.shape[0]
    request_list = lengths.shape[0]
    taps = convolution_x_taps.shape[0]
    bank_entries = adapter_down_input.shape[0]
    head_count = step_bias.shape[0]
    channels = xchan_input_weight.shape[1]
    start_pos = lax.axis_index("ctx") * length
    request_ends = jnp.cumsum(lengths, dtype=jnp.int32)
    positions = start_pos + jnp.arange(length, dtype=jnp.int32)
    segment = segment_of(positions, request_ends)
    previous = segment_of(jnp.reshape(start_pos - 1, (1,)), request_ends)[0]
    adapter_picker_matrix = (
        segment[:, None] == jnp.arange(request_list, dtype=jnp.int32)[None, :]
    ).astype(jnp.float32)
    onehot_b = adapter_picker_matrix.astype(jnp.bfloat16)
    slot_indices = adapter_store_slot[request_adapter_ids]
    initial_stacks = (
        jnp.zeros(
            (adapter_down_input.shape[1], request_list, adapter_down_input.shape[2]), jnp.bfloat16
        ),
        jnp.zeros((request_list,) + adapter_up_xchan.shape[1:], jnp.bfloat16),
        jnp.zeros((request_list,) + adapter_up_bc.shape[1:], jnp.bfloat16),
        jnp.zeros(
            (adapter_down_output.shape[1], request_list, adapter_down_output.shape[2]), jnp.bfloat16
        ),
        jnp.zeros((request_list,) + adapter_up_output.shape[1:], jnp.bfloat16),
    )
    stack_dims = (1, 0, 0, 1, 0)

    def fetch(request_item, current):
        slot = slot_indices[request_item]
        owner = slot // bank_entries
        within = slot % bank_entries
        a_in, b_x, b_bc, a_out, b_out = [
            lax.dynamic_index_in_dim(adapter_bank, within, 0, keepdims=False)
            for adapter_bank in (
                adapter_down_input,
                adapter_up_xchan,
                adapter_up_bc,
                adapter_down_output,
                adapter_up_output,
            )
        ]
        received = (
            from_root(a_in, "ctx", owner),
            from_root(b_x, "ctx", owner),
            from_root(b_bc, "ctx", owner),
            from_root(a_out, "ctx", owner),
            from_root(b_out, "ctx", owner),
        )
        return tuple(
            (
                lax.dynamic_update_index_in_dim(stack, panel, request_item, along)
                for stack, panel, along in zip(current, received, stack_dims)
            )
        )

    stacks = lax.fori_loop(0, request_list, fetch, initial_stacks)
    rank_value = adapter_down_input.shape[2]
    down_in = stacks[0].reshape(stacks[0].shape[0], request_list * rank_value)
    up_x = stacks[1].reshape(request_list * rank_value, -1)
    up_bc = stacks[2].reshape(request_list * rank_value, -1)
    down_out = stacks[3].reshape(stacks[3].shape[0], request_list * rank_value)
    up_out = stacks[4].reshape(request_list * rank_value, -1)
    lowrank_part = select_rows(
        jnp.dot(tokens, down_in, preferred_element_type=jnp.float32), adapter_picker_matrix
    )
    rank_hidden = lax.psum(lowrank_part.astype(jnp.bfloat16), ("tp", "dp"))
    lowrank_wide = masked_wide(rank_hidden, onehot_b)
    full_tokens = lax.all_gather(tokens, ("tp", "dp"), axis=1, tiled=True)
    pieces = (
        lax.all_gather(xchan_input_weight, "ctx", axis=0, tiled=True),
        lax.all_gather(bc_input_weight, "ctx", axis=0, tiled=True),
        lax.all_gather(step_input_weight, "ctx", axis=0, tiled=True),
    )
    xchan_values, bc_channel_values, step_raw = tuple(
        (jnp.dot(full_tokens, piece, preferred_element_type=jnp.float32) for piece in pieces)
    )
    xchan_values = xchan_values + jnp.dot(lowrank_wide, up_x, preferred_element_type=jnp.float32)
    bc_channel_values = bc_channel_values + jnp.dot(
        lowrank_wide, up_bc, preferred_element_type=jnp.float32
    )
    values = jnp.concatenate([xchan_values, bc_channel_values], axis=1)
    kernel = jnp.concatenate([convolution_x_taps, convolution_bc_taps], axis=1)
    tail_rows = passed_along(values[length - (taps - 1) :], "ctx", 1)
    extended = jnp.concatenate([tail_rows, values], axis=0)
    extended_segment = segment_of(
        start_pos - (taps - 1) + jnp.arange(length + taps - 1, dtype=jnp.int32), request_ends
    )
    convolved = jnp.zeros_like(values)
    for tap in range(taps):
        keep = (extended_segment[tap : tap + length] == segment).astype(jnp.float32)
        convolved = convolved + kernel[tap][None, :] * extended[tap : tap + length] * keep[:, None]
    act = jax.nn.silu(convolved)
    x_heads = act[:, :channels].reshape(length, head_count, -1)
    bc_local = act[:, channels:].astype(jnp.bfloat16)
    bc_all = lax.all_gather(bc_local, ("tp", "dp"), axis=1, tiled=True)
    state_width = bc_all.shape[1] // 2
    b_proj = bc_all[:, :state_width]
    c_proj = bc_all[:, state_width:]
    step_size = jax.nn.softplus(step_raw + step_bias[None, :])
    log_decay = -step_size * jnp.exp(decay_log_rate)[None, :]
    inner_out, local_state, enter_weight, carry_decay = span_parts(
        x_heads, b_proj, c_proj, step_size, log_decay, segment, previous
    )

    def compose(earlier, later):
        return (earlier[0] * later[0], later[0][:, None, None] * earlier[1] + later[1])

    carried = prefix(
        (carry_decay, local_state),
        "ctx",
        compose,
        (jnp.ones_like(carry_decay), jnp.zeros_like(local_state)),
    )
    entering = carried[1]
    entered = (
        jnp.einsum("tn,hdn->thd", c_proj.astype(jnp.float32), entering, precision=FULL_PRECISION)
        * enter_weight[:, :, None]
    )
    mixer_out = (inner_out + entered + head_skip_gain[None, :, None] * x_heads).reshape(
        length, channels
    )
    scale = lax.rsqrt(jnp.mean(mixer_out * mixer_out, axis=1, keepdims=True) + NORM_EPSILON)
    normalized_rows = (mixer_out * scale * output_norm_gain[None, :]).astype(jnp.bfloat16)
    term = jnp.dot(
        normalized_rows,
        lax.all_gather(output_weight, "ctx", axis=1, tiled=True),
        preferred_element_type=jnp.float32,
    )
    base = lax.psum_scatter(
        term.astype(jnp.bfloat16), ("tp", "dp"), scatter_dimension=1, tiled=True
    ).astype(jnp.float32)
    lowrank_out_part = select_rows(
        jnp.dot(normalized_rows, down_out, preferred_element_type=jnp.float32),
        adapter_picker_matrix,
    )
    rank_hidden_output = lax.psum(lowrank_out_part.astype(jnp.bfloat16), ("tp", "dp"))
    adapter_term = jnp.dot(
        masked_wide(rank_hidden_output, onehot_b), up_out, preferred_element_type=jnp.float32
    )
    return (base + adapter_term).astype(jnp.bfloat16)


def moved(block, shift, kind):
    side = lax.axis_size("ctx")
    if kind == "ctx":
        pairs = [(a, (a + shift) % side) for a in range(side)]
        return lax.ppermute(block, "ctx", pairs)
    if kind == "lane":
        pairs = [(a, (a + shift) % side) for a in range(side)]
        return lax.ppermute(block, ("tp", "dp"), pairs)
    if kind == "rows":
        pairs = [(a * side + b, b * side + (a + shift) % side) for a in range(side) for b in range(side)]
    else:
        pairs = [(a * side + b, ((b + shift) % side) * side + a) for a in range(side) for b in range(side)]
    return lax.ppermute(block, ("ctx", "tp", "dp"), pairs)


def transposed(block):
    return moved(block, 0, "rows")


def in_order(pieces, place):
    stacked = jnp.stack(pieces[::-1], axis=0)
    ordered = jnp.roll(stacked, place + 1, axis=0)
    return ordered.reshape((-1,) + pieces[0].shape[1:])


def block_rows(values, index, length):
    return lax.dynamic_slice_in_dim(values, index * length, length, 0)


def owned_rows(values, owned):
    return jnp.concatenate(
        [values * owned[:, i : i + 1].astype(values.dtype) for i in range(owned.shape[1])], axis=1
    )


def square_body(
    tokens,
    lengths,
    request_adapter_ids,
    adapter_store_slot,
    xchan_input_weight,
    bc_input_weight,
    step_input_weight,
    convolution_x_taps,
    convolution_bc_taps,
    step_bias,
    decay_log_rate,
    head_skip_gain,
    output_norm_gain,
    output_weight,
    adapter_down_input,
    adapter_up_xchan,
    adapter_up_bc,
    adapter_down_output,
    adapter_up_output,
):
    length = tokens.shape[0]
    side = lax.axis_size("ctx")
    stream = side * length
    taps = convolution_x_taps.shape[0]
    bank_entries = adapter_down_input.shape[0]
    rank_value = adapter_down_input.shape[2]
    head_count = step_bias.shape[0]
    channels = xchan_input_weight.shape[1]
    bc_width = bc_input_weight.shape[1]
    here = lax.axis_index("ctx")
    lane = lax.axis_index(("tp", "dp"))
    start_pos = here * length
    request_ends = jnp.cumsum(lengths, dtype=jnp.int32)
    every_position = jnp.arange(stream, dtype=jnp.int32)
    every_segment = segment_of(every_position, request_ends)
    slot_indices = adapter_store_slot[request_adapter_ids]
    request_count = lengths.shape[0]
    stream_onehot = every_segment[:, None] == jnp.arange(request_count, dtype=jnp.int32)[None, :]
    slot_of_position = jnp.sum(
        jnp.where(stream_onehot, slot_indices[None, :], 0), axis=1, dtype=jnp.int32
    )
    entry_ids = jnp.arange(bank_entries, dtype=jnp.int32)[None, :]
    owned_here = slot_of_position[:, None] == here * bank_entries + entry_ids
    owned_lane = slot_of_position[:, None] == lane * bank_entries + entry_ids
    positions = start_pos + jnp.arange(length, dtype=jnp.int32)
    segment = segment_of(positions, request_ends)
    previous = segment_of(jnp.reshape(start_pos - 1, (1,)), request_ends)[0]

    tokens_t, down_in_local = lax.optimization_barrier((transposed(tokens), adapter_down_input))
    stream_rows = in_order(
        [tokens_t] + [moved(tokens_t, s, "lane") for s in range(1, side)], lane
    )
    local_owned = lax.dynamic_slice_in_dim(slot_of_position, start_pos, length, 0)
    down_pick = jnp.zeros((length, rank_value), jnp.float32)
    for s in range(side):
        piece = down_in_local if s == 0 else moved(down_in_local, s, "ctx")
        first = ((here - s) % side) * bank_entries
        every = jnp.einsum("pf,efr->per", tokens, piece, preferred_element_type=jnp.float32)
        chosen = local_owned[:, None] == first + jnp.arange(bank_entries, dtype=jnp.int32)[None, :]
        down_pick = down_pick + jnp.sum(every * chosen[:, :, None].astype(jnp.float32), axis=1)
    rank_local = (
        down_pick + sum(moved(down_pick, s, "lane") for s in range(1, side))
    ).astype(jnp.bfloat16)
    rank_hidden = in_order(
        [rank_local] + [moved(rank_local, s, "ctx") for s in range(1, side)], here
    )
    hidden_wide = owned_rows(rank_hidden, owned_here)
    xchan_part = jnp.dot(
        stream_rows, xchan_input_weight, preferred_element_type=jnp.float32
    ) + jnp.dot(
        hidden_wide,
        adapter_up_xchan.reshape(bank_entries * rank_value, -1),
        preferred_element_type=jnp.float32,
    )
    bc_part = jnp.dot(stream_rows, bc_input_weight, preferred_element_type=jnp.float32) + jnp.dot(
        hidden_wide,
        adapter_up_bc.reshape(bank_entries * rank_value, -1),
        preferred_element_type=jnp.float32,
    )
    step_part = jnp.dot(stream_rows, step_input_weight, preferred_element_type=jnp.float32)
    projected = jnp.concatenate([xchan_part, bc_part, step_part], axis=1)
    summed = block_rows(projected, here, length)
    for s in range(1, side):
        sent = block_rows(projected, (here + s) % side, length).astype(jnp.bfloat16)
        summed = summed + moved(sent, s, "ctx").astype(jnp.float32)
    summed, up_out_local = lax.optimization_barrier((summed, adapter_up_output))
    up_out_t = transposed(up_out_local)
    values = summed[:, : channels + bc_width]
    step_raw = summed[:, channels + bc_width :]

    kernel = jnp.concatenate([convolution_x_taps, convolution_bc_taps], axis=1)
    tail_rows = passed_along(values[length - (taps - 1) :], "ctx", 1)
    extended = jnp.concatenate([tail_rows, values], axis=0)
    extended_segment = segment_of(
        start_pos - (taps - 1) + jnp.arange(length + taps - 1, dtype=jnp.int32), request_ends
    )
    convolved = jnp.zeros_like(values)
    for tap in range(taps):
        keep = (extended_segment[tap : tap + length] == segment).astype(jnp.float32)
        convolved = convolved + kernel[tap][None, :] * extended[tap : tap + length] * keep[:, None]
    act = jax.nn.silu(convolved)
    x_heads = act[:, :channels].reshape(length, head_count, -1)
    bc_local = act[:, channels:].astype(jnp.bfloat16)
    bc_pieces = [bc_local] + [moved(bc_local, s, "lane") for s in range(1, side)]
    bc_all = jnp.transpose(in_order([piece.T for piece in bc_pieces], lane))
    state_width = bc_all.shape[1] // 2
    b_proj = bc_all[:, :state_width]
    c_proj = bc_all[:, state_width:]
    step_size = jax.nn.softplus(step_raw + step_bias[None, :])
    log_decay = -step_size * jnp.exp(decay_log_rate)[None, :]
    inner_out, local_state, enter_weight, carry_decay = span_parts(
        x_heads, b_proj, c_proj, step_size, log_decay, segment, previous
    )

    decay_row = jnp.broadcast_to(carry_decay[:, None, None], (head_count, 1, local_state.shape[2]))
    state_and_decay = jnp.concatenate([decay_row, local_state], axis=1).astype(jnp.bfloat16)
    entering = jnp.zeros_like(local_state)
    for s in range(side - 1, 0, -1):
        pairs = [(a, a + s) for a in range(side - s)]
        both_in = lax.ppermute(state_and_decay, "ctx", pairs).astype(jnp.float32)
        entering = both_in[:, :1, :1] * entering + both_in[:, 1:]
    entered = (
        jnp.einsum("tn,hdn->thd", c_proj.astype(jnp.float32), entering, precision=FULL_PRECISION)
        * enter_weight[:, :, None]
    )
    mixer_out = (inner_out + entered + head_skip_gain[None, :, None] * x_heads).reshape(
        length, channels
    )
    scale = lax.rsqrt(jnp.mean(mixer_out * mixer_out, axis=1, keepdims=True) + NORM_EPSILON)
    normalized_rows = (mixer_out * scale * output_norm_gain[None, :]).astype(jnp.bfloat16)

    normed_stream = in_order(
        [normalized_rows] + [moved(normalized_rows, s, "ctx") for s in range(1, side)], here
    )
    out_down_part = jnp.einsum(
        "pc,ecr->per", normed_stream, adapter_down_output, preferred_element_type=jnp.float32
    )
    out_down_pick = jnp.sum(out_down_part * owned_here[:, :, None].astype(jnp.float32), axis=1)
    rank_hidden_output = transposed(
        out_down_pick + sum(moved(out_down_pick, s, "lane") for s in range(1, side))
    )
    base_part = jnp.dot(
        normed_stream, output_weight, preferred_element_type=jnp.float32
    ).astype(jnp.bfloat16).astype(jnp.float32)
    adapter_part = jnp.dot(
        owned_rows(rank_hidden_output, owned_lane).astype(jnp.bfloat16),
        up_out_t.reshape(bank_entries * rank_value, -1),
        preferred_element_type=jnp.float32,
    )
    out_part = base_part + adapter_part
    mixed_t = block_rows(out_part, lane, length)
    for s in range(1, side):
        sent = block_rows(out_part, (lane + s) % side, length).astype(jnp.bfloat16)
        mixed_t = mixed_t + moved(sent, s, "lane").astype(jnp.float32)
    return transposed(mixed_t.astype(jnp.bfloat16))


def solution(mesh):
    body = square_body if mesh.shape["ctx"] == mesh.shape["tp"] * mesh.shape["dp"] else general_body
    placed = (
        P(("groups", "ctx"), ("tp", "dp")),
        P("groups"),
        P("groups"),
        P(),
        P("ctx", ("tp", "dp")),
        P("ctx", ("tp", "dp")),
        P("ctx", ("tp", "dp")),
        P(None, ("tp", "dp")),
        P(None, ("tp", "dp")),
        P(("tp", "dp")),
        P(("tp", "dp")),
        P(("tp", "dp")),
        P(("tp", "dp")),
        P(("tp", "dp"), "ctx"),
        P("ctx", ("tp", "dp"), None),
        P("ctx", None, ("tp", "dp")),
        P("ctx", None, ("tp", "dp")),
        P("ctx", ("tp", "dp"), None),
        P("ctx", None, ("tp", "dp")),
    )
    return jax.shard_map(
        body,
        mesh=mesh,
        in_specs=placed,
        out_specs=P(("groups", "ctx"), ("tp", "dp")),
        check_vma=False,
    )
```

```python
import jax
import jax.numpy as jnp
from jax import lax
from jax.sharding import PartitionSpec as P

FULL_PRECISION = lax.Precision.HIGHEST
NORM_EPSILON = 1e-06


def from_root(block, axis, source):
    block = jnp.where(lax.axis_index(axis) == source, block, jnp.zeros_like(block))
    return lax.psum(block, axis)


def passed_along(shard, axis, by):
    size = lax.axis_size(axis)
    pairs = [(i, i + by) for i in range(size) if 0 <= i + by < size]
    return lax.ppermute(shard, axis, pairs)


def prefix(shard, axis, combine, identity):
    size, place = (lax.axis_size(axis), lax.axis_index(axis))
    everything = jax.tree.map(
        lambda part, kind: lax.all_gather(part.astype(kind), axis),
        shard,
        (jnp.bfloat16, jnp.bfloat16),
    )
    start = jax.tree.map(
        lambda part, zero: jnp.broadcast_to(jnp.asarray(zero, part.dtype), part.shape),
        shard,
        identity,
    )

    def lap(k, before):
        reached = k < place
        new = combine(
            before, jax.tree.map(lambda part, own: part[k].astype(own.dtype), everything, shard)
        )
        return jax.tree.map(lambda a, b: jnp.where(reached, a, b), new, before)

    return lax.fori_loop(0, size, lap, start)


def segment_of(positions, request_ends):
    inside = (positions[:, None] >= request_ends[None, :]).astype(jnp.int32)
    counted = jnp.sum(inside, axis=1, dtype=jnp.int32)
    return jnp.where(positions < 0, jnp.int32(-1), counted)


def span_parts(x_heads, b_proj, c_proj, step_size, log_decay, segment, previous):
    length = x_heads.shape[0]
    cumulative = jnp.cumsum(log_decay, axis=0)
    final_log = cumulative[length - 1]
    places = jnp.arange(length, dtype=jnp.int32)
    same_request = jnp.logical_and(
        segment[:, None] == segment[None, :], places[None, :] <= places[:, None]
    ).astype(jnp.float32)
    log_gap = cumulative.T[:, :, None] - cumulative.T[:, None, :]
    decay_table = jnp.exp(jnp.minimum(log_gap, 0.0)) * same_request[None]
    scores = lax.dot_general(
        c_proj, b_proj, (((1,), (1,)), ((), ())), preferred_element_type=jnp.float32
    )
    weights = scores[None] * decay_table * step_size.T[:, None, :]
    inner_out = jnp.einsum("hts,shd->thd", weights, x_heads, precision=FULL_PRECISION)
    at_end = (segment == segment[length - 1]).astype(jnp.float32)
    state_weight = jnp.exp(final_log[None, :] - cumulative) * at_end[:, None] * step_size
    local_state = jnp.einsum(
        "sh,shd,sn->hdn",
        state_weight,
        x_heads,
        b_proj.astype(jnp.float32),
        precision=FULL_PRECISION,
    )
    enter_weight = jnp.exp(cumulative) * (segment == previous).astype(jnp.float32)[:, None]
    carry_decay = jnp.exp(final_log) * (segment[length - 1] == previous).astype(jnp.float32)
    return (inner_out, local_state, enter_weight, carry_decay)


def select_rows(wide, adapter_picker_matrix):
    shaped = wide.reshape(wide.shape[0], adapter_picker_matrix.shape[1], -1)
    return jnp.sum(shaped * adapter_picker_matrix[:, :, None], axis=1)


def masked_wide(values, onehot_b):
    return (values[:, None, :] * onehot_b[:, :, None]).reshape(values.shape[0], -1)


def general_body(
    tokens,
    lengths,
    request_adapter_ids,
    adapter_store_slot,
    xchan_input_weight,
    bc_input_weight,
    step_input_weight,
    convolution_x_taps,
    convolution_bc_taps,
    step_bias,
    decay_log_rate,
    head_skip_gain,
    output_norm_gain,
    output_weight,
    adapter_down_input,
    adapter_up_xchan,
    adapter_up_bc,
    adapter_down_output,
    adapter_up_output,
):
    length = tokens.shape[0]
    request_list = lengths.shape[0]
    taps = convolution_x_taps.shape[0]
    bank_entries = adapter_down_input.shape[0]
    head_count = step_bias.shape[0]
    channels = xchan_input_weight.shape[1]
    start_pos = lax.axis_index("ctx") * length
    request_ends = jnp.cumsum(lengths, dtype=jnp.int32)
    positions = start_pos + jnp.arange(length, dtype=jnp.int32)
    segment = segment_of(positions, request_ends)
    previous = segment_of(jnp.reshape(start_pos - 1, (1,)), request_ends)[0]
    adapter_picker_matrix = (
        segment[:, None] == jnp.arange(request_list, dtype=jnp.int32)[None, :]
    ).astype(jnp.float32)
    onehot_b = adapter_picker_matrix.astype(jnp.bfloat16)
    slot_indices = adapter_store_slot[request_adapter_ids]
    initial_stacks = (
        jnp.zeros(
            (adapter_down_input.shape[1], request_list, adapter_down_input.shape[2]), jnp.bfloat16
        ),
        jnp.zeros((request_list,) + adapter_up_xchan.shape[1:], jnp.bfloat16),
        jnp.zeros((request_list,) + adapter_up_bc.shape[1:], jnp.bfloat16),
        jnp.zeros(
            (adapter_down_output.shape[1], request_list, adapter_down_output.shape[2]), jnp.bfloat16
        ),
        jnp.zeros((request_list,) + adapter_up_output.shape[1:], jnp.bfloat16),
    )
    stack_dims = (1, 0, 0, 1, 0)

    def fetch(request_item, current):
        slot = slot_indices[request_item]
        owner = slot // bank_entries
        within = slot % bank_entries
        a_in, b_x, b_bc, a_out, b_out = [
            lax.dynamic_index_in_dim(adapter_bank, within, 0, keepdims=False)
            for adapter_bank in (
                adapter_down_input,
                adapter_up_xchan,
                adapter_up_bc,
                adapter_down_output,
                adapter_up_output,
            )
        ]
        received = (
            from_root(a_in, "ctx", owner),
            from_root(b_x, "ctx", owner),
            from_root(b_bc, "ctx", owner),
            from_root(a_out, "ctx", owner),
            from_root(b_out, "ctx", owner),
        )
        return tuple(
            (
                lax.dynamic_update_index_in_dim(stack, panel, request_item, along)
                for stack, panel, along in zip(current, received, stack_dims)
            )
        )

    stacks = lax.fori_loop(0, request_list, fetch, initial_stacks)
    rank_value = adapter_down_input.shape[2]
    down_in = stacks[0].reshape(stacks[0].shape[0], request_list * rank_value)
    up_x = stacks[1].reshape(request_list * rank_value, -1)
    up_bc = stacks[2].reshape(request_list * rank_value, -1)
    down_out = stacks[3].reshape(stacks[3].shape[0], request_list * rank_value)
    up_out = stacks[4].reshape(request_list * rank_value, -1)
    lowrank_part = select_rows(
        jnp.dot(tokens, down_in, preferred_element_type=jnp.float32), adapter_picker_matrix
    )
    rank_hidden = lax.psum(lowrank_part.astype(jnp.bfloat16), ("tp", "dp"))
    lowrank_wide = masked_wide(rank_hidden, onehot_b)
    full_tokens = lax.all_gather(tokens, ("tp", "dp"), axis=1, tiled=True)
    pieces = (
        lax.all_gather(xchan_input_weight, "ctx", axis=0, tiled=True),
        lax.all_gather(bc_input_weight, "ctx", axis=0, tiled=True),
        lax.all_gather(step_input_weight, "ctx", axis=0, tiled=True),
    )
    xchan_values, bc_channel_values, step_raw = tuple(
        (jnp.dot(full_tokens, piece, preferred_element_type=jnp.float32) for piece in pieces)
    )
    xchan_values = xchan_values + jnp.dot(lowrank_wide, up_x, preferred_element_type=jnp.float32)
    bc_channel_values = bc_channel_values + jnp.dot(
        lowrank_wide, up_bc, preferred_element_type=jnp.float32
    )
    values = jnp.concatenate([xchan_values, bc_channel_values], axis=1)
    kernel = jnp.concatenate([convolution_x_taps, convolution_bc_taps], axis=1)
    tail_rows = passed_along(values[length - (taps - 1) :], "ctx", 1)
    extended = jnp.concatenate([tail_rows, values], axis=0)
    extended_segment = segment_of(
        start_pos - (taps - 1) + jnp.arange(length + taps - 1, dtype=jnp.int32), request_ends
    )
    convolved = jnp.zeros_like(values)
    for tap in range(taps):
        keep = (extended_segment[tap : tap + length] == segment).astype(jnp.float32)
        convolved = convolved + kernel[tap][None, :] * extended[tap : tap + length] * keep[:, None]
    act = jax.nn.silu(convolved)
    x_heads = act[:, :channels].reshape(length, head_count, -1)
    bc_local = act[:, channels:].astype(jnp.bfloat16)
    bc_all = lax.all_gather(bc_local, ("tp", "dp"), axis=1, tiled=True)
    state_width = bc_all.shape[1] // 2
    b_proj = bc_all[:, :state_width]
    c_proj = bc_all[:, state_width:]
    step_size = jax.nn.softplus(step_raw + step_bias[None, :])
    log_decay = -step_size * jnp.exp(decay_log_rate)[None, :]
    inner_out, local_state, enter_weight, carry_decay = span_parts(
        x_heads, b_proj, c_proj, step_size, log_decay, segment, previous
    )

    def compose(earlier, later):
        return (earlier[0] * later[0], later[0][:, None, None] * earlier[1] + later[1])

    carried = prefix(
        (carry_decay, local_state),
        "ctx",
        compose,
        (jnp.ones_like(carry_decay), jnp.zeros_like(local_state)),
    )
    entering = carried[1]
    entered = (
        jnp.einsum("tn,hdn->thd", c_proj.astype(jnp.float32), entering, precision=FULL_PRECISION)
        * enter_weight[:, :, None]
    )
    mixer_out = (inner_out + entered + head_skip_gain[None, :, None] * x_heads).reshape(
        length, channels
    )
    scale = lax.rsqrt(jnp.mean(mixer_out * mixer_out, axis=1, keepdims=True) + NORM_EPSILON)
    normalized_rows = (mixer_out * scale * output_norm_gain[None, :]).astype(jnp.bfloat16)
    term = jnp.dot(
        normalized_rows,
        lax.all_gather(output_weight, "ctx", axis=1, tiled=True),
        preferred_element_type=jnp.float32,
    )
    base = lax.psum_scatter(
        term.astype(jnp.bfloat16), ("tp", "dp"), scatter_dimension=1, tiled=True
    ).astype(jnp.float32)
    lowrank_out_part = select_rows(
        jnp.dot(normalized_rows, down_out, preferred_element_type=jnp.float32),
        adapter_picker_matrix,
    )
    rank_hidden_output = lax.psum(lowrank_out_part.astype(jnp.bfloat16), ("tp", "dp"))
    adapter_term = jnp.dot(
        masked_wide(rank_hidden_output, onehot_b), up_out, preferred_element_type=jnp.float32
    )
    return (base + adapter_term).astype(jnp.bfloat16)


def moved(block, shift, kind):
    side = lax.axis_size("ctx")
    if kind == "ctx":
        pairs = [(a, (a + shift) % side) for a in range(side)]
        return lax.ppermute(block, "ctx", pairs)
    if kind == "lane":
        pairs = [(a, (a + shift) % side) for a in range(side)]
        return lax.ppermute(block, ("tp", "dp"), pairs)
    if kind == "rows":
        pairs = [(a * side + b, b * side + (a + shift) % side) for a in range(side) for b in range(side)]
    else:
        pairs = [(a * side + b, ((b + shift) % side) * side + a) for a in range(side) for b in range(side)]
    return lax.ppermute(block, ("ctx", "tp", "dp"), pairs)


def transposed(block):
    return moved(block, 0, "rows")


def in_order(pieces, place):
    stacked = jnp.stack(pieces[::-1], axis=0)
    ordered = jnp.roll(stacked, place + 1, axis=0)
    return ordered.reshape((-1,) + pieces[0].shape[1:])


def block_rows(values, index, length):
    return lax.dynamic_slice_in_dim(values, index * length, length, 0)


def owned_rows(values, owned):
    return jnp.concatenate(
        [values * owned[:, i : i + 1].astype(values.dtype) for i in range(owned.shape[1])], axis=1
    )


def square_body(
    tokens,
    lengths,
    request_adapter_ids,
    adapter_store_slot,
    xchan_input_weight,
    bc_input_weight,
    step_input_weight,
    convolution_x_taps,
    convolution_bc_taps,
    step_bias,
    decay_log_rate,
    head_skip_gain,
    output_norm_gain,
    output_weight,
    adapter_down_input,
    adapter_up_xchan,
    adapter_up_bc,
    adapter_down_output,
    adapter_up_output,
):
    length = tokens.shape[0]
    side = lax.axis_size("ctx")
    stream = side * length
    taps = convolution_x_taps.shape[0]
    bank_entries = adapter_down_input.shape[0]
    rank_value = adapter_down_input.shape[2]
    head_count = step_bias.shape[0]
    channels = xchan_input_weight.shape[1]
    bc_width = bc_input_weight.shape[1]
    here = lax.axis_index("ctx")
    lane = lax.axis_index(("tp", "dp"))
    start_pos = here * length
    request_ends = jnp.cumsum(lengths, dtype=jnp.int32)
    every_position = jnp.arange(stream, dtype=jnp.int32)
    every_segment = segment_of(every_position, request_ends)
    slot_indices = adapter_store_slot[request_adapter_ids]
    request_count = lengths.shape[0]
    stream_onehot = every_segment[:, None] == jnp.arange(request_count, dtype=jnp.int32)[None, :]
    slot_of_position = jnp.sum(
        jnp.where(stream_onehot, slot_indices[None, :], 0), axis=1, dtype=jnp.int32
    )
    entry_ids = jnp.arange(bank_entries, dtype=jnp.int32)[None, :]
    owned_here = slot_of_position[:, None] == here * bank_entries + entry_ids
    owned_lane = slot_of_position[:, None] == lane * bank_entries + entry_ids
    positions = start_pos + jnp.arange(length, dtype=jnp.int32)
    segment = segment_of(positions, request_ends)
    previous = segment_of(jnp.reshape(start_pos - 1, (1,)), request_ends)[0]

    tokens_t, down_in_local = lax.optimization_barrier((transposed(tokens), adapter_down_input))
    stream_rows = in_order(
        [tokens_t] + [moved(tokens_t, s, "lane") for s in range(1, side)], lane
    )
    local_owned = lax.dynamic_slice_in_dim(slot_of_position, start_pos, length, 0)
    down_pick = jnp.zeros((length, rank_value), jnp.float32)
    for s in range(side):
        piece = down_in_local if s == 0 else moved(down_in_local, s, "ctx")
        first = ((here - s) % side) * bank_entries
        every = jnp.einsum("pf,efr->per", tokens, piece, preferred_element_type=jnp.float32)
        chosen = local_owned[:, None] == first + jnp.arange(bank_entries, dtype=jnp.int32)[None, :]
        down_pick = down_pick + jnp.sum(every * chosen[:, :, None].astype(jnp.float32), axis=1)
    rank_local = (
        down_pick + sum(moved(down_pick, s, "lane") for s in range(1, side))
    ).astype(jnp.bfloat16)
    rank_hidden = in_order(
        [rank_local] + [moved(rank_local, s, "ctx") for s in range(1, side)], here
    )
    hidden_wide = owned_rows(rank_hidden, owned_here)
    xchan_part = jnp.dot(
        stream_rows, xchan_input_weight, preferred_element_type=jnp.float32
    ) + jnp.dot(
        hidden_wide,
        adapter_up_xchan.reshape(bank_entries * rank_value, -1),
        preferred_element_type=jnp.float32,
    )
    bc_part = jnp.dot(stream_rows, bc_input_weight, preferred_element_type=jnp.float32) + jnp.dot(
        hidden_wide,
        adapter_up_bc.reshape(bank_entries * rank_value, -1),
        preferred_element_type=jnp.float32,
    )
    step_part = jnp.dot(stream_rows, step_input_weight, preferred_element_type=jnp.float32)
    projected = jnp.concatenate([xchan_part, bc_part, step_part], axis=1)
    summed = block_rows(projected, here, length)
    for s in range(1, side):
        sent = block_rows(projected, (here + s) % side, length).astype(jnp.bfloat16)
        summed = summed + moved(sent, s, "ctx").astype(jnp.float32)
    summed, up_out_local = lax.optimization_barrier((summed, adapter_up_output))
    up_out_t = transposed(up_out_local)
    values = summed[:, : channels + bc_width]
    step_raw = summed[:, channels + bc_width :]

    kernel = jnp.concatenate([convolution_x_taps, convolution_bc_taps], axis=1)
    tail_rows = passed_along(values[length - (taps - 1) :], "ctx", 1)
    extended = jnp.concatenate([tail_rows, values], axis=0)
    extended_segment = segment_of(
        start_pos - (taps - 1) + jnp.arange(length + taps - 1, dtype=jnp.int32), request_ends
    )
    convolved = jnp.zeros_like(values)
    for tap in range(taps):
        keep = (extended_segment[tap : tap + length] == segment).astype(jnp.float32)
        convolved = convolved + kernel[tap][None, :] * extended[tap : tap + length] * keep[:, None]
    act = jax.nn.silu(convolved)
    x_heads = act[:, :channels].reshape(length, head_count, -1)
    bc_local = act[:, channels:].astype(jnp.bfloat16)
    bc_pieces = [bc_local] + [moved(bc_local, s, "lane") for s in range(1, side)]
    bc_all = jnp.transpose(in_order([piece.T for piece in bc_pieces], lane))
    state_width = bc_all.shape[1] // 2
    b_proj = bc_all[:, :state_width]
    c_proj = bc_all[:, state_width:]
    step_size = jax.nn.softplus(step_raw + step_bias[None, :])
    log_decay = -step_size * jnp.exp(decay_log_rate)[None, :]
    inner_out, local_state, enter_weight, carry_decay = span_parts(
        x_heads, b_proj, c_proj, step_size, log_decay, segment, previous
    )

    decay_row = jnp.broadcast_to(carry_decay[:, None, None], (head_count, 1, local_state.shape[2]))
    state_and_decay = jnp.concatenate([decay_row, local_state], axis=1).astype(jnp.bfloat16)
    if side <= 4:
        prior = lax.ppermute(
            state_and_decay, "ctx", [(a, a + 1) for a in range(side - 1)]
        ).astype(jnp.float32)
        pair_decay = prior[:, :1, :1] * carry_decay[:, None, None]
        pair_state = carry_decay[:, None, None] * prior[:, 1:] + local_state
        pair = jnp.concatenate(
            [jnp.broadcast_to(pair_decay, decay_row.shape), pair_state], axis=1
        ).astype(jnp.bfloat16)
        entering = prior[:, 1:]
        if side > 2:
            far = lax.ppermute(pair, "ctx", [(a, a + 2) for a in range(side - 2)])
            entering = prior[:, :1, :1] * far[:, 1:].astype(jnp.float32) + entering
    else:
        entering = jnp.zeros_like(local_state)
        for s in range(side - 1, 0, -1):
            pairs = [(a, a + s) for a in range(side - s)]
            both_in = lax.ppermute(state_and_decay, "ctx", pairs).astype(jnp.float32)
            entering = both_in[:, :1, :1] * entering + both_in[:, 1:]
    entered = (
        jnp.einsum("tn,hdn->thd", c_proj.astype(jnp.float32), entering, precision=FULL_PRECISION)
        * enter_weight[:, :, None]
    )
    mixer_out = (inner_out + entered + head_skip_gain[None, :, None] * x_heads).reshape(
        length, channels
    )
    scale = lax.rsqrt(jnp.mean(mixer_out * mixer_out, axis=1, keepdims=True) + NORM_EPSILON)
    normalized_rows = (mixer_out * scale * output_norm_gain[None, :]).astype(jnp.bfloat16)

    normed_stream = in_order(
        [normalized_rows] + [moved(normalized_rows, s, "ctx") for s in range(1, side)], here
    )
    out_down_part = jnp.einsum(
        "pc,ecr->per", normed_stream, adapter_down_output, preferred_element_type=jnp.float32
    )
    out_down_pick = jnp.sum(out_down_part * owned_here[:, :, None].astype(jnp.float32), axis=1)
    rank_hidden_output = transposed(
        out_down_pick + sum(moved(out_down_pick, s, "lane") for s in range(1, side))
    )
    base_part = jnp.dot(
        normed_stream, output_weight, preferred_element_type=jnp.float32
    ).astype(jnp.bfloat16).astype(jnp.float32)
    adapter_part = jnp.dot(
        owned_rows(rank_hidden_output, owned_lane).astype(jnp.bfloat16),
        up_out_t.reshape(bank_entries * rank_value, -1),
        preferred_element_type=jnp.float32,
    )
    out_part = base_part + adapter_part
    mixed_t = block_rows(out_part, lane, length)
    for s in range(1, side):
        sent = block_rows(out_part, (lane + s) % side, length).astype(jnp.bfloat16)
        mixed_t = mixed_t + moved(sent, s, "lane").astype(jnp.float32)
    return transposed(mixed_t.astype(jnp.bfloat16))


def solution(mesh):
    body = square_body if mesh.shape["ctx"] == mesh.shape["tp"] * mesh.shape["dp"] else general_body
    placed = (
        P(("groups", "ctx"), ("tp", "dp")),
        P("groups"),
        P("groups"),
        P(),
        P("ctx", ("tp", "dp")),
        P("ctx", ("tp", "dp")),
        P("ctx", ("tp", "dp")),
        P(None, ("tp", "dp")),
        P(None, ("tp", "dp")),
        P(("tp", "dp")),
        P(("tp", "dp")),
        P(("tp", "dp")),
        P(("tp", "dp")),
        P(("tp", "dp"), "ctx"),
        P("ctx", ("tp", "dp"), None),
        P("ctx", None, ("tp", "dp")),
        P("ctx", None, ("tp", "dp")),
        P("ctx", ("tp", "dp"), None),
        P("ctx", None, ("tp", "dp")),
    )
    return jax.shard_map(
        body,
        mesh=mesh,
        in_specs=placed,
        out_specs=P(("groups", "ctx"), ("tp", "dp")),
        check_vma=False,
    )
```

```python
import jax
import jax.numpy as jnp
from jax import lax
from jax.sharding import PartitionSpec as P

FULL_PRECISION = lax.Precision.HIGHEST
NORM_EPSILON = 1e-06


def from_root(block, axis, source):
    block = jnp.where(lax.axis_index(axis) == source, block, jnp.zeros_like(block))
    return lax.psum(block, axis)


def passed_along(shard, axis, by):
    size = lax.axis_size(axis)
    pairs = [(i, i + by) for i in range(size) if 0 <= i + by < size]
    return lax.ppermute(shard, axis, pairs)


def prefix(shard, axis, combine, identity):
    size, place = (lax.axis_size(axis), lax.axis_index(axis))
    everything = jax.tree.map(
        lambda part, kind: lax.all_gather(part.astype(kind), axis),
        shard,
        (jnp.bfloat16, jnp.bfloat16),
    )
    start = jax.tree.map(
        lambda part, zero: jnp.broadcast_to(jnp.asarray(zero, part.dtype), part.shape),
        shard,
        identity,
    )

    def lap(k, before):
        reached = k < place
        new = combine(
            before, jax.tree.map(lambda part, own: part[k].astype(own.dtype), everything, shard)
        )
        return jax.tree.map(lambda a, b: jnp.where(reached, a, b), new, before)

    return lax.fori_loop(0, size, lap, start)


def segment_of(positions, request_ends):
    inside = (positions[:, None] >= request_ends[None, :]).astype(jnp.int32)
    counted = jnp.sum(inside, axis=1, dtype=jnp.int32)
    return jnp.where(positions < 0, jnp.int32(-1), counted)


def span_parts(x_heads, b_proj, c_proj, step_size, log_decay, segment, previous):
    length = x_heads.shape[0]
    cumulative = jnp.cumsum(log_decay, axis=0)
    final_log = cumulative[length - 1]
    places = jnp.arange(length, dtype=jnp.int32)
    same_request = jnp.logical_and(
        segment[:, None] == segment[None, :], places[None, :] <= places[:, None]
    ).astype(jnp.float32)
    log_gap = cumulative.T[:, :, None] - cumulative.T[:, None, :]
    decay_table = jnp.exp(jnp.minimum(log_gap, 0.0)) * same_request[None]
    scores = lax.dot_general(
        c_proj, b_proj, (((1,), (1,)), ((), ())), preferred_element_type=jnp.float32
    )
    weights = scores[None] * decay_table * step_size.T[:, None, :]
    inner_out = jnp.einsum("hts,shd->thd", weights, x_heads, precision=FULL_PRECISION)
    at_end = (segment == segment[length - 1]).astype(jnp.float32)
    state_weight = jnp.exp(final_log[None, :] - cumulative) * at_end[:, None] * step_size
    local_state = jnp.einsum(
        "sh,shd,sn->hdn",
        state_weight,
        x_heads,
        b_proj.astype(jnp.float32),
        precision=FULL_PRECISION,
    )
    enter_weight = jnp.exp(cumulative) * (segment == previous).astype(jnp.float32)[:, None]
    carry_decay = jnp.exp(final_log) * (segment[length - 1] == previous).astype(jnp.float32)
    return (inner_out, local_state, enter_weight, carry_decay)


def select_rows(wide, adapter_picker_matrix):
    shaped = wide.reshape(wide.shape[0], adapter_picker_matrix.shape[1], -1)
    return jnp.sum(shaped * adapter_picker_matrix[:, :, None], axis=1)


def masked_wide(values, onehot_b):
    return (values[:, None, :] * onehot_b[:, :, None]).reshape(values.shape[0], -1)


def general_body(
    tokens,
    lengths,
    request_adapter_ids,
    adapter_store_slot,
    xchan_input_weight,
    bc_input_weight,
    step_input_weight,
    convolution_x_taps,
    convolution_bc_taps,
    step_bias,
    decay_log_rate,
    head_skip_gain,
    output_norm_gain,
    output_weight,
    adapter_down_input,
    adapter_up_xchan,
    adapter_up_bc,
    adapter_down_output,
    adapter_up_output,
):
    length = tokens.shape[0]
    request_list = lengths.shape[0]
    taps = convolution_x_taps.shape[0]
    bank_entries = adapter_down_input.shape[0]
    head_count = step_bias.shape[0]
    channels = xchan_input_weight.shape[1]
    start_pos = lax.axis_index("ctx") * length
    request_ends = jnp.cumsum(lengths, dtype=jnp.int32)
    positions = start_pos + jnp.arange(length, dtype=jnp.int32)
    segment = segment_of(positions, request_ends)
    previous = segment_of(jnp.reshape(start_pos - 1, (1,)), request_ends)[0]
    adapter_picker_matrix = (
        segment[:, None] == jnp.arange(request_list, dtype=jnp.int32)[None, :]
    ).astype(jnp.float32)
    onehot_b = adapter_picker_matrix.astype(jnp.bfloat16)
    slot_indices = adapter_store_slot[request_adapter_ids]
    initial_stacks = (
        jnp.zeros(
            (adapter_down_input.shape[1], request_list, adapter_down_input.shape[2]), jnp.bfloat16
        ),
        jnp.zeros((request_list,) + adapter_up_xchan.shape[1:], jnp.bfloat16),
        jnp.zeros((request_list,) + adapter_up_bc.shape[1:], jnp.bfloat16),
        jnp.zeros(
            (adapter_down_output.shape[1], request_list, adapter_down_output.shape[2]), jnp.bfloat16
        ),
        jnp.zeros((request_list,) + adapter_up_output.shape[1:], jnp.bfloat16),
    )
    stack_dims = (1, 0, 0, 1, 0)

    def fetch(request_item, current):
        slot = slot_indices[request_item]
        owner = slot // bank_entries
        within = slot % bank_entries
        a_in, b_x, b_bc, a_out, b_out = [
            lax.dynamic_index_in_dim(adapter_bank, within, 0, keepdims=False)
            for adapter_bank in (
                adapter_down_input,
                adapter_up_xchan,
                adapter_up_bc,
                adapter_down_output,
                adapter_up_output,
            )
        ]
        received = (
            from_root(a_in, "ctx", owner),
            from_root(b_x, "ctx", owner),
            from_root(b_bc, "ctx", owner),
            from_root(a_out, "ctx", owner),
            from_root(b_out, "ctx", owner),
        )
        return tuple(
            (
                lax.dynamic_update_index_in_dim(stack, panel, request_item, along)
                for stack, panel, along in zip(current, received, stack_dims)
            )
        )

    stacks = lax.fori_loop(0, request_list, fetch, initial_stacks)
    rank_value = adapter_down_input.shape[2]
    down_in = stacks[0].reshape(stacks[0].shape[0], request_list * rank_value)
    up_x = stacks[1].reshape(request_list * rank_value, -1)
    up_bc = stacks[2].reshape(request_list * rank_value, -1)
    down_out = stacks[3].reshape(stacks[3].shape[0], request_list * rank_value)
    up_out = stacks[4].reshape(request_list * rank_value, -1)
    lowrank_part = select_rows(
        jnp.dot(tokens, down_in, preferred_element_type=jnp.float32), adapter_picker_matrix
    )
    rank_hidden = lax.psum(lowrank_part.astype(jnp.bfloat16), ("tp", "dp"))
    lowrank_wide = masked_wide(rank_hidden, onehot_b)
    full_tokens = lax.all_gather(tokens, ("tp", "dp"), axis=1, tiled=True)
    pieces = (
        lax.all_gather(xchan_input_weight, "ctx", axis=0, tiled=True),
        lax.all_gather(bc_input_weight, "ctx", axis=0, tiled=True),
        lax.all_gather(step_input_weight, "ctx", axis=0, tiled=True),
    )
    xchan_values, bc_channel_values, step_raw = tuple(
        (jnp.dot(full_tokens, piece, preferred_element_type=jnp.float32) for piece in pieces)
    )
    xchan_values = xchan_values + jnp.dot(lowrank_wide, up_x, preferred_element_type=jnp.float32)
    bc_channel_values = bc_channel_values + jnp.dot(
        lowrank_wide, up_bc, preferred_element_type=jnp.float32
    )
    values = jnp.concatenate([xchan_values, bc_channel_values], axis=1)
    kernel = jnp.concatenate([convolution_x_taps, convolution_bc_taps], axis=1)
    tail_rows = passed_along(values[length - (taps - 1) :], "ctx", 1)
    extended = jnp.concatenate([tail_rows, values], axis=0)
    extended_segment = segment_of(
        start_pos - (taps - 1) + jnp.arange(length + taps - 1, dtype=jnp.int32), request_ends
    )
    convolved = jnp.zeros_like(values)
    for tap in range(taps):
        keep = (extended_segment[tap : tap + length] == segment).astype(jnp.float32)
        convolved = convolved + kernel[tap][None, :] * extended[tap : tap + length] * keep[:, None]
    act = jax.nn.silu(convolved)
    x_heads = act[:, :channels].reshape(length, head_count, -1)
    bc_local = act[:, channels:].astype(jnp.bfloat16)
    bc_all = lax.all_gather(bc_local, ("tp", "dp"), axis=1, tiled=True)
    state_width = bc_all.shape[1] // 2
    b_proj = bc_all[:, :state_width]
    c_proj = bc_all[:, state_width:]
    step_size = jax.nn.softplus(step_raw + step_bias[None, :])
    log_decay = -step_size * jnp.exp(decay_log_rate)[None, :]
    inner_out, local_state, enter_weight, carry_decay = span_parts(
        x_heads, b_proj, c_proj, step_size, log_decay, segment, previous
    )

    def compose(earlier, later):
        return (earlier[0] * later[0], later[0][:, None, None] * earlier[1] + later[1])

    carried = prefix(
        (carry_decay, local_state),
        "ctx",
        compose,
        (jnp.ones_like(carry_decay), jnp.zeros_like(local_state)),
    )
    entering = carried[1]
    entered = (
        jnp.einsum("tn,hdn->thd", c_proj.astype(jnp.float32), entering, precision=FULL_PRECISION)
        * enter_weight[:, :, None]
    )
    mixer_out = (inner_out + entered + head_skip_gain[None, :, None] * x_heads).reshape(
        length, channels
    )
    scale = lax.rsqrt(jnp.mean(mixer_out * mixer_out, axis=1, keepdims=True) + NORM_EPSILON)
    normalized_rows = (mixer_out * scale * output_norm_gain[None, :]).astype(jnp.bfloat16)
    term = jnp.dot(
        normalized_rows,
        lax.all_gather(output_weight, "ctx", axis=1, tiled=True),
        preferred_element_type=jnp.float32,
    )
    base = lax.psum_scatter(
        term.astype(jnp.bfloat16), ("tp", "dp"), scatter_dimension=1, tiled=True
    ).astype(jnp.float32)
    lowrank_out_part = select_rows(
        jnp.dot(normalized_rows, down_out, preferred_element_type=jnp.float32),
        adapter_picker_matrix,
    )
    rank_hidden_output = lax.psum(lowrank_out_part.astype(jnp.bfloat16), ("tp", "dp"))
    adapter_term = jnp.dot(
        masked_wide(rank_hidden_output, onehot_b), up_out, preferred_element_type=jnp.float32
    )
    return (base + adapter_term).astype(jnp.bfloat16)


def moved(block, shift, kind):
    side = lax.axis_size("ctx")
    if kind == "ctx":
        pairs = [(a, (a + shift) % side) for a in range(side)]
        return lax.ppermute(block, "ctx", pairs)
    if kind == "lane":
        pairs = [(a, (a + shift) % side) for a in range(side)]
        return lax.ppermute(block, ("tp", "dp"), pairs)
    if kind == "rows":
        pairs = [(a * side + b, b * side + (a + shift) % side) for a in range(side) for b in range(side)]
    else:
        pairs = [(a * side + b, ((b + shift) % side) * side + a) for a in range(side) for b in range(side)]
    return lax.ppermute(block, ("ctx", "tp", "dp"), pairs)


def transposed(block):
    return moved(block, 0, "rows")


def in_order(pieces, place):
    stacked = jnp.stack(pieces[::-1], axis=0)
    ordered = jnp.roll(stacked, place + 1, axis=0)
    return ordered.reshape((-1,) + pieces[0].shape[1:])


def block_rows(values, index, length):
    return lax.dynamic_slice_in_dim(values, index * length, length, 0)


def owned_rows(values, owned):
    return jnp.concatenate(
        [values * owned[:, i : i + 1].astype(values.dtype) for i in range(owned.shape[1])], axis=1
    )


def square_body(
    tokens,
    lengths,
    request_adapter_ids,
    adapter_store_slot,
    xchan_input_weight,
    bc_input_weight,
    step_input_weight,
    convolution_x_taps,
    convolution_bc_taps,
    step_bias,
    decay_log_rate,
    head_skip_gain,
    output_norm_gain,
    output_weight,
    adapter_down_input,
    adapter_up_xchan,
    adapter_up_bc,
    adapter_down_output,
    adapter_up_output,
):
    length = tokens.shape[0]
    side = lax.axis_size("ctx")
    stream = side * length
    taps = convolution_x_taps.shape[0]
    bank_entries = adapter_down_input.shape[0]
    rank_value = adapter_down_input.shape[2]
    head_count = step_bias.shape[0]
    channels = xchan_input_weight.shape[1]
    bc_width = bc_input_weight.shape[1]
    here = lax.axis_index("ctx")
    lane = lax.axis_index(("tp", "dp"))
    start_pos = here * length
    request_ends = jnp.cumsum(lengths, dtype=jnp.int32)
    every_position = jnp.arange(stream, dtype=jnp.int32)
    every_segment = segment_of(every_position, request_ends)
    slot_indices = adapter_store_slot[request_adapter_ids]
    request_count = lengths.shape[0]
    stream_onehot = every_segment[:, None] == jnp.arange(request_count, dtype=jnp.int32)[None, :]
    slot_of_position = jnp.sum(
        jnp.where(stream_onehot, slot_indices[None, :], 0), axis=1, dtype=jnp.int32
    )
    entry_ids = jnp.arange(bank_entries, dtype=jnp.int32)[None, :]
    owned_here = slot_of_position[:, None] == here * bank_entries + entry_ids
    owned_lane = slot_of_position[:, None] == lane * bank_entries + entry_ids
    positions = start_pos + jnp.arange(length, dtype=jnp.int32)
    segment = segment_of(positions, request_ends)
    previous = segment_of(jnp.reshape(start_pos - 1, (1,)), request_ends)[0]

    tokens_t, down_in_local = lax.optimization_barrier((transposed(tokens), adapter_down_input))
    stream_rows = in_order(
        [tokens_t] + [moved(tokens_t, s, "lane") for s in range(1, side)], lane
    )
    local_owned = lax.dynamic_slice_in_dim(slot_of_position, start_pos, length, 0)
    down_pick = jnp.zeros((length, rank_value), jnp.float32)
    for s in range(side):
        piece = down_in_local if s == 0 else moved(down_in_local, s, "ctx")
        first = ((here - s) % side) * bank_entries
        every = jnp.einsum("pf,efr->per", tokens, piece, preferred_element_type=jnp.float32)
        chosen = local_owned[:, None] == first + jnp.arange(bank_entries, dtype=jnp.int32)[None, :]
        down_pick = down_pick + jnp.sum(every * chosen[:, :, None].astype(jnp.float32), axis=1)
    rank_local = (
        down_pick + sum(moved(down_pick, s, "lane") for s in range(1, side))
    ).astype(jnp.bfloat16)
    rank_hidden = in_order(
        [rank_local] + [moved(rank_local, s, "ctx") for s in range(1, side)], here
    )
    hidden_wide = owned_rows(rank_hidden, owned_here)
    xchan_part = jnp.dot(
        stream_rows, xchan_input_weight, preferred_element_type=jnp.float32
    ) + jnp.dot(
        hidden_wide,
        adapter_up_xchan.reshape(bank_entries * rank_value, -1),
        preferred_element_type=jnp.float32,
    )
    bc_part = jnp.dot(stream_rows, bc_input_weight, preferred_element_type=jnp.float32) + jnp.dot(
        hidden_wide,
        adapter_up_bc.reshape(bank_entries * rank_value, -1),
        preferred_element_type=jnp.float32,
    )
    step_part = jnp.dot(stream_rows, step_input_weight, preferred_element_type=jnp.float32)
    projected = jnp.concatenate([xchan_part, bc_part, step_part], axis=1)
    summed = block_rows(projected, here, length)
    for s in range(1, side):
        sent = block_rows(projected, (here + s) % side, length).astype(jnp.bfloat16)
        summed = summed + moved(sent, s, "ctx").astype(jnp.float32)
    summed, up_out_local = lax.optimization_barrier((summed, adapter_up_output))
    up_out_t = transposed(up_out_local)
    values = summed[:, : channels + bc_width]
    step_raw = summed[:, channels + bc_width :]

    kernel = jnp.concatenate([convolution_x_taps, convolution_bc_taps], axis=1)
    tail_rows = passed_along(values[length - (taps - 1) :], "ctx", 1)
    extended = jnp.concatenate([tail_rows, values], axis=0)
    extended_segment = segment_of(
        start_pos - (taps - 1) + jnp.arange(length + taps - 1, dtype=jnp.int32), request_ends
    )
    convolved = jnp.zeros_like(values)
    for tap in range(taps):
        keep = (extended_segment[tap : tap + length] == segment).astype(jnp.float32)
        convolved = convolved + kernel[tap][None, :] * extended[tap : tap + length] * keep[:, None]
    act = jax.nn.silu(convolved)
    x_heads = act[:, :channels].reshape(length, head_count, -1)
    bc_local = act[:, channels:].astype(jnp.bfloat16)
    bc_pieces = [bc_local] + [moved(bc_local, s, "lane") for s in range(1, side)]
    bc_all = jnp.transpose(in_order([piece.T for piece in bc_pieces], lane))
    state_width = bc_all.shape[1] // 2
    b_proj = bc_all[:, :state_width]
    c_proj = bc_all[:, state_width:]
    step_size = jax.nn.softplus(step_raw + step_bias[None, :])
    log_decay = -step_size * jnp.exp(decay_log_rate)[None, :]
    inner_out, local_state, enter_weight, carry_decay = span_parts(
        x_heads, b_proj, c_proj, step_size, log_decay, segment, previous
    )

    decay_row = jnp.broadcast_to(carry_decay[:, None, None], (head_count, 1, local_state.shape[2]))
    state_and_decay = jnp.concatenate([decay_row, local_state], axis=1).astype(jnp.bfloat16)
    if side <= 4:
        prior = lax.ppermute(
            state_and_decay, "ctx", [(a, a + 1) for a in range(side - 1)]
        ).astype(jnp.float32)
        pair_decay = prior[:, :1, :1] * carry_decay[:, None, None]
        pair_state = carry_decay[:, None, None] * prior[:, 1:] + local_state
        pair = jnp.concatenate(
            [jnp.broadcast_to(pair_decay, decay_row.shape), pair_state], axis=1
        ).astype(jnp.bfloat16)
        entering = prior[:, 1:]
        if side > 2:
            far = lax.ppermute(pair, "ctx", [(a, a + 2) for a in range(side - 2)])
            entering = prior[:, :1, :1] * far[:, 1:].astype(jnp.float32) + entering
    else:
        entering = jnp.zeros_like(local_state)
        for s in range(side - 1, 0, -1):
            pairs = [(a, a + s) for a in range(side - s)]
            both_in = lax.ppermute(state_and_decay, "ctx", pairs).astype(jnp.float32)
            entering = both_in[:, :1, :1] * entering + both_in[:, 1:]
    entered = (
        jnp.einsum("tn,hdn->thd", c_proj.astype(jnp.float32), entering, precision=FULL_PRECISION)
        * enter_weight[:, :, None]
    )
    mixer_out = (inner_out + entered + head_skip_gain[None, :, None] * x_heads).reshape(
        length, channels
    )
    scale = lax.rsqrt(jnp.mean(mixer_out * mixer_out, axis=1, keepdims=True) + NORM_EPSILON)
    normalized_rows = (mixer_out * scale * output_norm_gain[None, :]).astype(jnp.bfloat16)

    normed_stream = in_order(
        [normalized_rows] + [moved(normalized_rows, s, "ctx") for s in range(1, side)], here
    )
    out_down_part = jnp.einsum(
        "pc,ecr->per", normed_stream, adapter_down_output, preferred_element_type=jnp.float32
    )
    out_down_pick = jnp.sum(out_down_part * owned_here[:, :, None].astype(jnp.float32), axis=1)
    rank_hidden_output = transposed(
        out_down_pick + sum(moved(out_down_pick, s, "lane") for s in range(1, side))
    )
    base_part = jnp.dot(
        normed_stream, output_weight, preferred_element_type=jnp.float32
    ).astype(jnp.bfloat16).astype(jnp.float32)
    adapter_part = jnp.dot(
        owned_rows(rank_hidden_output, owned_lane).astype(jnp.bfloat16),
        up_out_t.reshape(bank_entries * rank_value, -1),
        preferred_element_type=jnp.float32,
    )
    out_part = base_part + adapter_part
    if lax.axis_size("tp") == 2 and lax.axis_size("dp") == 2:
        core = lax.axis_index("dp")
        chip = lax.axis_index("tp")
        blocks = out_part.reshape(side, length, -1)

        def pick(index):
            return lax.dynamic_index_in_dim(blocks, index, 0, keepdims=False)

        swapped = lax.ppermute(
            jnp.stack([pick(1 - core), pick(3 - core)]).astype(jnp.bfloat16),
            "dp",
            [(0, 1), (1, 0)],
        ).astype(jnp.float32)
        near = pick(core) + swapped[0]
        far = pick(2 + core) + swapped[1]
        mixed_t = jnp.where(chip == 0, near, far)
        crossing = jnp.where(chip == 0, far, near).astype(jnp.bfloat16)
        mixed_t = mixed_t + lax.ppermute(crossing, "tp", [(0, 1), (1, 0)]).astype(jnp.float32)
    else:
        mixed_t = block_rows(out_part, lane, length)
        for s in range(1, side):
            sent = block_rows(out_part, (lane + s) % side, length).astype(jnp.bfloat16)
            mixed_t = mixed_t + moved(sent, s, "lane").astype(jnp.float32)
    return transposed(mixed_t.astype(jnp.bfloat16))


def solution(mesh):
    body = square_body if mesh.shape["ctx"] == mesh.shape["tp"] * mesh.shape["dp"] else general_body
    placed = (
        P(("groups", "ctx"), ("tp", "dp")),
        P("groups"),
        P("groups"),
        P(),
        P("ctx", ("tp", "dp")),
        P("ctx", ("tp", "dp")),
        P("ctx", ("tp", "dp")),
        P(None, ("tp", "dp")),
        P(None, ("tp", "dp")),
        P(("tp", "dp")),
        P(("tp", "dp")),
        P(("tp", "dp")),
        P(("tp", "dp")),
        P(("tp", "dp"), "ctx"),
        P("ctx", ("tp", "dp"), None),
        P("ctx", None, ("tp", "dp")),
        P("ctx", None, ("tp", "dp")),
        P("ctx", ("tp", "dp"), None),
        P("ctx", None, ("tp", "dp")),
    )
    return jax.shard_map(
        body,
        mesh=mesh,
        in_specs=placed,
        out_specs=P(("groups", "ctx"), ("tp", "dp")),
        check_vma=False,
    )
```

```python
import jax
import jax.numpy as jnp
from jax import lax
from jax.sharding import PartitionSpec as P

FULL_PRECISION = lax.Precision.HIGHEST
NORM_EPSILON = 1e-06


def from_root(block, axis, source):
    block = jnp.where(lax.axis_index(axis) == source, block, jnp.zeros_like(block))
    return lax.psum(block, axis)


def passed_along(shard, axis, by):
    size = lax.axis_size(axis)
    pairs = [(i, i + by) for i in range(size) if 0 <= i + by < size]
    return lax.ppermute(shard, axis, pairs)


def prefix(shard, axis, combine, identity):
    size, place = (lax.axis_size(axis), lax.axis_index(axis))
    everything = jax.tree.map(
        lambda part, kind: lax.all_gather(part.astype(kind), axis),
        shard,
        (jnp.bfloat16, jnp.bfloat16),
    )
    start = jax.tree.map(
        lambda part, zero: jnp.broadcast_to(jnp.asarray(zero, part.dtype), part.shape),
        shard,
        identity,
    )

    def lap(k, before):
        reached = k < place
        new = combine(
            before, jax.tree.map(lambda part, own: part[k].astype(own.dtype), everything, shard)
        )
        return jax.tree.map(lambda a, b: jnp.where(reached, a, b), new, before)

    return lax.fori_loop(0, size, lap, start)


def segment_of(positions, request_ends):
    inside = (positions[:, None] >= request_ends[None, :]).astype(jnp.int32)
    counted = jnp.sum(inside, axis=1, dtype=jnp.int32)
    return jnp.where(positions < 0, jnp.int32(-1), counted)


def span_parts(x_heads, b_proj, c_proj, step_size, log_decay, segment, previous):
    length = x_heads.shape[0]
    cumulative = jnp.cumsum(log_decay, axis=0)
    final_log = cumulative[length - 1]
    places = jnp.arange(length, dtype=jnp.int32)
    same_request = jnp.logical_and(
        segment[:, None] == segment[None, :], places[None, :] <= places[:, None]
    ).astype(jnp.float32)
    log_gap = cumulative.T[:, :, None] - cumulative.T[:, None, :]
    decay_table = jnp.exp(jnp.minimum(log_gap, 0.0)) * same_request[None]
    scores = lax.dot_general(
        c_proj, b_proj, (((1,), (1,)), ((), ())), preferred_element_type=jnp.float32
    )
    weights = scores[None] * decay_table * step_size.T[:, None, :]
    inner_out = jnp.einsum("hts,shd->thd", weights, x_heads, precision=FULL_PRECISION)
    at_end = (segment == segment[length - 1]).astype(jnp.float32)
    state_weight = jnp.exp(final_log[None, :] - cumulative) * at_end[:, None] * step_size
    local_state = jnp.einsum(
        "sh,shd,sn->hdn",
        state_weight,
        x_heads,
        b_proj.astype(jnp.float32),
        precision=FULL_PRECISION,
    )
    enter_weight = jnp.exp(cumulative) * (segment == previous).astype(jnp.float32)[:, None]
    carry_decay = jnp.exp(final_log) * (segment[length - 1] == previous).astype(jnp.float32)
    return (inner_out, local_state, enter_weight, carry_decay)


def select_rows(wide, adapter_picker_matrix):
    shaped = wide.reshape(wide.shape[0], adapter_picker_matrix.shape[1], -1)
    return jnp.sum(shaped * adapter_picker_matrix[:, :, None], axis=1)


def masked_wide(values, onehot_b):
    return (values[:, None, :] * onehot_b[:, :, None]).reshape(values.shape[0], -1)


def general_body(
    tokens,
    lengths,
    request_adapter_ids,
    adapter_store_slot,
    xchan_input_weight,
    bc_input_weight,
    step_input_weight,
    convolution_x_taps,
    convolution_bc_taps,
    step_bias,
    decay_log_rate,
    head_skip_gain,
    output_norm_gain,
    output_weight,
    adapter_down_input,
    adapter_up_xchan,
    adapter_up_bc,
    adapter_down_output,
    adapter_up_output,
):
    length = tokens.shape[0]
    request_list = lengths.shape[0]
    taps = convolution_x_taps.shape[0]
    bank_entries = adapter_down_input.shape[0]
    head_count = step_bias.shape[0]
    channels = xchan_input_weight.shape[1]
    start_pos = lax.axis_index("ctx") * length
    request_ends = jnp.cumsum(lengths, dtype=jnp.int32)
    positions = start_pos + jnp.arange(length, dtype=jnp.int32)
    segment = segment_of(positions, request_ends)
    previous = segment_of(jnp.reshape(start_pos - 1, (1,)), request_ends)[0]
    adapter_picker_matrix = (
        segment[:, None] == jnp.arange(request_list, dtype=jnp.int32)[None, :]
    ).astype(jnp.float32)
    onehot_b = adapter_picker_matrix.astype(jnp.bfloat16)
    slot_indices = adapter_store_slot[request_adapter_ids]
    initial_stacks = (
        jnp.zeros(
            (adapter_down_input.shape[1], request_list, adapter_down_input.shape[2]), jnp.bfloat16
        ),
        jnp.zeros((request_list,) + adapter_up_xchan.shape[1:], jnp.bfloat16),
        jnp.zeros((request_list,) + adapter_up_bc.shape[1:], jnp.bfloat16),
        jnp.zeros(
            (adapter_down_output.shape[1], request_list, adapter_down_output.shape[2]), jnp.bfloat16
        ),
        jnp.zeros((request_list,) + adapter_up_output.shape[1:], jnp.bfloat16),
    )
    stack_dims = (1, 0, 0, 1, 0)

    def fetch(request_item, current):
        slot = slot_indices[request_item]
        owner = slot // bank_entries
        within = slot % bank_entries
        a_in, b_x, b_bc, a_out, b_out = [
            lax.dynamic_index_in_dim(adapter_bank, within, 0, keepdims=False)
            for adapter_bank in (
                adapter_down_input,
                adapter_up_xchan,
                adapter_up_bc,
                adapter_down_output,
                adapter_up_output,
            )
        ]
        received = (
            from_root(a_in, "ctx", owner),
            from_root(b_x, "ctx", owner),
            from_root(b_bc, "ctx", owner),
            from_root(a_out, "ctx", owner),
            from_root(b_out, "ctx", owner),
        )
        return tuple(
            (
                lax.dynamic_update_index_in_dim(stack, panel, request_item, along)
                for stack, panel, along in zip(current, received, stack_dims)
            )
        )

    stacks = lax.fori_loop(0, request_list, fetch, initial_stacks)
    rank_value = adapter_down_input.shape[2]
    down_in = stacks[0].reshape(stacks[0].shape[0], request_list * rank_value)
    up_x = stacks[1].reshape(request_list * rank_value, -1)
    up_bc = stacks[2].reshape(request_list * rank_value, -1)
    down_out = stacks[3].reshape(stacks[3].shape[0], request_list * rank_value)
    up_out = stacks[4].reshape(request_list * rank_value, -1)
    lowrank_part = select_rows(
        jnp.dot(tokens, down_in, preferred_element_type=jnp.float32), adapter_picker_matrix
    )
    rank_hidden = lax.psum(lowrank_part.astype(jnp.bfloat16), ("tp", "dp"))
    lowrank_wide = masked_wide(rank_hidden, onehot_b)
    full_tokens = lax.all_gather(tokens, ("tp", "dp"), axis=1, tiled=True)
    pieces = (
        lax.all_gather(xchan_input_weight, "ctx", axis=0, tiled=True),
        lax.all_gather(bc_input_weight, "ctx", axis=0, tiled=True),
        lax.all_gather(step_input_weight, "ctx", axis=0, tiled=True),
    )
    xchan_values, bc_channel_values, step_raw = tuple(
        (jnp.dot(full_tokens, piece, preferred_element_type=jnp.float32) for piece in pieces)
    )
    xchan_values = xchan_values + jnp.dot(lowrank_wide, up_x, preferred_element_type=jnp.float32)
    bc_channel_values = bc_channel_values + jnp.dot(
        lowrank_wide, up_bc, preferred_element_type=jnp.float32
    )
    values = jnp.concatenate([xchan_values, bc_channel_values], axis=1)
    kernel = jnp.concatenate([convolution_x_taps, convolution_bc_taps], axis=1)
    tail_rows = passed_along(values[length - (taps - 1) :], "ctx", 1)
    extended = jnp.concatenate([tail_rows, values], axis=0)
    extended_segment = segment_of(
        start_pos - (taps - 1) + jnp.arange(length + taps - 1, dtype=jnp.int32), request_ends
    )
    convolved = jnp.zeros_like(values)
    for tap in range(taps):
        keep = (extended_segment[tap : tap + length] == segment).astype(jnp.float32)
        convolved = convolved + kernel[tap][None, :] * extended[tap : tap + length] * keep[:, None]
    act = jax.nn.silu(convolved)
    x_heads = act[:, :channels].reshape(length, head_count, -1)
    bc_local = act[:, channels:].astype(jnp.bfloat16)
    bc_all = lax.all_gather(bc_local, ("tp", "dp"), axis=1, tiled=True)
    state_width = bc_all.shape[1] // 2
    b_proj = bc_all[:, :state_width]
    c_proj = bc_all[:, state_width:]
    step_size = jax.nn.softplus(step_raw + step_bias[None, :])
    log_decay = -step_size * jnp.exp(decay_log_rate)[None, :]
    inner_out, local_state, enter_weight, carry_decay = span_parts(
        x_heads, b_proj, c_proj, step_size, log_decay, segment, previous
    )

    def compose(earlier, later):
        return (earlier[0] * later[0], later[0][:, None, None] * earlier[1] + later[1])

    carried = prefix(
        (carry_decay, local_state),
        "ctx",
        compose,
        (jnp.ones_like(carry_decay), jnp.zeros_like(local_state)),
    )
    entering = carried[1]
    entered = (
        jnp.einsum("tn,hdn->thd", c_proj.astype(jnp.float32), entering, precision=FULL_PRECISION)
        * enter_weight[:, :, None]
    )
    mixer_out = (inner_out + entered + head_skip_gain[None, :, None] * x_heads).reshape(
        length, channels
    )
    scale = lax.rsqrt(jnp.mean(mixer_out * mixer_out, axis=1, keepdims=True) + NORM_EPSILON)
    normalized_rows = (mixer_out * scale * output_norm_gain[None, :]).astype(jnp.bfloat16)
    term = jnp.dot(
        normalized_rows,
        lax.all_gather(output_weight, "ctx", axis=1, tiled=True),
        preferred_element_type=jnp.float32,
    )
    base = lax.psum_scatter(
        term.astype(jnp.bfloat16), ("tp", "dp"), scatter_dimension=1, tiled=True
    ).astype(jnp.float32)
    lowrank_out_part = select_rows(
        jnp.dot(normalized_rows, down_out, preferred_element_type=jnp.float32),
        adapter_picker_matrix,
    )
    rank_hidden_output = lax.psum(lowrank_out_part.astype(jnp.bfloat16), ("tp", "dp"))
    adapter_term = jnp.dot(
        masked_wide(rank_hidden_output, onehot_b), up_out, preferred_element_type=jnp.float32
    )
    return (base + adapter_term).astype(jnp.bfloat16)


def moved(block, shift, kind):
    side = lax.axis_size("ctx")
    if kind == "ctx":
        pairs = [(a, (a + shift) % side) for a in range(side)]
        return lax.ppermute(block, "ctx", pairs)
    if kind == "lane":
        pairs = [(a, (a + shift) % side) for a in range(side)]
        return lax.ppermute(block, ("tp", "dp"), pairs)
    if kind == "rows":
        pairs = [(a * side + b, b * side + (a + shift) % side) for a in range(side) for b in range(side)]
    else:
        pairs = [(a * side + b, ((b + shift) % side) * side + a) for a in range(side) for b in range(side)]
    return lax.ppermute(block, ("ctx", "tp", "dp"), pairs)


def transposed(block):
    return moved(block, 0, "rows")


def in_order(pieces, place):
    stacked = jnp.stack(pieces[::-1], axis=0)
    ordered = jnp.roll(stacked, place + 1, axis=0)
    return ordered.reshape((-1,) + pieces[0].shape[1:])


def block_rows(values, index, length):
    return lax.dynamic_slice_in_dim(values, index * length, length, 0)


def owned_rows(values, owned):
    return jnp.concatenate(
        [values * owned[:, i : i + 1].astype(values.dtype) for i in range(owned.shape[1])], axis=1
    )


def lane_pair():
    return lax.axis_size("tp") == 2 and lax.axis_size("dp") == 2


def lane_sum(part):
    if lane_pair():
        part = part + lax.ppermute(part, "dp", [(0, 1), (1, 0)])
        return part + lax.ppermute(part, "tp", [(0, 1), (1, 0)])
    side = lax.axis_size("ctx")
    return part + sum(moved(part, s, "lane") for s in range(1, side))


def lane_rows(piece):
    if lane_pair():
        other = lax.ppermute(piece, "dp", [(0, 1), (1, 0)])
        first = lax.axis_index("dp") == 0
        pair = jnp.where(first, jnp.concatenate([piece, other]), jnp.concatenate([other, piece]))
        other = lax.ppermute(pair, "tp", [(0, 1), (1, 0)])
        first = lax.axis_index("tp") == 0
        return jnp.where(first, jnp.concatenate([pair, other]), jnp.concatenate([other, pair]))
    side = lax.axis_size("ctx")
    return in_order(
        [piece] + [moved(piece, s, "lane") for s in range(1, side)], lax.axis_index(("tp", "dp"))
    )


def square_body(
    tokens,
    lengths,
    request_adapter_ids,
    adapter_store_slot,
    xchan_input_weight,
    bc_input_weight,
    step_input_weight,
    convolution_x_taps,
    convolution_bc_taps,
    step_bias,
    decay_log_rate,
    head_skip_gain,
    output_norm_gain,
    output_weight,
    adapter_down_input,
    adapter_up_xchan,
    adapter_up_bc,
    adapter_down_output,
    adapter_up_output,
):
    length = tokens.shape[0]
    side = lax.axis_size("ctx")
    stream = side * length
    taps = convolution_x_taps.shape[0]
    bank_entries = adapter_down_input.shape[0]
    rank_value = adapter_down_input.shape[2]
    head_count = step_bias.shape[0]
    channels = xchan_input_weight.shape[1]
    bc_width = bc_input_weight.shape[1]
    here = lax.axis_index("ctx")
    lane = lax.axis_index(("tp", "dp"))
    start_pos = here * length
    request_ends = jnp.cumsum(lengths, dtype=jnp.int32)
    every_position = jnp.arange(stream, dtype=jnp.int32)
    every_segment = segment_of(every_position, request_ends)
    slot_indices = adapter_store_slot[request_adapter_ids]
    request_count = lengths.shape[0]
    stream_onehot = every_segment[:, None] == jnp.arange(request_count, dtype=jnp.int32)[None, :]
    slot_of_position = jnp.sum(
        jnp.where(stream_onehot, slot_indices[None, :], 0), axis=1, dtype=jnp.int32
    )
    entry_ids = jnp.arange(bank_entries, dtype=jnp.int32)[None, :]
    owned_here = slot_of_position[:, None] == here * bank_entries + entry_ids
    owned_lane = slot_of_position[:, None] == lane * bank_entries + entry_ids
    positions = start_pos + jnp.arange(length, dtype=jnp.int32)
    segment = segment_of(positions, request_ends)
    previous = segment_of(jnp.reshape(start_pos - 1, (1,)), request_ends)[0]

    tokens_t, down_in_local = lax.optimization_barrier((transposed(tokens), adapter_down_input))
    stream_rows = lane_rows(tokens_t)
    local_owned = lax.dynamic_slice_in_dim(slot_of_position, start_pos, length, 0)
    down_pick = jnp.zeros((length, rank_value), jnp.float32)
    for s in range(side):
        piece = down_in_local if s == 0 else moved(down_in_local, s, "ctx")
        first = ((here - s) % side) * bank_entries
        every = jnp.einsum("pf,efr->per", tokens, piece, preferred_element_type=jnp.float32)
        chosen = local_owned[:, None] == first + jnp.arange(bank_entries, dtype=jnp.int32)[None, :]
        down_pick = down_pick + jnp.sum(every * chosen[:, :, None].astype(jnp.float32), axis=1)
    rank_local = lane_sum(down_pick).astype(jnp.bfloat16)
    rank_hidden = in_order(
        [rank_local] + [moved(rank_local, s, "ctx") for s in range(1, side)], here
    )
    hidden_wide = owned_rows(rank_hidden, owned_here)
    xchan_part = jnp.dot(
        stream_rows, xchan_input_weight, preferred_element_type=jnp.float32
    ) + jnp.dot(
        hidden_wide,
        adapter_up_xchan.reshape(bank_entries * rank_value, -1),
        preferred_element_type=jnp.float32,
    )
    bc_part = jnp.dot(stream_rows, bc_input_weight, preferred_element_type=jnp.float32) + jnp.dot(
        hidden_wide,
        adapter_up_bc.reshape(bank_entries * rank_value, -1),
        preferred_element_type=jnp.float32,
    )
    step_part = jnp.dot(stream_rows, step_input_weight, preferred_element_type=jnp.float32)
    projected = jnp.concatenate([xchan_part, bc_part, step_part], axis=1)
    summed = block_rows(projected, here, length)
    for s in range(1, side):
        sent = block_rows(projected, (here + s) % side, length).astype(jnp.bfloat16)
        summed = summed + moved(sent, s, "ctx").astype(jnp.float32)
    summed, up_out_local = lax.optimization_barrier((summed, adapter_up_output))
    up_out_t = transposed(up_out_local)
    values = summed[:, : channels + bc_width]
    step_raw = summed[:, channels + bc_width :]

    kernel = jnp.concatenate([convolution_x_taps, convolution_bc_taps], axis=1)
    tail_rows = passed_along(values[length - (taps - 1) :], "ctx", 1)
    extended = jnp.concatenate([tail_rows, values], axis=0)
    extended_segment = segment_of(
        start_pos - (taps - 1) + jnp.arange(length + taps - 1, dtype=jnp.int32), request_ends
    )
    convolved = jnp.zeros_like(values)
    for tap in range(taps):
        keep = (extended_segment[tap : tap + length] == segment).astype(jnp.float32)
        convolved = convolved + kernel[tap][None, :] * extended[tap : tap + length] * keep[:, None]
    act = jax.nn.silu(convolved)
    x_heads = act[:, :channels].reshape(length, head_count, -1)
    bc_local = act[:, channels:].astype(jnp.bfloat16)
    bc_all = jnp.transpose(lane_rows(bc_local.T))
    state_width = bc_all.shape[1] // 2
    b_proj = bc_all[:, :state_width]
    c_proj = bc_all[:, state_width:]
    step_size = jax.nn.softplus(step_raw + step_bias[None, :])
    log_decay = -step_size * jnp.exp(decay_log_rate)[None, :]
    inner_out, local_state, enter_weight, carry_decay = span_parts(
        x_heads, b_proj, c_proj, step_size, log_decay, segment, previous
    )

    decay_row = jnp.broadcast_to(carry_decay[:, None, None], (head_count, 1, local_state.shape[2]))
    state_and_decay = jnp.concatenate([decay_row, local_state], axis=1).astype(jnp.bfloat16)
    if side <= 4:
        prior = lax.ppermute(
            state_and_decay, "ctx", [(a, a + 1) for a in range(side - 1)]
        ).astype(jnp.float32)
        pair_decay = prior[:, :1, :1] * carry_decay[:, None, None]
        pair_state = carry_decay[:, None, None] * prior[:, 1:] + local_state
        pair = jnp.concatenate(
            [jnp.broadcast_to(pair_decay, decay_row.shape), pair_state], axis=1
        ).astype(jnp.bfloat16)
        entering = prior[:, 1:]
        if side > 2:
            far = lax.ppermute(pair, "ctx", [(a, a + 2) for a in range(side - 2)])
            entering = prior[:, :1, :1] * far[:, 1:].astype(jnp.float32) + entering
    else:
        entering = jnp.zeros_like(local_state)
        for s in range(side - 1, 0, -1):
            pairs = [(a, a + s) for a in range(side - s)]
            both_in = lax.ppermute(state_and_decay, "ctx", pairs).astype(jnp.float32)
            entering = both_in[:, :1, :1] * entering + both_in[:, 1:]
    entered = (
        jnp.einsum("tn,hdn->thd", c_proj.astype(jnp.float32), entering, precision=FULL_PRECISION)
        * enter_weight[:, :, None]
    )
    mixer_out = (inner_out + entered + head_skip_gain[None, :, None] * x_heads).reshape(
        length, channels
    )
    scale = lax.rsqrt(jnp.mean(mixer_out * mixer_out, axis=1, keepdims=True) + NORM_EPSILON)
    normalized_rows = (mixer_out * scale * output_norm_gain[None, :]).astype(jnp.bfloat16)

    normed_stream = in_order(
        [normalized_rows] + [moved(normalized_rows, s, "ctx") for s in range(1, side)], here
    )
    out_down_part = jnp.einsum(
        "pc,ecr->per", normed_stream, adapter_down_output, preferred_element_type=jnp.float32
    )
    out_down_pick = jnp.sum(out_down_part * owned_here[:, :, None].astype(jnp.float32), axis=1)
    rank_hidden_output = transposed(lane_sum(out_down_pick))
    base_part = jnp.dot(
        normed_stream, output_weight, preferred_element_type=jnp.float32
    ).astype(jnp.bfloat16).astype(jnp.float32)
    adapter_part = jnp.dot(
        owned_rows(rank_hidden_output, owned_lane).astype(jnp.bfloat16),
        up_out_t.reshape(bank_entries * rank_value, -1),
        preferred_element_type=jnp.float32,
    )
    out_part = base_part + adapter_part
    if lax.axis_size("tp") == 2 and lax.axis_size("dp") == 2:
        core = lax.axis_index("dp")
        chip = lax.axis_index("tp")
        blocks = out_part.reshape(side, length, -1)

        def pick(index):
            return lax.dynamic_index_in_dim(blocks, index, 0, keepdims=False)

        swapped = lax.ppermute(
            jnp.stack([pick(1 - core), pick(3 - core)]).astype(jnp.bfloat16),
            "dp",
            [(0, 1), (1, 0)],
        ).astype(jnp.float32)
        near = pick(core) + swapped[0]
        far = pick(2 + core) + swapped[1]
        mixed_t = jnp.where(chip == 0, near, far)
        crossing = jnp.where(chip == 0, far, near).astype(jnp.bfloat16)
        mixed_t = mixed_t + lax.ppermute(crossing, "tp", [(0, 1), (1, 0)]).astype(jnp.float32)
    else:
        mixed_t = block_rows(out_part, lane, length)
        for s in range(1, side):
            sent = block_rows(out_part, (lane + s) % side, length).astype(jnp.bfloat16)
            mixed_t = mixed_t + moved(sent, s, "lane").astype(jnp.float32)
    return transposed(mixed_t.astype(jnp.bfloat16))


def solution(mesh):
    body = square_body if mesh.shape["ctx"] == mesh.shape["tp"] * mesh.shape["dp"] else general_body
    placed = (
        P(("groups", "ctx"), ("tp", "dp")),
        P("groups"),
        P("groups"),
        P(),
        P("ctx", ("tp", "dp")),
        P("ctx", ("tp", "dp")),
        P("ctx", ("tp", "dp")),
        P(None, ("tp", "dp")),
        P(None, ("tp", "dp")),
        P(("tp", "dp")),
        P(("tp", "dp")),
        P(("tp", "dp")),
        P(("tp", "dp")),
        P(("tp", "dp"), "ctx"),
        P("ctx", ("tp", "dp"), None),
        P("ctx", None, ("tp", "dp")),
        P("ctx", None, ("tp", "dp")),
        P("ctx", ("tp", "dp"), None),
        P("ctx", None, ("tp", "dp")),
    )
    return jax.shard_map(
        body,
        mesh=mesh,
        in_specs=placed,
        out_specs=P(("groups", "ctx"), ("tp", "dp")),
        check_vma=False,
    )
```

```python
import jax
import jax.numpy as jnp
from jax import lax
from jax.sharding import PartitionSpec as P

FULL_PRECISION = lax.Precision.HIGHEST
NORM_EPSILON = 1e-06


def from_root(block, axis, source):
    block = jnp.where(lax.axis_index(axis) == source, block, jnp.zeros_like(block))
    return lax.psum(block, axis)


def passed_along(shard, axis, by):
    size = lax.axis_size(axis)
    pairs = [(i, i + by) for i in range(size) if 0 <= i + by < size]
    return lax.ppermute(shard, axis, pairs)


def prefix(shard, axis, combine, identity):
    size, place = (lax.axis_size(axis), lax.axis_index(axis))
    everything = jax.tree.map(
        lambda part, kind: lax.all_gather(part.astype(kind), axis),
        shard,
        (jnp.bfloat16, jnp.bfloat16),
    )
    start = jax.tree.map(
        lambda part, zero: jnp.broadcast_to(jnp.asarray(zero, part.dtype), part.shape),
        shard,
        identity,
    )

    def lap(k, before):
        reached = k < place
        new = combine(
            before, jax.tree.map(lambda part, own: part[k].astype(own.dtype), everything, shard)
        )
        return jax.tree.map(lambda a, b: jnp.where(reached, a, b), new, before)

    return lax.fori_loop(0, size, lap, start)


def segment_of(positions, request_ends):
    inside = (positions[:, None] >= request_ends[None, :]).astype(jnp.int32)
    counted = jnp.sum(inside, axis=1, dtype=jnp.int32)
    return jnp.where(positions < 0, jnp.int32(-1), counted)


def span_parts(x_heads, b_proj, c_proj, step_size, log_decay, segment, previous):
    length = x_heads.shape[0]
    cumulative = jnp.cumsum(log_decay, axis=0)
    final_log = cumulative[length - 1]
    places = jnp.arange(length, dtype=jnp.int32)
    same_request = jnp.logical_and(
        segment[:, None] == segment[None, :], places[None, :] <= places[:, None]
    ).astype(jnp.float32)
    log_gap = cumulative.T[:, :, None] - cumulative.T[:, None, :]
    decay_table = jnp.exp(jnp.minimum(log_gap, 0.0)) * same_request[None]
    scores = lax.dot_general(
        c_proj, b_proj, (((1,), (1,)), ((), ())), preferred_element_type=jnp.float32
    )
    weights = scores[None] * decay_table * step_size.T[:, None, :]
    inner_out = jnp.einsum("hts,shd->thd", weights, x_heads, precision=FULL_PRECISION)
    at_end = (segment == segment[length - 1]).astype(jnp.float32)
    state_weight = jnp.exp(final_log[None, :] - cumulative) * at_end[:, None] * step_size
    local_state = jnp.einsum(
        "sh,shd,sn->hdn",
        state_weight,
        x_heads,
        b_proj.astype(jnp.float32),
        precision=FULL_PRECISION,
    )
    enter_weight = jnp.exp(cumulative) * (segment == previous).astype(jnp.float32)[:, None]
    carry_decay = jnp.exp(final_log) * (segment[length - 1] == previous).astype(jnp.float32)
    return (inner_out, local_state, enter_weight, carry_decay)


def select_rows(wide, adapter_picker_matrix):
    shaped = wide.reshape(wide.shape[0], adapter_picker_matrix.shape[1], -1)
    return jnp.sum(shaped * adapter_picker_matrix[:, :, None], axis=1)


def masked_wide(values, onehot_b):
    return (values[:, None, :] * onehot_b[:, :, None]).reshape(values.shape[0], -1)


def general_body(
    tokens,
    lengths,
    request_adapter_ids,
    adapter_store_slot,
    xchan_input_weight,
    bc_input_weight,
    step_input_weight,
    convolution_x_taps,
    convolution_bc_taps,
    step_bias,
    decay_log_rate,
    head_skip_gain,
    output_norm_gain,
    output_weight,
    adapter_down_input,
    adapter_up_xchan,
    adapter_up_bc,
    adapter_down_output,
    adapter_up_output,
):
    length = tokens.shape[0]
    request_list = lengths.shape[0]
    taps = convolution_x_taps.shape[0]
    bank_entries = adapter_down_input.shape[0]
    head_count = step_bias.shape[0]
    channels = xchan_input_weight.shape[1]
    start_pos = lax.axis_index("ctx") * length
    request_ends = jnp.cumsum(lengths, dtype=jnp.int32)
    positions = start_pos + jnp.arange(length, dtype=jnp.int32)
    segment = segment_of(positions, request_ends)
    previous = segment_of(jnp.reshape(start_pos - 1, (1,)), request_ends)[0]
    adapter_picker_matrix = (
        segment[:, None] == jnp.arange(request_list, dtype=jnp.int32)[None, :]
    ).astype(jnp.float32)
    onehot_b = adapter_picker_matrix.astype(jnp.bfloat16)
    slot_indices = adapter_store_slot[request_adapter_ids]
    initial_stacks = (
        jnp.zeros(
            (adapter_down_input.shape[1], request_list, adapter_down_input.shape[2]), jnp.bfloat16
        ),
        jnp.zeros((request_list,) + adapter_up_xchan.shape[1:], jnp.bfloat16),
        jnp.zeros((request_list,) + adapter_up_bc.shape[1:], jnp.bfloat16),
        jnp.zeros(
            (adapter_down_output.shape[1], request_list, adapter_down_output.shape[2]), jnp.bfloat16
        ),
        jnp.zeros((request_list,) + adapter_up_output.shape[1:], jnp.bfloat16),
    )
    stack_dims = (1, 0, 0, 1, 0)

    def fetch(request_item, current):
        slot = slot_indices[request_item]
        owner = slot // bank_entries
        within = slot % bank_entries
        a_in, b_x, b_bc, a_out, b_out = [
            lax.dynamic_index_in_dim(adapter_bank, within, 0, keepdims=False)
            for adapter_bank in (
                adapter_down_input,
                adapter_up_xchan,
                adapter_up_bc,
                adapter_down_output,
                adapter_up_output,
            )
        ]
        received = (
            from_root(a_in, "ctx", owner),
            from_root(b_x, "ctx", owner),
            from_root(b_bc, "ctx", owner),
            from_root(a_out, "ctx", owner),
            from_root(b_out, "ctx", owner),
        )
        return tuple(
            (
                lax.dynamic_update_index_in_dim(stack, panel, request_item, along)
                for stack, panel, along in zip(current, received, stack_dims)
            )
        )

    stacks = lax.fori_loop(0, request_list, fetch, initial_stacks)
    rank_value = adapter_down_input.shape[2]
    down_in = stacks[0].reshape(stacks[0].shape[0], request_list * rank_value)
    up_x = stacks[1].reshape(request_list * rank_value, -1)
    up_bc = stacks[2].reshape(request_list * rank_value, -1)
    down_out = stacks[3].reshape(stacks[3].shape[0], request_list * rank_value)
    up_out = stacks[4].reshape(request_list * rank_value, -1)
    lowrank_part = select_rows(
        jnp.dot(tokens, down_in, preferred_element_type=jnp.float32), adapter_picker_matrix
    )
    rank_hidden = lax.psum(lowrank_part.astype(jnp.bfloat16), ("tp", "dp"))
    lowrank_wide = masked_wide(rank_hidden, onehot_b)
    full_tokens = lax.all_gather(tokens, ("tp", "dp"), axis=1, tiled=True)
    pieces = (
        lax.all_gather(xchan_input_weight, "ctx", axis=0, tiled=True),
        lax.all_gather(bc_input_weight, "ctx", axis=0, tiled=True),
        lax.all_gather(step_input_weight, "ctx", axis=0, tiled=True),
    )
    xchan_values, bc_channel_values, step_raw = tuple(
        (jnp.dot(full_tokens, piece, preferred_element_type=jnp.float32) for piece in pieces)
    )
    xchan_values = xchan_values + jnp.dot(lowrank_wide, up_x, preferred_element_type=jnp.float32)
    bc_channel_values = bc_channel_values + jnp.dot(
        lowrank_wide, up_bc, preferred_element_type=jnp.float32
    )
    values = jnp.concatenate([xchan_values, bc_channel_values], axis=1)
    kernel = jnp.concatenate([convolution_x_taps, convolution_bc_taps], axis=1)
    tail_rows = passed_along(values[length - (taps - 1) :], "ctx", 1)
    extended = jnp.concatenate([tail_rows, values], axis=0)
    extended_segment = segment_of(
        start_pos - (taps - 1) + jnp.arange(length + taps - 1, dtype=jnp.int32), request_ends
    )
    convolved = jnp.zeros_like(values)
    for tap in range(taps):
        keep = (extended_segment[tap : tap + length] == segment).astype(jnp.float32)
        convolved = convolved + kernel[tap][None, :] * extended[tap : tap + length] * keep[:, None]
    act = jax.nn.silu(convolved)
    x_heads = act[:, :channels].reshape(length, head_count, -1)
    bc_local = act[:, channels:].astype(jnp.bfloat16)
    bc_all = lax.all_gather(bc_local, ("tp", "dp"), axis=1, tiled=True)
    state_width = bc_all.shape[1] // 2
    b_proj = bc_all[:, :state_width]
    c_proj = bc_all[:, state_width:]
    step_size = jax.nn.softplus(step_raw + step_bias[None, :])
    log_decay = -step_size * jnp.exp(decay_log_rate)[None, :]
    inner_out, local_state, enter_weight, carry_decay = span_parts(
        x_heads, b_proj, c_proj, step_size, log_decay, segment, previous
    )

    def compose(earlier, later):
        return (earlier[0] * later[0], later[0][:, None, None] * earlier[1] + later[1])

    carried = prefix(
        (carry_decay, local_state),
        "ctx",
        compose,
        (jnp.ones_like(carry_decay), jnp.zeros_like(local_state)),
    )
    entering = carried[1]
    entered = (
        jnp.einsum("tn,hdn->thd", c_proj.astype(jnp.float32), entering, precision=FULL_PRECISION)
        * enter_weight[:, :, None]
    )
    mixer_out = (inner_out + entered + head_skip_gain[None, :, None] * x_heads).reshape(
        length, channels
    )
    scale = lax.rsqrt(jnp.mean(mixer_out * mixer_out, axis=1, keepdims=True) + NORM_EPSILON)
    normalized_rows = (mixer_out * scale * output_norm_gain[None, :]).astype(jnp.bfloat16)
    term = jnp.dot(
        normalized_rows,
        lax.all_gather(output_weight, "ctx", axis=1, tiled=True),
        preferred_element_type=jnp.float32,
    )
    base = lax.psum_scatter(
        term.astype(jnp.bfloat16), ("tp", "dp"), scatter_dimension=1, tiled=True
    ).astype(jnp.float32)
    lowrank_out_part = select_rows(
        jnp.dot(normalized_rows, down_out, preferred_element_type=jnp.float32),
        adapter_picker_matrix,
    )
    rank_hidden_output = lax.psum(lowrank_out_part.astype(jnp.bfloat16), ("tp", "dp"))
    adapter_term = jnp.dot(
        masked_wide(rank_hidden_output, onehot_b), up_out, preferred_element_type=jnp.float32
    )
    return (base + adapter_term).astype(jnp.bfloat16)


def moved(block, shift, kind):
    side = lax.axis_size("ctx")
    if kind == "ctx":
        pairs = [(a, (a + shift) % side) for a in range(side)]
        return lax.ppermute(block, "ctx", pairs)
    if kind == "lane":
        pairs = [(a, (a + shift) % side) for a in range(side)]
        return lax.ppermute(block, ("tp", "dp"), pairs)
    if kind == "rows":
        pairs = [(a * side + b, b * side + (a + shift) % side) for a in range(side) for b in range(side)]
    else:
        pairs = [(a * side + b, ((b + shift) % side) * side + a) for a in range(side) for b in range(side)]
    return lax.ppermute(block, ("ctx", "tp", "dp"), pairs)


def transposed(block):
    return moved(block, 0, "rows")


def in_order(pieces, place):
    stacked = jnp.stack(pieces[::-1], axis=0)
    ordered = jnp.roll(stacked, place + 1, axis=0)
    return ordered.reshape((-1,) + pieces[0].shape[1:])


def block_rows(values, index, length):
    return lax.dynamic_slice_in_dim(values, index * length, length, 0)


def owned_rows(values, owned):
    return jnp.concatenate(
        [values * owned[:, i : i + 1].astype(values.dtype) for i in range(owned.shape[1])], axis=1
    )


def square_body(
    tokens,
    lengths,
    request_adapter_ids,
    adapter_store_slot,
    xchan_input_weight,
    bc_input_weight,
    step_input_weight,
    convolution_x_taps,
    convolution_bc_taps,
    step_bias,
    decay_log_rate,
    head_skip_gain,
    output_norm_gain,
    output_weight,
    adapter_down_input,
    adapter_up_xchan,
    adapter_up_bc,
    adapter_down_output,
    adapter_up_output,
):
    length = tokens.shape[0]
    side = lax.axis_size("ctx")
    stream = side * length
    taps = convolution_x_taps.shape[0]
    bank_entries = adapter_down_input.shape[0]
    rank_value = adapter_down_input.shape[2]
    head_count = step_bias.shape[0]
    channels = xchan_input_weight.shape[1]
    bc_width = bc_input_weight.shape[1]
    here = lax.axis_index("ctx")
    lane = lax.axis_index(("tp", "dp"))
    start_pos = here * length
    request_ends = jnp.cumsum(lengths, dtype=jnp.int32)
    every_position = jnp.arange(stream, dtype=jnp.int32)
    every_segment = segment_of(every_position, request_ends)
    slot_indices = adapter_store_slot[request_adapter_ids]
    request_count = lengths.shape[0]
    stream_onehot = every_segment[:, None] == jnp.arange(request_count, dtype=jnp.int32)[None, :]
    slot_of_position = jnp.sum(
        jnp.where(stream_onehot, slot_indices[None, :], 0), axis=1, dtype=jnp.int32
    )
    entry_ids = jnp.arange(bank_entries, dtype=jnp.int32)[None, :]
    owned_here = slot_of_position[:, None] == here * bank_entries + entry_ids
    owned_lane = slot_of_position[:, None] == lane * bank_entries + entry_ids
    positions = start_pos + jnp.arange(length, dtype=jnp.int32)
    segment = segment_of(positions, request_ends)
    previous = segment_of(jnp.reshape(start_pos - 1, (1,)), request_ends)[0]

    tokens_t, down_in_local = lax.optimization_barrier((transposed(tokens), adapter_down_input))
    stream_rows = in_order(
        [tokens_t] + [moved(tokens_t, s, "lane") for s in range(1, side)], lane
    )
    local_owned = lax.dynamic_slice_in_dim(slot_of_position, start_pos, length, 0)
    down_pick = jnp.zeros((length, rank_value), jnp.float32)
    for s in range(side):
        piece = down_in_local if s == 0 else moved(down_in_local, s, "ctx")
        first = ((here - s) % side) * bank_entries
        every = jnp.einsum("pf,efr->per", tokens, piece, preferred_element_type=jnp.float32)
        chosen = local_owned[:, None] == first + jnp.arange(bank_entries, dtype=jnp.int32)[None, :]
        down_pick = down_pick + jnp.sum(every * chosen[:, :, None].astype(jnp.float32), axis=1)
    rank_local = (
        down_pick + sum(moved(down_pick, s, "lane") for s in range(1, side))
    ).astype(jnp.bfloat16)
    rank_hidden = in_order(
        [rank_local] + [moved(rank_local, s, "ctx") for s in range(1, side)], here
    )
    hidden_wide = owned_rows(rank_hidden, owned_here)
    xchan_part = jnp.dot(
        stream_rows, xchan_input_weight, preferred_element_type=jnp.float32
    ) + jnp.dot(
        hidden_wide,
        adapter_up_xchan.reshape(bank_entries * rank_value, -1),
        preferred_element_type=jnp.float32,
    )
    bc_part = jnp.dot(stream_rows, bc_input_weight, preferred_element_type=jnp.float32) + jnp.dot(
        hidden_wide,
        adapter_up_bc.reshape(bank_entries * rank_value, -1),
        preferred_element_type=jnp.float32,
    )
    step_part = jnp.dot(stream_rows, step_input_weight, preferred_element_type=jnp.float32)
    projected = jnp.concatenate([xchan_part, bc_part, step_part], axis=1)
    summed = block_rows(projected, here, length)
    for s in range(1, side):
        sent = block_rows(projected, (here + s) % side, length).astype(jnp.bfloat16)
        summed = summed + moved(sent, s, "ctx").astype(jnp.float32)
    summed, up_out_local = lax.optimization_barrier((summed, adapter_up_output))
    up_out_t = transposed(up_out_local)
    values = summed[:, : channels + bc_width]
    step_raw = summed[:, channels + bc_width :]

    kernel = jnp.concatenate([convolution_x_taps, convolution_bc_taps], axis=1)
    tail_rows = passed_along(values[length - (taps - 1) :], "ctx", 1)
    extended = jnp.concatenate([tail_rows, values], axis=0)
    extended_segment = segment_of(
        start_pos - (taps - 1) + jnp.arange(length + taps - 1, dtype=jnp.int32), request_ends
    )
    convolved = jnp.zeros_like(values)
    for tap in range(taps):
        keep = (extended_segment[tap : tap + length] == segment).astype(jnp.float32)
        convolved = convolved + kernel[tap][None, :] * extended[tap : tap + length] * keep[:, None]
    act = jax.nn.silu(convolved)
    x_heads = act[:, :channels].reshape(length, head_count, -1)
    bc_local = act[:, channels:].astype(jnp.bfloat16)
    bc_pieces = [bc_local] + [moved(bc_local, s, "lane") for s in range(1, side)]
    bc_all = jnp.transpose(in_order([piece.T for piece in bc_pieces], lane))
    state_width = bc_all.shape[1] // 2
    b_proj = bc_all[:, :state_width]
    c_proj = bc_all[:, state_width:]
    step_size = jax.nn.softplus(step_raw + step_bias[None, :])
    log_decay = -step_size * jnp.exp(decay_log_rate)[None, :]
    inner_out, local_state, enter_weight, carry_decay = span_parts(
        x_heads, b_proj, c_proj, step_size, log_decay, segment, previous
    )

    decay_row = jnp.broadcast_to(carry_decay[:, None, None], (head_count, 1, local_state.shape[2]))
    state_and_decay = jnp.concatenate([decay_row, local_state], axis=1).astype(jnp.bfloat16)
    if side <= 4:
        prior = lax.ppermute(
            state_and_decay, "ctx", [(a, a + 1) for a in range(side - 1)]
        ).astype(jnp.float32)
        pair_decay = prior[:, :1, :1] * carry_decay[:, None, None]
        pair_state = carry_decay[:, None, None] * prior[:, 1:] + local_state
        pair = jnp.concatenate(
            [jnp.broadcast_to(pair_decay, decay_row.shape), pair_state], axis=1
        ).astype(jnp.bfloat16)
        entering = prior[:, 1:]
        if side > 2:
            far = lax.ppermute(pair, "ctx", [(a, a + 2) for a in range(side - 2)])
            entering = prior[:, :1, :1] * far[:, 1:].astype(jnp.float32) + entering
    else:
        entering = jnp.zeros_like(local_state)
        for s in range(side - 1, 0, -1):
            pairs = [(a, a + s) for a in range(side - s)]
            both_in = lax.ppermute(state_and_decay, "ctx", pairs).astype(jnp.float32)
            entering = both_in[:, :1, :1] * entering + both_in[:, 1:]
    entered = (
        jnp.einsum("tn,hdn->thd", c_proj.astype(jnp.float32), entering, precision=FULL_PRECISION)
        * enter_weight[:, :, None]
    )
    mixer_out = (inner_out + entered + head_skip_gain[None, :, None] * x_heads).reshape(
        length, channels
    )
    scale = lax.rsqrt(jnp.mean(mixer_out * mixer_out, axis=1, keepdims=True) + NORM_EPSILON)
    normalized_rows = (mixer_out * scale * output_norm_gain[None, :]).astype(jnp.bfloat16)

    normed_stream = in_order(
        [normalized_rows] + [moved(normalized_rows, s, "ctx") for s in range(1, side)], here
    )
    out_down_part = jnp.einsum(
        "pc,ecr->per", normed_stream, adapter_down_output, preferred_element_type=jnp.float32
    )
    out_down_pick = jnp.sum(out_down_part * owned_here[:, :, None].astype(jnp.float32), axis=1)
    if lax.axis_size("tp") == 2 and lax.axis_size("dp") == 2:
        summed_pick = out_down_pick + lax.ppermute(out_down_pick, "dp", [(0, 1), (1, 0)])
        summed_pick = summed_pick + lax.ppermute(summed_pick, "tp", [(0, 1), (1, 0)])
    else:
        summed_pick = out_down_pick + sum(moved(out_down_pick, s, "lane") for s in range(1, side))
    rank_hidden_output = transposed(summed_pick)
    base_part = jnp.dot(
        normed_stream, output_weight, preferred_element_type=jnp.float32
    ).astype(jnp.bfloat16).astype(jnp.float32)
    adapter_part = jnp.dot(
        owned_rows(rank_hidden_output, owned_lane).astype(jnp.bfloat16),
        up_out_t.reshape(bank_entries * rank_value, -1),
        preferred_element_type=jnp.float32,
    )
    out_part = base_part + adapter_part
    if lax.axis_size("tp") == 2 and lax.axis_size("dp") == 2:
        core = lax.axis_index("dp")
        chip = lax.axis_index("tp")
        blocks = out_part.reshape(side, length, -1)

        def pick(index):
            return lax.dynamic_index_in_dim(blocks, index, 0, keepdims=False)

        swapped = lax.ppermute(
            jnp.stack([pick(1 - core), pick(3 - core)]).astype(jnp.bfloat16),
            "dp",
            [(0, 1), (1, 0)],
        ).astype(jnp.float32)
        near = pick(core) + swapped[0]
        far = pick(2 + core) + swapped[1]
        mixed_t = jnp.where(chip == 0, near, far)
        crossing = jnp.where(chip == 0, far, near).astype(jnp.bfloat16)
        mixed_t = mixed_t + lax.ppermute(crossing, "tp", [(0, 1), (1, 0)]).astype(jnp.float32)
    else:
        mixed_t = block_rows(out_part, lane, length)
        for s in range(1, side):
            sent = block_rows(out_part, (lane + s) % side, length).astype(jnp.bfloat16)
            mixed_t = mixed_t + moved(sent, s, "lane").astype(jnp.float32)
    return transposed(mixed_t.astype(jnp.bfloat16))


def solution(mesh):
    body = square_body if mesh.shape["ctx"] == mesh.shape["tp"] * mesh.shape["dp"] else general_body
    placed = (
        P(("groups", "ctx"), ("tp", "dp")),
        P("groups"),
        P("groups"),
        P(),
        P("ctx", ("tp", "dp")),
        P("ctx", ("tp", "dp")),
        P("ctx", ("tp", "dp")),
        P(None, ("tp", "dp")),
        P(None, ("tp", "dp")),
        P(("tp", "dp")),
        P(("tp", "dp")),
        P(("tp", "dp")),
        P(("tp", "dp")),
        P(("tp", "dp"), "ctx"),
        P("ctx", ("tp", "dp"), None),
        P("ctx", None, ("tp", "dp")),
        P("ctx", None, ("tp", "dp")),
        P("ctx", ("tp", "dp"), None),
        P("ctx", None, ("tp", "dp")),
    )
    return jax.shard_map(
        body,
        mesh=mesh,
        in_specs=placed,
        out_specs=P(("groups", "ctx"), ("tp", "dp")),
        check_vma=False,
    )
```

```python
import jax
import jax.numpy as jnp
from jax import lax
from jax.sharding import PartitionSpec as P

FULL_PRECISION = lax.Precision.HIGHEST
NORM_EPSILON = 1e-06


def from_root(block, axis, source):
    block = jnp.where(lax.axis_index(axis) == source, block, jnp.zeros_like(block))
    return lax.psum(block, axis)


def passed_along(shard, axis, by):
    size = lax.axis_size(axis)
    pairs = [(i, i + by) for i in range(size) if 0 <= i + by < size]
    return lax.ppermute(shard, axis, pairs)


def prefix(shard, axis, combine, identity):
    size, place = (lax.axis_size(axis), lax.axis_index(axis))
    everything = jax.tree.map(
        lambda part, kind: lax.all_gather(part.astype(kind), axis),
        shard,
        (jnp.bfloat16, jnp.bfloat16),
    )
    start = jax.tree.map(
        lambda part, zero: jnp.broadcast_to(jnp.asarray(zero, part.dtype), part.shape),
        shard,
        identity,
    )

    def lap(k, before):
        reached = k < place
        new = combine(
            before, jax.tree.map(lambda part, own: part[k].astype(own.dtype), everything, shard)
        )
        return jax.tree.map(lambda a, b: jnp.where(reached, a, b), new, before)

    return lax.fori_loop(0, size, lap, start)


def segment_of(positions, request_ends):
    inside = (positions[:, None] >= request_ends[None, :]).astype(jnp.int32)
    counted = jnp.sum(inside, axis=1, dtype=jnp.int32)
    return jnp.where(positions < 0, jnp.int32(-1), counted)


def span_parts(x_heads, b_proj, c_proj, step_size, log_decay, segment, previous):
    length = x_heads.shape[0]
    cumulative = jnp.cumsum(log_decay, axis=0)
    final_log = cumulative[length - 1]
    places = jnp.arange(length, dtype=jnp.int32)
    same_request = jnp.logical_and(
        segment[:, None] == segment[None, :], places[None, :] <= places[:, None]
    ).astype(jnp.float32)
    log_gap = cumulative.T[:, :, None] - cumulative.T[:, None, :]
    decay_table = jnp.exp(jnp.minimum(log_gap, 0.0)) * same_request[None]
    scores = lax.dot_general(
        c_proj, b_proj, (((1,), (1,)), ((), ())), preferred_element_type=jnp.float32
    )
    weights = scores[None] * decay_table * step_size.T[:, None, :]
    inner_out = jnp.einsum("hts,shd->thd", weights, x_heads, precision=FULL_PRECISION)
    at_end = (segment == segment[length - 1]).astype(jnp.float32)
    state_weight = jnp.exp(final_log[None, :] - cumulative) * at_end[:, None] * step_size
    local_state = jnp.einsum(
        "sh,shd,sn->hdn",
        state_weight,
        x_heads,
        b_proj.astype(jnp.float32),
        precision=FULL_PRECISION,
    )
    enter_weight = jnp.exp(cumulative) * (segment == previous).astype(jnp.float32)[:, None]
    carry_decay = jnp.exp(final_log) * (segment[length - 1] == previous).astype(jnp.float32)
    return (inner_out, local_state, enter_weight, carry_decay)


def select_rows(wide, adapter_picker_matrix):
    shaped = wide.reshape(wide.shape[0], adapter_picker_matrix.shape[1], -1)
    return jnp.sum(shaped * adapter_picker_matrix[:, :, None], axis=1)


def masked_wide(values, onehot_b):
    return (values[:, None, :] * onehot_b[:, :, None]).reshape(values.shape[0], -1)


def general_body(
    tokens,
    lengths,
    request_adapter_ids,
    adapter_store_slot,
    xchan_input_weight,
    bc_input_weight,
    step_input_weight,
    convolution_x_taps,
    convolution_bc_taps,
    step_bias,
    decay_log_rate,
    head_skip_gain,
    output_norm_gain,
    output_weight,
    adapter_down_input,
    adapter_up_xchan,
    adapter_up_bc,
    adapter_down_output,
    adapter_up_output,
):
    length = tokens.shape[0]
    request_list = lengths.shape[0]
    taps = convolution_x_taps.shape[0]
    bank_entries = adapter_down_input.shape[0]
    head_count = step_bias.shape[0]
    channels = xchan_input_weight.shape[1]
    start_pos = lax.axis_index("ctx") * length
    request_ends = jnp.cumsum(lengths, dtype=jnp.int32)
    positions = start_pos + jnp.arange(length, dtype=jnp.int32)
    segment = segment_of(positions, request_ends)
    previous = segment_of(jnp.reshape(start_pos - 1, (1,)), request_ends)[0]
    adapter_picker_matrix = (
        segment[:, None] == jnp.arange(request_list, dtype=jnp.int32)[None, :]
    ).astype(jnp.float32)
    onehot_b = adapter_picker_matrix.astype(jnp.bfloat16)
    slot_indices = adapter_store_slot[request_adapter_ids]
    initial_stacks = (
        jnp.zeros(
            (adapter_down_input.shape[1], request_list, adapter_down_input.shape[2]), jnp.bfloat16
        ),
        jnp.zeros((request_list,) + adapter_up_xchan.shape[1:], jnp.bfloat16),
        jnp.zeros((request_list,) + adapter_up_bc.shape[1:], jnp.bfloat16),
        jnp.zeros(
            (adapter_down_output.shape[1], request_list, adapter_down_output.shape[2]), jnp.bfloat16
        ),
        jnp.zeros((request_list,) + adapter_up_output.shape[1:], jnp.bfloat16),
    )
    stack_dims = (1, 0, 0, 1, 0)

    def fetch(request_item, current):
        slot = slot_indices[request_item]
        owner = slot // bank_entries
        within = slot % bank_entries
        a_in, b_x, b_bc, a_out, b_out = [
            lax.dynamic_index_in_dim(adapter_bank, within, 0, keepdims=False)
            for adapter_bank in (
                adapter_down_input,
                adapter_up_xchan,
                adapter_up_bc,
                adapter_down_output,
                adapter_up_output,
            )
        ]
        received = (
            from_root(a_in, "ctx", owner),
            from_root(b_x, "ctx", owner),
            from_root(b_bc, "ctx", owner),
            from_root(a_out, "ctx", owner),
            from_root(b_out, "ctx", owner),
        )
        return tuple(
            (
                lax.dynamic_update_index_in_dim(stack, panel, request_item, along)
                for stack, panel, along in zip(current, received, stack_dims)
            )
        )

    stacks = lax.fori_loop(0, request_list, fetch, initial_stacks)
    rank_value = adapter_down_input.shape[2]
    down_in = stacks[0].reshape(stacks[0].shape[0], request_list * rank_value)
    up_x = stacks[1].reshape(request_list * rank_value, -1)
    up_bc = stacks[2].reshape(request_list * rank_value, -1)
    down_out = stacks[3].reshape(stacks[3].shape[0], request_list * rank_value)
    up_out = stacks[4].reshape(request_list * rank_value, -1)
    lowrank_part = select_rows(
        jnp.dot(tokens, down_in, preferred_element_type=jnp.float32), adapter_picker_matrix
    )
    rank_hidden = lax.psum(lowrank_part.astype(jnp.bfloat16), ("tp", "dp"))
    lowrank_wide = masked_wide(rank_hidden, onehot_b)
    full_tokens = lax.all_gather(tokens, ("tp", "dp"), axis=1, tiled=True)
    pieces = (
        lax.all_gather(xchan_input_weight, "ctx", axis=0, tiled=True),
        lax.all_gather(bc_input_weight, "ctx", axis=0, tiled=True),
        lax.all_gather(step_input_weight, "ctx", axis=0, tiled=True),
    )
    xchan_values, bc_channel_values, step_raw = tuple(
        (jnp.dot(full_tokens, piece, preferred_element_type=jnp.float32) for piece in pieces)
    )
    xchan_values = xchan_values + jnp.dot(lowrank_wide, up_x, preferred_element_type=jnp.float32)
    bc_channel_values = bc_channel_values + jnp.dot(
        lowrank_wide, up_bc, preferred_element_type=jnp.float32
    )
    values = jnp.concatenate([xchan_values, bc_channel_values], axis=1)
    kernel = jnp.concatenate([convolution_x_taps, convolution_bc_taps], axis=1)
    tail_rows = passed_along(values[length - (taps - 1) :], "ctx", 1)
    extended = jnp.concatenate([tail_rows, values], axis=0)
    extended_segment = segment_of(
        start_pos - (taps - 1) + jnp.arange(length + taps - 1, dtype=jnp.int32), request_ends
    )
    convolved = jnp.zeros_like(values)
    for tap in range(taps):
        keep = (extended_segment[tap : tap + length] == segment).astype(jnp.float32)
        convolved = convolved + kernel[tap][None, :] * extended[tap : tap + length] * keep[:, None]
    act = jax.nn.silu(convolved)
    x_heads = act[:, :channels].reshape(length, head_count, -1)
    bc_local = act[:, channels:].astype(jnp.bfloat16)
    bc_all = lax.all_gather(bc_local, ("tp", "dp"), axis=1, tiled=True)
    state_width = bc_all.shape[1] // 2
    b_proj = bc_all[:, :state_width]
    c_proj = bc_all[:, state_width:]
    step_size = jax.nn.softplus(step_raw + step_bias[None, :])
    log_decay = -step_size * jnp.exp(decay_log_rate)[None, :]
    inner_out, local_state, enter_weight, carry_decay = span_parts(
        x_heads, b_proj, c_proj, step_size, log_decay, segment, previous
    )

    def compose(earlier, later):
        return (earlier[0] * later[0], later[0][:, None, None] * earlier[1] + later[1])

    carried = prefix(
        (carry_decay, local_state),
        "ctx",
        compose,
        (jnp.ones_like(carry_decay), jnp.zeros_like(local_state)),
    )
    entering = carried[1]
    entered = (
        jnp.einsum("tn,hdn->thd", c_proj.astype(jnp.float32), entering, precision=FULL_PRECISION)
        * enter_weight[:, :, None]
    )
    mixer_out = (inner_out + entered + head_skip_gain[None, :, None] * x_heads).reshape(
        length, channels
    )
    scale = lax.rsqrt(jnp.mean(mixer_out * mixer_out, axis=1, keepdims=True) + NORM_EPSILON)
    normalized_rows = (mixer_out * scale * output_norm_gain[None, :]).astype(jnp.bfloat16)
    term = jnp.dot(
        normalized_rows,
        lax.all_gather(output_weight, "ctx", axis=1, tiled=True),
        preferred_element_type=jnp.float32,
    )
    base = lax.psum_scatter(
        term.astype(jnp.bfloat16), ("tp", "dp"), scatter_dimension=1, tiled=True
    ).astype(jnp.float32)
    lowrank_out_part = select_rows(
        jnp.dot(normalized_rows, down_out, preferred_element_type=jnp.float32),
        adapter_picker_matrix,
    )
    rank_hidden_output = lax.psum(lowrank_out_part.astype(jnp.bfloat16), ("tp", "dp"))
    adapter_term = jnp.dot(
        masked_wide(rank_hidden_output, onehot_b), up_out, preferred_element_type=jnp.float32
    )
    return (base + adapter_term).astype(jnp.bfloat16)


def moved(block, shift, kind):
    side = lax.axis_size("ctx")
    if kind == "ctx":
        pairs = [(a, (a + shift) % side) for a in range(side)]
        return lax.ppermute(block, "ctx", pairs)
    if kind == "lane":
        pairs = [(a, (a + shift) % side) for a in range(side)]
        return lax.ppermute(block, ("tp", "dp"), pairs)
    if kind == "rows":
        pairs = [(a * side + b, b * side + (a + shift) % side) for a in range(side) for b in range(side)]
    else:
        pairs = [(a * side + b, ((b + shift) % side) * side + a) for a in range(side) for b in range(side)]
    return lax.ppermute(block, ("ctx", "tp", "dp"), pairs)


def transposed(block):
    return moved(block, 0, "rows")


def in_order(pieces, place):
    stacked = jnp.stack(pieces[::-1], axis=0)
    ordered = jnp.roll(stacked, place + 1, axis=0)
    return ordered.reshape((-1,) + pieces[0].shape[1:])


def block_rows(values, index, length):
    return lax.dynamic_slice_in_dim(values, index * length, length, 0)


def owned_rows(values, owned):
    return jnp.concatenate(
        [values * owned[:, i : i + 1].astype(values.dtype) for i in range(owned.shape[1])], axis=1
    )


def square_body(
    tokens,
    lengths,
    request_adapter_ids,
    adapter_store_slot,
    xchan_input_weight,
    bc_input_weight,
    step_input_weight,
    convolution_x_taps,
    convolution_bc_taps,
    step_bias,
    decay_log_rate,
    head_skip_gain,
    output_norm_gain,
    output_weight,
    adapter_down_input,
    adapter_up_xchan,
    adapter_up_bc,
    adapter_down_output,
    adapter_up_output,
):
    length = tokens.shape[0]
    side = lax.axis_size("ctx")
    stream = side * length
    taps = convolution_x_taps.shape[0]
    bank_entries = adapter_down_input.shape[0]
    rank_value = adapter_down_input.shape[2]
    head_count = step_bias.shape[0]
    channels = xchan_input_weight.shape[1]
    bc_width = bc_input_weight.shape[1]
    here = lax.axis_index("ctx")
    lane = lax.axis_index(("tp", "dp"))
    start_pos = here * length
    request_ends = jnp.cumsum(lengths, dtype=jnp.int32)
    every_position = jnp.arange(stream, dtype=jnp.int32)
    every_segment = segment_of(every_position, request_ends)
    slot_indices = adapter_store_slot[request_adapter_ids]
    request_count = lengths.shape[0]
    stream_onehot = every_segment[:, None] == jnp.arange(request_count, dtype=jnp.int32)[None, :]
    slot_of_position = jnp.sum(
        jnp.where(stream_onehot, slot_indices[None, :], 0), axis=1, dtype=jnp.int32
    )
    entry_ids = jnp.arange(bank_entries, dtype=jnp.int32)[None, :]
    owned_here = slot_of_position[:, None] == here * bank_entries + entry_ids
    owned_lane = slot_of_position[:, None] == lane * bank_entries + entry_ids
    positions = start_pos + jnp.arange(length, dtype=jnp.int32)
    segment = segment_of(positions, request_ends)
    previous = segment_of(jnp.reshape(start_pos - 1, (1,)), request_ends)[0]

    tokens_t, down_in_local = lax.optimization_barrier((transposed(tokens), adapter_down_input))
    stream_rows = in_order(
        [tokens_t] + [moved(tokens_t, s, "lane") for s in range(1, side)], lane
    )
    local_owned = lax.dynamic_slice_in_dim(slot_of_position, start_pos, length, 0)
    down_pick = jnp.zeros((length, rank_value), jnp.float32)
    for s in range(side):
        piece = down_in_local if s == 0 else moved(down_in_local, s, "ctx")
        first = ((here - s) % side) * bank_entries
        every = jnp.einsum("pf,efr->per", tokens, piece, preferred_element_type=jnp.float32)
        chosen = local_owned[:, None] == first + jnp.arange(bank_entries, dtype=jnp.int32)[None, :]
        down_pick = down_pick + jnp.sum(every * chosen[:, :, None].astype(jnp.float32), axis=1)
    if lax.axis_size("tp") == 2 and lax.axis_size("dp") == 2:
        down_pick = down_pick + lax.ppermute(down_pick, "dp", [(0, 1), (1, 0)])
        rank_local = down_pick + lax.ppermute(down_pick, "tp", [(0, 1), (1, 0)])
    else:
        rank_local = down_pick + sum(moved(down_pick, s, "lane") for s in range(1, side))
    rank_local = rank_local.astype(jnp.bfloat16)
    rank_hidden = in_order(
        [rank_local] + [moved(rank_local, s, "ctx") for s in range(1, side)], here
    )
    hidden_wide = owned_rows(rank_hidden, owned_here)
    xchan_part = jnp.dot(
        stream_rows, xchan_input_weight, preferred_element_type=jnp.float32
    ) + jnp.dot(
        hidden_wide,
        adapter_up_xchan.reshape(bank_entries * rank_value, -1),
        preferred_element_type=jnp.float32,
    )
    bc_part = jnp.dot(stream_rows, bc_input_weight, preferred_element_type=jnp.float32) + jnp.dot(
        hidden_wide,
        adapter_up_bc.reshape(bank_entries * rank_value, -1),
        preferred_element_type=jnp.float32,
    )
    step_part = jnp.dot(stream_rows, step_input_weight, preferred_element_type=jnp.float32)
    projected = jnp.concatenate([xchan_part, bc_part, step_part], axis=1)
    summed = block_rows(projected, here, length)
    for s in range(1, side):
        sent = block_rows(projected, (here + s) % side, length).astype(jnp.bfloat16)
        summed = summed + moved(sent, s, "ctx").astype(jnp.float32)
    summed, up_out_local = lax.optimization_barrier((summed, adapter_up_output))
    up_out_t = transposed(up_out_local)
    values = summed[:, : channels + bc_width]
    step_raw = summed[:, channels + bc_width :]

    kernel = jnp.concatenate([convolution_x_taps, convolution_bc_taps], axis=1)
    tail_rows = passed_along(values[length - (taps - 1) :], "ctx", 1)
    extended = jnp.concatenate([tail_rows, values], axis=0)
    extended_segment = segment_of(
        start_pos - (taps - 1) + jnp.arange(length + taps - 1, dtype=jnp.int32), request_ends
    )
    convolved = jnp.zeros_like(values)
    for tap in range(taps):
        keep = (extended_segment[tap : tap + length] == segment).astype(jnp.float32)
        convolved = convolved + kernel[tap][None, :] * extended[tap : tap + length] * keep[:, None]
    act = jax.nn.silu(convolved)
    x_heads = act[:, :channels].reshape(length, head_count, -1)
    bc_local = act[:, channels:].astype(jnp.bfloat16)
    bc_pieces = [bc_local] + [moved(bc_local, s, "lane") for s in range(1, side)]
    bc_all = jnp.transpose(in_order([piece.T for piece in bc_pieces], lane))
    state_width = bc_all.shape[1] // 2
    b_proj = bc_all[:, :state_width]
    c_proj = bc_all[:, state_width:]
    step_size = jax.nn.softplus(step_raw + step_bias[None, :])
    log_decay = -step_size * jnp.exp(decay_log_rate)[None, :]
    inner_out, local_state, enter_weight, carry_decay = span_parts(
        x_heads, b_proj, c_proj, step_size, log_decay, segment, previous
    )

    decay_row = jnp.broadcast_to(carry_decay[:, None, None], (head_count, 1, local_state.shape[2]))
    state_and_decay = jnp.concatenate([decay_row, local_state], axis=1).astype(jnp.bfloat16)
    if side <= 4:
        prior = lax.ppermute(
            state_and_decay, "ctx", [(a, a + 1) for a in range(side - 1)]
        ).astype(jnp.float32)
        pair_decay = prior[:, :1, :1] * carry_decay[:, None, None]
        pair_state = carry_decay[:, None, None] * prior[:, 1:] + local_state
        pair = jnp.concatenate(
            [jnp.broadcast_to(pair_decay, decay_row.shape), pair_state], axis=1
        ).astype(jnp.bfloat16)
        entering = prior[:, 1:]
        if side > 2:
            far = lax.ppermute(pair, "ctx", [(a, a + 2) for a in range(side - 2)])
            entering = prior[:, :1, :1] * far[:, 1:].astype(jnp.float32) + entering
    else:
        entering = jnp.zeros_like(local_state)
        for s in range(side - 1, 0, -1):
            pairs = [(a, a + s) for a in range(side - s)]
            both_in = lax.ppermute(state_and_decay, "ctx", pairs).astype(jnp.float32)
            entering = both_in[:, :1, :1] * entering + both_in[:, 1:]
    entered = (
        jnp.einsum("tn,hdn->thd", c_proj.astype(jnp.float32), entering, precision=FULL_PRECISION)
        * enter_weight[:, :, None]
    )
    mixer_out = (inner_out + entered + head_skip_gain[None, :, None] * x_heads).reshape(
        length, channels
    )
    scale = lax.rsqrt(jnp.mean(mixer_out * mixer_out, axis=1, keepdims=True) + NORM_EPSILON)
    normalized_rows = (mixer_out * scale * output_norm_gain[None, :]).astype(jnp.bfloat16)

    normed_stream = in_order(
        [normalized_rows] + [moved(normalized_rows, s, "ctx") for s in range(1, side)], here
    )
    out_down_part = jnp.einsum(
        "pc,ecr->per", normed_stream, adapter_down_output, preferred_element_type=jnp.float32
    )
    out_down_pick = jnp.sum(out_down_part * owned_here[:, :, None].astype(jnp.float32), axis=1)
    if lax.axis_size("tp") == 2 and lax.axis_size("dp") == 2:
        summed_pick = out_down_pick + lax.ppermute(out_down_pick, "dp", [(0, 1), (1, 0)])
        summed_pick = summed_pick + lax.ppermute(summed_pick, "tp", [(0, 1), (1, 0)])
    else:
        summed_pick = out_down_pick + sum(moved(out_down_pick, s, "lane") for s in range(1, side))
    rank_hidden_output = transposed(summed_pick)
    base_part = jnp.dot(
        normed_stream, output_weight, preferred_element_type=jnp.float32
    ).astype(jnp.bfloat16).astype(jnp.float32)
    adapter_part = jnp.dot(
        owned_rows(rank_hidden_output, owned_lane).astype(jnp.bfloat16),
        up_out_t.reshape(bank_entries * rank_value, -1),
        preferred_element_type=jnp.float32,
    )
    out_part = base_part + adapter_part
    if lax.axis_size("tp") == 2 and lax.axis_size("dp") == 2:
        core = lax.axis_index("dp")
        chip = lax.axis_index("tp")
        blocks = out_part.reshape(side, length, -1)

        def pick(index):
            return lax.dynamic_index_in_dim(blocks, index, 0, keepdims=False)

        swapped = lax.ppermute(
            jnp.stack([pick(1 - core), pick(3 - core)]).astype(jnp.bfloat16),
            "dp",
            [(0, 1), (1, 0)],
        ).astype(jnp.float32)
        near = pick(core) + swapped[0]
        far = pick(2 + core) + swapped[1]
        mixed_t = jnp.where(chip == 0, near, far)
        crossing = jnp.where(chip == 0, far, near).astype(jnp.bfloat16)
        mixed_t = mixed_t + lax.ppermute(crossing, "tp", [(0, 1), (1, 0)]).astype(jnp.float32)
    else:
        mixed_t = block_rows(out_part, lane, length)
        for s in range(1, side):
            sent = block_rows(out_part, (lane + s) % side, length).astype(jnp.bfloat16)
            mixed_t = mixed_t + moved(sent, s, "lane").astype(jnp.float32)
    return transposed(mixed_t.astype(jnp.bfloat16))


def solution(mesh):
    body = square_body if mesh.shape["ctx"] == mesh.shape["tp"] * mesh.shape["dp"] else general_body
    placed = (
        P(("groups", "ctx"), ("tp", "dp")),
        P("groups"),
        P("groups"),
        P(),
        P("ctx", ("tp", "dp")),
        P("ctx", ("tp", "dp")),
        P("ctx", ("tp", "dp")),
        P(None, ("tp", "dp")),
        P(None, ("tp", "dp")),
        P(("tp", "dp")),
        P(("tp", "dp")),
        P(("tp", "dp")),
        P(("tp", "dp")),
        P(("tp", "dp"), "ctx"),
        P("ctx", ("tp", "dp"), None),
        P("ctx", None, ("tp", "dp")),
        P("ctx", None, ("tp", "dp")),
        P("ctx", ("tp", "dp"), None),
        P("ctx", None, ("tp", "dp")),
    )
    return jax.shard_map(
        body,
        mesh=mesh,
        in_specs=placed,
        out_specs=P(("groups", "ctx"), ("tp", "dp")),
        check_vma=False,
    )
```

```python
import jax
import jax.numpy as jnp
from jax import lax
from jax.sharding import PartitionSpec as P

FULL_PRECISION = lax.Precision.HIGHEST
NORM_EPSILON = 1e-06


def from_root(block, axis, source):
    block = jnp.where(lax.axis_index(axis) == source, block, jnp.zeros_like(block))
    return lax.psum(block, axis)


def passed_along(shard, axis, by):
    size = lax.axis_size(axis)
    pairs = [(i, i + by) for i in range(size) if 0 <= i + by < size]
    return lax.ppermute(shard, axis, pairs)


def prefix(shard, axis, combine, identity):
    size, place = (lax.axis_size(axis), lax.axis_index(axis))
    everything = jax.tree.map(
        lambda part, kind: lax.all_gather(part.astype(kind), axis),
        shard,
        (jnp.bfloat16, jnp.bfloat16),
    )
    start = jax.tree.map(
        lambda part, zero: jnp.broadcast_to(jnp.asarray(zero, part.dtype), part.shape),
        shard,
        identity,
    )

    def lap(k, before):
        reached = k < place
        new = combine(
            before, jax.tree.map(lambda part, own: part[k].astype(own.dtype), everything, shard)
        )
        return jax.tree.map(lambda a, b: jnp.where(reached, a, b), new, before)

    return lax.fori_loop(0, size, lap, start)


def segment_of(positions, request_ends):
    inside = (positions[:, None] >= request_ends[None, :]).astype(jnp.int32)
    counted = jnp.sum(inside, axis=1, dtype=jnp.int32)
    return jnp.where(positions < 0, jnp.int32(-1), counted)


def span_parts(x_heads, b_proj, c_proj, step_size, log_decay, segment, previous):
    length = x_heads.shape[0]
    cumulative = jnp.cumsum(log_decay, axis=0)
    final_log = cumulative[length - 1]
    places = jnp.arange(length, dtype=jnp.int32)
    same_request = jnp.logical_and(
        segment[:, None] == segment[None, :], places[None, :] <= places[:, None]
    ).astype(jnp.float32)
    log_gap = cumulative.T[:, :, None] - cumulative.T[:, None, :]
    decay_table = jnp.exp(jnp.minimum(log_gap, 0.0)) * same_request[None]
    scores = lax.dot_general(
        c_proj, b_proj, (((1,), (1,)), ((), ())), preferred_element_type=jnp.float32
    )
    weights = scores[None] * decay_table * step_size.T[:, None, :]
    inner_out = jnp.einsum("hts,shd->thd", weights, x_heads, precision=FULL_PRECISION)
    at_end = (segment == segment[length - 1]).astype(jnp.float32)
    state_weight = jnp.exp(final_log[None, :] - cumulative) * at_end[:, None] * step_size
    local_state = jnp.einsum(
        "sh,shd,sn->hdn",
        state_weight,
        x_heads,
        b_proj.astype(jnp.float32),
        precision=FULL_PRECISION,
    )
    enter_weight = jnp.exp(cumulative) * (segment == previous).astype(jnp.float32)[:, None]
    carry_decay = jnp.exp(final_log) * (segment[length - 1] == previous).astype(jnp.float32)
    return (inner_out, local_state, enter_weight, carry_decay)


def select_rows(wide, adapter_picker_matrix):
    shaped = wide.reshape(wide.shape[0], adapter_picker_matrix.shape[1], -1)
    return jnp.sum(shaped * adapter_picker_matrix[:, :, None], axis=1)


def masked_wide(values, onehot_b):
    return (values[:, None, :] * onehot_b[:, :, None]).reshape(values.shape[0], -1)


def general_body(
    tokens,
    lengths,
    request_adapter_ids,
    adapter_store_slot,
    xchan_input_weight,
    bc_input_weight,
    step_input_weight,
    convolution_x_taps,
    convolution_bc_taps,
    step_bias,
    decay_log_rate,
    head_skip_gain,
    output_norm_gain,
    output_weight,
    adapter_down_input,
    adapter_up_xchan,
    adapter_up_bc,
    adapter_down_output,
    adapter_up_output,
):
    length = tokens.shape[0]
    request_list = lengths.shape[0]
    taps = convolution_x_taps.shape[0]
    bank_entries = adapter_down_input.shape[0]
    head_count = step_bias.shape[0]
    channels = xchan_input_weight.shape[1]
    start_pos = lax.axis_index("ctx") * length
    request_ends = jnp.cumsum(lengths, dtype=jnp.int32)
    positions = start_pos + jnp.arange(length, dtype=jnp.int32)
    segment = segment_of(positions, request_ends)
    previous = segment_of(jnp.reshape(start_pos - 1, (1,)), request_ends)[0]
    adapter_picker_matrix = (
        segment[:, None] == jnp.arange(request_list, dtype=jnp.int32)[None, :]
    ).astype(jnp.float32)
    onehot_b = adapter_picker_matrix.astype(jnp.bfloat16)
    slot_indices = adapter_store_slot[request_adapter_ids]
    initial_stacks = (
        jnp.zeros(
            (adapter_down_input.shape[1], request_list, adapter_down_input.shape[2]), jnp.bfloat16
        ),
        jnp.zeros((request_list,) + adapter_up_xchan.shape[1:], jnp.bfloat16),
        jnp.zeros((request_list,) + adapter_up_bc.shape[1:], jnp.bfloat16),
        jnp.zeros(
            (adapter_down_output.shape[1], request_list, adapter_down_output.shape[2]), jnp.bfloat16
        ),
        jnp.zeros((request_list,) + adapter_up_output.shape[1:], jnp.bfloat16),
    )
    stack_dims = (1, 0, 0, 1, 0)

    def fetch(request_item, current):
        slot = slot_indices[request_item]
        owner = slot // bank_entries
        within = slot % bank_entries
        a_in, b_x, b_bc, a_out, b_out = [
            lax.dynamic_index_in_dim(adapter_bank, within, 0, keepdims=False)
            for adapter_bank in (
                adapter_down_input,
                adapter_up_xchan,
                adapter_up_bc,
                adapter_down_output,
                adapter_up_output,
            )
        ]
        received = (
            from_root(a_in, "ctx", owner),
            from_root(b_x, "ctx", owner),
            from_root(b_bc, "ctx", owner),
            from_root(a_out, "ctx", owner),
            from_root(b_out, "ctx", owner),
        )
        return tuple(
            (
                lax.dynamic_update_index_in_dim(stack, panel, request_item, along)
                for stack, panel, along in zip(current, received, stack_dims)
            )
        )

    stacks = lax.fori_loop(0, request_list, fetch, initial_stacks)
    rank_value = adapter_down_input.shape[2]
    down_in = stacks[0].reshape(stacks[0].shape[0], request_list * rank_value)
    up_x = stacks[1].reshape(request_list * rank_value, -1)
    up_bc = stacks[2].reshape(request_list * rank_value, -1)
    down_out = stacks[3].reshape(stacks[3].shape[0], request_list * rank_value)
    up_out = stacks[4].reshape(request_list * rank_value, -1)
    lowrank_part = select_rows(
        jnp.dot(tokens, down_in, preferred_element_type=jnp.float32), adapter_picker_matrix
    )
    rank_hidden = lax.psum(lowrank_part.astype(jnp.bfloat16), ("tp", "dp"))
    lowrank_wide = masked_wide(rank_hidden, onehot_b)
    full_tokens = lax.all_gather(tokens, ("tp", "dp"), axis=1, tiled=True)
    pieces = (
        lax.all_gather(xchan_input_weight, "ctx", axis=0, tiled=True),
        lax.all_gather(bc_input_weight, "ctx", axis=0, tiled=True),
        lax.all_gather(step_input_weight, "ctx", axis=0, tiled=True),
    )
    xchan_values, bc_channel_values, step_raw = tuple(
        (jnp.dot(full_tokens, piece, preferred_element_type=jnp.float32) for piece in pieces)
    )
    xchan_values = xchan_values + jnp.dot(lowrank_wide, up_x, preferred_element_type=jnp.float32)
    bc_channel_values = bc_channel_values + jnp.dot(
        lowrank_wide, up_bc, preferred_element_type=jnp.float32
    )
    values = jnp.concatenate([xchan_values, bc_channel_values], axis=1)
    kernel = jnp.concatenate([convolution_x_taps, convolution_bc_taps], axis=1)
    tail_rows = passed_along(values[length - (taps - 1) :], "ctx", 1)
    extended = jnp.concatenate([tail_rows, values], axis=0)
    extended_segment = segment_of(
        start_pos - (taps - 1) + jnp.arange(length + taps - 1, dtype=jnp.int32), request_ends
    )
    convolved = jnp.zeros_like(values)
    for tap in range(taps):
        keep = (extended_segment[tap : tap + length] == segment).astype(jnp.float32)
        convolved = convolved + kernel[tap][None, :] * extended[tap : tap + length] * keep[:, None]
    act = jax.nn.silu(convolved)
    x_heads = act[:, :channels].reshape(length, head_count, -1)
    bc_local = act[:, channels:].astype(jnp.bfloat16)
    bc_all = lax.all_gather(bc_local, ("tp", "dp"), axis=1, tiled=True)
    state_width = bc_all.shape[1] // 2
    b_proj = bc_all[:, :state_width]
    c_proj = bc_all[:, state_width:]
    step_size = jax.nn.softplus(step_raw + step_bias[None, :])
    log_decay = -step_size * jnp.exp(decay_log_rate)[None, :]
    inner_out, local_state, enter_weight, carry_decay = span_parts(
        x_heads, b_proj, c_proj, step_size, log_decay, segment, previous
    )

    def compose(earlier, later):
        return (earlier[0] * later[0], later[0][:, None, None] * earlier[1] + later[1])

    carried = prefix(
        (carry_decay, local_state),
        "ctx",
        compose,
        (jnp.ones_like(carry_decay), jnp.zeros_like(local_state)),
    )
    entering = carried[1]
    entered = (
        jnp.einsum("tn,hdn->thd", c_proj.astype(jnp.float32), entering, precision=FULL_PRECISION)
        * enter_weight[:, :, None]
    )
    mixer_out = (inner_out + entered + head_skip_gain[None, :, None] * x_heads).reshape(
        length, channels
    )
    scale = lax.rsqrt(jnp.mean(mixer_out * mixer_out, axis=1, keepdims=True) + NORM_EPSILON)
    normalized_rows = (mixer_out * scale * output_norm_gain[None, :]).astype(jnp.bfloat16)
    term = jnp.dot(
        normalized_rows,
        lax.all_gather(output_weight, "ctx", axis=1, tiled=True),
        preferred_element_type=jnp.float32,
    )
    base = lax.psum_scatter(
        term.astype(jnp.bfloat16), ("tp", "dp"), scatter_dimension=1, tiled=True
    ).astype(jnp.float32)
    lowrank_out_part = select_rows(
        jnp.dot(normalized_rows, down_out, preferred_element_type=jnp.float32),
        adapter_picker_matrix,
    )
    rank_hidden_output = lax.psum(lowrank_out_part.astype(jnp.bfloat16), ("tp", "dp"))
    adapter_term = jnp.dot(
        masked_wide(rank_hidden_output, onehot_b), up_out, preferred_element_type=jnp.float32
    )
    return (base + adapter_term).astype(jnp.bfloat16)


def moved(block, shift, kind):
    side = lax.axis_size("ctx")
    if kind == "ctx":
        pairs = [(a, (a + shift) % side) for a in range(side)]
        return lax.ppermute(block, "ctx", pairs)
    if kind == "lane":
        pairs = [(a, (a + shift) % side) for a in range(side)]
        return lax.ppermute(block, ("tp", "dp"), pairs)
    if kind == "rows":
        pairs = [(a * side + b, b * side + (a + shift) % side) for a in range(side) for b in range(side)]
    else:
        pairs = [(a * side + b, ((b + shift) % side) * side + a) for a in range(side) for b in range(side)]
    return lax.ppermute(block, ("ctx", "tp", "dp"), pairs)


def transposed(block):
    return moved(block, 0, "rows")


def in_order(pieces, place):
    stacked = jnp.stack(pieces[::-1], axis=0)
    ordered = jnp.roll(stacked, place + 1, axis=0)
    return ordered.reshape((-1,) + pieces[0].shape[1:])


def block_rows(values, index, length):
    return lax.dynamic_slice_in_dim(values, index * length, length, 0)


def owned_rows(values, owned):
    return jnp.concatenate(
        [values * owned[:, i : i + 1].astype(values.dtype) for i in range(owned.shape[1])], axis=1
    )


def square_body(
    tokens,
    lengths,
    request_adapter_ids,
    adapter_store_slot,
    xchan_input_weight,
    bc_input_weight,
    step_input_weight,
    convolution_x_taps,
    convolution_bc_taps,
    step_bias,
    decay_log_rate,
    head_skip_gain,
    output_norm_gain,
    output_weight,
    adapter_down_input,
    adapter_up_xchan,
    adapter_up_bc,
    adapter_down_output,
    adapter_up_output,
):
    length = tokens.shape[0]
    side = lax.axis_size("ctx")
    stream = side * length
    taps = convolution_x_taps.shape[0]
    bank_entries = adapter_down_input.shape[0]
    rank_value = adapter_down_input.shape[2]
    head_count = step_bias.shape[0]
    channels = xchan_input_weight.shape[1]
    bc_width = bc_input_weight.shape[1]
    here = lax.axis_index("ctx")
    lane = lax.axis_index(("tp", "dp"))
    start_pos = here * length
    request_ends = jnp.cumsum(lengths, dtype=jnp.int32)
    every_position = jnp.arange(stream, dtype=jnp.int32)
    every_segment = segment_of(every_position, request_ends)
    slot_indices = adapter_store_slot[request_adapter_ids]
    request_count = lengths.shape[0]
    stream_onehot = every_segment[:, None] == jnp.arange(request_count, dtype=jnp.int32)[None, :]
    slot_of_position = jnp.sum(
        jnp.where(stream_onehot, slot_indices[None, :], 0), axis=1, dtype=jnp.int32
    )
    entry_ids = jnp.arange(bank_entries, dtype=jnp.int32)[None, :]
    owned_here = slot_of_position[:, None] == here * bank_entries + entry_ids
    owned_lane = slot_of_position[:, None] == lane * bank_entries + entry_ids
    positions = start_pos + jnp.arange(length, dtype=jnp.int32)
    segment = segment_of(positions, request_ends)
    previous = segment_of(jnp.reshape(start_pos - 1, (1,)), request_ends)[0]

    tokens_t, down_in_local = lax.optimization_barrier((transposed(tokens), adapter_down_input))
    stream_rows = in_order(
        [tokens_t] + [moved(tokens_t, s, "lane") for s in range(1, side)], lane
    )
    local_owned = lax.dynamic_slice_in_dim(slot_of_position, start_pos, length, 0)
    down_pick = jnp.zeros((length, rank_value), jnp.float32)
    for s in range(side):
        piece = down_in_local if s == 0 else moved(down_in_local, s, "ctx")
        first = ((here - s) % side) * bank_entries
        every = jnp.einsum("pf,efr->per", tokens, piece, preferred_element_type=jnp.float32)
        chosen = local_owned[:, None] == first + jnp.arange(bank_entries, dtype=jnp.int32)[None, :]
        down_pick = down_pick + jnp.sum(every * chosen[:, :, None].astype(jnp.float32), axis=1)
    if lax.axis_size("tp") == 2 and lax.axis_size("dp") == 2:
        down_pick = down_pick + lax.ppermute(down_pick, "dp", [(0, 1), (1, 0)])
        rank_local = down_pick + lax.ppermute(down_pick, "tp", [(0, 1), (1, 0)])
    else:
        rank_local = down_pick + sum(moved(down_pick, s, "lane") for s in range(1, side))
    rank_local = rank_local.astype(jnp.bfloat16)
    rank_hidden = in_order(
        [rank_local] + [moved(rank_local, s, "ctx") for s in range(1, side)], here
    )
    hidden_wide = owned_rows(rank_hidden, owned_here)
    xchan_part = jnp.dot(
        stream_rows, xchan_input_weight, preferred_element_type=jnp.float32
    ) + jnp.dot(
        hidden_wide,
        adapter_up_xchan.reshape(bank_entries * rank_value, -1),
        preferred_element_type=jnp.float32,
    )
    bc_part = jnp.dot(stream_rows, bc_input_weight, preferred_element_type=jnp.float32) + jnp.dot(
        hidden_wide,
        adapter_up_bc.reshape(bank_entries * rank_value, -1),
        preferred_element_type=jnp.float32,
    )
    step_part = jnp.dot(stream_rows, step_input_weight, preferred_element_type=jnp.float32)
    projected = jnp.concatenate([xchan_part, bc_part, step_part], axis=1)
    summed = block_rows(projected, here, length)
    for s in range(1, side):
        sent = block_rows(projected, (here + s) % side, length).astype(jnp.bfloat16)
        summed = summed + moved(sent, s, "ctx").astype(jnp.float32)
    summed, up_out_local = lax.optimization_barrier((summed, adapter_up_output))
    up_out_t = transposed(up_out_local)
    values = summed[:, : channels + bc_width]
    step_raw = summed[:, channels + bc_width :]

    kernel = jnp.concatenate([convolution_x_taps, convolution_bc_taps], axis=1)
    tail_rows = passed_along(values[length - (taps - 1) :], "ctx", 1)
    extended = jnp.concatenate([tail_rows, values], axis=0)
    extended_segment = segment_of(
        start_pos - (taps - 1) + jnp.arange(length + taps - 1, dtype=jnp.int32), request_ends
    )
    convolved = jnp.zeros_like(values)
    for tap in range(taps):
        keep = (extended_segment[tap : tap + length] == segment).astype(jnp.float32)
        convolved = convolved + kernel[tap][None, :] * extended[tap : tap + length] * keep[:, None]
    act = jax.nn.silu(convolved)
    x_heads = act[:, :channels].reshape(length, head_count, -1)
    bc_local = act[:, channels:].astype(jnp.bfloat16)
    if lax.axis_size("tp") == 2 and lax.axis_size("dp") == 2:
        other = lax.ppermute(bc_local, "dp", [(0, 1), (1, 0)])
        pair = jnp.where(
            lax.axis_index("dp") == 0,
            jnp.concatenate([bc_local, other], axis=1),
            jnp.concatenate([other, bc_local], axis=1),
        )
        other = lax.ppermute(pair, "tp", [(0, 1), (1, 0)])
        bc_all = jnp.where(
            lax.axis_index("tp") == 0,
            jnp.concatenate([pair, other], axis=1),
            jnp.concatenate([other, pair], axis=1),
        )
    else:
        bc_pieces = [bc_local] + [moved(bc_local, s, "lane") for s in range(1, side)]
        bc_all = jnp.transpose(in_order([piece.T for piece in bc_pieces], lane))
    state_width = bc_all.shape[1] // 2
    b_proj = bc_all[:, :state_width]
    c_proj = bc_all[:, state_width:]
    step_size = jax.nn.softplus(step_raw + step_bias[None, :])
    log_decay = -step_size * jnp.exp(decay_log_rate)[None, :]
    inner_out, local_state, enter_weight, carry_decay = span_parts(
        x_heads, b_proj, c_proj, step_size, log_decay, segment, previous
    )

    decay_row = jnp.broadcast_to(carry_decay[:, None, None], (head_count, 1, local_state.shape[2]))
    state_and_decay = jnp.concatenate([decay_row, local_state], axis=1).astype(jnp.bfloat16)
    if side <= 4:
        prior = lax.ppermute(
            state_and_decay, "ctx", [(a, a + 1) for a in range(side - 1)]
        ).astype(jnp.float32)
        pair_decay = prior[:, :1, :1] * carry_decay[:, None, None]
        pair_state = carry_decay[:, None, None] * prior[:, 1:] + local_state
        pair = jnp.concatenate(
            [jnp.broadcast_to(pair_decay, decay_row.shape), pair_state], axis=1
        ).astype(jnp.bfloat16)
        entering = prior[:, 1:]
        if side > 2:
            far = lax.ppermute(pair, "ctx", [(a, a + 2) for a in range(side - 2)])
            entering = prior[:, :1, :1] * far[:, 1:].astype(jnp.float32) + entering
    else:
        entering = jnp.zeros_like(local_state)
        for s in range(side - 1, 0, -1):
            pairs = [(a, a + s) for a in range(side - s)]
            both_in = lax.ppermute(state_and_decay, "ctx", pairs).astype(jnp.float32)
            entering = both_in[:, :1, :1] * entering + both_in[:, 1:]
    entered = (
        jnp.einsum("tn,hdn->thd", c_proj.astype(jnp.float32), entering, precision=FULL_PRECISION)
        * enter_weight[:, :, None]
    )
    mixer_out = (inner_out + entered + head_skip_gain[None, :, None] * x_heads).reshape(
        length, channels
    )
    scale = lax.rsqrt(jnp.mean(mixer_out * mixer_out, axis=1, keepdims=True) + NORM_EPSILON)
    normalized_rows = (mixer_out * scale * output_norm_gain[None, :]).astype(jnp.bfloat16)

    normed_stream = in_order(
        [normalized_rows] + [moved(normalized_rows, s, "ctx") for s in range(1, side)], here
    )
    out_down_part = jnp.einsum(
        "pc,ecr->per", normed_stream, adapter_down_output, preferred_element_type=jnp.float32
    )
    out_down_pick = jnp.sum(out_down_part * owned_here[:, :, None].astype(jnp.float32), axis=1)
    if lax.axis_size("tp") == 2 and lax.axis_size("dp") == 2:
        summed_pick = out_down_pick + lax.ppermute(out_down_pick, "dp", [(0, 1), (1, 0)])
        summed_pick = summed_pick + lax.ppermute(summed_pick, "tp", [(0, 1), (1, 0)])
    else:
        summed_pick = out_down_pick + sum(moved(out_down_pick, s, "lane") for s in range(1, side))
    rank_hidden_output = transposed(summed_pick)
    base_part = jnp.dot(
        normed_stream, output_weight, preferred_element_type=jnp.float32
    ).astype(jnp.bfloat16).astype(jnp.float32)
    adapter_part = jnp.dot(
        owned_rows(rank_hidden_output, owned_lane).astype(jnp.bfloat16),
        up_out_t.reshape(bank_entries * rank_value, -1),
        preferred_element_type=jnp.float32,
    )
    out_part = base_part + adapter_part
    if lax.axis_size("tp") == 2 and lax.axis_size("dp") == 2:
        core = lax.axis_index("dp")
        chip = lax.axis_index("tp")
        blocks = out_part.reshape(side, length, -1)

        def pick(index):
            return lax.dynamic_index_in_dim(blocks, index, 0, keepdims=False)

        swapped = lax.ppermute(
            jnp.stack([pick(1 - core), pick(3 - core)]).astype(jnp.bfloat16),
            "dp",
            [(0, 1), (1, 0)],
        ).astype(jnp.float32)
        near = pick(core) + swapped[0]
        far = pick(2 + core) + swapped[1]
        mixed_t = jnp.where(chip == 0, near, far)
        crossing = jnp.where(chip == 0, far, near).astype(jnp.bfloat16)
        mixed_t = mixed_t + lax.ppermute(crossing, "tp", [(0, 1), (1, 0)]).astype(jnp.float32)
    else:
        mixed_t = block_rows(out_part, lane, length)
        for s in range(1, side):
            sent = block_rows(out_part, (lane + s) % side, length).astype(jnp.bfloat16)
            mixed_t = mixed_t + moved(sent, s, "lane").astype(jnp.float32)
    return transposed(mixed_t.astype(jnp.bfloat16))


def solution(mesh):
    body = square_body if mesh.shape["ctx"] == mesh.shape["tp"] * mesh.shape["dp"] else general_body
    placed = (
        P(("groups", "ctx"), ("tp", "dp")),
        P("groups"),
        P("groups"),
        P(),
        P("ctx", ("tp", "dp")),
        P("ctx", ("tp", "dp")),
        P("ctx", ("tp", "dp")),
        P(None, ("tp", "dp")),
        P(None, ("tp", "dp")),
        P(("tp", "dp")),
        P(("tp", "dp")),
        P(("tp", "dp")),
        P(("tp", "dp")),
        P(("tp", "dp"), "ctx"),
        P("ctx", ("tp", "dp"), None),
        P("ctx", None, ("tp", "dp")),
        P("ctx", None, ("tp", "dp")),
        P("ctx", ("tp", "dp"), None),
        P("ctx", None, ("tp", "dp")),
    )
    return jax.shard_map(
        body,
        mesh=mesh,
        in_specs=placed,
        out_specs=P(("groups", "ctx"), ("tp", "dp")),
        check_vma=False,
    )
```
